32 devices in a mesh: group: 2 (over x), ctx: 16 (over z, y, core).
Axes of the slice: x: 2, y: 2, z: 4, core: 2. Of those that a mesh axis runs over, the one named last changes fastest.
Arguments:
- xbc: bfloat16 [16384, 5120], P(('group', 'ctx')), parts along dimension 0, may hold values from -6 to 6
- z_gate: bfloat16 [16384, 4096], P(('group', 'ctx')), parts along dimension 0, may hold values from -6 to 6
- dt_raw: bfloat16 [16384, 64], P(('group', 'ctx')), parts along dimension 0, may hold values from -4 to 4
- lengths: int32 [8], P('group'), parts along dimension 0, may hold values from 1 to 6144, 8192 in all
- conv_weight: float32 [4, 5120], replicated, may hold values from -3 to 3
- conv_bias: float32 [5120], replicated, may hold values from -3 to 3
- dt_bias: float32 [64], replicated, may hold values from -3 to -1
- a_log: float32 [64], replicated, may hold values from -14 to 0
- d_skip: float32 [64], replicated, may hold values from 0.5 to 2
- norm_gain: float32 [4096], replicated, may hold values from 0.5 to 1.5
Outputs:
- mixed: bfloat16 [16384, 4096], P(('group', 'ctx')), parts along dimension 0
The draws below stay inside these ranges and needn't reach their ends.
There are 2 independent parts, one for each index of `group`. The reference program is written for one: setup_inputs(seed, part) draws one part's arguments, and reference() takes and returns one part's arrays. A program takes and returns all parts, laid end to end along the dimension named above; an argument that names none is the same for every part. Nothing has to cross between parts.
Inputs may be any that keep to these rules, and one draw needn't show every extreme that they name: `lengths`: the 4 prompts lie one after another and fill all 8192 positions; the longest has exactly 6144 tokens.
All inputs are finite; a program needn't handle non-finite values.
Results may differ from the reference program's by a relative error of at most 0.0035.
Values may be sent and summed in bfloat16 or wider, within the bound.
No kernel may reach another device: no remote copies, remote signals or barrier semaphores. Data moves between devices by JAX's collectives and lax.ppermute only.
A program may use at most 128 MiB of HBM per device.

```python
import math
import jax
import jax.numpy as jnp
import numpy as np
from jax import lax

HEADS = 64
HEAD_DIM = 64
STATE = 256
GROUPS = 2
CONV = 4
STRETCH = 256
PROMPTS = 4
TOKENS = 8192
INNER = 4096
CHANNELS = 5120


def draw_a_log(key, part):
    k_pick, k_slow, k_fast = jax.random.split(key, 3)
    share = 0.5
    slow = jax.random.uniform(k_pick, (HEADS,)) < share
    slow_rate = jnp.log(0.5 / TOKENS) + jnp.log(16.0) * jax.random.uniform(k_slow, (HEADS,))
    fast_rate = jnp.log(0.1) + jnp.log(3.0) * jax.random.uniform(k_fast, (HEADS,))
    return jnp.where(slow, slow_rate, fast_rate).astype(jnp.float32)


def level_of(rng, extent, shards, low, top_value):
    def one(position, parts):
        heights = jax.random.uniform(jax.random.fold_in(jax.random.fold_in(rng, 6), position), (parts,), jnp.float32, low / len(shards), top_value / len(shards))
        return jnp.repeat(jnp.exp(heights), extent[position] // parts).reshape((-1,) + (1,) * (len(extent) - position - 1))

    loudness = one(*shards[0])
    for cut in shards[1:]:
        loudness = loudness * one(*cut)
    return loudness


def profile(count, total, most, lean):
    weights = [(1 << 20) // math.isqrt(standing ** lean) + 1 for standing in range(2, count + 1)]
    rest, holding = total - most - (count - 1), [1] * (count - 1)
    while rest > 0:
        candidates = [i for i in range(count - 1) if holding[i] < most]
        whole, budget = sum([weights[i] for i in candidates]), rest
        for i in candidates:
            extra = min(most - holding[i], max(1, budget * weights[i] // whole), rest)
            holding[i] = holding[i] + extra
            rest = rest - extra
    return np.array([most] + holding)


def uneven(key, amount, total, most, skew):
    if amount == 2:
        one = jax.random.randint(key, (), max(1, total - most), min(most, total - 1) + 1)
        return jnp.stack([one, total - one])
    sizes = jnp.asarray(profile(amount, total, most, skew), jnp.int32)
    pairs = (amount - 1) // 2
    source_of, receiver = sizes[1:1 + 2 * pairs:2], sizes[2:2 + 2 * pairs:2]
    margin = jnp.minimum(source_of - 1, most - receiver)
    shifted = jax.random.randint(jax.random.fold_in(key, 1), (pairs,), 0, 1 << 20) % (margin + 1)
    sizes = sizes.at[1:1 + 2 * pairs:2].set(source_of - shifted).at[2:2 + 2 * pairs:2].set(receiver + shifted)
    return sizes[jax.random.permutation(jax.random.fold_in(key, 2), amount)]


def normal_values(own_key, shape, deviation, most, pieces=(), kind=jnp.bfloat16):
    factor_of = level_of(own_key, shape, pieces, -0.22, 0.18) if pieces else 1.0
    array = jax.random.normal(own_key, shape, jnp.float32) * deviation * factor_of
    return jnp.minimum(jnp.maximum(array, -most), most).astype(kind)


def setup_inputs(seed: int = 0, part: int = 0) -> dict:
    keys = jax.random.split(jax.random.key(seed), 11)
    part_splits = jax.random.split(jax.random.fold_in(keys[10], part), 11)
    return {
        "xbc": normal_values(part_splits[0], (TOKENS, CHANNELS), 1.0, 6.0, ((0, 16),)),
        "z_gate": normal_values(part_splits[1], (TOKENS, INNER), 1.0, 6.0, ((0, 16),)),
        "dt_raw": normal_values(part_splits[2], (TOKENS, HEADS), 1.0, 4.0, ((0, 16),)),
        "lengths": uneven(part_splits[3], PROMPTS, TOKENS, TOKENS * 3 // 4, 2).astype(jnp.int32),
        "conv_weight": normal_values(keys[4], (CONV, CHANNELS), CONV ** -0.5, 3.0, (), jnp.float32),
        "conv_bias": normal_values(keys[5], (CHANNELS,), 0.5, 3.0, (), jnp.float32),
        "dt_bias": jnp.clip(jax.random.uniform(keys[6], (HEADS,), jnp.float32, -3.0, -1.0), -3.0, -1.0),
        "a_log": draw_a_log(jax.random.fold_in(keys[10], 71), part),
        "d_skip": jnp.clip(jax.random.uniform(keys[8], (HEADS,), jnp.float32, 0.5, 2.0), 0.5, 2.0),
        "norm_gain": jnp.clip(1.0 + 0.1 * jax.random.normal(keys[9], (INNER,), jnp.float32), 0.5, 1.5),
    }


def segment_of(positions, lengths):
    prompt_ends = jnp.cumsum(lengths).astype(jnp.int32)
    hits = (prompt_ends[None, :] <= positions[:, None]).astype(jnp.int32)
    return lax.optimization_barrier(jnp.sum(hits, axis=1)).astype(jnp.int32)

def causal_conv(extended, positions, lengths, conv_weight, conv_bias):
    out_rows = extended.shape[0] - (CONV - 1)
    segments = segment_of(positions, lengths)
    inside = positions >= 0
    target = segments[CONV - 1:]
    summed = jnp.zeros((out_rows, extended.shape[1]), jnp.float32)
    for tap in range(CONV):
        kept = inside[tap:tap + out_rows] & (segments[tap:tap + out_rows] == target)
        term = extended[tap:tap + out_rows].astype(jnp.float32) * conv_weight[tap][None, :]
        summed = summed + jnp.where(kept[:, None], term, 0.0)
    return jax.nn.silu(summed + conv_bias[None, :]).astype(jnp.bfloat16)

def stretch_local(block, step_size, segments, seg_before, decay_rate, d_skip):
    span = block.shape[0]
    inner = HEADS * HEAD_DIM
    bc_width = GROUPS * STATE
    per_group = HEADS // GROUPS
    values = block[:, :inner]
    b_rows = block[:, inner:inner + bc_width].reshape(span, GROUPS, STATE)
    c_rows = block[:, inner + bc_width:].reshape(span, GROUPS, STATE)
    log_cum = jnp.cumsum(-step_size * decay_rate[None, :], axis=0)
    scaled = (values.astype(jnp.float32).reshape(span, HEADS, HEAD_DIM) * step_size[:, :, None]).astype(jnp.bfloat16)
    scaled_groups = scaled.reshape(span, GROUPS, per_group, HEAD_DIM).astype(jnp.float32)
    order = jnp.arange(span)
    kept = (segments[:, None] == segments[None, :]) & (order[:, None] >= order[None, :])
    gaps = jnp.where(kept[:, :, None], log_cum[:, None, :] - log_cum[None, :, :], 0.0)
    decay = jnp.where(kept[:, :, None], jnp.exp(gaps), 0.0)
    scores = jnp.einsum('tgn,sgn->tsg', c_rows.astype(jnp.float32), b_rows.astype(jnp.float32))
    weights = (decay.reshape(span, span, GROUPS, per_group) * scores[:, :, :, None]).astype(jnp.bfloat16)
    intra = jnp.einsum('tsgk,sgkp->tgkp', weights.astype(jnp.float32), scaled_groups).reshape(span, inner)
    end_seg = segments[span - 1]
    end_weight = jnp.where((segments == end_seg)[:, None], jnp.exp(log_cum[span - 1][None, :] - log_cum), 0.0)
    weighted_b = (b_rows.astype(jnp.float32)[:, :, None, :] * end_weight.reshape(span, GROUPS, per_group)[:, :, :, None]).astype(jnp.bfloat16)
    state_end = jnp.einsum('sgkp,sgkn->gkpn', scaled_groups, weighted_b.astype(jnp.float32)).reshape(HEADS, HEAD_DIM, STATE)
    decay_stretch = jnp.where(end_seg == seg_before, jnp.exp(log_cum[span - 1]), 0.0)
    in_weight = jnp.where((segments == seg_before)[:, None], jnp.exp(log_cum), 0.0)
    skip = values.astype(jnp.float32).reshape(span, HEADS, HEAD_DIM) * d_skip[None, :, None]
    local_out = intra + skip.reshape(span, inner)
    return (local_out, in_weight, decay_stretch, state_end, c_rows)

def from_state(state, c_rows, in_weight):
    span = c_rows.shape[0]
    per_group = HEADS // GROUPS
    state_low = state.astype(jnp.bfloat16).reshape(GROUPS, per_group, HEAD_DIM, STATE)
    term = jnp.einsum('tgn,gkpn->tgkp', c_rows.astype(jnp.float32), state_low.astype(jnp.float32))
    term = term * in_weight.reshape(span, GROUPS, per_group)[:, :, :, None]
    return term.reshape(span, HEADS * HEAD_DIM)

def finish(mixed_out, z_block, norm_gain):
    span = mixed_out.shape[0]
    inner = HEADS * HEAD_DIM
    gated = mixed_out * jax.nn.silu(z_block.astype(jnp.float32))
    grouped = gated.reshape(span, GROUPS, inner // GROUPS)
    mean_square = lax.optimization_barrier(jnp.mean(grouped * grouped, axis=2, keepdims=True)) + 1e-05
    normed = (grouped * lax.rsqrt(mean_square)).reshape(span, inner)
    return (normed * norm_gain[None, :]).astype(jnp.bfloat16)

def reference(xbc, z_gate, dt_raw, lengths, conv_weight, conv_bias, dt_bias, a_log, d_skip, norm_gain):
    total = xbc.shape[0]
    channels = xbc.shape[1]
    extended = jnp.concatenate([jnp.zeros((CONV - 1, channels), jnp.bfloat16), xbc], axis=0)
    positions = (jnp.arange(total + CONV - 1) - (CONV - 1)).astype(jnp.int32)
    conv_out = causal_conv(extended, positions, lengths, conv_weight, conv_bias)
    step_size = jax.nn.softplus(dt_raw.astype(jnp.float32) + dt_bias[None, :])
    decay_rate = jnp.exp(a_log)
    segments = segment_of(jnp.arange(total).astype(jnp.int32), lengths)
    stretch_count = total // STRETCH
    seg_before = segment_of((jnp.arange(stretch_count) * STRETCH - 1).astype(jnp.int32), lengths)
    inputs = (conv_out.reshape(stretch_count, STRETCH, channels), step_size.reshape(stretch_count, STRETCH, HEADS), segments.reshape(stretch_count, STRETCH), seg_before, z_gate.reshape(stretch_count, STRETCH, HEADS * HEAD_DIM))

    def advance(state, item):
        block, step_block, seg_block, seg_prev, z_block = item
        local_out, in_weight, decay_stretch, state_end, c_rows = stretch_local(block, step_block, seg_block, seg_prev, decay_rate, d_skip)
        mixed_out = local_out + from_state(state, c_rows, in_weight)
        new_state = decay_stretch[:, None, None] * state + state_end
        return (new_state, finish(mixed_out, z_block, norm_gain))
    start_state = jnp.zeros((HEADS, HEAD_DIM, STATE), jnp.float32)
    _, outputs = lax.scan(advance, start_state, inputs)
    return outputs.reshape(total, HEADS * HEAD_DIM)
```

```python
import jax
import jax.numpy as jnp
from jax import lax
from jax.experimental import pallas as pl
from jax.experimental.pallas import tpu as pltpu
from jax.sharding import PartitionSpec as P

HEADS = 64
HEAD_DIM = 64
STATE = 256
GROUPS = 2
CONV = 4
STRETCH = 256
CHANNELS = 5120
INNER = HEADS * HEAD_DIM
PER_GROUP = HEADS // GROUPS
GROUP_COLS = INNER // GROUPS


def shifted(value, axis, by):
    peers = lax.axis_size(axis)
    pairs = [(i, i + by) for i in range(peers) if 0 <= i + by < peers]
    return lax.ppermute(value, axis, pairs)


def segment_of(positions, lengths):
    prompt_ends = jnp.cumsum(lengths)
    hits = (prompt_ends[None, :] <= positions[:, None]).astype(jnp.int32)
    return jnp.sum(hits, axis=1)


def causal_conv(extended, positions, lengths, conv_weight, conv_bias):
    out_rows = extended.shape[0] - (CONV - 1)
    segments = segment_of(positions, lengths)
    inside = positions >= 0
    target = segments[CONV - 1 :]
    summed = jnp.zeros((out_rows, extended.shape[1]), jnp.float32)
    for tap in range(CONV):
        kept = inside[tap : tap + out_rows] & (segments[tap : tap + out_rows] == target)
        term = extended[tap : tap + out_rows].astype(jnp.float32) * conv_weight[tap][None, :]
        summed = summed + jnp.where(kept[:, None], term, 0.0)
    return jax.nn.silu(summed + conv_bias[None, :]).astype(jnp.bfloat16)


def state_kernel(bt_ref, u_ref, cum_ref, segc_ref, out_ref, uw_ref):
    cum = cum_ref[0]
    segc = segc_ref[:, 0:1]
    last = cum[STRETCH - 1 : STRETCH, :]
    seg_last = segc[STRETCH - 1 : STRETCH, :]
    w = jnp.where(segc == seg_last, jnp.exp(last - cum), 0.0)
    for j in range(PER_GROUP):
        cols = slice(j * HEAD_DIM, (j + 1) * HEAD_DIM)
        uw_ref[:, cols] = (u_ref[:, cols].astype(jnp.float32) * w[:, j : j + 1]).astype(jnp.bfloat16)
    out_ref[0] = jnp.dot(bt_ref[...], uw_ref[...], preferred_element_type=jnp.float32)


def block_states(bt, u, cum_g, segc):
    tok = u.shape[0]
    nb = tok // STRETCH
    return pl.pallas_call(
        state_kernel,
        grid=(nb, GROUPS),
        in_specs=[
            pl.BlockSpec((STATE, STRETCH), lambda b, g: (g, b)),
            pl.BlockSpec((STRETCH, GROUP_COLS), lambda b, g: (b, g)),
            pl.BlockSpec((1, STRETCH, PER_GROUP), lambda b, g: (g, b, 0)),
            pl.BlockSpec((STRETCH, 128), lambda b, g: (b, 0)),
        ],
        out_specs=pl.BlockSpec((1, STATE, GROUP_COLS), lambda b, g: (b, 0, g)),
        out_shape=jax.ShapeDtypeStruct((nb, STATE, INNER), jnp.float32),
        scratch_shapes=[pltpu.VMEM((STRETCH, GROUP_COLS), jnp.bfloat16)],
    )(bt, u, cum_g, segc)


def mix_kernel(
    c_ref, b_ref, x_ref, u_ref, z_ref, hbt_ref, cum_ref, cumt_ref, segc_ref, segr_ref, eb_ref,
    dsk_ref, gain_ref, out_ref, y_ref,
):
    cmat = c_ref[...]
    gram = lax.dot_general(
        cmat, b_ref[...], (((1,), (1,)), ((), ())), preferred_element_type=jnp.float32
    )
    segc = segc_ref[:, 0:1]
    segr = segr_ref[0:1, :]
    rows = lax.broadcasted_iota(jnp.int32, (STRETCH, STRETCH), 0)
    cols = lax.broadcasted_iota(jnp.int32, (STRETCH, STRETCH), 1)
    gram = jnp.where((segc == segr) & (cols <= rows), gram, 0.0)
    cum = cum_ref[0]
    cumt = cumt_ref[0]
    entry = eb_ref[0:1, 0:1]
    in_weight = jnp.where(segc == entry, jnp.exp(cum), 0.0)
    inter = jnp.dot(cmat, hbt_ref[0], preferred_element_type=jnp.float32)
    for j in range(PER_GROUP):
        hc = slice(j * HEAD_DIM, (j + 1) * HEAD_DIM)
        gap = jnp.minimum(cum[:, j : j + 1] - cumt[j : j + 1, :], 0.0)
        weights = (gram * jnp.exp(gap)).astype(jnp.bfloat16)
        intra = jnp.dot(weights, u_ref[:, hc], preferred_element_type=jnp.float32)
        y_ref[:, hc] = intra + inter[:, hc] * in_weight[:, j : j + 1]
    y = y_ref[...] + dsk_ref[...] * x_ref[...].astype(jnp.float32)
    zf = z_ref[...].astype(jnp.float32)
    gated = y * (zf * jax.nn.sigmoid(zf))
    mean_square = jnp.mean(gated * gated, axis=1, keepdims=True) + 1e-05
    out_ref[...] = (gated * lax.rsqrt(mean_square) * gain_ref[...]).astype(jnp.bfloat16)


def mix(conv, u, z_gate, hbt, cum_g, cumt_g, segc, segr, eb, dsk, gain):
    tok = u.shape[0]
    nb = tok // STRETCH
    b_col = INNER // STATE
    c_col = b_col + GROUPS
    return pl.pallas_call(
        mix_kernel,
        grid=(nb, GROUPS),
        in_specs=[
            pl.BlockSpec((STRETCH, STATE), lambda b, g: (b, c_col + g)),
            pl.BlockSpec((STRETCH, STATE), lambda b, g: (b, b_col + g)),
            pl.BlockSpec((STRETCH, GROUP_COLS), lambda b, g: (b, g)),
            pl.BlockSpec((STRETCH, GROUP_COLS), lambda b, g: (b, g)),
            pl.BlockSpec((STRETCH, GROUP_COLS), lambda b, g: (b, g)),
            pl.BlockSpec((1, STATE, GROUP_COLS), lambda b, g: (b, 0, g)),
            pl.BlockSpec((1, STRETCH, PER_GROUP), lambda b, g: (g, b, 0)),
            pl.BlockSpec((1, PER_GROUP, STRETCH), lambda b, g: (g, 0, b)),
            pl.BlockSpec((STRETCH, 128), lambda b, g: (b, 0)),
            pl.BlockSpec((8, STRETCH), lambda b, g: (0, b)),
            pl.BlockSpec((8, 128), lambda b, g: (b, 0)),
            pl.BlockSpec((1, GROUP_COLS), lambda b, g: (0, g)),
            pl.BlockSpec((1, GROUP_COLS), lambda b, g: (0, g)),
        ],
        out_specs=pl.BlockSpec((STRETCH, GROUP_COLS), lambda b, g: (b, g)),
        out_shape=jax.ShapeDtypeStruct((tok, INNER), jnp.bfloat16),
        scratch_shapes=[pltpu.VMEM((STRETCH, GROUP_COLS), jnp.float32)],
    )(conv, conv, conv, u, z_gate, hbt, cum_g, cumt_g, segc, segr, eb, dsk, gain)


def compose(state_dev, decay_dev):
    peers = lax.axis_size("ctx")
    width = INNER // peers
    pieces = state_dev.reshape(STATE, peers, width).transpose(1, 0, 2)
    payload = jnp.concatenate([pieces, decay_dev.reshape(peers, 1, width)], axis=1)
    got = lax.all_to_all(payload, "ctx", split_axis=0, concat_axis=0, tiled=True)
    states = got[:, :STATE, :]
    span = max(1, width // HEAD_DIM)
    sub = width // span
    decays = got[:, STATE, :].reshape(peers, span, sub)[:, :, 0].T
    dest = lax.broadcasted_iota(jnp.int32, (peers, peers, peers), 0)
    src = lax.broadcasted_iota(jnp.int32, (peers, peers, peers), 1)
    mid = lax.broadcasted_iota(jnp.int32, (peers, peers, peers), 2)
    between = (mid > src) & (mid < dest)
    factors = jnp.where(between[None], decays[:, None, None, :], 1.0)
    links = jnp.prod(factors, axis=3)
    links = jnp.where((src[:, :, 0] < dest[:, :, 0])[None], links, 0.0)
    entering = jnp.einsum(
        "hdj,jnhp->dnhp",
        links,
        states.reshape(peers, STATE, span, sub),
        precision=lax.Precision.HIGHEST,
    ).reshape(peers, STATE, width)
    back = lax.all_to_all(
        entering.astype(jnp.bfloat16), "ctx", split_axis=0, concat_axis=0, tiled=True
    )
    return back.transpose(1, 0, 2).reshape(STATE, INNER).astype(jnp.float32)


def local(xbc, z_gate, dt_raw, lengths, conv_weight, conv_bias, dt_bias, a_log, d_skip, norm_gain):
    tok = xbc.shape[0]
    nb = tok // STRETCH
    first_pos = lax.axis_index("ctx") * tok
    rim_rows = shifted(xbc[tok - (CONV - 1) :], "ctx", 1)
    extended = jnp.concatenate([rim_rows, xbc], axis=0)
    positions = first_pos - (CONV - 1) + jnp.arange(tok + CONV - 1)
    conv = causal_conv(extended, positions, lengths, conv_weight, conv_bias)
    step = jax.nn.softplus(dt_raw.astype(jnp.float32) + dt_bias[None, :])
    log_decay = -step * jnp.exp(a_log)[None, :]
    cum = jnp.cumsum(log_decay.reshape(nb, STRETCH, HEADS), axis=1).reshape(tok, HEADS)
    u = (
        conv[:, :INNER].astype(jnp.float32).reshape(tok, HEADS, HEAD_DIM) * step[:, :, None]
    ).astype(jnp.bfloat16).reshape(tok, INNER)
    segments = segment_of(first_pos + jnp.arange(tok), lengths)
    seg_before = segment_of(first_pos + jnp.arange(nb) * STRETCH - 1, lengths)
    seg_last = segments.reshape(nb, STRETCH)[:, -1]
    cum_last = cum.reshape(nb, STRETCH, HEADS)[:, -1, :]
    block_decay = jnp.where((seg_last == seg_before)[:, None], jnp.exp(cum_last), 0.0)

    cum_g = cum.reshape(tok, GROUPS, PER_GROUP).transpose(1, 0, 2)
    cumt_g = cum.T.reshape(GROUPS, PER_GROUP, tok)
    segc = jnp.broadcast_to(segments[:, None], (tok, 128)).astype(jnp.int32)
    segr = jnp.broadcast_to(segments[None, :], (8, tok)).astype(jnp.int32)
    eb = jnp.broadcast_to(seg_before[:, None, None], (nb, 8, 128)).reshape(nb * 8, 128)
    eb = eb.astype(jnp.int32)
    bt = conv[:, INNER : INNER + GROUPS * STATE].T

    ends = block_states(bt, u, cum_g, segc)
    col_decay = jnp.repeat(block_decay, HEAD_DIM, axis=1)
    state_dev = ends[0]
    decay_dev = col_decay[0]
    for b in range(1, nb):
        state_dev = col_decay[b][None, :] * state_dev + ends[b]
        decay_dev = decay_dev * col_decay[b]
    state_in = compose(state_dev, decay_dev)
    entering = [state_in]
    for b in range(1, nb):
        entering.append(col_decay[b - 1][None, :] * entering[-1] + ends[b - 1])
    hbt = jnp.stack(entering).astype(jnp.bfloat16)

    dsk = jnp.repeat(d_skip, HEAD_DIM)[None, :]
    gain = norm_gain[None, :]
    return mix(conv, u, z_gate, hbt, cum_g, cumt_g, segc, segr, eb, dsk, gain)


def solution(mesh):
    return jax.shard_map(
        local,
        mesh=mesh,
        in_specs=(
            P(("group", "ctx"), None),
            P(("group", "ctx"), None),
            P(("group", "ctx"), None),
            P("group"),
            P(),
            P(),
            P(),
            P(),
            P(),
            P(),
        ),
        out_specs=P(("group", "ctx"), None),
        check_vma=False,
    )
```

```python
import jax
import jax.numpy as jnp
from jax import lax
from jax.experimental import pallas as pl
from jax.experimental.pallas import tpu as pltpu
from jax.sharding import PartitionSpec as P

HEADS = 64
HEAD_DIM = 64
STATE = 256
GROUPS = 2
CONV = 4
STRETCH = 256
CHANNELS = 5120
INNER = HEADS * HEAD_DIM
PER_GROUP = HEADS // GROUPS
GROUP_COLS = INNER // GROUPS


def shifted(value, axis, by):
    peers = lax.axis_size(axis)
    pairs = [(i, i + by) for i in range(peers) if 0 <= i + by < peers]
    return lax.ppermute(value, axis, pairs)


def segment_of(positions, lengths):
    prompt_ends = jnp.cumsum(lengths)
    hits = (prompt_ends[None, :] <= positions[:, None]).astype(jnp.int32)
    return jnp.sum(hits, axis=1)


def causal_conv(extended, positions, lengths, conv_weight, conv_bias):
    out_rows = extended.shape[0] - (CONV - 1)
    segments = segment_of(positions, lengths)
    inside = positions >= 0
    target = segments[CONV - 1 :]
    summed = jnp.zeros((out_rows, extended.shape[1]), jnp.float32)
    for tap in range(CONV):
        kept = inside[tap : tap + out_rows] & (segments[tap : tap + out_rows] == target)
        term = extended[tap : tap + out_rows].astype(jnp.float32) * conv_weight[tap][None, :]
        summed = summed + jnp.where(kept[:, None], term, 0.0)
    return jax.nn.silu(summed + conv_bias[None, :]).astype(jnp.bfloat16)


def state_kernel(bt_ref, x_ref, dt_ref, cum_ref, segc_ref, out_ref, uw_ref):
    cum = cum_ref[0]
    step = dt_ref[0]
    segc = segc_ref[:, 0:1]
    last = cum[STRETCH - 1 : STRETCH, :]
    seg_last = segc[STRETCH - 1 : STRETCH, :]
    w = jnp.where(segc == seg_last, jnp.exp(last - cum), 0.0)
    for j in range(PER_GROUP):
        cols = slice(j * HEAD_DIM, (j + 1) * HEAD_DIM)
        scaled = (x_ref[:, cols].astype(jnp.float32) * step[:, j : j + 1]).astype(jnp.bfloat16)
        uw_ref[:, cols] = (scaled.astype(jnp.float32) * w[:, j : j + 1]).astype(jnp.bfloat16)
    out_ref[0] = jnp.dot(bt_ref[...], uw_ref[...], preferred_element_type=jnp.float32)


def block_states(bt, conv, dt_g, cum_g, segc):
    tok = conv.shape[0]
    nb = tok // STRETCH
    return pl.pallas_call(
        state_kernel,
        grid=(nb, GROUPS),
        in_specs=[
            pl.BlockSpec((STATE, STRETCH), lambda b, g: (g, b)),
            pl.BlockSpec((STRETCH, GROUP_COLS), lambda b, g: (b, g)),
            pl.BlockSpec((1, STRETCH, PER_GROUP), lambda b, g: (g, b, 0)),
            pl.BlockSpec((1, STRETCH, PER_GROUP), lambda b, g: (g, b, 0)),
            pl.BlockSpec((STRETCH, 128), lambda b, g: (b, 0)),
        ],
        out_specs=pl.BlockSpec((1, STATE, GROUP_COLS), lambda b, g: (b, 0, g)),
        out_shape=jax.ShapeDtypeStruct((nb, STATE, INNER), jnp.float32),
        scratch_shapes=[pltpu.VMEM((STRETCH, GROUP_COLS), jnp.bfloat16)],
    )(bt, conv, dt_g, cum_g, segc)


def mix_kernel(
    c_ref, b_ref, x_ref, dt_ref, z_ref, hbt_ref, cum_ref, cumt_ref, segc_ref, segr_ref, eb_ref,
    dsk_ref, gain_ref, out_ref, y_ref,
):
    cmat = c_ref[...]
    gram = lax.dot_general(
        cmat, b_ref[...], (((1,), (1,)), ((), ())), preferred_element_type=jnp.float32
    )
    segc = segc_ref[:, 0:1]
    segr = segr_ref[0:1, :]
    rows = lax.broadcasted_iota(jnp.int32, (STRETCH, STRETCH), 0)
    cols = lax.broadcasted_iota(jnp.int32, (STRETCH, STRETCH), 1)
    gram = jnp.where((segc == segr) & (cols <= rows), gram, 0.0)
    cum = cum_ref[0]
    cumt = cumt_ref[0]
    step = dt_ref[0]
    entry = eb_ref[0:1, 0:1]
    in_weight = jnp.where(segc == entry, jnp.exp(cum), 0.0)
    inter = jnp.dot(cmat, hbt_ref[0], preferred_element_type=jnp.float32)
    for j in range(PER_GROUP):
        hc = slice(j * HEAD_DIM, (j + 1) * HEAD_DIM)
        gap = jnp.minimum(cum[:, j : j + 1] - cumt[j : j + 1, :], 0.0)
        weights = (gram * jnp.exp(gap)).astype(jnp.bfloat16)
        scaled = (x_ref[:, hc].astype(jnp.float32) * step[:, j : j + 1]).astype(jnp.bfloat16)
        intra = jnp.dot(weights, scaled, preferred_element_type=jnp.float32)
        y_ref[:, hc] = intra + inter[:, hc] * in_weight[:, j : j + 1]
    y = y_ref[...] + dsk_ref[...] * x_ref[...].astype(jnp.float32)
    zf = z_ref[...].astype(jnp.float32)
    gated = y * (zf * jax.nn.sigmoid(zf))
    mean_square = jnp.mean(gated * gated, axis=1, keepdims=True) + 1e-05
    out_ref[...] = (gated * lax.rsqrt(mean_square) * gain_ref[...]).astype(jnp.bfloat16)


def mix(conv, dt_g, z_gate, hbt, cum_g, cumt_g, segc, segr, eb, dsk, gain):
    tok = conv.shape[0]
    nb = tok // STRETCH
    b_col = INNER // STATE
    c_col = b_col + GROUPS
    return pl.pallas_call(
        mix_kernel,
        grid=(nb, GROUPS),
        in_specs=[
            pl.BlockSpec((STRETCH, STATE), lambda b, g: (b, c_col + g)),
            pl.BlockSpec((STRETCH, STATE), lambda b, g: (b, b_col + g)),
            pl.BlockSpec((STRETCH, GROUP_COLS), lambda b, g: (b, g)),
            pl.BlockSpec((1, STRETCH, PER_GROUP), lambda b, g: (g, b, 0)),
            pl.BlockSpec((STRETCH, GROUP_COLS), lambda b, g: (b, g)),
            pl.BlockSpec((1, STATE, GROUP_COLS), lambda b, g: (b, 0, g)),
            pl.BlockSpec((1, STRETCH, PER_GROUP), lambda b, g: (g, b, 0)),
            pl.BlockSpec((1, PER_GROUP, STRETCH), lambda b, g: (g, 0, b)),
            pl.BlockSpec((STRETCH, 128), lambda b, g: (b, 0)),
            pl.BlockSpec((8, STRETCH), lambda b, g: (0, b)),
            pl.BlockSpec((8, 128), lambda b, g: (b, 0)),
            pl.BlockSpec((1, GROUP_COLS), lambda b, g: (0, g)),
            pl.BlockSpec((1, GROUP_COLS), lambda b, g: (0, g)),
        ],
        out_specs=pl.BlockSpec((STRETCH, GROUP_COLS), lambda b, g: (b, g)),
        out_shape=jax.ShapeDtypeStruct((tok, INNER), jnp.bfloat16),
        scratch_shapes=[pltpu.VMEM((STRETCH, GROUP_COLS), jnp.float32)],
    )(conv, conv, conv, dt_g, z_gate, hbt, cum_g, cumt_g, segc, segr, eb, dsk, gain)


def compose(state_dev, decay_dev):
    peers = lax.axis_size("ctx")
    width = INNER // peers
    pieces = state_dev.reshape(STATE, peers, width).transpose(1, 0, 2)
    decay_hi = decay_dev.astype(jnp.bfloat16)
    decay_lo = (decay_dev - decay_hi.astype(jnp.float32)).astype(jnp.bfloat16)
    payload = jnp.concatenate(
        [
            pieces.astype(jnp.bfloat16),
            decay_hi.reshape(peers, 1, width),
            decay_lo.reshape(peers, 1, width),
        ],
        axis=1,
    )
    got = lax.all_to_all(payload, "ctx", split_axis=0, concat_axis=0, tiled=True)
    states = got[:, :STATE, :].astype(jnp.float32)
    span = max(1, width // HEAD_DIM)
    sub = width // span
    decay_rows = got[:, STATE, :].astype(jnp.float32) + got[:, STATE + 1, :].astype(jnp.float32)
    decays = decay_rows.reshape(peers, span, sub)[:, :, 0].T
    dest = lax.broadcasted_iota(jnp.int32, (peers, peers, peers), 0)
    src = lax.broadcasted_iota(jnp.int32, (peers, peers, peers), 1)
    mid = lax.broadcasted_iota(jnp.int32, (peers, peers, peers), 2)
    between = (mid > src) & (mid < dest)
    factors = jnp.where(between[None], decays[:, None, None, :], 1.0)
    links = jnp.prod(factors, axis=3)
    links = jnp.where((src[:, :, 0] < dest[:, :, 0])[None], links, 0.0)
    entering = jnp.einsum(
        "hdj,jnhp->dnhp",
        links,
        states.reshape(peers, STATE, span, sub),
        precision=lax.Precision.HIGHEST,
    ).reshape(peers, STATE, width)
    back = lax.all_to_all(
        entering.astype(jnp.bfloat16), "ctx", split_axis=0, concat_axis=0, tiled=True
    )
    return back.transpose(1, 0, 2).reshape(STATE, INNER).astype(jnp.float32)


def local(xbc, z_gate, dt_raw, lengths, conv_weight, conv_bias, dt_bias, a_log, d_skip, norm_gain):
    tok = xbc.shape[0]
    nb = tok // STRETCH
    first_pos = lax.axis_index("ctx") * tok
    rim_rows = shifted(xbc[tok - (CONV - 1) :], "ctx", 1)
    extended = jnp.concatenate([rim_rows, xbc], axis=0)
    positions = first_pos - (CONV - 1) + jnp.arange(tok + CONV - 1)
    conv = causal_conv(extended, positions, lengths, conv_weight, conv_bias)
    step = jax.nn.softplus(dt_raw.astype(jnp.float32) + dt_bias[None, :])
    log_decay = -step * jnp.exp(a_log)[None, :]
    cum = jnp.cumsum(log_decay.reshape(nb, STRETCH, HEADS), axis=1).reshape(tok, HEADS)
    segments = segment_of(first_pos + jnp.arange(tok), lengths)
    seg_before = segment_of(first_pos + jnp.arange(nb) * STRETCH - 1, lengths)
    seg_last = segments.reshape(nb, STRETCH)[:, -1]
    cum_last = cum.reshape(nb, STRETCH, HEADS)[:, -1, :]
    block_decay = jnp.where((seg_last == seg_before)[:, None], jnp.exp(cum_last), 0.0)

    cum_g = cum.reshape(tok, GROUPS, PER_GROUP).transpose(1, 0, 2)
    dt_g = step.reshape(tok, GROUPS, PER_GROUP).transpose(1, 0, 2)
    cumt_g = cum.T.reshape(GROUPS, PER_GROUP, tok)
    segc = jnp.broadcast_to(segments[:, None], (tok, 128)).astype(jnp.int32)
    segr = jnp.broadcast_to(segments[None, :], (8, tok)).astype(jnp.int32)
    eb = jnp.broadcast_to(seg_before[:, None, None], (nb, 8, 128)).reshape(nb * 8, 128)
    eb = eb.astype(jnp.int32)
    bt = conv[:, INNER : INNER + GROUPS * STATE].T

    ends = block_states(bt, conv, dt_g, cum_g, segc)
    col_decay = jnp.repeat(block_decay, HEAD_DIM, axis=1)
    state_dev = ends[0]
    decay_dev = col_decay[0]
    for b in range(1, nb):
        state_dev = col_decay[b][None, :] * state_dev + ends[b]
        decay_dev = decay_dev * col_decay[b]
    state_in = compose(state_dev, decay_dev)
    entering = [state_in]
    for b in range(1, nb):
        entering.append(col_decay[b - 1][None, :] * entering[-1] + ends[b - 1])
    hbt = jnp.stack(entering).astype(jnp.bfloat16)

    dsk = jnp.repeat(d_skip, HEAD_DIM)[None, :]
    gain = norm_gain[None, :]
    return mix(conv, dt_g, z_gate, hbt, cum_g, cumt_g, segc, segr, eb, dsk, gain)


def solution(mesh):
    return jax.shard_map(
        local,
        mesh=mesh,
        in_specs=(
            P(("group", "ctx"), None),
            P(("group", "ctx"), None),
            P(("group", "ctx"), None),
            P("group"),
            P(),
            P(),
            P(),
            P(),
            P(),
            P(),
        ),
        out_specs=P(("group", "ctx"), None),
        check_vma=False,
    )
```

```python
import jax
import jax.numpy as jnp
from jax import lax
from jax.experimental import pallas as pl
from jax.experimental.pallas import tpu as pltpu
from jax.sharding import PartitionSpec as P

HEADS = 64
HEAD_DIM = 64
STATE = 256
GROUPS = 2
CONV = 4
STRETCH = 256
CHANNELS = 5120
INNER = HEADS * HEAD_DIM
PER_GROUP = HEADS // GROUPS
GROUP_COLS = INNER // GROUPS


def shifted(value, axis, by):
    peers = lax.axis_size(axis)
    pairs = [(i, i + by) for i in range(peers) if 0 <= i + by < peers]
    return lax.ppermute(value, axis, pairs)


def segment_of(positions, lengths):
    prompt_ends = jnp.cumsum(lengths)
    hits = (prompt_ends[None, :] <= positions[:, None]).astype(jnp.int32)
    return jnp.sum(hits, axis=1)


def causal_conv(extended, positions, lengths, conv_weight, conv_bias):
    out_rows = extended.shape[0] - (CONV - 1)
    segments = segment_of(positions, lengths)
    inside = positions >= 0
    target = segments[CONV - 1 :]
    summed = jnp.zeros((out_rows, extended.shape[1]), jnp.float32)
    for tap in range(CONV):
        kept = inside[tap : tap + out_rows] & (segments[tap : tap + out_rows] == target)
        term = extended[tap : tap + out_rows].astype(jnp.float32) * conv_weight[tap][None, :]
        summed = summed + jnp.where(kept[:, None], term, 0.0)
    return jax.nn.silu(summed + conv_bias[None, :]).astype(jnp.bfloat16)


def state_kernel(bt_ref, x_ref, dt_ref, cum_ref, segc_ref, out_ref, uw_ref):
    cum = cum_ref[0]
    step = dt_ref[0]
    segc = segc_ref[:, 0:1]
    last = cum[STRETCH - 1 : STRETCH, :]
    seg_last = segc[STRETCH - 1 : STRETCH, :]
    w = jnp.where(segc == seg_last, jnp.exp(last - cum), 0.0)
    for j in range(PER_GROUP):
        cols = slice(j * HEAD_DIM, (j + 1) * HEAD_DIM)
        scaled = (x_ref[:, cols].astype(jnp.float32) * step[:, j : j + 1]).astype(jnp.bfloat16)
        uw_ref[:, cols] = (scaled.astype(jnp.float32) * w[:, j : j + 1]).astype(jnp.bfloat16)
    out_ref[0] = jnp.dot(bt_ref[...], uw_ref[...], preferred_element_type=jnp.float32)


def block_states(bt, conv, dt_g, cum_g, segc):
    tok = conv.shape[0]
    nb = tok // STRETCH
    return pl.pallas_call(
        state_kernel,
        grid=(nb, GROUPS),
        in_specs=[
            pl.BlockSpec((STATE, STRETCH), lambda b, g: (g, b)),
            pl.BlockSpec((STRETCH, GROUP_COLS), lambda b, g: (b, g)),
            pl.BlockSpec((1, STRETCH, PER_GROUP), lambda b, g: (g, b, 0)),
            pl.BlockSpec((1, STRETCH, PER_GROUP), lambda b, g: (g, b, 0)),
            pl.BlockSpec((STRETCH, 128), lambda b, g: (b, 0)),
        ],
        out_specs=pl.BlockSpec((1, STATE, GROUP_COLS), lambda b, g: (b, 0, g)),
        out_shape=jax.ShapeDtypeStruct((nb, STATE, INNER), jnp.float32),
        scratch_shapes=[pltpu.VMEM((STRETCH, GROUP_COLS), jnp.bfloat16)],
    )(bt, conv, dt_g, cum_g, segc)


def intra_kernel(
    c_ref, b_ref, x_ref, dt_ref, cum_ref, cumt_ref, segc_ref, segr_ref, dsk_ref, out_ref
):
    gram = lax.dot_general(
        c_ref[...], b_ref[...], (((1,), (1,)), ((), ())), preferred_element_type=jnp.float32
    )
    segc = segc_ref[:, 0:1]
    segr = segr_ref[0:1, :]
    rows = lax.broadcasted_iota(jnp.int32, (STRETCH, STRETCH), 0)
    cols = lax.broadcasted_iota(jnp.int32, (STRETCH, STRETCH), 1)
    gram = jnp.where((segc == segr) & (cols <= rows), gram, 0.0)
    cum = cum_ref[0]
    cumt = cumt_ref[0]
    step = dt_ref[0]
    for j in range(PER_GROUP):
        hc = slice(j * HEAD_DIM, (j + 1) * HEAD_DIM)
        gap = jnp.minimum(cum[:, j : j + 1] - cumt[j : j + 1, :], 0.0)
        weights = (gram * jnp.exp(gap)).astype(jnp.bfloat16)
        xf = x_ref[:, hc].astype(jnp.float32)
        scaled = (xf * step[:, j : j + 1]).astype(jnp.bfloat16)
        intra = jnp.dot(weights, scaled, preferred_element_type=jnp.float32)
        out_ref[:, hc] = intra + dsk_ref[:, hc] * xf


def intra_part(conv, dt_g, cum_g, cumt_g, segc, segr, dsk):
    tok = conv.shape[0]
    nb = tok // STRETCH
    b_col = INNER // STATE
    c_col = b_col + GROUPS
    return pl.pallas_call(
        intra_kernel,
        grid=(nb, GROUPS),
        in_specs=[
            pl.BlockSpec((STRETCH, STATE), lambda b, g: (b, c_col + g)),
            pl.BlockSpec((STRETCH, STATE), lambda b, g: (b, b_col + g)),
            pl.BlockSpec((STRETCH, GROUP_COLS), lambda b, g: (b, g)),
            pl.BlockSpec((1, STRETCH, PER_GROUP), lambda b, g: (g, b, 0)),
            pl.BlockSpec((1, STRETCH, PER_GROUP), lambda b, g: (g, b, 0)),
            pl.BlockSpec((1, PER_GROUP, STRETCH), lambda b, g: (g, 0, b)),
            pl.BlockSpec((STRETCH, 128), lambda b, g: (b, 0)),
            pl.BlockSpec((8, STRETCH), lambda b, g: (0, b)),
            pl.BlockSpec((1, GROUP_COLS), lambda b, g: (0, g)),
        ],
        out_specs=pl.BlockSpec((STRETCH, GROUP_COLS), lambda b, g: (b, g)),
        out_shape=jax.ShapeDtypeStruct((tok, INNER), jnp.float32),
    )(conv, conv, conv, dt_g, cum_g, cumt_g, segc, segr, dsk)


def mix_kernel(
    c_ref, y_ref, z_ref, hbt_ref, cum_ref, segc_ref, eb_ref, gain_ref, out_ref, acc_ref
):
    segc = segc_ref[:, 0:1]
    entry = eb_ref[0:1, 0:1]
    in_weight = jnp.where(segc == entry, jnp.exp(cum_ref[0]), 0.0)
    inter = jnp.dot(c_ref[...], hbt_ref[0], preferred_element_type=jnp.float32)
    for j in range(PER_GROUP):
        hc = slice(j * HEAD_DIM, (j + 1) * HEAD_DIM)
        acc_ref[:, hc] = inter[:, hc] * in_weight[:, j : j + 1]
    y = y_ref[...] + acc_ref[...]
    zf = z_ref[...].astype(jnp.float32)
    gated = y * (zf * jax.nn.sigmoid(zf))
    mean_square = jnp.mean(gated * gated, axis=1, keepdims=True) + 1e-05
    out_ref[...] = (gated * lax.rsqrt(mean_square) * gain_ref[...]).astype(jnp.bfloat16)


def mix(conv, y_local, z_gate, hbt, cum_g, segc, eb, gain):
    tok = conv.shape[0]
    nb = tok // STRETCH
    c_col = INNER // STATE + GROUPS
    return pl.pallas_call(
        mix_kernel,
        grid=(nb, GROUPS),
        in_specs=[
            pl.BlockSpec((STRETCH, STATE), lambda b, g: (b, c_col + g)),
            pl.BlockSpec((STRETCH, GROUP_COLS), lambda b, g: (b, g)),
            pl.BlockSpec((STRETCH, GROUP_COLS), lambda b, g: (b, g)),
            pl.BlockSpec((1, STATE, GROUP_COLS), lambda b, g: (b, 0, g)),
            pl.BlockSpec((1, STRETCH, PER_GROUP), lambda b, g: (g, b, 0)),
            pl.BlockSpec((STRETCH, 128), lambda b, g: (b, 0)),
            pl.BlockSpec((8, 128), lambda b, g: (b, 0)),
            pl.BlockSpec((1, GROUP_COLS), lambda b, g: (0, g)),
        ],
        out_specs=pl.BlockSpec((STRETCH, GROUP_COLS), lambda b, g: (b, g)),
        out_shape=jax.ShapeDtypeStruct((tok, INNER), jnp.bfloat16),
        scratch_shapes=[pltpu.VMEM((STRETCH, GROUP_COLS), jnp.float32)],
    )(conv, y_local, z_gate, hbt, cum_g, segc, eb, gain)


def compose(state_dev, decay_dev):
    peers = lax.axis_size("ctx")
    width = INNER // peers
    pieces = state_dev.reshape(STATE, peers, width).transpose(1, 0, 2)
    decay_hi = decay_dev.astype(jnp.bfloat16)
    decay_lo = (decay_dev - decay_hi.astype(jnp.float32)).astype(jnp.bfloat16)
    payload = jnp.concatenate(
        [
            pieces.astype(jnp.bfloat16),
            decay_hi.reshape(peers, 1, width),
            decay_lo.reshape(peers, 1, width),
        ],
        axis=1,
    )
    got = lax.all_to_all(payload, "ctx", split_axis=0, concat_axis=0, tiled=True)
    states = got[:, :STATE, :].astype(jnp.float32)
    span = max(1, width // HEAD_DIM)
    sub = width // span
    decay_rows = got[:, STATE, :].astype(jnp.float32) + got[:, STATE + 1, :].astype(jnp.float32)
    decays = decay_rows.reshape(peers, span, sub)[:, :, 0].T
    dest = lax.broadcasted_iota(jnp.int32, (peers, peers, peers), 0)
    src = lax.broadcasted_iota(jnp.int32, (peers, peers, peers), 1)
    mid = lax.broadcasted_iota(jnp.int32, (peers, peers, peers), 2)
    between = (mid > src) & (mid < dest)
    factors = jnp.where(between[None], decays[:, None, None, :], 1.0)
    links = jnp.prod(factors, axis=3)
    links = jnp.where((src[:, :, 0] < dest[:, :, 0])[None], links, 0.0)
    entering = jnp.einsum(
        "hdj,jnhp->dnhp",
        links,
        states.reshape(peers, STATE, span, sub),
        precision=lax.Precision.HIGHEST,
    ).reshape(peers, STATE, width)
    back = lax.all_to_all(
        entering.astype(jnp.bfloat16), "ctx", split_axis=0, concat_axis=0, tiled=True
    )
    return back.transpose(1, 0, 2).reshape(STATE, INNER).astype(jnp.float32)


def local(xbc, z_gate, dt_raw, lengths, conv_weight, conv_bias, dt_bias, a_log, d_skip, norm_gain):
    tok = xbc.shape[0]
    nb = tok // STRETCH
    first_pos = lax.axis_index("ctx") * tok
    rim_rows = shifted(xbc[tok - (CONV - 1) :], "ctx", 1)
    extended = jnp.concatenate([rim_rows, xbc], axis=0)
    positions = first_pos - (CONV - 1) + jnp.arange(tok + CONV - 1)
    conv = causal_conv(extended, positions, lengths, conv_weight, conv_bias)
    step = jax.nn.softplus(dt_raw.astype(jnp.float32) + dt_bias[None, :])
    log_decay = -step * jnp.exp(a_log)[None, :]
    cum = jnp.cumsum(log_decay.reshape(nb, STRETCH, HEADS), axis=1).reshape(tok, HEADS)
    segments = segment_of(first_pos + jnp.arange(tok), lengths)
    seg_before = segment_of(first_pos + jnp.arange(nb) * STRETCH - 1, lengths)
    seg_last = segments.reshape(nb, STRETCH)[:, -1]
    cum_last = cum.reshape(nb, STRETCH, HEADS)[:, -1, :]
    block_decay = jnp.where((seg_last == seg_before)[:, None], jnp.exp(cum_last), 0.0)

    cum_g = cum.reshape(tok, GROUPS, PER_GROUP).transpose(1, 0, 2)
    dt_g = step.reshape(tok, GROUPS, PER_GROUP).transpose(1, 0, 2)
    cumt_g = cum.T.reshape(GROUPS, PER_GROUP, tok)
    segc = jnp.broadcast_to(segments[:, None], (tok, 128)).astype(jnp.int32)
    segr = jnp.broadcast_to(segments[None, :], (8, tok)).astype(jnp.int32)
    eb = jnp.broadcast_to(seg_before[:, None, None], (nb, 8, 128)).reshape(nb * 8, 128)
    eb = eb.astype(jnp.int32)
    bt = conv[:, INNER : INNER + GROUPS * STATE].T

    ends = block_states(bt, conv, dt_g, cum_g, segc)
    dsk = jnp.repeat(d_skip, HEAD_DIM)[None, :]
    y_local = intra_part(conv, dt_g, cum_g, cumt_g, segc, segr, dsk)
    col_decay = jnp.repeat(block_decay, HEAD_DIM, axis=1)
    state_dev = ends[0]
    decay_dev = col_decay[0]
    for b in range(1, nb):
        state_dev = col_decay[b][None, :] * state_dev + ends[b]
        decay_dev = decay_dev * col_decay[b]
    state_in = compose(state_dev, decay_dev)
    entering = [state_in]
    for b in range(1, nb):
        entering.append(col_decay[b - 1][None, :] * entering[-1] + ends[b - 1])
    hbt = jnp.stack(entering).astype(jnp.bfloat16)
    gain = norm_gain[None, :]
    return mix(conv, y_local, z_gate, hbt, cum_g, segc, eb, gain)


def solution(mesh):
    return jax.shard_map(
        local,
        mesh=mesh,
        in_specs=(
            P(("group", "ctx"), None),
            P(("group", "ctx"), None),
            P(("group", "ctx"), None),
            P("group"),
            P(),
            P(),
            P(),
            P(),
            P(),
            P(),
        ),
        out_specs=P(("group", "ctx"), None),
        check_vma=False,
    )
```

```python
import jax
import jax.numpy as jnp
from jax import lax
from jax.experimental import pallas as pl
from jax.experimental.pallas import tpu as pltpu
from jax.sharding import PartitionSpec as P

HEADS = 64
HEAD_DIM = 64
STATE = 256
GROUPS = 2
CONV = 4
STRETCH = 256
CHANNELS = 5120
INNER = HEADS * HEAD_DIM
PER_GROUP = HEADS // GROUPS
GROUP_COLS = INNER // GROUPS


def shifted(value, axis, by):
    peers = lax.axis_size(axis)
    pairs = [(i, i + by) for i in range(peers) if 0 <= i + by < peers]
    return lax.ppermute(value, axis, pairs)


def segment_of(positions, lengths):
    prompt_ends = jnp.cumsum(lengths)
    hits = (prompt_ends[None, :] <= positions[:, None]).astype(jnp.int32)
    return jnp.sum(hits, axis=1)


def causal_conv(extended, positions, lengths, conv_weight, conv_bias):
    out_rows = extended.shape[0] - (CONV - 1)
    segments = segment_of(positions, lengths)
    inside = positions >= 0
    target = segments[CONV - 1 :]
    summed = jnp.zeros((out_rows, extended.shape[1]), jnp.float32)
    for tap in range(CONV):
        kept = inside[tap : tap + out_rows] & (segments[tap : tap + out_rows] == target)
        term = extended[tap : tap + out_rows].astype(jnp.float32) * conv_weight[tap][None, :]
        summed = summed + jnp.where(kept[:, None], term, 0.0)
    return jax.nn.silu(summed + conv_bias[None, :]).astype(jnp.bfloat16)


def state_kernel(bt_ref, x_ref, dt_ref, cum_ref, segc_ref, out_ref, uw_ref):
    cum = cum_ref[0]
    step = dt_ref[0]
    segc = segc_ref[:, 0:1]
    last = cum[STRETCH - 1 : STRETCH, :]
    seg_last = segc[STRETCH - 1 : STRETCH, :]
    w = jnp.where(segc == seg_last, jnp.exp(last - cum), 0.0)
    for j in range(PER_GROUP):
        cols = slice(j * HEAD_DIM, (j + 1) * HEAD_DIM)
        scaled = (x_ref[:, cols].astype(jnp.float32) * step[:, j : j + 1]).astype(jnp.bfloat16)
        uw_ref[:, cols] = (scaled.astype(jnp.float32) * w[:, j : j + 1]).astype(jnp.bfloat16)
    out_ref[0] = jnp.dot(bt_ref[...], uw_ref[...], preferred_element_type=jnp.float32)


def block_states(bt, conv, dt_g, cum_g, segc, g):
    tok = conv.shape[0]
    nb = tok // STRETCH
    return pl.pallas_call(
        state_kernel,
        grid=(nb,),
        in_specs=[
            pl.BlockSpec((STATE, STRETCH), lambda b: (g, b)),
            pl.BlockSpec((STRETCH, GROUP_COLS), lambda b: (b, g)),
            pl.BlockSpec((1, STRETCH, PER_GROUP), lambda b: (g, b, 0)),
            pl.BlockSpec((1, STRETCH, PER_GROUP), lambda b: (g, b, 0)),
            pl.BlockSpec((STRETCH, 128), lambda b: (b, 0)),
        ],
        out_specs=pl.BlockSpec((1, STATE, GROUP_COLS), lambda b: (b, 0, 0)),
        out_shape=jax.ShapeDtypeStruct((nb, STATE, GROUP_COLS), jnp.float32),
        scratch_shapes=[pltpu.VMEM((STRETCH, GROUP_COLS), jnp.bfloat16)],
    )(bt, conv, dt_g, cum_g, segc)


def intra_kernel(
    c_ref, b_ref, x_ref, dt_ref, cum_ref, cumt_ref, segc_ref, segr_ref, dsk_ref, out_ref
):
    gram = lax.dot_general(
        c_ref[...], b_ref[...], (((1,), (1,)), ((), ())), preferred_element_type=jnp.float32
    )
    segc = segc_ref[:, 0:1]
    segr = segr_ref[0:1, :]
    rows = lax.broadcasted_iota(jnp.int32, (STRETCH, STRETCH), 0)
    cols = lax.broadcasted_iota(jnp.int32, (STRETCH, STRETCH), 1)
    gram = jnp.where((segc == segr) & (cols <= rows), gram, 0.0)
    cum = cum_ref[0]
    cumt = cumt_ref[0]
    step = dt_ref[0]
    for j in range(PER_GROUP):
        hc = slice(j * HEAD_DIM, (j + 1) * HEAD_DIM)
        gap = jnp.minimum(cum[:, j : j + 1] - cumt[j : j + 1, :], 0.0)
        weights = (gram * jnp.exp(gap)).astype(jnp.bfloat16)
        xf = x_ref[:, hc].astype(jnp.float32)
        scaled = (xf * step[:, j : j + 1]).astype(jnp.bfloat16)
        intra = jnp.dot(weights, scaled, preferred_element_type=jnp.float32)
        out_ref[:, hc] = intra + dsk_ref[:, hc] * xf


def intra_part(conv, dt_g, cum_g, cumt_g, segc, segr, dsk):
    tok = conv.shape[0]
    nb = tok // STRETCH
    b_col = INNER // STATE
    c_col = b_col + GROUPS
    return pl.pallas_call(
        intra_kernel,
        grid=(nb, GROUPS),
        in_specs=[
            pl.BlockSpec((STRETCH, STATE), lambda b, g: (b, c_col + g)),
            pl.BlockSpec((STRETCH, STATE), lambda b, g: (b, b_col + g)),
            pl.BlockSpec((STRETCH, GROUP_COLS), lambda b, g: (b, g)),
            pl.BlockSpec((1, STRETCH, PER_GROUP), lambda b, g: (g, b, 0)),
            pl.BlockSpec((1, STRETCH, PER_GROUP), lambda b, g: (g, b, 0)),
            pl.BlockSpec((1, PER_GROUP, STRETCH), lambda b, g: (g, 0, b)),
            pl.BlockSpec((STRETCH, 128), lambda b, g: (b, 0)),
            pl.BlockSpec((8, STRETCH), lambda b, g: (0, b)),
            pl.BlockSpec((1, GROUP_COLS), lambda b, g: (0, g)),
        ],
        out_specs=pl.BlockSpec((STRETCH, GROUP_COLS), lambda b, g: (b, g)),
        out_shape=jax.ShapeDtypeStruct((tok, INNER), jnp.float32),
    )(conv, conv, conv, dt_g, cum_g, cumt_g, segc, segr, dsk)


def mix_kernel(
    c_ref, y_ref, z_ref, hbt_ref, cum_ref, segc_ref, eb_ref, gain_ref, out_ref, acc_ref
):
    segc = segc_ref[:, 0:1]
    entry = eb_ref[0:1, 0:1]
    in_weight = jnp.where(segc == entry, jnp.exp(cum_ref[0]), 0.0)
    inter = jnp.dot(c_ref[...], hbt_ref[0], preferred_element_type=jnp.float32)
    for j in range(PER_GROUP):
        hc = slice(j * HEAD_DIM, (j + 1) * HEAD_DIM)
        acc_ref[:, hc] = inter[:, hc] * in_weight[:, j : j + 1]
    y = y_ref[...] + acc_ref[...]
    zf = z_ref[...].astype(jnp.float32)
    gated = y * (zf * jax.nn.sigmoid(zf))
    mean_square = jnp.mean(gated * gated, axis=1, keepdims=True) + 1e-05
    out_ref[...] = (gated * lax.rsqrt(mean_square) * gain_ref[...]).astype(jnp.bfloat16)


def mix(conv, y_local, z_gate, hbt, cum_g, segc, eb, gain, g):
    tok = conv.shape[0]
    nb = tok // STRETCH
    c_col = INNER // STATE + GROUPS
    return pl.pallas_call(
        mix_kernel,
        grid=(nb,),
        in_specs=[
            pl.BlockSpec((STRETCH, STATE), lambda b: (b, c_col + g)),
            pl.BlockSpec((STRETCH, GROUP_COLS), lambda b: (b, g)),
            pl.BlockSpec((STRETCH, GROUP_COLS), lambda b: (b, g)),
            pl.BlockSpec((1, STATE, GROUP_COLS), lambda b: (b, 0, 0)),
            pl.BlockSpec((1, STRETCH, PER_GROUP), lambda b: (g, b, 0)),
            pl.BlockSpec((STRETCH, 128), lambda b: (b, 0)),
            pl.BlockSpec((8, 128), lambda b: (b, 0)),
            pl.BlockSpec((1, GROUP_COLS), lambda b: (0, g)),
        ],
        out_specs=pl.BlockSpec((STRETCH, GROUP_COLS), lambda b: (b, 0)),
        out_shape=jax.ShapeDtypeStruct((tok, GROUP_COLS), jnp.bfloat16),
        scratch_shapes=[pltpu.VMEM((STRETCH, GROUP_COLS), jnp.float32)],
    )(conv, y_local, z_gate, hbt, cum_g, segc, eb, gain)


def compose(state_dev, decay_dev):
    peers = lax.axis_size("ctx")
    total = state_dev.shape[1]
    width = total // peers
    pieces = state_dev.reshape(STATE, peers, width).transpose(1, 0, 2)
    decay_hi = decay_dev.astype(jnp.bfloat16)
    decay_lo = (decay_dev - decay_hi.astype(jnp.float32)).astype(jnp.bfloat16)
    payload = jnp.concatenate(
        [
            pieces.astype(jnp.bfloat16),
            decay_hi.reshape(peers, 1, width),
            decay_lo.reshape(peers, 1, width),
        ],
        axis=1,
    )
    got = lax.all_to_all(payload, "ctx", split_axis=0, concat_axis=0, tiled=True)
    states = got[:, :STATE, :].astype(jnp.float32)
    span = max(1, width // HEAD_DIM)
    sub = width // span
    decay_rows = got[:, STATE, :].astype(jnp.float32) + got[:, STATE + 1, :].astype(jnp.float32)
    decays = decay_rows.reshape(peers, span, sub)[:, :, 0].T
    dest = lax.broadcasted_iota(jnp.int32, (peers, peers, peers), 0)
    src = lax.broadcasted_iota(jnp.int32, (peers, peers, peers), 1)
    mid = lax.broadcasted_iota(jnp.int32, (peers, peers, peers), 2)
    between = (mid > src) & (mid < dest)
    factors = jnp.where(between[None], decays[:, None, None, :], 1.0)
    links = jnp.prod(factors, axis=3)
    links = jnp.where((src[:, :, 0] < dest[:, :, 0])[None], links, 0.0)
    entering = jnp.einsum(
        "hdj,jnhp->dnhp",
        links,
        states.reshape(peers, STATE, span, sub),
        precision=lax.Precision.HIGHEST,
    ).reshape(peers, STATE, width)
    back = lax.all_to_all(
        entering.astype(jnp.bfloat16), "ctx", split_axis=0, concat_axis=0, tiled=True
    )
    return back.transpose(1, 0, 2).reshape(STATE, total).astype(jnp.float32)


def local(xbc, z_gate, dt_raw, lengths, conv_weight, conv_bias, dt_bias, a_log, d_skip, norm_gain):
    tok = xbc.shape[0]
    nb = tok // STRETCH
    first_pos = lax.axis_index("ctx") * tok
    rim_rows = shifted(xbc[tok - (CONV - 1) :], "ctx", 1)
    extended = jnp.concatenate([rim_rows, xbc], axis=0)
    positions = first_pos - (CONV - 1) + jnp.arange(tok + CONV - 1)
    conv = causal_conv(extended, positions, lengths, conv_weight, conv_bias)
    step = jax.nn.softplus(dt_raw.astype(jnp.float32) + dt_bias[None, :])
    log_decay = -step * jnp.exp(a_log)[None, :]
    cum = jnp.cumsum(log_decay.reshape(nb, STRETCH, HEADS), axis=1).reshape(tok, HEADS)
    segments = segment_of(first_pos + jnp.arange(tok), lengths)
    seg_before = segment_of(first_pos + jnp.arange(nb) * STRETCH - 1, lengths)
    seg_last = segments.reshape(nb, STRETCH)[:, -1]
    cum_last = cum.reshape(nb, STRETCH, HEADS)[:, -1, :]
    block_decay = jnp.where((seg_last == seg_before)[:, None], jnp.exp(cum_last), 0.0)

    cum_g = cum.reshape(tok, GROUPS, PER_GROUP).transpose(1, 0, 2)
    dt_g = step.reshape(tok, GROUPS, PER_GROUP).transpose(1, 0, 2)
    cumt_g = cum.T.reshape(GROUPS, PER_GROUP, tok)
    segc = jnp.broadcast_to(segments[:, None], (tok, 128)).astype(jnp.int32)
    segr = jnp.broadcast_to(segments[None, :], (8, tok)).astype(jnp.int32)
    eb = jnp.broadcast_to(seg_before[:, None, None], (nb, 8, 128)).reshape(nb * 8, 128)
    eb = eb.astype(jnp.int32)
    bt = conv[:, INNER : INNER + GROUPS * STATE].T

    dsk = jnp.repeat(d_skip, HEAD_DIM)[None, :]
    gain = norm_gain[None, :]
    col_decay = jnp.repeat(block_decay, HEAD_DIM, axis=1).reshape(nb, GROUPS, GROUP_COLS)
    y_local = intra_part(conv, dt_g, cum_g, cumt_g, segc, segr, dsk)
    outs = []
    for g in range(GROUPS):
        ends = block_states(bt, conv, dt_g, cum_g, segc, g)
        state_dev = ends[0]
        decay_dev = col_decay[0, g]
        for b in range(1, nb):
            state_dev = col_decay[b, g][None, :] * state_dev + ends[b]
            decay_dev = decay_dev * col_decay[b, g]
        state_in = compose(state_dev, decay_dev)
        entering = [state_in]
        for b in range(1, nb):
            entering.append(col_decay[b - 1, g][None, :] * entering[-1] + ends[b - 1])
        hbt = jnp.stack(entering).astype(jnp.bfloat16)
        outs.append(mix(conv, y_local, z_gate, hbt, cum_g, segc, eb, gain, g))
    return jnp.concatenate(outs, axis=1)


def solution(mesh):
    return jax.shard_map(
        local,
        mesh=mesh,
        in_specs=(
            P(("group", "ctx"), None),
            P(("group", "ctx"), None),
            P(("group", "ctx"), None),
            P("group"),
            P(),
            P(),
            P(),
            P(),
            P(),
            P(),
        ),
        out_specs=P(("group", "ctx"), None),
        check_vma=False,
    )
```

```python
import jax
import jax.numpy as jnp
from jax import lax
from jax.experimental import pallas as pl
from jax.experimental.pallas import tpu as pltpu
from jax.sharding import PartitionSpec as P

HEADS = 64
HEAD_DIM = 64
STATE = 256
GROUPS = 2
CONV = 4
STRETCH = 256
CHANNELS = 5120
INNER = HEADS * HEAD_DIM
PER_GROUP = HEADS // GROUPS
GROUP_COLS = INNER // GROUPS


def shifted(value, axis, by):
    peers = lax.axis_size(axis)
    pairs = [(i, i + by) for i in range(peers) if 0 <= i + by < peers]
    return lax.ppermute(value, axis, pairs)


def segment_of(positions, lengths):
    prompt_ends = jnp.cumsum(lengths)
    hits = (prompt_ends[None, :] <= positions[:, None]).astype(jnp.int32)
    return jnp.sum(hits, axis=1)


CONV_COLS = 640


def conv_kernel(x_ref, rim_ref, w_ref, bias_ref, m_ref, out_ref):
    x = x_ref[...].astype(jnp.float32)
    rim = rim_ref[...].astype(jnp.float32)
    rows8 = lax.broadcasted_iota(jnp.int32, rim.shape, 0)
    summed = jnp.zeros(x.shape, jnp.float32)
    top = jnp.zeros(rim.shape, jnp.float32)
    for tap in range(CONV):
        by = CONV - 1 - tap
        wk = w_ref[tap : tap + 1, :]
        kept = m_ref[:, tap : tap + 1] > 0.0
        if by == 0:
            term = x
            top_term = x[0:8]
        else:
            term = pltpu.roll(x, by, 0)
            top_term = jnp.where(rows8 < by, pltpu.roll(rim, by, 0), term[0:8])
        summed = summed + jnp.where(kept, term * wk, 0.0)
        top = top + jnp.where(kept[0:8], top_term * wk, 0.0)
    out_ref[...] = jax.nn.silu(summed + bias_ref[...]).astype(jnp.bfloat16)
    out_ref[0:8, :] = jax.nn.silu(top + bias_ref[...]).astype(jnp.bfloat16)


def conv_part(xbc, rim8, w8, bias, masks):
    tok, chans = xbc.shape
    return pl.pallas_call(
        conv_kernel,
        grid=(chans // CONV_COLS,),
        in_specs=[
            pl.BlockSpec((tok, CONV_COLS), lambda c: (0, c)),
            pl.BlockSpec((8, CONV_COLS), lambda c: (0, c)),
            pl.BlockSpec((8, CONV_COLS), lambda c: (0, c)),
            pl.BlockSpec((1, CONV_COLS), lambda c: (0, c)),
            pl.BlockSpec((tok, 128), lambda c: (0, 0)),
        ],
        out_specs=pl.BlockSpec((tok, CONV_COLS), lambda c: (0, c)),
        out_shape=jax.ShapeDtypeStruct((tok, chans), jnp.bfloat16),
    )(xbc, rim8, w8, bias, masks)


def state_kernel(
    bt_ref, x_ref, dt_ref, cum_ref, segc_ref, bdec_ref, local_ref, cdec_ref, pay_ref,
    uw_ref, acc_ref, dec_ref,
):
    b = pl.program_id(1)

    @pl.when(b == 0)
    def _():
        acc_ref[...] = jnp.zeros(acc_ref.shape, jnp.float32)
        dec_ref[...] = jnp.ones(dec_ref.shape, jnp.float32)

    local_ref[0] = acc_ref[...]
    cdec_ref[0] = dec_ref[...]
    cum = cum_ref[0]
    step = dt_ref[0]
    segc = segc_ref[:, 0:1]
    last = cum[STRETCH - 1 : STRETCH, :]
    seg_last = segc[STRETCH - 1 : STRETCH, :]
    w = jnp.where(segc == seg_last, jnp.exp(last - cum), 0.0)
    for j in range(PER_GROUP):
        cols = slice(j * HEAD_DIM, (j + 1) * HEAD_DIM)
        scaled = (x_ref[:, cols].astype(jnp.float32) * step[:, j : j + 1]).astype(jnp.bfloat16)
        uw_ref[:, cols] = (scaled.astype(jnp.float32) * w[:, j : j + 1]).astype(jnp.bfloat16)
    block_state = jnp.dot(bt_ref[...], uw_ref[...], preferred_element_type=jnp.float32)
    decay = bdec_ref[0]
    acc_ref[...] = decay * acc_ref[...] + block_state
    dec_ref[...] = dec_ref[...] * decay

    @pl.when(b == pl.num_programs(1) - 1)
    def _():
        pieces, _, width = pay_ref.shape
        total = acc_ref[...]
        dec = dec_ref[...]
        hi = dec.astype(jnp.bfloat16)
        lo = (dec - hi.astype(jnp.float32)).astype(jnp.bfloat16)
        for k in range(pieces):
            cols = slice(k * width, (k + 1) * width)
            pay_ref[k, 0:STATE, :] = total[:, cols].astype(jnp.bfloat16)
            pay_ref[k, STATE : STATE + 1, :] = hi[:, cols]
            pay_ref[k, STATE + 1 : STATE + 2, :] = lo[:, cols]


def block_states(bt, conv, dt_g, cum_g, segc, bdec, peers):
    tok = conv.shape[0]
    nb = tok // STRETCH
    width = INNER // peers
    per = peers // GROUPS
    return pl.pallas_call(
        state_kernel,
        grid=(GROUPS, nb),
        in_specs=[
            pl.BlockSpec((STATE, STRETCH), lambda g, b: (g, b)),
            pl.BlockSpec((STRETCH, GROUP_COLS), lambda g, b: (b, g)),
            pl.BlockSpec((1, STRETCH, PER_GROUP), lambda g, b: (g, b, 0)),
            pl.BlockSpec((1, STRETCH, PER_GROUP), lambda g, b: (g, b, 0)),
            pl.BlockSpec((STRETCH, 128), lambda g, b: (b, 0)),
            pl.BlockSpec((1, 1, GROUP_COLS), lambda g, b: (b, 0, g)),
        ],
        out_specs=[
            pl.BlockSpec((1, STATE, GROUP_COLS), lambda g, b: (b, 0, g)),
            pl.BlockSpec((1, 1, GROUP_COLS), lambda g, b: (b, 0, g)),
            pl.BlockSpec((per, STATE + 2, width), lambda g, b: (g, 0, 0)),
        ],
        out_shape=[
            jax.ShapeDtypeStruct((nb, STATE, INNER), jnp.float32),
            jax.ShapeDtypeStruct((nb, 1, INNER), jnp.float32),
            jax.ShapeDtypeStruct((peers, STATE + 2, width), jnp.bfloat16),
        ],
        scratch_shapes=[
            pltpu.VMEM((STRETCH, GROUP_COLS), jnp.bfloat16),
            pltpu.VMEM((STATE, GROUP_COLS), jnp.float32),
            pltpu.VMEM((1, GROUP_COLS), jnp.float32),
        ],
    )(bt, conv, dt_g, cum_g, segc, bdec)


def intra_kernel(
    c_ref, b_ref, x_ref, dt_ref, cum_ref, cumt_ref, segc_ref, segr_ref, dsk_ref, out_ref
):
    gram = lax.dot_general(
        c_ref[...], b_ref[...], (((1,), (1,)), ((), ())), preferred_element_type=jnp.float32
    )
    segc = segc_ref[:, 0:1]
    segr = segr_ref[0:1, :]
    rows = lax.broadcasted_iota(jnp.int32, (STRETCH, STRETCH), 0)
    cols = lax.broadcasted_iota(jnp.int32, (STRETCH, STRETCH), 1)
    gram = jnp.where((segc == segr) & (cols <= rows), gram, 0.0)
    cum = cum_ref[0]
    cumt = cumt_ref[0]
    step = dt_ref[0]
    for j in range(PER_GROUP):
        hc = slice(j * HEAD_DIM, (j + 1) * HEAD_DIM)
        gap = jnp.minimum(cum[:, j : j + 1] - cumt[j : j + 1, :], 0.0)
        weights = (gram * jnp.exp(gap)).astype(jnp.bfloat16)
        xf = x_ref[:, hc].astype(jnp.float32)
        scaled = (xf * step[:, j : j + 1]).astype(jnp.bfloat16)
        intra = jnp.dot(weights, scaled, preferred_element_type=jnp.float32)
        out_ref[:, hc] = intra + dsk_ref[:, hc] * xf


def intra_part(conv, dt_g, cum_g, cumt_g, segc, segr, dsk):
    tok = conv.shape[0]
    nb = tok // STRETCH
    b_col = INNER // STATE
    c_col = b_col + GROUPS
    return pl.pallas_call(
        intra_kernel,
        grid=(nb, GROUPS),
        in_specs=[
            pl.BlockSpec((STRETCH, STATE), lambda b, g: (b, c_col + g)),
            pl.BlockSpec((STRETCH, STATE), lambda b, g: (b, b_col + g)),
            pl.BlockSpec((STRETCH, GROUP_COLS), lambda b, g: (b, g)),
            pl.BlockSpec((1, STRETCH, PER_GROUP), lambda b, g: (g, b, 0)),
            pl.BlockSpec((1, STRETCH, PER_GROUP), lambda b, g: (g, b, 0)),
            pl.BlockSpec((1, PER_GROUP, STRETCH), lambda b, g: (g, 0, b)),
            pl.BlockSpec((STRETCH, 128), lambda b, g: (b, 0)),
            pl.BlockSpec((8, STRETCH), lambda b, g: (0, b)),
            pl.BlockSpec((1, GROUP_COLS), lambda b, g: (0, g)),
        ],
        out_specs=pl.BlockSpec((STRETCH, GROUP_COLS), lambda b, g: (b, g)),
        out_shape=jax.ShapeDtypeStruct((tok, INNER), jnp.float32),
    )(conv, conv, conv, dt_g, cum_g, cumt_g, segc, segr, dsk)


def mix_kernel(
    c_ref, y_ref, z_ref, back_ref, local_ref, cdec_ref, cum_ref, segc_ref, eb_ref, gain_ref,
    out_ref, hin_ref, acc_ref,
):
    pieces, _, width = back_ref.shape
    for k in range(pieces):
        hin_ref[:, k * width : (k + 1) * width] = back_ref[k].astype(jnp.float32)
    state = cdec_ref[0] * hin_ref[...] + local_ref[0]
    segc = segc_ref[:, 0:1]
    entry = eb_ref[0:1, 0:1]
    in_weight = jnp.where(segc == entry, jnp.exp(cum_ref[0]), 0.0)
    inter = jnp.dot(c_ref[...], state.astype(jnp.bfloat16), preferred_element_type=jnp.float32)
    for j in range(PER_GROUP):
        hc = slice(j * HEAD_DIM, (j + 1) * HEAD_DIM)
        acc_ref[:, hc] = inter[:, hc] * in_weight[:, j : j + 1]
    y = y_ref[...] + acc_ref[...]
    zf = z_ref[...].astype(jnp.float32)
    gated = y * (zf * jax.nn.sigmoid(zf))
    mean_square = jnp.mean(gated * gated, axis=1, keepdims=True) + 1e-05
    out_ref[...] = (gated * lax.rsqrt(mean_square) * gain_ref[...]).astype(jnp.bfloat16)


def mix(conv, y_local, z_gate, back, local_states, cdec, cum_g, segc, eb, gain):
    tok = conv.shape[0]
    nb = tok // STRETCH
    c_col = INNER // STATE + GROUPS
    peers, _, width = back.shape
    per = peers // GROUPS
    return pl.pallas_call(
        mix_kernel,
        grid=(nb, GROUPS),
        in_specs=[
            pl.BlockSpec((STRETCH, STATE), lambda b, g: (b, c_col + g)),
            pl.BlockSpec((STRETCH, GROUP_COLS), lambda b, g: (b, g)),
            pl.BlockSpec((STRETCH, GROUP_COLS), lambda b, g: (b, g)),
            pl.BlockSpec((per, STATE, width), lambda b, g: (g, 0, 0)),
            pl.BlockSpec((1, STATE, GROUP_COLS), lambda b, g: (b, 0, g)),
            pl.BlockSpec((1, 1, GROUP_COLS), lambda b, g: (b, 0, g)),
            pl.BlockSpec((1, STRETCH, PER_GROUP), lambda b, g: (g, b, 0)),
            pl.BlockSpec((STRETCH, 128), lambda b, g: (b, 0)),
            pl.BlockSpec((8, 128), lambda b, g: (b, 0)),
            pl.BlockSpec((1, GROUP_COLS), lambda b, g: (0, g)),
        ],
        out_specs=pl.BlockSpec((STRETCH, GROUP_COLS), lambda b, g: (b, g)),
        out_shape=jax.ShapeDtypeStruct((tok, INNER), jnp.bfloat16),
        scratch_shapes=[
            pltpu.VMEM((STATE, GROUP_COLS), jnp.float32),
            pltpu.VMEM((STRETCH, GROUP_COLS), jnp.float32),
        ],
    )(conv, y_local, z_gate, back, local_states, cdec, cum_g, segc, eb, gain)


def scan_kernel(got_ref, out_ref):
    peers = got_ref.shape[0]

    def body(d, carry):
        out_ref[d] = carry.astype(jnp.bfloat16)
        decay = got_ref[d, STATE : STATE + 1, :].astype(jnp.float32) + got_ref[
            d, STATE + 1 : STATE + 2, :
        ].astype(jnp.float32)
        return decay * carry + got_ref[d, 0:STATE, :].astype(jnp.float32)

    lax.fori_loop(0, peers, body, jnp.zeros(out_ref.shape[1:], jnp.float32))


def compose(payload):
    peers, _, width = payload.shape
    got = lax.all_to_all(payload, "ctx", split_axis=0, concat_axis=0, tiled=True)
    entering = pl.pallas_call(
        scan_kernel,
        out_shape=jax.ShapeDtypeStruct((peers, STATE, width), jnp.bfloat16),
    )(got)
    return lax.all_to_all(entering, "ctx", split_axis=0, concat_axis=0, tiled=True)


def local(xbc, z_gate, dt_raw, lengths, conv_weight, conv_bias, dt_bias, a_log, d_skip, norm_gain):
    tok = xbc.shape[0]
    nb = tok // STRETCH
    peers = lax.axis_size("ctx")
    first_pos = lax.axis_index("ctx") * tok
    rim_rows = shifted(xbc[tok - (CONV - 1) :], "ctx", 1)
    rim8 = jnp.concatenate([jnp.zeros((8 - (CONV - 1), CHANNELS), xbc.dtype), rim_rows], axis=0)
    ext_pos = first_pos - (CONV - 1) + jnp.arange(tok + CONV - 1)
    ext_seg = segment_of(ext_pos, lengths)
    target = ext_seg[CONV - 1 :]
    kept = [
        (ext_pos[tap : tap + tok] >= 0) & (ext_seg[tap : tap + tok] == target) for tap in range(CONV)
    ]
    masks = jnp.stack(kept, axis=1).astype(jnp.float32)
    masks = jnp.concatenate([masks, jnp.zeros((tok, 128 - CONV), jnp.float32)], axis=1)
    w8 = jnp.concatenate([conv_weight, jnp.zeros((8 - CONV, CHANNELS), jnp.float32)], axis=0)
    conv = conv_part(xbc, rim8, w8, conv_bias[None, :], masks)
    step = jax.nn.softplus(dt_raw.astype(jnp.float32) + dt_bias[None, :])
    log_decay = -step * jnp.exp(a_log)[None, :]
    cum = jnp.cumsum(log_decay.reshape(nb, STRETCH, HEADS), axis=1).reshape(tok, HEADS)
    segments = segment_of(first_pos + jnp.arange(tok), lengths)
    seg_before = segment_of(first_pos + jnp.arange(nb) * STRETCH - 1, lengths)
    seg_last = segments.reshape(nb, STRETCH)[:, -1]
    cum_last = cum.reshape(nb, STRETCH, HEADS)[:, -1, :]
    block_decay = jnp.where((seg_last == seg_before)[:, None], jnp.exp(cum_last), 0.0)

    cum_g = cum.reshape(tok, GROUPS, PER_GROUP).transpose(1, 0, 2)
    dt_g = step.reshape(tok, GROUPS, PER_GROUP).transpose(1, 0, 2)
    cumt_g = cum.T.reshape(GROUPS, PER_GROUP, tok)
    segc = jnp.broadcast_to(segments[:, None], (tok, 128)).astype(jnp.int32)
    segr = jnp.broadcast_to(segments[None, :], (8, tok)).astype(jnp.int32)
    eb = jnp.broadcast_to(seg_before[:, None, None], (nb, 8, 128)).reshape(nb * 8, 128)
    eb = eb.astype(jnp.int32)
    bt = conv[:, INNER : INNER + GROUPS * STATE].T
    bdec = jnp.repeat(block_decay, HEAD_DIM, axis=1)[:, None, :]

    local_states, cdec, payload = block_states(bt, conv, dt_g, cum_g, segc, bdec, peers)
    dsk = jnp.repeat(d_skip, HEAD_DIM)[None, :]
    y_local = intra_part(conv, dt_g, cum_g, cumt_g, segc, segr, dsk)
    back = compose(payload)
    gain = norm_gain[None, :]
    return mix(conv, y_local, z_gate, back, local_states, cdec, cum_g, segc, eb, gain)


def solution(mesh):
    return jax.shard_map(
        local,
        mesh=mesh,
        in_specs=(
            P(("group", "ctx"), None),
            P(("group", "ctx"), None),
            P(("group", "ctx"), None),
            P("group"),
            P(),
            P(),
            P(),
            P(),
            P(),
            P(),
        ),
        out_specs=P(("group", "ctx"), None),
        check_vma=False,
    )
```

```python
import jax
import jax.numpy as jnp
from jax import lax
from jax.experimental import pallas as pl
from jax.experimental.pallas import tpu as pltpu
from jax.sharding import PartitionSpec as P

HEADS = 64
HEAD_DIM = 64
STATE = 256
GROUPS = 2
CONV = 4
STRETCH = 256
CHANNELS = 5120
INNER = HEADS * HEAD_DIM
PER_GROUP = HEADS // GROUPS
GROUP_COLS = INNER // GROUPS


def shifted(value, axis, by):
    peers = lax.axis_size(axis)
    pairs = [(i, i + by) for i in range(peers) if 0 <= i + by < peers]
    return lax.ppermute(value, axis, pairs)


def segment_of(positions, lengths):
    prompt_ends = jnp.cumsum(lengths)
    hits = (prompt_ends[None, :] <= positions[:, None]).astype(jnp.int32)
    return jnp.sum(hits, axis=1)


def expand_heads(v):
    heads = lax.broadcasted_iota(jnp.int32, (PER_GROUP, GROUP_COLS), 0)
    cols = lax.broadcasted_iota(jnp.int32, (PER_GROUP, GROUP_COLS), 1)
    spread = (cols // HEAD_DIM == heads).astype(jnp.bfloat16)
    hi = v.astype(jnp.bfloat16)
    rest = v - hi.astype(jnp.float32)
    mid = rest.astype(jnp.bfloat16)
    lo = (rest - mid.astype(jnp.float32)).astype(jnp.bfloat16)
    out = jnp.dot(hi, spread, preferred_element_type=jnp.float32)
    out = out + jnp.dot(mid, spread, preferred_element_type=jnp.float32)
    return out + jnp.dot(lo, spread, preferred_element_type=jnp.float32)


CONV_COLS = 640


def conv_kernel(x_ref, rim_ref, w_ref, bias_ref, m_ref, out_ref):
    x = x_ref[...].astype(jnp.float32)
    rim = rim_ref[...].astype(jnp.float32)
    rows8 = lax.broadcasted_iota(jnp.int32, rim.shape, 0)
    summed = jnp.zeros(x.shape, jnp.float32)
    top = jnp.zeros(rim.shape, jnp.float32)
    for tap in range(CONV):
        by = CONV - 1 - tap
        wk = w_ref[tap : tap + 1, :]
        kept = m_ref[:, tap : tap + 1] > 0.0
        if by == 0:
            term = x
            top_term = x[0:8]
        else:
            term = pltpu.roll(x, by, 0)
            top_term = jnp.where(rows8 < by, pltpu.roll(rim, by, 0), term[0:8])
        summed = summed + jnp.where(kept, term * wk, 0.0)
        top = top + jnp.where(kept[0:8], top_term * wk, 0.0)
    out_ref[...] = jax.nn.silu(summed + bias_ref[...]).astype(jnp.bfloat16)
    out_ref[0:8, :] = jax.nn.silu(top + bias_ref[...]).astype(jnp.bfloat16)


def conv_part(xbc, rim8, w8, bias, masks):
    tok, chans = xbc.shape
    return pl.pallas_call(
        conv_kernel,
        grid=(chans // CONV_COLS,),
        in_specs=[
            pl.BlockSpec((tok, CONV_COLS), lambda c: (0, c)),
            pl.BlockSpec((8, CONV_COLS), lambda c: (0, c)),
            pl.BlockSpec((8, CONV_COLS), lambda c: (0, c)),
            pl.BlockSpec((1, CONV_COLS), lambda c: (0, c)),
            pl.BlockSpec((tok, 128), lambda c: (0, 0)),
        ],
        out_specs=pl.BlockSpec((tok, CONV_COLS), lambda c: (0, c)),
        out_shape=jax.ShapeDtypeStruct((tok, chans), jnp.bfloat16),
    )(xbc, rim8, w8, bias, masks)


def state_kernel(
    bt_ref, x_ref, dt_ref, cum_ref, segc_ref, bdec_ref, local_ref, cdec_ref, pay_ref,
    acc_ref, dec_ref,
):
    b = pl.program_id(1)

    @pl.when(b == 0)
    def _():
        acc_ref[...] = jnp.zeros(acc_ref.shape, jnp.float32)
        dec_ref[...] = jnp.ones(dec_ref.shape, jnp.float32)

    local_ref[0] = acc_ref[...]
    cdec_ref[0] = dec_ref[...]
    cum = cum_ref[0]
    step = dt_ref[0]
    segc = segc_ref[:, 0:1]
    last = cum[STRETCH - 1 : STRETCH, :]
    seg_last = segc[STRETCH - 1 : STRETCH, :]
    w = jnp.where(segc == seg_last, jnp.exp(last - cum), 0.0)
    scaled = (x_ref[...].astype(jnp.float32) * expand_heads(step)).astype(jnp.bfloat16)
    weighted = (scaled.astype(jnp.float32) * expand_heads(w)).astype(jnp.bfloat16)
    block_state = jnp.dot(bt_ref[...], weighted, preferred_element_type=jnp.float32)
    decay = bdec_ref[0]
    acc_ref[...] = decay * acc_ref[...] + block_state
    dec_ref[...] = dec_ref[...] * decay

    @pl.when(b == pl.num_programs(1) - 1)
    def _():
        pieces, _, width = pay_ref.shape
        total = acc_ref[...]
        dec = dec_ref[...]
        hi = dec.astype(jnp.bfloat16)
        lo = (dec - hi.astype(jnp.float32)).astype(jnp.bfloat16)
        for k in range(pieces):
            cols = slice(k * width, (k + 1) * width)
            pay_ref[k, 0:STATE, :] = total[:, cols].astype(jnp.bfloat16)
            pay_ref[k, STATE : STATE + 1, :] = hi[:, cols]
            pay_ref[k, STATE + 1 : STATE + 2, :] = lo[:, cols]


def block_states(bt, conv, dt_g, cum_g, segc, bdec, peers):
    tok = conv.shape[0]
    nb = tok // STRETCH
    width = INNER // peers
    per = peers // GROUPS
    return pl.pallas_call(
        state_kernel,
        grid=(GROUPS, nb),
        in_specs=[
            pl.BlockSpec((STATE, STRETCH), lambda g, b: (g, b)),
            pl.BlockSpec((STRETCH, GROUP_COLS), lambda g, b: (b, g)),
            pl.BlockSpec((1, STRETCH, PER_GROUP), lambda g, b: (g, b, 0)),
            pl.BlockSpec((1, STRETCH, PER_GROUP), lambda g, b: (g, b, 0)),
            pl.BlockSpec((STRETCH, 128), lambda g, b: (b, 0)),
            pl.BlockSpec((1, 1, GROUP_COLS), lambda g, b: (b, 0, g)),
        ],
        out_specs=[
            pl.BlockSpec((1, STATE, GROUP_COLS), lambda g, b: (b, 0, g)),
            pl.BlockSpec((1, 1, GROUP_COLS), lambda g, b: (b, 0, g)),
            pl.BlockSpec((per, STATE + 2, width), lambda g, b: (g, 0, 0)),
        ],
        out_shape=[
            jax.ShapeDtypeStruct((nb, STATE, INNER), jnp.float32),
            jax.ShapeDtypeStruct((nb, 1, INNER), jnp.float32),
            jax.ShapeDtypeStruct((peers, STATE + 2, width), jnp.bfloat16),
        ],
        scratch_shapes=[
            pltpu.VMEM((STATE, GROUP_COLS), jnp.float32),
            pltpu.VMEM((1, GROUP_COLS), jnp.float32),
        ],
    )(bt, conv, dt_g, cum_g, segc, bdec)


def intra_kernel(
    c_ref, b_ref, x_ref, dt_ref, cum_ref, cumt_ref, segc_ref, segr_ref, dsk_ref, out_ref
):
    gram = lax.dot_general(
        c_ref[...], b_ref[...], (((1,), (1,)), ((), ())), preferred_element_type=jnp.float32
    )
    segc = segc_ref[:, 0:1]
    segr = segr_ref[0:1, :]
    rows = lax.broadcasted_iota(jnp.int32, (STRETCH, STRETCH), 0)
    cols = lax.broadcasted_iota(jnp.int32, (STRETCH, STRETCH), 1)
    gram = jnp.where((segc == segr) & (cols <= rows), gram, 0.0)
    cum = cum_ref[0]
    cumt = cumt_ref[0]
    step = dt_ref[0]
    for j in range(PER_GROUP):
        hc = slice(j * HEAD_DIM, (j + 1) * HEAD_DIM)
        gap = jnp.minimum(cum[:, j : j + 1] - cumt[j : j + 1, :], 0.0)
        weights = (gram * jnp.exp(gap)).astype(jnp.bfloat16)
        xf = x_ref[:, hc].astype(jnp.float32)
        scaled = (xf * step[:, j : j + 1]).astype(jnp.bfloat16)
        intra = jnp.dot(weights, scaled, preferred_element_type=jnp.float32)
        out_ref[:, hc] = intra + dsk_ref[:, hc] * xf


def intra_part(conv, dt_g, cum_g, cumt_g, segc, segr, dsk, g):
    tok = conv.shape[0]
    nb = tok // STRETCH
    b_col = INNER // STATE
    c_col = b_col + GROUPS
    return pl.pallas_call(
        intra_kernel,
        grid=(nb,),
        in_specs=[
            pl.BlockSpec((STRETCH, STATE), lambda b: (b, c_col + g)),
            pl.BlockSpec((STRETCH, STATE), lambda b: (b, b_col + g)),
            pl.BlockSpec((STRETCH, GROUP_COLS), lambda b: (b, g)),
            pl.BlockSpec((1, STRETCH, PER_GROUP), lambda b: (g, b, 0)),
            pl.BlockSpec((1, STRETCH, PER_GROUP), lambda b: (g, b, 0)),
            pl.BlockSpec((1, PER_GROUP, STRETCH), lambda b: (g, 0, b)),
            pl.BlockSpec((STRETCH, 128), lambda b: (b, 0)),
            pl.BlockSpec((8, STRETCH), lambda b: (0, b)),
            pl.BlockSpec((1, GROUP_COLS), lambda b: (0, g)),
        ],
        out_specs=pl.BlockSpec((STRETCH, GROUP_COLS), lambda b: (b, 0)),
        out_shape=jax.ShapeDtypeStruct((tok, GROUP_COLS), jnp.float32),
    )(conv, conv, conv, dt_g, cum_g, cumt_g, segc, segr, dsk)


def mix_kernel(
    c_ref, y_ref, z_ref, back_ref, local_ref, cdec_ref, cum_ref, segc_ref, eb_ref, gain_ref,
    out_ref, hin_ref,
):
    pieces, _, width = back_ref.shape
    for k in range(pieces):
        hin_ref[:, k * width : (k + 1) * width] = back_ref[k].astype(jnp.float32)
    state = cdec_ref[0] * hin_ref[...] + local_ref[0]
    segc = segc_ref[:, 0:1]
    entry = eb_ref[0:1, 0:1]
    in_weight = jnp.where(segc == entry, jnp.exp(cum_ref[0]), 0.0)
    inter = jnp.dot(c_ref[...], state.astype(jnp.bfloat16), preferred_element_type=jnp.float32)
    y = y_ref[...] + inter * expand_heads(in_weight)
    zf = z_ref[...].astype(jnp.float32)
    gated = y * (zf * jax.nn.sigmoid(zf))
    mean_square = jnp.mean(gated * gated, axis=1, keepdims=True) + 1e-05
    out_ref[...] = (gated * lax.rsqrt(mean_square) * gain_ref[...]).astype(jnp.bfloat16)


def mix(conv, y_local, z_gate, back, local_states, cdec, cum_g, segc, eb, gain):
    tok = conv.shape[0]
    nb = tok // STRETCH
    c_col = INNER // STATE + GROUPS
    peers, _, width = back.shape
    per = peers // GROUPS
    return pl.pallas_call(
        mix_kernel,
        grid=(nb, GROUPS),
        in_specs=[
            pl.BlockSpec((STRETCH, STATE), lambda b, g: (b, c_col + g)),
            pl.BlockSpec((STRETCH, GROUP_COLS), lambda b, g: (b, g)),
            pl.BlockSpec((STRETCH, GROUP_COLS), lambda b, g: (b, g)),
            pl.BlockSpec((per, STATE, width), lambda b, g: (g, 0, 0)),
            pl.BlockSpec((1, STATE, GROUP_COLS), lambda b, g: (b, 0, g)),
            pl.BlockSpec((1, 1, GROUP_COLS), lambda b, g: (b, 0, g)),
            pl.BlockSpec((1, STRETCH, PER_GROUP), lambda b, g: (g, b, 0)),
            pl.BlockSpec((STRETCH, 128), lambda b, g: (b, 0)),
            pl.BlockSpec((8, 128), lambda b, g: (b, 0)),
            pl.BlockSpec((1, GROUP_COLS), lambda b, g: (0, g)),
        ],
        out_specs=pl.BlockSpec((STRETCH, GROUP_COLS), lambda b, g: (b, g)),
        out_shape=jax.ShapeDtypeStruct((tok, INNER), jnp.bfloat16),
        scratch_shapes=[pltpu.VMEM((STATE, GROUP_COLS), jnp.float32)],
    )(conv, y_local, z_gate, back, local_states, cdec, cum_g, segc, eb, gain)


def scan_kernel(got_ref, out_ref):
    peers = got_ref.shape[0]

    def body(d, carry):
        out_ref[d] = carry.astype(jnp.bfloat16)
        decay = got_ref[d, STATE : STATE + 1, :].astype(jnp.float32) + got_ref[
            d, STATE + 1 : STATE + 2, :
        ].astype(jnp.float32)
        return decay * carry + got_ref[d, 0:STATE, :].astype(jnp.float32)

    lax.fori_loop(0, peers, body, jnp.zeros(out_ref.shape[1:], jnp.float32))


def compose(payload):
    peers, _, width = payload.shape
    got = lax.all_to_all(payload, "ctx", split_axis=0, concat_axis=0, tiled=True)
    entering = pl.pallas_call(
        scan_kernel,
        out_shape=jax.ShapeDtypeStruct((peers, STATE, width), jnp.bfloat16),
    )(got)
    return lax.all_to_all(entering, "ctx", split_axis=0, concat_axis=0, tiled=True)


def local(xbc, z_gate, dt_raw, lengths, conv_weight, conv_bias, dt_bias, a_log, d_skip, norm_gain):
    tok = xbc.shape[0]
    nb = tok // STRETCH
    peers = lax.axis_size("ctx")
    first_pos = lax.axis_index("ctx") * tok
    rim_rows = shifted(xbc[tok - (CONV - 1) :], "ctx", 1)
    rim8 = jnp.concatenate([jnp.zeros((8 - (CONV - 1), CHANNELS), xbc.dtype), rim_rows], axis=0)
    ext_pos = first_pos - (CONV - 1) + jnp.arange(tok + CONV - 1)
    ext_seg = segment_of(ext_pos, lengths)
    target = ext_seg[CONV - 1 :]
    kept = [
        (ext_pos[tap : tap + tok] >= 0) & (ext_seg[tap : tap + tok] == target) for tap in range(CONV)
    ]
    masks = jnp.stack(kept, axis=1).astype(jnp.float32)
    masks = jnp.concatenate([masks, jnp.zeros((tok, 128 - CONV), jnp.float32)], axis=1)
    w8 = jnp.concatenate([conv_weight, jnp.zeros((8 - CONV, CHANNELS), jnp.float32)], axis=0)
    conv = conv_part(xbc, rim8, w8, conv_bias[None, :], masks)
    step = jax.nn.softplus(dt_raw.astype(jnp.float32) + dt_bias[None, :])
    log_decay = -step * jnp.exp(a_log)[None, :]
    cum = jnp.cumsum(log_decay.reshape(nb, STRETCH, HEADS), axis=1).reshape(tok, HEADS)
    segments = segment_of(first_pos + jnp.arange(tok), lengths)
    seg_before = segment_of(first_pos + jnp.arange(nb) * STRETCH - 1, lengths)
    seg_last = segments.reshape(nb, STRETCH)[:, -1]
    cum_last = cum.reshape(nb, STRETCH, HEADS)[:, -1, :]
    block_decay = jnp.where((seg_last == seg_before)[:, None], jnp.exp(cum_last), 0.0)

    cum_g = cum.reshape(tok, GROUPS, PER_GROUP).transpose(1, 0, 2)
    dt_g = step.reshape(tok, GROUPS, PER_GROUP).transpose(1, 0, 2)
    cumt_g = cum.T.reshape(GROUPS, PER_GROUP, tok)
    segc = jnp.broadcast_to(segments[:, None], (tok, 128)).astype(jnp.int32)
    segr = jnp.broadcast_to(segments[None, :], (8, tok)).astype(jnp.int32)
    eb = jnp.broadcast_to(seg_before[:, None, None], (nb, 8, 128)).reshape(nb * 8, 128)
    eb = eb.astype(jnp.int32)
    bt = conv[:, INNER : INNER + GROUPS * STATE].T
    bdec = jnp.repeat(block_decay, HEAD_DIM, axis=1)[:, None, :]

    local_states, cdec, payload = block_states(bt, conv, dt_g, cum_g, segc, bdec, peers)
    dsk = jnp.repeat(d_skip, HEAD_DIM)[None, :]
    y_local = jnp.concatenate(
        [intra_part(conv, dt_g, cum_g, cumt_g, segc, segr, dsk, g) for g in range(GROUPS)], axis=1
    )
    back = compose(payload)
    gain = norm_gain[None, :]
    return mix(conv, y_local, z_gate, back, local_states, cdec, cum_g, segc, eb, gain)


def solution(mesh):
    return jax.shard_map(
        local,
        mesh=mesh,
        in_specs=(
            P(("group", "ctx"), None),
            P(("group", "ctx"), None),
            P(("group", "ctx"), None),
            P("group"),
            P(),
            P(),
            P(),
            P(),
            P(),
            P(),
        ),
        out_specs=P(("group", "ctx"), None),
        check_vma=False,
    )
```

```python
import jax
import jax.numpy as jnp
from jax import lax
from jax.experimental import pallas as pl
from jax.experimental.pallas import tpu as pltpu
from jax.sharding import Mesh, PartitionSpec as P

HEADS = 64
HEAD_DIM = 64
STATE = 256
GROUPS = 2
CONV = 4
STRETCH = 256
CHANNELS = 5120
INNER = HEADS * HEAD_DIM
PER_GROUP = HEADS // GROUPS
GROUP_COLS = INNER // GROUPS


def shifted(value, axis, by):
    peers = lax.axis_size(axis)
    pairs = [(i, i + by) for i in range(peers) if 0 <= i + by < peers]
    return lax.ppermute(value, axis, pairs)


def segment_of(positions, lengths):
    prompt_ends = jnp.cumsum(lengths)
    hits = (prompt_ends[None, :] <= positions[:, None]).astype(jnp.int32)
    return jnp.sum(hits, axis=1)


def expand_heads(v):
    heads = lax.broadcasted_iota(jnp.int32, (PER_GROUP, GROUP_COLS), 0)
    cols = lax.broadcasted_iota(jnp.int32, (PER_GROUP, GROUP_COLS), 1)
    spread = (cols // HEAD_DIM == heads).astype(jnp.bfloat16)
    hi = v.astype(jnp.bfloat16)
    rest = v - hi.astype(jnp.float32)
    mid = rest.astype(jnp.bfloat16)
    lo = (rest - mid.astype(jnp.float32)).astype(jnp.bfloat16)
    out = jnp.dot(hi, spread, preferred_element_type=jnp.float32)
    out = out + jnp.dot(mid, spread, preferred_element_type=jnp.float32)
    return out + jnp.dot(lo, spread, preferred_element_type=jnp.float32)


CONV_COLS = 640


def conv_kernel(x_ref, rim_ref, w_ref, bias_ref, m_ref, out_ref):
    x = x_ref[...].astype(jnp.float32)
    rim = rim_ref[...].astype(jnp.float32)
    rows8 = lax.broadcasted_iota(jnp.int32, rim.shape, 0)
    summed = jnp.zeros(x.shape, jnp.float32)
    top = jnp.zeros(rim.shape, jnp.float32)
    for tap in range(CONV):
        by = CONV - 1 - tap
        wk = w_ref[tap : tap + 1, :]
        kept = m_ref[:, tap : tap + 1] > 0.0
        if by == 0:
            term = x
            top_term = x[0:8]
        else:
            term = pltpu.roll(x, by, 0)
            top_term = jnp.where(rows8 < by, pltpu.roll(rim, by, 0), term[0:8])
        summed = summed + jnp.where(kept, term * wk, 0.0)
        top = top + jnp.where(kept[0:8], top_term * wk, 0.0)
    out_ref[...] = jax.nn.silu(summed + bias_ref[...]).astype(jnp.bfloat16)
    out_ref[0:8, :] = jax.nn.silu(top + bias_ref[...]).astype(jnp.bfloat16)


def conv_part(xbc, rim8, w8, bias, masks):
    tok, chans = xbc.shape
    return pl.pallas_call(
        conv_kernel,
        grid=(chans // CONV_COLS,),
        in_specs=[
            pl.BlockSpec((tok, CONV_COLS), lambda c: (0, c)),
            pl.BlockSpec((8, CONV_COLS), lambda c: (0, c)),
            pl.BlockSpec((8, CONV_COLS), lambda c: (0, c)),
            pl.BlockSpec((1, CONV_COLS), lambda c: (0, c)),
            pl.BlockSpec((tok, 128), lambda c: (0, 0)),
        ],
        out_specs=pl.BlockSpec((tok, CONV_COLS), lambda c: (0, c)),
        out_shape=jax.ShapeDtypeStruct((tok, chans), jnp.bfloat16),
    )(xbc, rim8, w8, bias, masks)


def state_kernel(
    bt_ref, x_ref, dt_ref, cum_ref, segc_ref, bdec_ref, local_ref, cdec_ref, tot_ref, tdec_ref,
    acc_ref, dec_ref,
):
    b = pl.program_id(1)

    @pl.when(b == 0)
    def _():
        acc_ref[...] = jnp.zeros(acc_ref.shape, jnp.float32)
        dec_ref[...] = jnp.ones(dec_ref.shape, jnp.float32)

    local_ref[0] = acc_ref[...]
    cdec_ref[0] = dec_ref[...]
    cum = cum_ref[0]
    step = dt_ref[0]
    segc = segc_ref[:, 0:1]
    last = cum[STRETCH - 1 : STRETCH, :]
    seg_last = segc[STRETCH - 1 : STRETCH, :]
    w = jnp.where(segc == seg_last, jnp.exp(last - cum), 0.0)
    scaled = (x_ref[...].astype(jnp.float32) * expand_heads(step)).astype(jnp.bfloat16)
    weighted = (scaled.astype(jnp.float32) * expand_heads(w)).astype(jnp.bfloat16)
    block_state = jnp.dot(bt_ref[...], weighted, preferred_element_type=jnp.float32)
    decay = bdec_ref[0]
    acc_ref[...] = decay * acc_ref[...] + block_state
    dec_ref[...] = dec_ref[...] * decay

    @pl.when(b == pl.num_programs(1) - 1)
    def _():
        tot_ref[...] = acc_ref[...]
        tdec_ref[...] = dec_ref[...]


def block_states(bt, conv, dt_g, cum_g, segc, bdec):
    tok = conv.shape[0]
    nb = tok // STRETCH
    return pl.pallas_call(
        state_kernel,
        grid=(GROUPS, nb),
        in_specs=[
            pl.BlockSpec((STATE, STRETCH), lambda g, b: (g, b)),
            pl.BlockSpec((STRETCH, GROUP_COLS), lambda g, b: (b, g)),
            pl.BlockSpec((1, STRETCH, PER_GROUP), lambda g, b: (g, b, 0)),
            pl.BlockSpec((1, STRETCH, PER_GROUP), lambda g, b: (g, b, 0)),
            pl.BlockSpec((STRETCH, 128), lambda g, b: (b, 0)),
            pl.BlockSpec((1, 1, GROUP_COLS), lambda g, b: (b, 0, g)),
        ],
        out_specs=[
            pl.BlockSpec((1, STATE, GROUP_COLS), lambda g, b: (b, 0, g)),
            pl.BlockSpec((1, 1, GROUP_COLS), lambda g, b: (b, 0, g)),
            pl.BlockSpec((STATE, GROUP_COLS), lambda g, b: (0, g)),
            pl.BlockSpec((1, GROUP_COLS), lambda g, b: (0, g)),
        ],
        out_shape=[
            jax.ShapeDtypeStruct((nb, STATE, INNER), jnp.float32),
            jax.ShapeDtypeStruct((nb, 1, INNER), jnp.float32),
            jax.ShapeDtypeStruct((STATE, INNER), jnp.float32),
            jax.ShapeDtypeStruct((1, INNER), jnp.float32),
        ],
        scratch_shapes=[
            pltpu.VMEM((STATE, GROUP_COLS), jnp.float32),
            pltpu.VMEM((1, GROUP_COLS), jnp.float32),
        ],
    )(bt, conv, dt_g, cum_g, segc, bdec)


def intra_kernel(
    c_ref, b_ref, x_ref, dt_ref, cum_ref, cumt_ref, segc_ref, segr_ref, dsk_ref, out_ref
):
    gram = lax.dot_general(
        c_ref[...], b_ref[...], (((1,), (1,)), ((), ())), preferred_element_type=jnp.float32
    )
    segc = segc_ref[:, 0:1]
    segr = segr_ref[0:1, :]
    rows = lax.broadcasted_iota(jnp.int32, (STRETCH, STRETCH), 0)
    cols = lax.broadcasted_iota(jnp.int32, (STRETCH, STRETCH), 1)
    gram = jnp.where((segc == segr) & (cols <= rows), gram, 0.0)
    cum = cum_ref[0]
    cumt = cumt_ref[0]
    step = dt_ref[0]
    for j in range(PER_GROUP):
        hc = slice(j * HEAD_DIM, (j + 1) * HEAD_DIM)
        gap = jnp.minimum(cum[:, j : j + 1] - cumt[j : j + 1, :], 0.0)
        weights = (gram * jnp.exp(gap)).astype(jnp.bfloat16)
        xf = x_ref[:, hc].astype(jnp.float32)
        scaled = (xf * step[:, j : j + 1]).astype(jnp.bfloat16)
        intra = jnp.dot(weights, scaled, preferred_element_type=jnp.float32)
        out_ref[:, hc] = intra + dsk_ref[:, hc] * xf


def intra_part(conv, dt_g, cum_g, cumt_g, segc, segr, dsk, g, into=None):
    tok = conv.shape[0]
    nb = tok // STRETCH
    b_col = INNER // STATE
    c_col = b_col + GROUPS
    operands = [conv, conv, conv, dt_g, cum_g, cumt_g, segc, segr, dsk]
    specs = [
        pl.BlockSpec((STRETCH, STATE), lambda b: (b, c_col + g)),
        pl.BlockSpec((STRETCH, STATE), lambda b: (b, b_col + g)),
        pl.BlockSpec((STRETCH, GROUP_COLS), lambda b: (b, g)),
        pl.BlockSpec((1, STRETCH, PER_GROUP), lambda b: (g, b, 0)),
        pl.BlockSpec((1, STRETCH, PER_GROUP), lambda b: (g, b, 0)),
        pl.BlockSpec((1, PER_GROUP, STRETCH), lambda b: (g, 0, b)),
        pl.BlockSpec((STRETCH, 128), lambda b: (b, 0)),
        pl.BlockSpec((8, STRETCH), lambda b: (0, b)),
        pl.BlockSpec((1, GROUP_COLS), lambda b: (0, g)),
    ]
    kernel = intra_kernel
    aliases = {}
    if into is not None:
        operands.append(into)
        specs.append(pl.BlockSpec(memory_space=pl.ANY))
        aliases = {len(operands) - 1: 0}

        def kernel(*refs):
            intra_kernel(*refs[:-2], refs[-1])

    return pl.pallas_call(
        kernel,
        grid=(nb,),
        in_specs=specs,
        out_specs=pl.BlockSpec((STRETCH, GROUP_COLS), lambda b: (b, g)),
        out_shape=jax.ShapeDtypeStruct((tok, INNER), jnp.float32),
        input_output_aliases=aliases,
    )(*operands)


def mix_kernel(
    c_ref, y_ref, z_ref, hin_ref, local_ref, cdec_ref, cum_ref, segc_ref, eb_ref, gain_ref,
    out_ref,
):
    state = cdec_ref[0] * hin_ref[...].astype(jnp.float32) + local_ref[0]
    segc = segc_ref[:, 0:1]
    entry = eb_ref[0:1, 0:1]
    in_weight = jnp.where(segc == entry, jnp.exp(cum_ref[0]), 0.0)
    inter = jnp.dot(c_ref[...], state.astype(jnp.bfloat16), preferred_element_type=jnp.float32)
    y = y_ref[...] + inter * expand_heads(in_weight)
    zf = z_ref[...].astype(jnp.float32)
    gated = y * (zf * jax.nn.sigmoid(zf))
    mean_square = jnp.mean(gated * gated, axis=1, keepdims=True) + 1e-05
    out_ref[...] = (gated * lax.rsqrt(mean_square) * gain_ref[...]).astype(jnp.bfloat16)


def mix(conv, y_local, z_gate, back, local_states, cdec, cum_g, segc, eb, gain):
    tok = conv.shape[0]
    nb = tok // STRETCH
    c_col = INNER // STATE + GROUPS
    return pl.pallas_call(
        mix_kernel,
        grid=(nb, GROUPS),
        in_specs=[
            pl.BlockSpec((STRETCH, STATE), lambda b, g: (b, c_col + g)),
            pl.BlockSpec((STRETCH, GROUP_COLS), lambda b, g: (b, g)),
            pl.BlockSpec((STRETCH, GROUP_COLS), lambda b, g: (b, g)),
            pl.BlockSpec((STATE, GROUP_COLS), lambda b, g: (0, g)),
            pl.BlockSpec((1, STATE, GROUP_COLS), lambda b, g: (b, 0, g)),
            pl.BlockSpec((1, 1, GROUP_COLS), lambda b, g: (b, 0, g)),
            pl.BlockSpec((1, STRETCH, PER_GROUP), lambda b, g: (g, b, 0)),
            pl.BlockSpec((STRETCH, 128), lambda b, g: (b, 0)),
            pl.BlockSpec((8, 128), lambda b, g: (b, 0)),
            pl.BlockSpec((1, GROUP_COLS), lambda b, g: (0, g)),
        ],
        out_specs=pl.BlockSpec((STRETCH, GROUP_COLS), lambda b, g: (b, g)),
        out_shape=jax.ShapeDtypeStruct((tok, INNER), jnp.bfloat16),
    )(conv, y_local, z_gate, back, local_states, cdec, cum_g, segc, eb, gain)


def scan_kernel(got_ref, out_ref):
    peers = got_ref.shape[0]

    def body(d, carry):
        out_ref[d] = carry.astype(jnp.bfloat16)
        decay = got_ref[d, STATE : STATE + 1, :].astype(jnp.float32) + got_ref[
            d, STATE + 1 : STATE + 2, :
        ].astype(jnp.float32)
        return decay * carry + got_ref[d, 0:STATE, :].astype(jnp.float32)

    lax.fori_loop(0, peers, body, jnp.zeros(out_ref.shape[1:], jnp.float32))


def swap_cores(value):
    return lax.ppermute(value, "core", [(0, 1), (1, 0)])


def compose(total, total_decay):
    core = lax.axis_index("core")
    chips = lax.axis_size("chip")
    half = INNER // 2
    width = half // chips
    both = jnp.concatenate([total, total_decay], axis=0)
    mine = lax.dynamic_slice_in_dim(both, core * half, half, axis=1)
    theirs = swap_cores(lax.dynamic_slice_in_dim(both, (1 - core) * half, half, axis=1))
    first = jnp.where(core == 0, mine, theirs)
    second = jnp.where(core == 0, theirs, mine)
    first_decay = first[STATE:]
    chip_state = second[STATE:] * first[:STATE] + second[:STATE]
    chip_decay = first_decay * second[STATE:]
    decay_hi = chip_decay.astype(jnp.bfloat16)
    decay_lo = (chip_decay - decay_hi.astype(jnp.float32)).astype(jnp.bfloat16)
    payload = jnp.concatenate(
        [chip_state.astype(jnp.bfloat16), decay_hi, decay_lo], axis=0
    ).reshape(STATE + 2, chips, width).transpose(1, 0, 2)
    got = lax.all_to_all(payload, "chip", split_axis=0, concat_axis=0, tiled=True)
    entering = pl.pallas_call(
        scan_kernel,
        out_shape=jax.ShapeDtypeStruct((chips, STATE, width), jnp.bfloat16),
    )(got)
    back = lax.all_to_all(entering, "chip", split_axis=0, concat_axis=0, tiled=True)
    chip_in = back.transpose(1, 0, 2).reshape(STATE, half).astype(jnp.float32)
    later_in = first_decay * chip_in + first[:STATE]
    keep = jnp.where(core == 0, chip_in, later_in).astype(jnp.bfloat16)
    other = swap_cores(jnp.where(core == 0, later_in, chip_in).astype(jnp.bfloat16))
    return jnp.where(
        core == 0,
        jnp.concatenate([keep, other], axis=1),
        jnp.concatenate([other, keep], axis=1),
    )


def local(xbc, z_gate, dt_raw, lengths, conv_weight, conv_bias, dt_bias, a_log, d_skip, norm_gain):
    tok = xbc.shape[0]
    nb = tok // STRETCH
    first_pos = (lax.axis_index("chip") * lax.axis_size("core") + lax.axis_index("core")) * tok
    rim_rows = shifted(xbc[tok - (CONV - 1) :], ("chip", "core"), 1)
    rim8 = jnp.concatenate([jnp.zeros((8 - (CONV - 1), CHANNELS), xbc.dtype), rim_rows], axis=0)
    ext_pos = first_pos - (CONV - 1) + jnp.arange(tok + CONV - 1)
    ext_seg = segment_of(ext_pos, lengths)
    target = ext_seg[CONV - 1 :]
    kept = [
        (ext_pos[tap : tap + tok] >= 0) & (ext_seg[tap : tap + tok] == target) for tap in range(CONV)
    ]
    masks = jnp.stack(kept, axis=1).astype(jnp.float32)
    masks = jnp.concatenate([masks, jnp.zeros((tok, 128 - CONV), jnp.float32)], axis=1)
    w8 = jnp.concatenate([conv_weight, jnp.zeros((8 - CONV, CHANNELS), jnp.float32)], axis=0)
    conv = conv_part(xbc, rim8, w8, conv_bias[None, :], masks)
    step = jax.nn.softplus(dt_raw.astype(jnp.float32) + dt_bias[None, :])
    log_decay = -step * jnp.exp(a_log)[None, :]
    cum = jnp.cumsum(log_decay.reshape(nb, STRETCH, HEADS), axis=1).reshape(tok, HEADS)
    segments = segment_of(first_pos + jnp.arange(tok), lengths)
    seg_before = segment_of(first_pos + jnp.arange(nb) * STRETCH - 1, lengths)
    seg_last = segments.reshape(nb, STRETCH)[:, -1]
    cum_last = cum.reshape(nb, STRETCH, HEADS)[:, -1, :]
    block_decay = jnp.where((seg_last == seg_before)[:, None], jnp.exp(cum_last), 0.0)

    cum_g = cum.reshape(tok, GROUPS, PER_GROUP).transpose(1, 0, 2)
    dt_g = step.reshape(tok, GROUPS, PER_GROUP).transpose(1, 0, 2)
    cumt_g = cum.T.reshape(GROUPS, PER_GROUP, tok)
    segc = jnp.broadcast_to(segments[:, None], (tok, 128)).astype(jnp.int32)
    segr = jnp.broadcast_to(segments[None, :], (8, tok)).astype(jnp.int32)
    eb = jnp.broadcast_to(seg_before[:, None, None], (nb, 8, 128)).reshape(nb * 8, 128)
    eb = eb.astype(jnp.int32)
    bt = conv[:, INNER : INNER + GROUPS * STATE].T
    bdec = jnp.repeat(block_decay, HEAD_DIM, axis=1)[:, None, :]

    local_states, cdec, total, total_decay = block_states(bt, conv, dt_g, cum_g, segc, bdec)
    dsk = jnp.repeat(d_skip, HEAD_DIM)[None, :]
    y_local = None
    for g in range(GROUPS):
        y_local = intra_part(conv, dt_g, cum_g, cumt_g, segc, segr, dsk, g, y_local)
    back = compose(total, total_decay)
    gain = norm_gain[None, :]
    return mix(conv, y_local, z_gate, back, local_states, cdec, cum_g, segc, eb, gain)


def solution(mesh):
    groups, peers = mesh.devices.shape
    split = Mesh(mesh.devices.reshape(groups, peers // 2, 2), ("group", "chip", "core"))
    rows = P(("group", "chip", "core"), None)
    return jax.shard_map(
        local,
        mesh=split,
        in_specs=(rows, rows, rows, P("group"), P(), P(), P(), P(), P(), P()),
        out_specs=rows,
        check_vma=False,
    )
```

```python
import jax
import jax.numpy as jnp
from jax import lax
from jax.experimental import pallas as pl
from jax.experimental.pallas import tpu as pltpu
from jax.sharding import PartitionSpec as P

HEADS = 64
HEAD_DIM = 64
STATE = 256
GROUPS = 2
CONV = 4
STRETCH = 256
CHANNELS = 5120
INNER = HEADS * HEAD_DIM
PER_GROUP = HEADS // GROUPS
GROUP_COLS = INNER // GROUPS


def shifted(value, axis, by):
    peers = lax.axis_size(axis)
    pairs = [(i, i + by) for i in range(peers) if 0 <= i + by < peers]
    return lax.ppermute(value, axis, pairs)


def segment_of(positions, lengths):
    prompt_ends = jnp.cumsum(lengths)
    hits = (prompt_ends[None, :] <= positions[:, None]).astype(jnp.int32)
    return jnp.sum(hits, axis=1)


def expand_heads(v):
    heads = lax.broadcasted_iota(jnp.int32, (PER_GROUP, GROUP_COLS), 0)
    cols = lax.broadcasted_iota(jnp.int32, (PER_GROUP, GROUP_COLS), 1)
    spread = (cols // HEAD_DIM == heads).astype(jnp.bfloat16)
    hi = v.astype(jnp.bfloat16)
    rest = v - hi.astype(jnp.float32)
    mid = rest.astype(jnp.bfloat16)
    lo = (rest - mid.astype(jnp.float32)).astype(jnp.bfloat16)
    out = jnp.dot(hi, spread, preferred_element_type=jnp.float32)
    out = out + jnp.dot(mid, spread, preferred_element_type=jnp.float32)
    return out + jnp.dot(lo, spread, preferred_element_type=jnp.float32)


CONV_COLS = 640


def conv_kernel(x_ref, rim_ref, w_ref, bias_ref, m_ref, out_ref):
    x = x_ref[...].astype(jnp.float32)
    rim = rim_ref[...].astype(jnp.float32)
    rows8 = lax.broadcasted_iota(jnp.int32, rim.shape, 0)
    summed = jnp.zeros(x.shape, jnp.float32)
    top = jnp.zeros(rim.shape, jnp.float32)
    for tap in range(CONV):
        by = CONV - 1 - tap
        wk = w_ref[tap : tap + 1, :]
        kept = m_ref[:, tap : tap + 1] > 0.0
        if by == 0:
            term = x
            top_term = x[0:8]
        else:
            term = pltpu.roll(x, by, 0)
            top_term = jnp.where(rows8 < by, pltpu.roll(rim, by, 0), term[0:8])
        summed = summed + jnp.where(kept, term * wk, 0.0)
        top = top + jnp.where(kept[0:8], top_term * wk, 0.0)
    out_ref[...] = jax.nn.silu(summed + bias_ref[...]).astype(jnp.bfloat16)
    out_ref[0:8, :] = jax.nn.silu(top + bias_ref[...]).astype(jnp.bfloat16)


def conv_part(xbc, rim8, w8, bias, masks):
    tok, chans = xbc.shape
    return pl.pallas_call(
        conv_kernel,
        grid=(chans // CONV_COLS,),
        in_specs=[
            pl.BlockSpec((tok, CONV_COLS), lambda c: (0, c)),
            pl.BlockSpec((8, CONV_COLS), lambda c: (0, c)),
            pl.BlockSpec((8, CONV_COLS), lambda c: (0, c)),
            pl.BlockSpec((1, CONV_COLS), lambda c: (0, c)),
            pl.BlockSpec((tok, 128), lambda c: (0, 0)),
        ],
        out_specs=pl.BlockSpec((tok, CONV_COLS), lambda c: (0, c)),
        out_shape=jax.ShapeDtypeStruct((tok, chans), jnp.bfloat16),
    )(xbc, rim8, w8, bias, masks)


def state_kernel(
    bt_ref, x_ref, dt_ref, cum_ref, segc_ref, bdec_ref, local_ref, cdec_ref, pay_ref,
    acc_ref, dec_ref,
):
    b = pl.program_id(1)

    @pl.when(b == 0)
    def _():
        acc_ref[...] = jnp.zeros(acc_ref.shape, jnp.float32)
        dec_ref[...] = jnp.ones(dec_ref.shape, jnp.float32)

    local_ref[0] = acc_ref[...]
    cdec_ref[0] = dec_ref[...]
    cum = cum_ref[0]
    step = dt_ref[0]
    segc = segc_ref[:, 0:1]
    last = cum[STRETCH - 1 : STRETCH, :]
    seg_last = segc[STRETCH - 1 : STRETCH, :]
    w = jnp.where(segc == seg_last, jnp.exp(last - cum), 0.0)
    scaled = (x_ref[...].astype(jnp.float32) * expand_heads(step)).astype(jnp.bfloat16)
    weighted = (scaled.astype(jnp.float32) * expand_heads(w)).astype(jnp.bfloat16)
    block_state = jnp.dot(bt_ref[...], weighted, preferred_element_type=jnp.float32)
    decay = bdec_ref[0]
    acc_ref[...] = decay * acc_ref[...] + block_state
    dec_ref[...] = dec_ref[...] * decay

    @pl.when(b == pl.num_programs(1) - 1)
    def _():
        pieces, _, width = pay_ref.shape
        total = acc_ref[...]
        dec = dec_ref[...]
        hi = dec.astype(jnp.bfloat16)
        lo = (dec - hi.astype(jnp.float32)).astype(jnp.bfloat16)
        for k in range(pieces):
            cols = slice(k * width, (k + 1) * width)
            pay_ref[k, 0:STATE, :] = total[:, cols].astype(jnp.bfloat16)
            pay_ref[k, STATE : STATE + 1, :] = hi[:, cols]
            pay_ref[k, STATE + 1 : STATE + 2, :] = lo[:, cols]


def block_states(bt, conv, dt_g, cum_g, segc, bdec, peers):
    tok = conv.shape[0]
    nb = tok // STRETCH
    width = INNER // peers
    per = peers // GROUPS
    return pl.pallas_call(
        state_kernel,
        grid=(GROUPS, nb),
        in_specs=[
            pl.BlockSpec((STATE, STRETCH), lambda g, b: (g, b)),
            pl.BlockSpec((STRETCH, GROUP_COLS), lambda g, b: (b, g)),
            pl.BlockSpec((1, STRETCH, PER_GROUP), lambda g, b: (g, b, 0)),
            pl.BlockSpec((1, STRETCH, PER_GROUP), lambda g, b: (g, b, 0)),
            pl.BlockSpec((STRETCH, 128), lambda g, b: (b, 0)),
            pl.BlockSpec((1, 1, GROUP_COLS), lambda g, b: (b, 0, g)),
        ],
        out_specs=[
            pl.BlockSpec((1, STATE, GROUP_COLS), lambda g, b: (b, 0, g)),
            pl.BlockSpec((1, 1, GROUP_COLS), lambda g, b: (b, 0, g)),
            pl.BlockSpec((per, STATE + 2, width), lambda g, b: (g, 0, 0)),
        ],
        out_shape=[
            jax.ShapeDtypeStruct((nb, STATE, INNER), jnp.float32),
            jax.ShapeDtypeStruct((nb, 1, INNER), jnp.float32),
            jax.ShapeDtypeStruct((peers, STATE + 2, width), jnp.bfloat16),
        ],
        scratch_shapes=[
            pltpu.VMEM((STATE, GROUP_COLS), jnp.float32),
            pltpu.VMEM((1, GROUP_COLS), jnp.float32),
        ],
    )(bt, conv, dt_g, cum_g, segc, bdec)


def intra_kernel(
    c_ref, b_ref, x_ref, dt_ref, cum_ref, cumt_ref, segc_ref, segr_ref, dsk_ref, out_ref
):
    gram = lax.dot_general(
        c_ref[...], b_ref[...], (((1,), (1,)), ((), ())), preferred_element_type=jnp.float32
    )
    segc = segc_ref[:, 0:1]
    segr = segr_ref[0:1, :]
    rows = lax.broadcasted_iota(jnp.int32, (STRETCH, STRETCH), 0)
    cols = lax.broadcasted_iota(jnp.int32, (STRETCH, STRETCH), 1)
    gram = jnp.where((segc == segr) & (cols <= rows), gram, 0.0)
    cum = cum_ref[0]
    cumt = cumt_ref[0]
    step = dt_ref[0]
    for j in range(PER_GROUP):
        hc = slice(j * HEAD_DIM, (j + 1) * HEAD_DIM)
        gap = jnp.minimum(cum[:, j : j + 1] - cumt[j : j + 1, :], 0.0)
        weights = (gram * jnp.exp(gap)).astype(jnp.bfloat16)
        xf = x_ref[:, hc].astype(jnp.float32)
        scaled = (xf * step[:, j : j + 1]).astype(jnp.bfloat16)
        intra = jnp.dot(weights, scaled, preferred_element_type=jnp.float32)
        out_ref[:, hc] = intra + dsk_ref[:, hc] * xf


def intra_part(conv, dt_g, cum_g, cumt_g, segc, segr, dsk, g, into=None):
    tok = conv.shape[0]
    nb = tok // STRETCH
    b_col = INNER // STATE
    c_col = b_col + GROUPS
    operands = [conv, conv, conv, dt_g, cum_g, cumt_g, segc, segr, dsk]
    specs = [
        pl.BlockSpec((STRETCH, STATE), lambda b: (b, c_col + g)),
        pl.BlockSpec((STRETCH, STATE), lambda b: (b, b_col + g)),
        pl.BlockSpec((STRETCH, GROUP_COLS), lambda b: (b, g)),
        pl.BlockSpec((1, STRETCH, PER_GROUP), lambda b: (g, b, 0)),
        pl.BlockSpec((1, STRETCH, PER_GROUP), lambda b: (g, b, 0)),
        pl.BlockSpec((1, PER_GROUP, STRETCH), lambda b: (g, 0, b)),
        pl.BlockSpec((STRETCH, 128), lambda b: (b, 0)),
        pl.BlockSpec((8, STRETCH), lambda b: (0, b)),
        pl.BlockSpec((1, GROUP_COLS), lambda b: (0, g)),
    ]
    kernel = intra_kernel
    aliases = {}
    if into is not None:
        operands.append(into)
        specs.append(pl.BlockSpec(memory_space=pl.ANY))
        aliases = {len(operands) - 1: 0}

        def kernel(*refs):
            intra_kernel(*refs[:-2], refs[-1])

    return pl.pallas_call(
        kernel,
        grid=(nb,),
        in_specs=specs,
        out_specs=pl.BlockSpec((STRETCH, GROUP_COLS), lambda b: (b, g)),
        out_shape=jax.ShapeDtypeStruct((tok, INNER), jnp.float32),
        input_output_aliases=aliases,
    )(*operands)


def mix_kernel(
    c_ref, y_ref, z_ref, back_ref, local_ref, cdec_ref, cum_ref, segc_ref, eb_ref, gain_ref,
    out_ref, hin_ref,
):
    pieces, _, width = back_ref.shape
    for k in range(pieces):
        hin_ref[:, k * width : (k + 1) * width] = back_ref[k].astype(jnp.float32)
    state = cdec_ref[0] * hin_ref[...] + local_ref[0]
    segc = segc_ref[:, 0:1]
    entry = eb_ref[0:1, 0:1]
    in_weight = jnp.where(segc == entry, jnp.exp(cum_ref[0]), 0.0)
    inter = jnp.dot(c_ref[...], state.astype(jnp.bfloat16), preferred_element_type=jnp.float32)
    y = y_ref[...] + inter * expand_heads(in_weight)
    zf = z_ref[...].astype(jnp.float32)
    gated = y * (zf * jax.nn.sigmoid(zf))
    mean_square = jnp.mean(gated * gated, axis=1, keepdims=True) + 1e-05
    out_ref[...] = (gated * lax.rsqrt(mean_square) * gain_ref[...]).astype(jnp.bfloat16)


def mix(conv, y_local, z_gate, back, local_states, cdec, cum_g, segc, eb, gain):
    tok = conv.shape[0]
    nb = tok // STRETCH
    c_col = INNER // STATE + GROUPS
    peers, _, width = back.shape
    per = peers // GROUPS
    return pl.pallas_call(
        mix_kernel,
        grid=(nb, GROUPS),
        in_specs=[
            pl.BlockSpec((STRETCH, STATE), lambda b, g: (b, c_col + g)),
            pl.BlockSpec((STRETCH, GROUP_COLS), lambda b, g: (b, g)),
            pl.BlockSpec((STRETCH, GROUP_COLS), lambda b, g: (b, g)),
            pl.BlockSpec((per, STATE, width), lambda b, g: (g, 0, 0)),
            pl.BlockSpec((1, STATE, GROUP_COLS), lambda b, g: (b, 0, g)),
            pl.BlockSpec((1, 1, GROUP_COLS), lambda b, g: (b, 0, g)),
            pl.BlockSpec((1, STRETCH, PER_GROUP), lambda b, g: (g, b, 0)),
            pl.BlockSpec((STRETCH, 128), lambda b, g: (b, 0)),
            pl.BlockSpec((8, 128), lambda b, g: (b, 0)),
            pl.BlockSpec((1, GROUP_COLS), lambda b, g: (0, g)),
        ],
        out_specs=pl.BlockSpec((STRETCH, GROUP_COLS), lambda b, g: (b, g)),
        out_shape=jax.ShapeDtypeStruct((tok, INNER), jnp.bfloat16),
        scratch_shapes=[pltpu.VMEM((STATE, GROUP_COLS), jnp.float32)],
    )(conv, y_local, z_gate, back, local_states, cdec, cum_g, segc, eb, gain)


def scan_kernel(got_ref, out_ref):
    peers = got_ref.shape[0]

    def body(d, carry):
        out_ref[d] = carry.astype(jnp.bfloat16)
        decay = got_ref[d, STATE : STATE + 1, :].astype(jnp.float32) + got_ref[
            d, STATE + 1 : STATE + 2, :
        ].astype(jnp.float32)
        return decay * carry + got_ref[d, 0:STATE, :].astype(jnp.float32)

    lax.fori_loop(0, peers, body, jnp.zeros(out_ref.shape[1:], jnp.float32))


def compose(payload):
    peers, _, width = payload.shape
    got = lax.all_to_all(payload, "ctx", split_axis=0, concat_axis=0, tiled=True)
    entering = pl.pallas_call(
        scan_kernel,
        out_shape=jax.ShapeDtypeStruct((peers, STATE, width), jnp.bfloat16),
    )(got)
    return lax.all_to_all(entering, "ctx", split_axis=0, concat_axis=0, tiled=True)


def local(xbc, z_gate, dt_raw, lengths, conv_weight, conv_bias, dt_bias, a_log, d_skip, norm_gain):
    tok = xbc.shape[0]
    nb = tok // STRETCH
    peers = lax.axis_size("ctx")
    first_pos = lax.axis_index("ctx") * tok
    rim_rows = shifted(xbc[tok - (CONV - 1) :], "ctx", 1)
    rim8 = jnp.concatenate([jnp.zeros((8 - (CONV - 1), CHANNELS), xbc.dtype), rim_rows], axis=0)
    ext_pos = first_pos - (CONV - 1) + jnp.arange(tok + CONV - 1)
    ext_seg = segment_of(ext_pos, lengths)
    target = ext_seg[CONV - 1 :]
    kept = [
        (ext_pos[tap : tap + tok] >= 0) & (ext_seg[tap : tap + tok] == target) for tap in range(CONV)
    ]
    masks = jnp.stack(kept, axis=1).astype(jnp.float32)
    masks = jnp.concatenate([masks, jnp.zeros((tok, 128 - CONV), jnp.float32)], axis=1)
    w8 = jnp.concatenate([conv_weight, jnp.zeros((8 - CONV, CHANNELS), jnp.float32)], axis=0)
    conv = conv_part(xbc, rim8, w8, conv_bias[None, :], masks)
    step = jax.nn.softplus(dt_raw.astype(jnp.float32) + dt_bias[None, :])
    log_decay = -step * jnp.exp(a_log)[None, :]
    cum = jnp.cumsum(log_decay.reshape(nb, STRETCH, HEADS), axis=1).reshape(tok, HEADS)
    segments = segment_of(first_pos + jnp.arange(tok), lengths)
    seg_before = segment_of(first_pos + jnp.arange(nb) * STRETCH - 1, lengths)
    seg_last = segments.reshape(nb, STRETCH)[:, -1]
    cum_last = cum.reshape(nb, STRETCH, HEADS)[:, -1, :]
    block_decay = jnp.where((seg_last == seg_before)[:, None], jnp.exp(cum_last), 0.0)

    cum_g = cum.reshape(tok, GROUPS, PER_GROUP).transpose(1, 0, 2)
    dt_g = step.reshape(tok, GROUPS, PER_GROUP).transpose(1, 0, 2)
    cumt_g = cum.T.reshape(GROUPS, PER_GROUP, tok)
    segc = jnp.broadcast_to(segments[:, None], (tok, 128)).astype(jnp.int32)
    segr = jnp.broadcast_to(segments[None, :], (8, tok)).astype(jnp.int32)
    eb = jnp.broadcast_to(seg_before[:, None, None], (nb, 8, 128)).reshape(nb * 8, 128)
    eb = eb.astype(jnp.int32)
    bt = conv[:, INNER : INNER + GROUPS * STATE].T
    bdec = jnp.repeat(block_decay, HEAD_DIM, axis=1)[:, None, :]

    local_states, cdec, payload = block_states(bt, conv, dt_g, cum_g, segc, bdec, peers)
    dsk = jnp.repeat(d_skip, HEAD_DIM)[None, :]
    y_local = None
    for g in range(GROUPS):
        y_local = intra_part(conv, dt_g, cum_g, cumt_g, segc, segr, dsk, g, y_local)
    back = compose(payload)
    gain = norm_gain[None, :]
    return mix(conv, y_local, z_gate, back, local_states, cdec, cum_g, segc, eb, gain)


def solution(mesh):
    return jax.shard_map(
        local,
        mesh=mesh,
        in_specs=(
            P(("group", "ctx"), None),
            P(("group", "ctx"), None),
            P(("group", "ctx"), None),
            P("group"),
            P(),
            P(),
            P(),
            P(),
            P(),
            P(),
        ),
        out_specs=P(("group", "ctx"), None),
        check_vma=False,
    )
```

```python
import jax
import jax.numpy as jnp
from jax import lax
from jax.experimental import pallas as pl
from jax.experimental.pallas import tpu as pltpu
from jax.sharding import Mesh, PartitionSpec as P

HEADS = 64
HEAD_DIM = 64
STATE = 256
GROUPS = 2
CONV = 4
STRETCH = 256
CHANNELS = 5120
INNER = HEADS * HEAD_DIM
PER_GROUP = HEADS // GROUPS
GROUP_COLS = INNER // GROUPS


def shifted(value, axis, by):
    peers = lax.axis_size(axis)
    pairs = [(i, i + by) for i in range(peers) if 0 <= i + by < peers]
    return lax.ppermute(value, axis, pairs)


def segment_of(positions, lengths):
    prompt_ends = jnp.cumsum(lengths)
    hits = (prompt_ends[None, :] <= positions[:, None]).astype(jnp.int32)
    return jnp.sum(hits, axis=1)


def expand_heads(v):
    heads = lax.broadcasted_iota(jnp.int32, (PER_GROUP, GROUP_COLS), 0)
    cols = lax.broadcasted_iota(jnp.int32, (PER_GROUP, GROUP_COLS), 1)
    spread = (cols // HEAD_DIM == heads).astype(jnp.bfloat16)
    hi = v.astype(jnp.bfloat16)
    rest = v - hi.astype(jnp.float32)
    mid = rest.astype(jnp.bfloat16)
    lo = (rest - mid.astype(jnp.float32)).astype(jnp.bfloat16)
    out = jnp.dot(hi, spread, preferred_element_type=jnp.float32)
    out = out + jnp.dot(mid, spread, preferred_element_type=jnp.float32)
    return out + jnp.dot(lo, spread, preferred_element_type=jnp.float32)


CONV_COLS = 640


def conv_kernel(x_ref, rim_ref, w_ref, bias_ref, m_ref, out_ref):
    x = x_ref[...].astype(jnp.float32)
    rim = rim_ref[...].astype(jnp.float32)
    rows8 = lax.broadcasted_iota(jnp.int32, rim.shape, 0)
    summed = jnp.zeros(x.shape, jnp.float32)
    top = jnp.zeros(rim.shape, jnp.float32)
    for tap in range(CONV):
        by = CONV - 1 - tap
        wk = w_ref[tap : tap + 1, :]
        kept = m_ref[:, tap : tap + 1] > 0.0
        if by == 0:
            term = x
            top_term = x[0:8]
        else:
            term = pltpu.roll(x, by, 0)
            top_term = jnp.where(rows8 < by, pltpu.roll(rim, by, 0), term[0:8])
        summed = summed + jnp.where(kept, term * wk, 0.0)
        top = top + jnp.where(kept[0:8], top_term * wk, 0.0)
    out_ref[...] = jax.nn.silu(summed + bias_ref[...]).astype(jnp.bfloat16)
    out_ref[0:8, :] = jax.nn.silu(top + bias_ref[...]).astype(jnp.bfloat16)


def conv_part(xbc, rim8, w8, bias, masks):
    tok, chans = xbc.shape
    return pl.pallas_call(
        conv_kernel,
        grid=(chans // CONV_COLS,),
        in_specs=[
            pl.BlockSpec((tok, CONV_COLS), lambda c: (0, c)),
            pl.BlockSpec((8, CONV_COLS), lambda c: (0, c)),
            pl.BlockSpec((8, CONV_COLS), lambda c: (0, c)),
            pl.BlockSpec((1, CONV_COLS), lambda c: (0, c)),
            pl.BlockSpec((tok, 128), lambda c: (0, 0)),
        ],
        out_specs=pl.BlockSpec((tok, CONV_COLS), lambda c: (0, c)),
        out_shape=jax.ShapeDtypeStruct((tok, chans), jnp.bfloat16),
    )(xbc, rim8, w8, bias, masks)


def state_kernel(
    bt_ref, x_ref, dt_ref, cum_ref, segc_ref, bdec_ref, local_ref, cdec_ref, tot_ref,
    acc_ref, dec_ref,
):
    b = pl.program_id(1)

    @pl.when(b == 0)
    def _():
        acc_ref[...] = jnp.zeros(acc_ref.shape, jnp.float32)
        dec_ref[...] = jnp.ones(dec_ref.shape, jnp.float32)

    local_ref[0] = acc_ref[...]
    cdec_ref[0] = dec_ref[...]
    cum = cum_ref[0]
    step = dt_ref[0]
    segc = segc_ref[:, 0:1]
    last = cum[STRETCH - 1 : STRETCH, :]
    seg_last = segc[STRETCH - 1 : STRETCH, :]
    w = jnp.where(segc == seg_last, jnp.exp(last - cum), 0.0)
    scaled = (x_ref[...].astype(jnp.float32) * expand_heads(step)).astype(jnp.bfloat16)
    weighted = (scaled.astype(jnp.float32) * expand_heads(w)).astype(jnp.bfloat16)
    block_state = jnp.dot(bt_ref[...], weighted, preferred_element_type=jnp.float32)
    decay = bdec_ref[0]
    acc_ref[...] = decay * acc_ref[...] + block_state
    dec_ref[...] = dec_ref[...] * decay

    @pl.when(b == pl.num_programs(1) - 1)
    def _():
        tot_ref[0, 0:STATE, :] = acc_ref[...]
        tot_ref[0, STATE : STATE + 1, :] = dec_ref[...]


def block_states(bt, conv, dt_g, cum_g, segc, bdec):
    tok = conv.shape[0]
    nb = tok // STRETCH
    return pl.pallas_call(
        state_kernel,
        grid=(GROUPS, nb),
        in_specs=[
            pl.BlockSpec((STATE, STRETCH), lambda g, b: (g, b)),
            pl.BlockSpec((STRETCH, GROUP_COLS), lambda g, b: (b, g)),
            pl.BlockSpec((1, STRETCH, PER_GROUP), lambda g, b: (g, b, 0)),
            pl.BlockSpec((1, STRETCH, PER_GROUP), lambda g, b: (g, b, 0)),
            pl.BlockSpec((STRETCH, 128), lambda g, b: (b, 0)),
            pl.BlockSpec((1, 1, GROUP_COLS), lambda g, b: (b, 0, g)),
        ],
        out_specs=[
            pl.BlockSpec((1, STATE, GROUP_COLS), lambda g, b: (b, 0, g)),
            pl.BlockSpec((1, 1, GROUP_COLS), lambda g, b: (b, 0, g)),
            pl.BlockSpec((1, STATE + 1, GROUP_COLS), lambda g, b: (g, 0, 0)),
        ],
        out_shape=[
            jax.ShapeDtypeStruct((nb, STATE, INNER), jnp.float32),
            jax.ShapeDtypeStruct((nb, 1, INNER), jnp.float32),
            jax.ShapeDtypeStruct((GROUPS, STATE + 1, GROUP_COLS), jnp.float32),
        ],
        scratch_shapes=[
            pltpu.VMEM((STATE, GROUP_COLS), jnp.float32),
            pltpu.VMEM((1, GROUP_COLS), jnp.float32),
        ],
    )(bt, conv, dt_g, cum_g, segc, bdec)


def intra_kernel(
    c_ref, b_ref, x_ref, dt_ref, cum_ref, cumt_ref, segc_ref, segr_ref, dsk_ref, out_ref
):
    gram = lax.dot_general(
        c_ref[...], b_ref[...], (((1,), (1,)), ((), ())), preferred_element_type=jnp.float32
    )
    segc = segc_ref[:, 0:1]
    segr = segr_ref[0:1, :]
    rows = lax.broadcasted_iota(jnp.int32, (STRETCH, STRETCH), 0)
    cols = lax.broadcasted_iota(jnp.int32, (STRETCH, STRETCH), 1)
    gram = jnp.where((segc == segr) & (cols <= rows), gram, 0.0)
    cum = cum_ref[0]
    cumt = cumt_ref[0]
    step = dt_ref[0]
    for j in range(PER_GROUP):
        hc = slice(j * HEAD_DIM, (j + 1) * HEAD_DIM)
        gap = jnp.minimum(cum[:, j : j + 1] - cumt[j : j + 1, :], 0.0)
        weights = (gram * jnp.exp(gap)).astype(jnp.bfloat16)
        xf = x_ref[:, hc].astype(jnp.float32)
        scaled = (xf * step[:, j : j + 1]).astype(jnp.bfloat16)
        intra = jnp.dot(weights, scaled, preferred_element_type=jnp.float32)
        out_ref[:, hc] = intra + dsk_ref[:, hc] * xf


def intra_part(conv, dt_g, cum_g, cumt_g, segc, segr, dsk, g, into=None):
    tok = conv.shape[0]
    nb = tok // STRETCH
    b_col = INNER // STATE
    c_col = b_col + GROUPS
    operands = [conv, conv, conv, dt_g, cum_g, cumt_g, segc, segr, dsk]
    specs = [
        pl.BlockSpec((STRETCH, STATE), lambda b: (b, c_col + g)),
        pl.BlockSpec((STRETCH, STATE), lambda b: (b, b_col + g)),
        pl.BlockSpec((STRETCH, GROUP_COLS), lambda b: (b, g)),
        pl.BlockSpec((1, STRETCH, PER_GROUP), lambda b: (g, b, 0)),
        pl.BlockSpec((1, STRETCH, PER_GROUP), lambda b: (g, b, 0)),
        pl.BlockSpec((1, PER_GROUP, STRETCH), lambda b: (g, 0, b)),
        pl.BlockSpec((STRETCH, 128), lambda b: (b, 0)),
        pl.BlockSpec((8, STRETCH), lambda b: (0, b)),
        pl.BlockSpec((1, GROUP_COLS), lambda b: (0, g)),
    ]
    kernel = intra_kernel
    aliases = {}
    if into is not None:
        operands.append(into)
        specs.append(pl.BlockSpec(memory_space=pl.ANY))
        aliases = {len(operands) - 1: 0}

        def kernel(*refs):
            intra_kernel(*refs[:-2], refs[-1])

    return pl.pallas_call(
        kernel,
        grid=(nb,),
        in_specs=specs,
        out_specs=pl.BlockSpec((STRETCH, GROUP_COLS), lambda b: (b, g)),
        out_shape=jax.ShapeDtypeStruct((tok, INNER), jnp.float32),
        input_output_aliases=aliases,
    )(*operands)


def mix_kernel(
    c_ref, y_ref, z_ref, hin_ref, local_ref, cdec_ref, cum_ref, segc_ref, eb_ref, gain_ref,
    out_ref,
):
    state = cdec_ref[0] * hin_ref[...].astype(jnp.float32) + local_ref[0]
    segc = segc_ref[:, 0:1]
    entry = eb_ref[0:1, 0:1]
    in_weight = jnp.where(segc == entry, jnp.exp(cum_ref[0]), 0.0)
    inter = jnp.dot(c_ref[...], state.astype(jnp.bfloat16), preferred_element_type=jnp.float32)
    y = y_ref[...] + inter * expand_heads(in_weight)
    zf = z_ref[...].astype(jnp.float32)
    gated = y * (zf * jax.nn.sigmoid(zf))
    mean_square = jnp.mean(gated * gated, axis=1, keepdims=True) + 1e-05
    out_ref[...] = (gated * lax.rsqrt(mean_square) * gain_ref[...]).astype(jnp.bfloat16)


def mix(conv, y_local, z_gate, back, local_states, cdec, cum_g, segc, eb, gain):
    tok = conv.shape[0]
    nb = tok // STRETCH
    c_col = INNER // STATE + GROUPS
    return pl.pallas_call(
        mix_kernel,
        grid=(nb, GROUPS),
        in_specs=[
            pl.BlockSpec((STRETCH, STATE), lambda b, g: (b, c_col + g)),
            pl.BlockSpec((STRETCH, GROUP_COLS), lambda b, g: (b, g)),
            pl.BlockSpec((STRETCH, GROUP_COLS), lambda b, g: (b, g)),
            pl.BlockSpec((STATE, GROUP_COLS), lambda b, g: (0, g)),
            pl.BlockSpec((1, STATE, GROUP_COLS), lambda b, g: (b, 0, g)),
            pl.BlockSpec((1, 1, GROUP_COLS), lambda b, g: (b, 0, g)),
            pl.BlockSpec((1, STRETCH, PER_GROUP), lambda b, g: (g, b, 0)),
            pl.BlockSpec((STRETCH, 128), lambda b, g: (b, 0)),
            pl.BlockSpec((8, 128), lambda b, g: (b, 0)),
            pl.BlockSpec((1, GROUP_COLS), lambda b, g: (0, g)),
        ],
        out_specs=pl.BlockSpec((STRETCH, GROUP_COLS), lambda b, g: (b, g)),
        out_shape=jax.ShapeDtypeStruct((tok, INNER), jnp.bfloat16),
    )(conv, y_local, z_gate, back, local_states, cdec, cum_g, segc, eb, gain)


def scan_kernel(got_ref, out_ref):
    peers = got_ref.shape[0]

    def body(d, carry):
        out_ref[d] = carry.astype(jnp.bfloat16)
        decay = got_ref[d, STATE : STATE + 1, :].astype(jnp.float32) + got_ref[
            d, STATE + 1 : STATE + 2, :
        ].astype(jnp.float32)
        return decay * carry + got_ref[d, 0:STATE, :].astype(jnp.float32)

    lax.fori_loop(0, peers, body, jnp.zeros(out_ref.shape[1:], jnp.float32))


def swap_cores(value):
    return lax.ppermute(value, "core", [(0, 1), (1, 0)])


def exchange(value, axis):
    count = lax.axis_size(axis)
    me = lax.axis_index(axis)
    got = [lax.dynamic_index_in_dim(value, me, 0, keepdims=False)]
    for by in range(1, count):
        piece = lax.dynamic_index_in_dim(value, (me + by) % count, 0, keepdims=False)
        pairs = [(i, (i + by) % count) for i in range(count)]
        got.append(lax.ppermute(piece, axis, pairs))
    stacked = jnp.stack(got)
    return jnp.take(stacked, (me - jnp.arange(count)) % count, axis=0)


def compose(both):
    core = lax.axis_index("core")
    chips = lax.axis_size("chip")
    half = GROUP_COLS
    width = half // chips
    mine = lax.dynamic_index_in_dim(both, core, 0, keepdims=False)
    theirs = swap_cores(lax.dynamic_index_in_dim(both, 1 - core, 0, keepdims=False))
    first = jnp.where(core == 0, mine, theirs)
    second = jnp.where(core == 0, theirs, mine)
    first_decay = first[STATE:]
    chip_state = second[STATE:] * first[:STATE] + second[:STATE]
    chip_decay = first_decay * second[STATE:]
    decay_hi = chip_decay.astype(jnp.bfloat16)
    decay_lo = (chip_decay - decay_hi.astype(jnp.float32)).astype(jnp.bfloat16)
    payload = jnp.concatenate(
        [chip_state.astype(jnp.bfloat16), decay_hi, decay_lo], axis=0
    ).reshape(STATE + 2, chips, width).transpose(1, 0, 2)
    got = exchange(payload, "chip")
    entering = pl.pallas_call(
        scan_kernel,
        out_shape=jax.ShapeDtypeStruct((chips, STATE, width), jnp.bfloat16),
    )(got)
    back = exchange(entering, "chip")
    chip_in = back.transpose(1, 0, 2).reshape(STATE, half).astype(jnp.float32)
    later_in = first_decay * chip_in + first[:STATE]
    keep = jnp.where(core == 0, chip_in, later_in).astype(jnp.bfloat16)
    other = swap_cores(jnp.where(core == 0, later_in, chip_in).astype(jnp.bfloat16))
    return jnp.where(
        core == 0,
        jnp.concatenate([keep, other], axis=1),
        jnp.concatenate([other, keep], axis=1),
    )


def local(xbc, z_gate, dt_raw, lengths, conv_weight, conv_bias, dt_bias, a_log, d_skip, norm_gain):
    tok = xbc.shape[0]
    nb = tok // STRETCH
    first_pos = (lax.axis_index("chip") * lax.axis_size("core") + lax.axis_index("core")) * tok
    rim_rows = shifted(xbc[tok - (CONV - 1) :], ("chip", "core"), 1)
    rim8 = jnp.concatenate([jnp.zeros((8 - (CONV - 1), CHANNELS), xbc.dtype), rim_rows], axis=0)
    ext_pos = first_pos - (CONV - 1) + jnp.arange(tok + CONV - 1)
    ext_seg = segment_of(ext_pos, lengths)
    target = ext_seg[CONV - 1 :]
    kept = [
        (ext_pos[tap : tap + tok] >= 0) & (ext_seg[tap : tap + tok] == target) for tap in range(CONV)
    ]
    masks = jnp.stack(kept, axis=1).astype(jnp.float32)
    masks = jnp.concatenate([masks, jnp.zeros((tok, 128 - CONV), jnp.float32)], axis=1)
    w8 = jnp.concatenate([conv_weight, jnp.zeros((8 - CONV, CHANNELS), jnp.float32)], axis=0)
    conv = conv_part(xbc, rim8, w8, conv_bias[None, :], masks)
    step = jax.nn.softplus(dt_raw.astype(jnp.float32) + dt_bias[None, :])
    log_decay = -step * jnp.exp(a_log)[None, :]
    cum = jnp.cumsum(log_decay.reshape(nb, STRETCH, HEADS), axis=1).reshape(tok, HEADS)
    segments = segment_of(first_pos + jnp.arange(tok), lengths)
    seg_before = segment_of(first_pos + jnp.arange(nb) * STRETCH - 1, lengths)
    seg_last = segments.reshape(nb, STRETCH)[:, -1]
    cum_last = cum.reshape(nb, STRETCH, HEADS)[:, -1, :]
    block_decay = jnp.where((seg_last == seg_before)[:, None], jnp.exp(cum_last), 0.0)

    cum_g = cum.reshape(tok, GROUPS, PER_GROUP).transpose(1, 0, 2)
    dt_g = step.reshape(tok, GROUPS, PER_GROUP).transpose(1, 0, 2)
    cumt_g = cum.T.reshape(GROUPS, PER_GROUP, tok)
    segc = jnp.broadcast_to(segments[:, None], (tok, 128)).astype(jnp.int32)
    segr = jnp.broadcast_to(segments[None, :], (8, tok)).astype(jnp.int32)
    eb = jnp.broadcast_to(seg_before[:, None, None], (nb, 8, 128)).reshape(nb * 8, 128)
    eb = eb.astype(jnp.int32)
    bt = conv[:, INNER : INNER + GROUPS * STATE].T
    bdec = jnp.repeat(block_decay, HEAD_DIM, axis=1)[:, None, :]

    local_states, cdec, both = block_states(bt, conv, dt_g, cum_g, segc, bdec)
    dsk = jnp.repeat(d_skip, HEAD_DIM)[None, :]
    y_local = None
    for g in range(GROUPS):
        y_local = intra_part(conv, dt_g, cum_g, cumt_g, segc, segr, dsk, g, y_local)
    back = compose(both)
    gain = norm_gain[None, :]
    return mix(conv, y_local, z_gate, back, local_states, cdec, cum_g, segc, eb, gain)


def solution(mesh):
    groups, peers = mesh.devices.shape
    split = Mesh(mesh.devices.reshape(groups, peers // 2, 2), ("group", "chip", "core"))
    rows = P(("group", "chip", "core"), None)
    return jax.shard_map(
        local,
        mesh=split,
        in_specs=(rows, rows, rows, P("group"), P(), P(), P(), P(), P(), P()),
        out_specs=rows,
        check_vma=False,
    )
```

```python
import jax
import jax.numpy as jnp
from jax import lax
from jax.experimental import pallas as pl
from jax.experimental.pallas import tpu as pltpu
from jax.sharding import Mesh, PartitionSpec as P

HEADS = 64
HEAD_DIM = 64
STATE = 256
GROUPS = 2
CONV = 4
STRETCH = 256
CHANNELS = 5120
INNER = HEADS * HEAD_DIM
PER_GROUP = HEADS // GROUPS
GROUP_COLS = INNER // GROUPS


def shifted(value, axis, by):
    peers = lax.axis_size(axis)
    pairs = [(i, i + by) for i in range(peers) if 0 <= i + by < peers]
    return lax.ppermute(value, axis, pairs)


def segment_of(positions, lengths):
    prompt_ends = jnp.cumsum(lengths)
    hits = (prompt_ends[None, :] <= positions[:, None]).astype(jnp.int32)
    return jnp.sum(hits, axis=1)


def expand_heads(v):
    heads = lax.broadcasted_iota(jnp.int32, (PER_GROUP, GROUP_COLS), 0)
    cols = lax.broadcasted_iota(jnp.int32, (PER_GROUP, GROUP_COLS), 1)
    spread = (cols // HEAD_DIM == heads).astype(jnp.bfloat16)
    hi = v.astype(jnp.bfloat16)
    rest = v - hi.astype(jnp.float32)
    mid = rest.astype(jnp.bfloat16)
    lo = (rest - mid.astype(jnp.float32)).astype(jnp.bfloat16)
    out = jnp.dot(hi, spread, preferred_element_type=jnp.float32)
    out = out + jnp.dot(mid, spread, preferred_element_type=jnp.float32)
    return out + jnp.dot(lo, spread, preferred_element_type=jnp.float32)


CONV_COLS = 640


def conv_kernel(x_ref, rim_ref, w_ref, bias_ref, m_ref, out_ref):
    x = x_ref[...].astype(jnp.float32)
    rim = rim_ref[...].astype(jnp.float32)
    rows8 = lax.broadcasted_iota(jnp.int32, rim.shape, 0)
    summed = jnp.zeros(x.shape, jnp.float32)
    top = jnp.zeros(rim.shape, jnp.float32)
    for tap in range(CONV):
        by = CONV - 1 - tap
        wk = w_ref[tap : tap + 1, :]
        kept = m_ref[:, tap : tap + 1] > 0.0
        if by == 0:
            term = x
            top_term = x[0:8]
        else:
            term = pltpu.roll(x, by, 0)
            top_term = jnp.where(rows8 < by, pltpu.roll(rim, by, 0), term[0:8])
        summed = summed + jnp.where(kept, term * wk, 0.0)
        top = top + jnp.where(kept[0:8], top_term * wk, 0.0)
    out_ref[...] = jax.nn.silu(summed + bias_ref[...]).astype(jnp.bfloat16)
    out_ref[0:8, :] = jax.nn.silu(top + bias_ref[...]).astype(jnp.bfloat16)


def conv_part(xbc, rim8, w8, bias, masks):
    tok, chans = xbc.shape
    return pl.pallas_call(
        conv_kernel,
        grid=(chans // CONV_COLS,),
        in_specs=[
            pl.BlockSpec((tok, CONV_COLS), lambda c: (0, c)),
            pl.BlockSpec((8, CONV_COLS), lambda c: (0, c)),
            pl.BlockSpec((8, CONV_COLS), lambda c: (0, c)),
            pl.BlockSpec((1, CONV_COLS), lambda c: (0, c)),
            pl.BlockSpec((tok, 128), lambda c: (0, 0)),
        ],
        out_specs=pl.BlockSpec((tok, CONV_COLS), lambda c: (0, c)),
        out_shape=jax.ShapeDtypeStruct((tok, chans), jnp.bfloat16),
    )(xbc, rim8, w8, bias, masks)


def state_kernel(
    bt_ref, x_ref, dt_ref, cum_ref, segc_ref, bdec_ref, local_ref, cdec_ref, tot_ref,
    acc_ref, dec_ref,
):
    b = pl.program_id(1)

    @pl.when(b == 0)
    def _():
        acc_ref[...] = jnp.zeros(acc_ref.shape, jnp.float32)
        dec_ref[...] = jnp.ones(dec_ref.shape, jnp.float32)

    local_ref[0] = acc_ref[...]
    cdec_ref[0] = dec_ref[...]
    cum = cum_ref[0]
    step = dt_ref[0]
    segc = segc_ref[:, 0:1]
    last = cum[STRETCH - 1 : STRETCH, :]
    seg_last = segc[STRETCH - 1 : STRETCH, :]
    w = jnp.where(segc == seg_last, jnp.exp(last - cum), 0.0)
    scaled = (x_ref[...].astype(jnp.float32) * expand_heads(step)).astype(jnp.bfloat16)
    weighted = (scaled.astype(jnp.float32) * expand_heads(w)).astype(jnp.bfloat16)
    block_state = jnp.dot(bt_ref[...], weighted, preferred_element_type=jnp.float32)
    decay = bdec_ref[0]
    acc_ref[...] = decay * acc_ref[...] + block_state
    dec_ref[...] = dec_ref[...] * decay

    @pl.when(b == pl.num_programs(1) - 1)
    def _():
        tot_ref[0, 0:STATE, :] = acc_ref[...]
        tot_ref[0, STATE : STATE + 1, :] = dec_ref[...]


def block_states(bt, conv, dt_g, cum_g, segc, bdec):
    tok = conv.shape[0]
    nb = tok // STRETCH
    return pl.pallas_call(
        state_kernel,
        grid=(GROUPS, nb),
        in_specs=[
            pl.BlockSpec((STATE, STRETCH), lambda g, b: (g, b)),
            pl.BlockSpec((STRETCH, GROUP_COLS), lambda g, b: (b, g)),
            pl.BlockSpec((1, STRETCH, PER_GROUP), lambda g, b: (g, b, 0)),
            pl.BlockSpec((1, STRETCH, PER_GROUP), lambda g, b: (g, b, 0)),
            pl.BlockSpec((STRETCH, 128), lambda g, b: (b, 0)),
            pl.BlockSpec((1, 1, GROUP_COLS), lambda g, b: (b, 0, g)),
        ],
        out_specs=[
            pl.BlockSpec((1, STATE, GROUP_COLS), lambda g, b: (b, 0, g)),
            pl.BlockSpec((1, 1, GROUP_COLS), lambda g, b: (b, 0, g)),
            pl.BlockSpec((1, STATE + 1, GROUP_COLS), lambda g, b: (g, 0, 0)),
        ],
        out_shape=[
            jax.ShapeDtypeStruct((nb, STATE, INNER), jnp.float32),
            jax.ShapeDtypeStruct((nb, 1, INNER), jnp.float32),
            jax.ShapeDtypeStruct((GROUPS, STATE + 1, GROUP_COLS), jnp.float32),
        ],
        scratch_shapes=[
            pltpu.VMEM((STATE, GROUP_COLS), jnp.float32),
            pltpu.VMEM((1, GROUP_COLS), jnp.float32),
        ],
    )(bt, conv, dt_g, cum_g, segc, bdec)


def intra_kernel(
    c_ref, b_ref, x_ref, dt_ref, cum_ref, cumt_ref, segc_ref, segr_ref, dsk_ref, out_ref
):
    gram = lax.dot_general(
        c_ref[...], b_ref[...], (((1,), (1,)), ((), ())), preferred_element_type=jnp.float32
    )
    segc = segc_ref[:, 0:1]
    segr = segr_ref[0:1, :]
    rows = lax.broadcasted_iota(jnp.int32, (STRETCH, STRETCH), 0)
    cols = lax.broadcasted_iota(jnp.int32, (STRETCH, STRETCH), 1)
    gram = jnp.where((segc == segr) & (cols <= rows), gram, 0.0)
    cum = cum_ref[0]
    cumt = cumt_ref[0]
    step = dt_ref[0]
    for j in range(PER_GROUP):
        hc = slice(j * HEAD_DIM, (j + 1) * HEAD_DIM)
        gap = jnp.minimum(cum[:, j : j + 1] - cumt[j : j + 1, :], 0.0)
        weights = (gram * jnp.exp(gap)).astype(jnp.bfloat16)
        xf = x_ref[:, hc].astype(jnp.float32)
        scaled = (xf * step[:, j : j + 1]).astype(jnp.bfloat16)
        intra = jnp.dot(weights, scaled, preferred_element_type=jnp.float32)
        out_ref[:, hc] = intra + dsk_ref[:, hc] * xf


def intra_part(conv, dt_g, cum_g, cumt_g, segc, segr, dsk, g, into=None):
    tok = conv.shape[0]
    nb = tok // STRETCH
    b_col = INNER // STATE
    c_col = b_col + GROUPS
    operands = [conv, conv, conv, dt_g, cum_g, cumt_g, segc, segr, dsk]
    specs = [
        pl.BlockSpec((STRETCH, STATE), lambda b: (b, c_col + g)),
        pl.BlockSpec((STRETCH, STATE), lambda b: (b, b_col + g)),
        pl.BlockSpec((STRETCH, GROUP_COLS), lambda b: (b, g)),
        pl.BlockSpec((1, STRETCH, PER_GROUP), lambda b: (g, b, 0)),
        pl.BlockSpec((1, STRETCH, PER_GROUP), lambda b: (g, b, 0)),
        pl.BlockSpec((1, PER_GROUP, STRETCH), lambda b: (g, 0, b)),
        pl.BlockSpec((STRETCH, 128), lambda b: (b, 0)),
        pl.BlockSpec((8, STRETCH), lambda b: (0, b)),
        pl.BlockSpec((1, GROUP_COLS), lambda b: (0, g)),
    ]
    kernel = intra_kernel
    aliases = {}
    if into is not None:
        operands.append(into)
        specs.append(pl.BlockSpec(memory_space=pl.ANY))
        aliases = {len(operands) - 1: 0}

        def kernel(*refs):
            intra_kernel(*refs[:-2], refs[-1])

    return pl.pallas_call(
        kernel,
        grid=(nb,),
        in_specs=specs,
        out_specs=pl.BlockSpec((STRETCH, GROUP_COLS), lambda b: (b, g)),
        out_shape=jax.ShapeDtypeStruct((tok, INNER), jnp.float32),
        input_output_aliases=aliases,
    )(*operands)


def mix_kernel(
    c_ref, y_ref, z_ref, hin_ref, local_ref, cdec_ref, cum_ref, segc_ref, eb_ref, gain_ref,
    out_ref,
):
    state = cdec_ref[0] * hin_ref[...].astype(jnp.float32) + local_ref[0]
    segc = segc_ref[:, 0:1]
    entry = eb_ref[0:1, 0:1]
    in_weight = jnp.where(segc == entry, jnp.exp(cum_ref[0]), 0.0)
    inter = jnp.dot(c_ref[...], state.astype(jnp.bfloat16), preferred_element_type=jnp.float32)
    y = y_ref[...] + inter * expand_heads(in_weight)
    zf = z_ref[...].astype(jnp.float32)
    gated = y * (zf * jax.nn.sigmoid(zf))
    mean_square = jnp.mean(gated * gated, axis=1, keepdims=True) + 1e-05
    out_ref[...] = (gated * lax.rsqrt(mean_square) * gain_ref[...]).astype(jnp.bfloat16)


def mix(conv, y_local, z_gate, back, local_states, cdec, cum_g, segc, eb, gain):
    tok = conv.shape[0]
    nb = tok // STRETCH
    c_col = INNER // STATE + GROUPS
    return pl.pallas_call(
        mix_kernel,
        grid=(nb, GROUPS),
        in_specs=[
            pl.BlockSpec((STRETCH, STATE), lambda b, g: (b, c_col + g)),
            pl.BlockSpec((STRETCH, GROUP_COLS), lambda b, g: (b, g)),
            pl.BlockSpec((STRETCH, GROUP_COLS), lambda b, g: (b, g)),
            pl.BlockSpec((STATE, GROUP_COLS), lambda b, g: (0, g)),
            pl.BlockSpec((1, STATE, GROUP_COLS), lambda b, g: (b, 0, g)),
            pl.BlockSpec((1, 1, GROUP_COLS), lambda b, g: (b, 0, g)),
            pl.BlockSpec((1, STRETCH, PER_GROUP), lambda b, g: (g, b, 0)),
            pl.BlockSpec((STRETCH, 128), lambda b, g: (b, 0)),
            pl.BlockSpec((8, 128), lambda b, g: (b, 0)),
            pl.BlockSpec((1, GROUP_COLS), lambda b, g: (0, g)),
        ],
        out_specs=pl.BlockSpec((STRETCH, GROUP_COLS), lambda b, g: (b, g)),
        out_shape=jax.ShapeDtypeStruct((tok, INNER), jnp.bfloat16),
    )(conv, y_local, z_gate, back, local_states, cdec, cum_g, segc, eb, gain)


def scan_kernel(got_ref, out_ref):
    peers = got_ref.shape[0]

    def body(d, carry):
        out_ref[d] = carry.astype(jnp.bfloat16)
        decay = got_ref[d, STATE : STATE + 1, :].astype(jnp.float32) + got_ref[
            d, STATE + 1 : STATE + 2, :
        ].astype(jnp.float32)
        return decay * carry + got_ref[d, 0:STATE, :].astype(jnp.float32)

    lax.fori_loop(0, peers, body, jnp.zeros(out_ref.shape[1:], jnp.float32))


def swap_cores(value):
    return lax.ppermute(value, "core", [(0, 1), (1, 0)])


def exchange(value, axis):
    count = lax.axis_size(axis)
    me = lax.axis_index(axis)
    got = [lax.dynamic_index_in_dim(value, me, 0, keepdims=False)]
    for by in range(1, count):
        piece = lax.dynamic_index_in_dim(value, (me + by) % count, 0, keepdims=False)
        pairs = [(i, (i + by) % count) for i in range(count)]
        got.append(lax.ppermute(piece, axis, pairs))
    stacked = jnp.stack(got)
    return jnp.take(stacked, (me - jnp.arange(count)) % count, axis=0)


def tie(value, *after):
    def kernel(*refs):
        del refs

    return pl.pallas_call(
        kernel,
        in_specs=[pl.BlockSpec(memory_space=pl.ANY) for _ in range(1 + len(after))],
        out_specs=pl.BlockSpec(memory_space=pl.ANY),
        out_shape=jax.ShapeDtypeStruct(value.shape, value.dtype),
        input_output_aliases={0: 0},
    )(value, *after)


def compose(both, first_work, second_work):
    core = lax.axis_index("core")
    chips = lax.axis_size("chip")
    half = GROUP_COLS
    width = half // chips
    mine = lax.dynamic_index_in_dim(both, core, 0, keepdims=False)
    theirs = swap_cores(lax.dynamic_index_in_dim(both, 1 - core, 0, keepdims=False))
    first = jnp.where(core == 0, mine, theirs)
    second = jnp.where(core == 0, theirs, mine)
    first_decay = first[STATE:]
    chip_state = second[STATE:] * first[:STATE] + second[:STATE]
    chip_decay = first_decay * second[STATE:]
    decay_hi = chip_decay.astype(jnp.bfloat16)
    decay_lo = (chip_decay - decay_hi.astype(jnp.float32)).astype(jnp.bfloat16)
    payload = jnp.concatenate(
        [chip_state.astype(jnp.bfloat16), decay_hi, decay_lo], axis=0
    ).reshape(STATE + 2, chips, width).transpose(1, 0, 2)
    work = first_work()
    got = tie(exchange(payload, "chip"), work)
    entering = pl.pallas_call(
        scan_kernel,
        out_shape=jax.ShapeDtypeStruct((chips, STATE, width), jnp.bfloat16),
    )(got)
    work = second_work(work)
    back = tie(exchange(entering, "chip"), work)
    chip_in = back.transpose(1, 0, 2).reshape(STATE, half).astype(jnp.float32)
    later_in = first_decay * chip_in + first[:STATE]
    keep = jnp.where(core == 0, chip_in, later_in).astype(jnp.bfloat16)
    other = swap_cores(jnp.where(core == 0, later_in, chip_in).astype(jnp.bfloat16))
    hin = jnp.where(
        core == 0,
        jnp.concatenate([keep, other], axis=1),
        jnp.concatenate([other, keep], axis=1),
    )
    return hin, work


def local(xbc, z_gate, dt_raw, lengths, conv_weight, conv_bias, dt_bias, a_log, d_skip, norm_gain):
    tok = xbc.shape[0]
    nb = tok // STRETCH
    first_pos = (lax.axis_index("chip") * lax.axis_size("core") + lax.axis_index("core")) * tok
    rim_rows = shifted(xbc[tok - (CONV - 1) :], ("chip", "core"), 1)
    rim8 = jnp.concatenate([jnp.zeros((8 - (CONV - 1), CHANNELS), xbc.dtype), rim_rows], axis=0)
    ext_pos = first_pos - (CONV - 1) + jnp.arange(tok + CONV - 1)
    ext_seg = segment_of(ext_pos, lengths)
    target = ext_seg[CONV - 1 :]
    kept = [
        (ext_pos[tap : tap + tok] >= 0) & (ext_seg[tap : tap + tok] == target) for tap in range(CONV)
    ]
    masks = jnp.stack(kept, axis=1).astype(jnp.float32)
    masks = jnp.concatenate([masks, jnp.zeros((tok, 128 - CONV), jnp.float32)], axis=1)
    w8 = jnp.concatenate([conv_weight, jnp.zeros((8 - CONV, CHANNELS), jnp.float32)], axis=0)
    conv = conv_part(xbc, rim8, w8, conv_bias[None, :], masks)
    step = jax.nn.softplus(dt_raw.astype(jnp.float32) + dt_bias[None, :])
    log_decay = -step * jnp.exp(a_log)[None, :]
    cum = jnp.cumsum(log_decay.reshape(nb, STRETCH, HEADS), axis=1).reshape(tok, HEADS)
    segments = segment_of(first_pos + jnp.arange(tok), lengths)
    seg_before = segment_of(first_pos + jnp.arange(nb) * STRETCH - 1, lengths)
    seg_last = segments.reshape(nb, STRETCH)[:, -1]
    cum_last = cum.reshape(nb, STRETCH, HEADS)[:, -1, :]
    block_decay = jnp.where((seg_last == seg_before)[:, None], jnp.exp(cum_last), 0.0)

    cum_g = cum.reshape(tok, GROUPS, PER_GROUP).transpose(1, 0, 2)
    dt_g = step.reshape(tok, GROUPS, PER_GROUP).transpose(1, 0, 2)
    cumt_g = cum.T.reshape(GROUPS, PER_GROUP, tok)
    segc = jnp.broadcast_to(segments[:, None], (tok, 128)).astype(jnp.int32)
    segr = jnp.broadcast_to(segments[None, :], (8, tok)).astype(jnp.int32)
    eb = jnp.broadcast_to(seg_before[:, None, None], (nb, 8, 128)).reshape(nb * 8, 128)
    eb = eb.astype(jnp.int32)
    bt = conv[:, INNER : INNER + GROUPS * STATE].T
    bdec = jnp.repeat(block_decay, HEAD_DIM, axis=1)[:, None, :]

    local_states, cdec, both = block_states(bt, conv, dt_g, cum_g, segc, bdec)
    dsk = jnp.repeat(d_skip, HEAD_DIM)[None, :]
    def first_work():
        return intra_part(conv, dt_g, cum_g, cumt_g, segc, segr, dsk, 0)

    def second_work(done):
        return intra_part(conv, dt_g, cum_g, cumt_g, segc, segr, dsk, 1, done)

    back, y_local = compose(both, first_work, second_work)
    gain = norm_gain[None, :]
    return mix(conv, y_local, z_gate, back, local_states, cdec, cum_g, segc, eb, gain)


def solution(mesh):
    groups, peers = mesh.devices.shape
    split = Mesh(mesh.devices.reshape(groups, peers // 2, 2), ("group", "chip", "core"))
    rows = P(("group", "chip", "core"), None)
    return jax.shard_map(
        local,
        mesh=split,
        in_specs=(rows, rows, rows, P("group"), P(), P(), P(), P(), P(), P()),
        out_specs=rows,
        check_vma=False,
    )
```

```python
import jax
import jax.numpy as jnp
from jax import lax
from jax.experimental import pallas as pl
from jax.experimental.pallas import tpu as pltpu
from jax.sharding import PartitionSpec as P

HEADS = 64
HEAD_DIM = 64
STATE = 256
GROUPS = 2
CONV = 4
STRETCH = 256
CHANNELS = 5120
INNER = HEADS * HEAD_DIM
PER_GROUP = HEADS // GROUPS
GROUP_COLS = INNER // GROUPS


def shifted(value, axis, by):
    peers = lax.axis_size(axis)
    pairs = [(i, i + by) for i in range(peers) if 0 <= i + by < peers]
    return lax.ppermute(value, axis, pairs)


def segment_of(positions, lengths):
    prompt_ends = jnp.cumsum(lengths)
    hits = (prompt_ends[None, :] <= positions[:, None]).astype(jnp.int32)
    return jnp.sum(hits, axis=1)


def expand_heads(v):
    heads = lax.broadcasted_iota(jnp.int32, (PER_GROUP, GROUP_COLS), 0)
    cols = lax.broadcasted_iota(jnp.int32, (PER_GROUP, GROUP_COLS), 1)
    spread = (cols // HEAD_DIM == heads).astype(jnp.bfloat16)
    hi = v.astype(jnp.bfloat16)
    rest = v - hi.astype(jnp.float32)
    mid = rest.astype(jnp.bfloat16)
    lo = (rest - mid.astype(jnp.float32)).astype(jnp.bfloat16)
    out = jnp.dot(hi, spread, preferred_element_type=jnp.float32)
    out = out + jnp.dot(mid, spread, preferred_element_type=jnp.float32)
    return out + jnp.dot(lo, spread, preferred_element_type=jnp.float32)


CONV_COLS = 640


def conv_kernel(x_ref, rim_ref, w_ref, bias_ref, m_ref, out_ref):
    x = x_ref[...].astype(jnp.float32)
    rim = rim_ref[...].astype(jnp.float32)
    rows8 = lax.broadcasted_iota(jnp.int32, rim.shape, 0)
    summed = jnp.zeros(x.shape, jnp.float32)
    top = jnp.zeros(rim.shape, jnp.float32)
    for tap in range(CONV):
        by = CONV - 1 - tap
        wk = w_ref[tap : tap + 1, :]
        kept = m_ref[:, tap : tap + 1] > 0.0
        if by == 0:
            term = x
            top_term = x[0:8]
        else:
            term = pltpu.roll(x, by, 0)
            top_term = jnp.where(rows8 < by, pltpu.roll(rim, by, 0), term[0:8])
        summed = summed + jnp.where(kept, term * wk, 0.0)
        top = top + jnp.where(kept[0:8], top_term * wk, 0.0)
    out_ref[...] = jax.nn.silu(summed + bias_ref[...]).astype(jnp.bfloat16)
    out_ref[0:8, :] = jax.nn.silu(top + bias_ref[...]).astype(jnp.bfloat16)


def conv_part(xbc, rim8, w8, bias, masks):
    tok, chans = xbc.shape
    return pl.pallas_call(
        conv_kernel,
        grid=(chans // CONV_COLS,),
        in_specs=[
            pl.BlockSpec((tok, CONV_COLS), lambda c: (0, c)),
            pl.BlockSpec((8, CONV_COLS), lambda c: (0, c)),
            pl.BlockSpec((8, CONV_COLS), lambda c: (0, c)),
            pl.BlockSpec((1, CONV_COLS), lambda c: (0, c)),
            pl.BlockSpec((tok, 128), lambda c: (0, 0)),
        ],
        out_specs=pl.BlockSpec((tok, CONV_COLS), lambda c: (0, c)),
        out_shape=jax.ShapeDtypeStruct((tok, chans), jnp.bfloat16),
    )(xbc, rim8, w8, bias, masks)


def state_kernel(
    bt_ref, x_ref, dt_ref, cum_ref, segc_ref, bdec_ref, local_ref, cdec_ref, pay_ref, drow_ref,
    acc_ref, dec_ref,
):
    b = pl.program_id(1)

    @pl.when(b == 0)
    def _():
        acc_ref[...] = jnp.zeros(acc_ref.shape, jnp.float32)
        dec_ref[...] = jnp.ones(dec_ref.shape, jnp.float32)

    @pl.when(b > 0)
    def _():
        local_ref[0] = acc_ref[...]
        cdec_ref[0] = dec_ref[...]

    cum = cum_ref[0]
    step = dt_ref[0]
    segc = segc_ref[:, 0:1]
    last = cum[STRETCH - 1 : STRETCH, :]
    seg_last = segc[STRETCH - 1 : STRETCH, :]
    w = jnp.where(segc == seg_last, jnp.exp(last - cum), 0.0)
    scaled = (x_ref[...].astype(jnp.float32) * expand_heads(step)).astype(jnp.bfloat16)
    weighted = (scaled.astype(jnp.float32) * expand_heads(w)).astype(jnp.bfloat16)
    block_state = jnp.dot(bt_ref[...], weighted, preferred_element_type=jnp.float32)
    decay = bdec_ref[0]
    acc_ref[...] = decay * acc_ref[...] + block_state
    dec_ref[...] = dec_ref[...] * decay

    @pl.when(b == pl.num_programs(1) - 1)
    def _():
        pieces, _, width = pay_ref.shape
        total = acc_ref[...]
        dec = dec_ref[...]
        hi = dec.astype(jnp.bfloat16)
        lo = (dec - hi.astype(jnp.float32)).astype(jnp.bfloat16)
        for k in range(pieces):
            cols = slice(k * width, (k + 1) * width)
            pay_ref[k] = total[:, cols].astype(jnp.bfloat16)
            drow_ref[k, 0:1, :] = hi[:, cols]
            drow_ref[k, 1:2, :] = lo[:, cols]


def block_states(bt, conv, dt_g, cum_g, segc, bdec, peers):
    tok = conv.shape[0]
    nb = tok // STRETCH
    width = INNER // peers
    per = peers // GROUPS
    return pl.pallas_call(
        state_kernel,
        grid=(GROUPS, nb),
        in_specs=[
            pl.BlockSpec((STATE, STRETCH), lambda g, b: (g, b)),
            pl.BlockSpec((STRETCH, GROUP_COLS), lambda g, b: (b, g)),
            pl.BlockSpec((1, STRETCH, PER_GROUP), lambda g, b: (g, b, 0)),
            pl.BlockSpec((1, STRETCH, PER_GROUP), lambda g, b: (g, b, 0)),
            pl.BlockSpec((STRETCH, 128), lambda g, b: (b, 0)),
            pl.BlockSpec((1, 1, GROUP_COLS), lambda g, b: (b, 0, g)),
        ],
        out_specs=[
            pl.BlockSpec((1, STATE, GROUP_COLS), lambda g, b: (jnp.maximum(b - 1, 0), 0, g)),
            pl.BlockSpec((1, 1, GROUP_COLS), lambda g, b: (jnp.maximum(b - 1, 0), 0, g)),
            pl.BlockSpec((per, STATE, width), lambda g, b: (g, 0, 0)),
            pl.BlockSpec((per, 2, width), lambda g, b: (g, 0, 0)),
        ],
        out_shape=[
            jax.ShapeDtypeStruct((max(nb - 1, 1), STATE, INNER), jnp.float32),
            jax.ShapeDtypeStruct((max(nb - 1, 1), 1, INNER), jnp.float32),
            jax.ShapeDtypeStruct((peers, STATE, width), jnp.bfloat16),
            jax.ShapeDtypeStruct((peers, 2, width), jnp.bfloat16),
        ],
        scratch_shapes=[
            pltpu.VMEM((STATE, GROUP_COLS), jnp.float32),
            pltpu.VMEM((1, GROUP_COLS), jnp.float32),
        ],
    )(bt, conv, dt_g, cum_g, segc, bdec)


def intra_kernel(
    c_ref, b_ref, x_ref, dt_ref, cum_ref, cumt_ref, segc_ref, segr_ref, dsk_ref, out_ref
):
    gram = lax.dot_general(
        c_ref[...], b_ref[...], (((1,), (1,)), ((), ())), preferred_element_type=jnp.float32
    )
    segc = segc_ref[:, 0:1]
    segr = segr_ref[0:1, :]
    rows = lax.broadcasted_iota(jnp.int32, (STRETCH, STRETCH), 0)
    cols = lax.broadcasted_iota(jnp.int32, (STRETCH, STRETCH), 1)
    gram = jnp.where((segc == segr) & (cols <= rows), gram, 0.0)
    cum = cum_ref[0]
    cumt = cumt_ref[0]
    step = dt_ref[0]
    for j in range(PER_GROUP):
        hc = slice(j * HEAD_DIM, (j + 1) * HEAD_DIM)
        gap = jnp.minimum(cum[:, j : j + 1] - cumt[j : j + 1, :], 0.0)
        weights = (gram * jnp.exp(gap)).astype(jnp.bfloat16)
        xf = x_ref[:, hc].astype(jnp.float32)
        scaled = (xf * step[:, j : j + 1]).astype(jnp.bfloat16)
        intra = jnp.dot(weights, scaled, preferred_element_type=jnp.float32)
        out_ref[:, hc] = intra + dsk_ref[:, hc] * xf


def intra_part(conv, dt_g, cum_g, cumt_g, segc, segr, dsk, g, into=None):
    tok = conv.shape[0]
    nb = tok // STRETCH
    b_col = INNER // STATE
    c_col = b_col + GROUPS
    operands = [conv, conv, conv, dt_g, cum_g, cumt_g, segc, segr, dsk]
    specs = [
        pl.BlockSpec((STRETCH, STATE), lambda b: (b, c_col + g)),
        pl.BlockSpec((STRETCH, STATE), lambda b: (b, b_col + g)),
        pl.BlockSpec((STRETCH, GROUP_COLS), lambda b: (b, g)),
        pl.BlockSpec((1, STRETCH, PER_GROUP), lambda b: (g, b, 0)),
        pl.BlockSpec((1, STRETCH, PER_GROUP), lambda b: (g, b, 0)),
        pl.BlockSpec((1, PER_GROUP, STRETCH), lambda b: (g, 0, b)),
        pl.BlockSpec((STRETCH, 128), lambda b: (b, 0)),
        pl.BlockSpec((8, STRETCH), lambda b: (0, b)),
        pl.BlockSpec((1, GROUP_COLS), lambda b: (0, g)),
    ]
    kernel = intra_kernel
    aliases = {}
    if into is not None:
        operands.append(into)
        specs.append(pl.BlockSpec(memory_space=pl.ANY))
        aliases = {len(operands) - 1: 0}

        def kernel(*refs):
            intra_kernel(*refs[:-2], refs[-1])

    return pl.pallas_call(
        kernel,
        grid=(nb,),
        in_specs=specs,
        out_specs=pl.BlockSpec((STRETCH, GROUP_COLS), lambda b: (b, g)),
        out_shape=jax.ShapeDtypeStruct((tok, INNER), jnp.float32),
        input_output_aliases=aliases,
    )(*operands)


def mix_kernel(
    c_ref, y_ref, z_ref, back_ref, local_ref, cdec_ref, cum_ref, segc_ref, eb_ref, gain_ref,
    out_ref, hin_ref, state_ref,
):
    b = pl.program_id(1)
    pieces, _, width = back_ref.shape

    @pl.when(b == 0)
    def _():
        for k in range(pieces):
            hin_ref[:, k * width : (k + 1) * width] = back_ref[k].astype(jnp.float32)
        state_ref[...] = hin_ref[...].astype(jnp.bfloat16)

    @pl.when(b > 0)
    def _():
        state_ref[...] = (cdec_ref[0] * hin_ref[...] + local_ref[0]).astype(jnp.bfloat16)

    segc = segc_ref[:, 0:1]
    entry = eb_ref[0:1, 0:1]
    in_weight = jnp.where(segc == entry, jnp.exp(cum_ref[0]), 0.0)
    inter = jnp.dot(c_ref[...], state_ref[...], preferred_element_type=jnp.float32)
    y = y_ref[...] + inter * expand_heads(in_weight)
    zf = z_ref[...].astype(jnp.float32)
    gated = y * (zf * jax.nn.sigmoid(zf))
    mean_square = jnp.mean(gated * gated, axis=1, keepdims=True) + 1e-05
    out_ref[...] = (gated * lax.rsqrt(mean_square) * gain_ref[...]).astype(jnp.bfloat16)


def mix(conv, y_local, z_gate, back, local_states, cdec, cum_g, segc, eb, gain):
    tok = conv.shape[0]
    nb = tok // STRETCH
    c_col = INNER // STATE + GROUPS
    peers, _, width = back.shape
    per = peers // GROUPS
    return pl.pallas_call(
        mix_kernel,
        grid=(GROUPS, nb),
        in_specs=[
            pl.BlockSpec((STRETCH, STATE), lambda g, b: (b, c_col + g)),
            pl.BlockSpec((STRETCH, GROUP_COLS), lambda g, b: (b, g)),
            pl.BlockSpec((STRETCH, GROUP_COLS), lambda g, b: (b, g)),
            pl.BlockSpec((per, STATE, width), lambda g, b: (g, 0, 0)),
            pl.BlockSpec((1, STATE, GROUP_COLS), lambda g, b: (jnp.maximum(b - 1, 0), 0, g)),
            pl.BlockSpec((1, 1, GROUP_COLS), lambda g, b: (jnp.maximum(b - 1, 0), 0, g)),
            pl.BlockSpec((1, STRETCH, PER_GROUP), lambda g, b: (g, b, 0)),
            pl.BlockSpec((STRETCH, 128), lambda g, b: (b, 0)),
            pl.BlockSpec((8, 128), lambda g, b: (b, 0)),
            pl.BlockSpec((1, GROUP_COLS), lambda g, b: (0, g)),
        ],
        out_specs=pl.BlockSpec((STRETCH, GROUP_COLS), lambda g, b: (b, g)),
        out_shape=jax.ShapeDtypeStruct((tok, INNER), jnp.bfloat16),
        scratch_shapes=[
            pltpu.VMEM((STATE, GROUP_COLS), jnp.float32),
            pltpu.VMEM((STATE, GROUP_COLS), jnp.bfloat16),
        ],
    )(conv, y_local, z_gate, back, local_states, cdec, cum_g, segc, eb, gain)


def scan_kernel(got_ref, out_ref):
    peers = got_ref.shape[0]

    def body(d, carry):
        out_ref[d] = carry.astype(jnp.bfloat16)
        decay = got_ref[d, STATE : STATE + 1, :].astype(jnp.float32) + got_ref[
            d, STATE + 1 : STATE + 2, :
        ].astype(jnp.float32)
        return decay * carry + got_ref[d, 0:STATE, :].astype(jnp.float32)

    lax.fori_loop(0, peers, body, jnp.zeros(out_ref.shape[1:], jnp.float32))


def tie(value, *after):
    def kernel(*refs):
        del refs

    return pl.pallas_call(
        kernel,
        in_specs=[pl.BlockSpec(memory_space=pl.ANY) for _ in range(1 + len(after))],
        out_specs=pl.BlockSpec(memory_space=pl.ANY),
        out_shape=jax.ShapeDtypeStruct(value.shape, value.dtype),
        input_output_aliases={0: 0},
    )(value, *after)


def compose(pieces, rows, first_work, second_work):
    peers, _, width = pieces.shape
    payload = jnp.concatenate([pieces, rows], axis=1)
    work = first_work()
    got = tie(lax.all_to_all(payload, "ctx", split_axis=0, concat_axis=0, tiled=True), work)
    entering = pl.pallas_call(
        scan_kernel,
        out_shape=jax.ShapeDtypeStruct((peers, STATE, width), jnp.bfloat16),
    )(got)
    work = second_work(work)
    back = lax.all_to_all(entering, "ctx", split_axis=0, concat_axis=0, tiled=True)
    return tie(back, work), work


def local(xbc, z_gate, dt_raw, lengths, conv_weight, conv_bias, dt_bias, a_log, d_skip, norm_gain):
    tok = xbc.shape[0]
    nb = tok // STRETCH
    peers = lax.axis_size("ctx")
    first_pos = lax.axis_index("ctx") * tok
    rim_rows = shifted(xbc[tok - (CONV - 1) :], "ctx", 1)
    rim8 = jnp.concatenate([jnp.zeros((8 - (CONV - 1), CHANNELS), xbc.dtype), rim_rows], axis=0)
    ext_pos = first_pos - (CONV - 1) + jnp.arange(tok + CONV - 1)
    ext_seg = segment_of(ext_pos, lengths)
    target = ext_seg[CONV - 1 :]
    kept = [
        (ext_pos[tap : tap + tok] >= 0) & (ext_seg[tap : tap + tok] == target) for tap in range(CONV)
    ]
    masks = jnp.stack(kept, axis=1).astype(jnp.float32)
    masks = jnp.concatenate([masks, jnp.zeros((tok, 128 - CONV), jnp.float32)], axis=1)
    w8 = jnp.concatenate([conv_weight, jnp.zeros((8 - CONV, CHANNELS), jnp.float32)], axis=0)
    conv = conv_part(xbc, rim8, w8, conv_bias[None, :], masks)
    step = jax.nn.softplus(dt_raw.astype(jnp.float32) + dt_bias[None, :])
    log_decay = -step * jnp.exp(a_log)[None, :]
    cum = jnp.cumsum(log_decay.reshape(nb, STRETCH, HEADS), axis=1).reshape(tok, HEADS)
    segments = segment_of(first_pos + jnp.arange(tok), lengths)
    seg_before = segment_of(first_pos + jnp.arange(nb) * STRETCH - 1, lengths)
    seg_last = segments.reshape(nb, STRETCH)[:, -1]
    cum_last = cum.reshape(nb, STRETCH, HEADS)[:, -1, :]
    block_decay = jnp.where((seg_last == seg_before)[:, None], jnp.exp(cum_last), 0.0)

    cum_g = cum.reshape(tok, GROUPS, PER_GROUP).transpose(1, 0, 2)
    dt_g = step.reshape(tok, GROUPS, PER_GROUP).transpose(1, 0, 2)
    cumt_g = cum.T.reshape(GROUPS, PER_GROUP, tok)
    segc = jnp.broadcast_to(segments[:, None], (tok, 128)).astype(jnp.int32)
    segr = jnp.broadcast_to(segments[None, :], (8, tok)).astype(jnp.int32)
    eb = jnp.broadcast_to(seg_before[:, None, None], (nb, 8, 128)).reshape(nb * 8, 128)
    eb = eb.astype(jnp.int32)
    bt = conv[:, INNER : INNER + GROUPS * STATE].T
    bdec = jnp.repeat(block_decay, HEAD_DIM, axis=1)[:, None, :]

    local_states, cdec, pieces, rows = block_states(bt, conv, dt_g, cum_g, segc, bdec, peers)
    dsk = jnp.repeat(d_skip, HEAD_DIM)[None, :]
    def first_work():
        return intra_part(conv, dt_g, cum_g, cumt_g, segc, segr, dsk, 0)

    def second_work(done):
        return intra_part(conv, dt_g, cum_g, cumt_g, segc, segr, dsk, 1, done)

    back, y_local = compose(pieces, rows, first_work, second_work)
    gain = norm_gain[None, :]
    return mix(conv, y_local, z_gate, back, local_states, cdec, cum_g, segc, eb, gain)


def solution(mesh):
    return jax.shard_map(
        local,
        mesh=mesh,
        in_specs=(
            P(("group", "ctx"), None),
            P(("group", "ctx"), None),
            P(("group", "ctx"), None),
            P("group"),
            P(),
            P(),
            P(),
            P(),
            P(),
            P(),
        ),
        out_specs=P(("group", "ctx"), None),
        check_vma=False,
    )
```

```python
import jax
import jax.numpy as jnp
from jax import lax
from jax.experimental import pallas as pl
from jax.experimental.pallas import tpu as pltpu
from jax.sharding import Mesh, PartitionSpec as P

HEADS = 64
HEAD_DIM = 64
STATE = 256
GROUPS = 2
CONV = 4
STRETCH = 256
CHANNELS = 5120
INNER = HEADS * HEAD_DIM
PER_GROUP = HEADS // GROUPS
GROUP_COLS = INNER // GROUPS


def shifted(value, axis, by):
    peers = lax.axis_size(axis)
    pairs = [(i, i + by) for i in range(peers) if 0 <= i + by < peers]
    return lax.ppermute(value, axis, pairs)


def segment_of(positions, lengths):
    prompt_ends = jnp.cumsum(lengths)
    hits = (prompt_ends[None, :] <= positions[:, None]).astype(jnp.int32)
    return jnp.sum(hits, axis=1)


def expand_heads(v):
    heads = lax.broadcasted_iota(jnp.int32, (PER_GROUP, GROUP_COLS), 0)
    cols = lax.broadcasted_iota(jnp.int32, (PER_GROUP, GROUP_COLS), 1)
    spread = (cols // HEAD_DIM == heads).astype(jnp.bfloat16)
    hi = v.astype(jnp.bfloat16)
    rest = v - hi.astype(jnp.float32)
    mid = rest.astype(jnp.bfloat16)
    lo = (rest - mid.astype(jnp.float32)).astype(jnp.bfloat16)
    out = jnp.dot(hi, spread, preferred_element_type=jnp.float32)
    out = out + jnp.dot(mid, spread, preferred_element_type=jnp.float32)
    return out + jnp.dot(lo, spread, preferred_element_type=jnp.float32)


CONV_COLS = 640


def conv_kernel(x_ref, rim_ref, w_ref, bias_ref, m_ref, out_ref):
    x = x_ref[...].astype(jnp.float32)
    rim = rim_ref[...].astype(jnp.float32)
    rows8 = lax.broadcasted_iota(jnp.int32, rim.shape, 0)
    summed = jnp.zeros(x.shape, jnp.float32)
    top = jnp.zeros(rim.shape, jnp.float32)
    for tap in range(CONV):
        by = CONV - 1 - tap
        wk = w_ref[tap : tap + 1, :]
        kept = m_ref[:, tap : tap + 1] > 0.0
        if by == 0:
            term = x
            top_term = x[0:8]
        else:
            term = pltpu.roll(x, by, 0)
            top_term = jnp.where(rows8 < by, pltpu.roll(rim, by, 0), term[0:8])
        summed = summed + jnp.where(kept, term * wk, 0.0)
        top = top + jnp.where(kept[0:8], top_term * wk, 0.0)
    out_ref[...] = jax.nn.silu(summed + bias_ref[...]).astype(jnp.bfloat16)
    out_ref[0:8, :] = jax.nn.silu(top + bias_ref[...]).astype(jnp.bfloat16)


def conv_part(xbc, rim8, w8, bias, masks):
    tok, chans = xbc.shape
    return pl.pallas_call(
        conv_kernel,
        grid=(chans // CONV_COLS,),
        in_specs=[
            pl.BlockSpec((tok, CONV_COLS), lambda c: (0, c)),
            pl.BlockSpec((8, CONV_COLS), lambda c: (0, c)),
            pl.BlockSpec((8, CONV_COLS), lambda c: (0, c)),
            pl.BlockSpec((1, CONV_COLS), lambda c: (0, c)),
            pl.BlockSpec((tok, 128), lambda c: (0, 0)),
        ],
        out_specs=pl.BlockSpec((tok, CONV_COLS), lambda c: (0, c)),
        out_shape=jax.ShapeDtypeStruct((tok, chans), jnp.bfloat16),
    )(xbc, rim8, w8, bias, masks)


def state_kernel(
    bt_ref, x_ref, dt_ref, cum_ref, segc_ref, bdec_ref, local_ref, cdec_ref, tot_ref,
    acc_ref, dec_ref,
):
    b = pl.program_id(1)

    @pl.when(b == 0)
    def _():
        acc_ref[...] = jnp.zeros(acc_ref.shape, jnp.float32)
        dec_ref[...] = jnp.ones(dec_ref.shape, jnp.float32)

    local_ref[0] = acc_ref[...]
    cdec_ref[0] = dec_ref[...]
    cum = cum_ref[0]
    step = dt_ref[0]
    segc = segc_ref[:, 0:1]
    last = cum[STRETCH - 1 : STRETCH, :]
    seg_last = segc[STRETCH - 1 : STRETCH, :]
    w = jnp.where(segc == seg_last, jnp.exp(last - cum), 0.0)
    scaled = (x_ref[...].astype(jnp.float32) * expand_heads(step)).astype(jnp.bfloat16)
    weighted = (scaled.astype(jnp.float32) * expand_heads(w)).astype(jnp.bfloat16)
    block_state = jnp.dot(bt_ref[...], weighted, preferred_element_type=jnp.float32)
    decay = bdec_ref[0]
    acc_ref[...] = decay * acc_ref[...] + block_state
    dec_ref[...] = dec_ref[...] * decay

    @pl.when(b == pl.num_programs(1) - 1)
    def _():
        tot_ref[0, 0:STATE, :] = acc_ref[...]
        tot_ref[0, STATE : STATE + 1, :] = dec_ref[...]


def block_states(bt, conv, dt_g, cum_g, segc, bdec):
    tok = conv.shape[0]
    nb = tok // STRETCH
    return pl.pallas_call(
        state_kernel,
        grid=(GROUPS, nb),
        in_specs=[
            pl.BlockSpec((STATE, STRETCH), lambda g, b: (g, b)),
            pl.BlockSpec((STRETCH, GROUP_COLS), lambda g, b: (b, g)),
            pl.BlockSpec((1, STRETCH, PER_GROUP), lambda g, b: (g, b, 0)),
            pl.BlockSpec((1, STRETCH, PER_GROUP), lambda g, b: (g, b, 0)),
            pl.BlockSpec((STRETCH, 128), lambda g, b: (b, 0)),
            pl.BlockSpec((1, 1, GROUP_COLS), lambda g, b: (b, 0, g)),
        ],
        out_specs=[
            pl.BlockSpec((1, STATE, GROUP_COLS), lambda g, b: (b, 0, g)),
            pl.BlockSpec((1, 1, GROUP_COLS), lambda g, b: (b, 0, g)),
            pl.BlockSpec((1, STATE + 1, GROUP_COLS), lambda g, b: (g, 0, 0)),
        ],
        out_shape=[
            jax.ShapeDtypeStruct((nb, STATE, INNER), jnp.float32),
            jax.ShapeDtypeStruct((nb, 1, INNER), jnp.float32),
            jax.ShapeDtypeStruct((GROUPS, STATE + 1, GROUP_COLS), jnp.float32),
        ],
        scratch_shapes=[
            pltpu.VMEM((STATE, GROUP_COLS), jnp.float32),
            pltpu.VMEM((1, GROUP_COLS), jnp.float32),
        ],
    )(bt, conv, dt_g, cum_g, segc, bdec)


def intra_kernel(
    c_ref, b_ref, x_ref, dt_ref, cum_ref, cumt_ref, segc_ref, segr_ref, dsk_ref, out_ref
):
    gram = lax.dot_general(
        c_ref[...], b_ref[...], (((1,), (1,)), ((), ())), preferred_element_type=jnp.float32
    )
    segc = segc_ref[:, 0:1]
    segr = segr_ref[0:1, :]
    rows = lax.broadcasted_iota(jnp.int32, (STRETCH, STRETCH), 0)
    cols = lax.broadcasted_iota(jnp.int32, (STRETCH, STRETCH), 1)
    gram = jnp.where((segc == segr) & (cols <= rows), gram, 0.0)
    cum = cum_ref[0]
    cumt = cumt_ref[0]
    step = dt_ref[0]
    for j in range(PER_GROUP):
        hc = slice(j * HEAD_DIM, (j + 1) * HEAD_DIM)
        gap = jnp.minimum(cum[:, j : j + 1] - cumt[j : j + 1, :], 0.0)
        weights = (gram * jnp.exp(gap)).astype(jnp.bfloat16)
        xf = x_ref[:, hc].astype(jnp.float32)
        scaled = (xf * step[:, j : j + 1]).astype(jnp.bfloat16)
        intra = jnp.dot(weights, scaled, preferred_element_type=jnp.float32)
        out_ref[:, hc] = intra + dsk_ref[:, hc] * xf


def intra_part(conv, dt_g, cum_g, cumt_g, segc, segr, dsk, g, into=None):
    tok = conv.shape[0]
    nb = tok // STRETCH
    b_col = INNER // STATE
    c_col = b_col + GROUPS
    operands = [conv, conv, conv, dt_g, cum_g, cumt_g, segc, segr, dsk]
    specs = [
        pl.BlockSpec((STRETCH, STATE), lambda b: (b, c_col + g)),
        pl.BlockSpec((STRETCH, STATE), lambda b: (b, b_col + g)),
        pl.BlockSpec((STRETCH, GROUP_COLS), lambda b: (b, g)),
        pl.BlockSpec((1, STRETCH, PER_GROUP), lambda b: (g, b, 0)),
        pl.BlockSpec((1, STRETCH, PER_GROUP), lambda b: (g, b, 0)),
        pl.BlockSpec((1, PER_GROUP, STRETCH), lambda b: (g, 0, b)),
        pl.BlockSpec((STRETCH, 128), lambda b: (b, 0)),
        pl.BlockSpec((8, STRETCH), lambda b: (0, b)),
        pl.BlockSpec((1, GROUP_COLS), lambda b: (0, g)),
    ]
    kernel = intra_kernel
    aliases = {}
    if into is not None:
        operands.append(into)
        specs.append(pl.BlockSpec(memory_space=pl.ANY))
        aliases = {len(operands) - 1: 0}

        def kernel(*refs):
            intra_kernel(*refs[:-2], refs[-1])

    return pl.pallas_call(
        kernel,
        grid=(nb,),
        in_specs=specs,
        out_specs=pl.BlockSpec((STRETCH, GROUP_COLS), lambda b: (b, g)),
        out_shape=jax.ShapeDtypeStruct((tok, INNER), jnp.float32),
        input_output_aliases=aliases,
    )(*operands)


def mix_kernel(
    c_ref, y_ref, z_ref, hin_ref, local_ref, cdec_ref, cum_ref, segc_ref, eb_ref, gain_ref,
    out_ref,
):
    state = cdec_ref[0] * hin_ref[...].astype(jnp.float32) + local_ref[0]
    segc = segc_ref[:, 0:1]
    entry = eb_ref[0:1, 0:1]
    in_weight = jnp.where(segc == entry, jnp.exp(cum_ref[0]), 0.0)
    inter = jnp.dot(c_ref[...], state.astype(jnp.bfloat16), preferred_element_type=jnp.float32)
    y = y_ref[...] + inter * expand_heads(in_weight)
    zf = z_ref[...].astype(jnp.float32)
    gated = y * (zf * jax.nn.sigmoid(zf))
    mean_square = jnp.mean(gated * gated, axis=1, keepdims=True) + 1e-05
    out_ref[...] = (gated * lax.rsqrt(mean_square) * gain_ref[...]).astype(jnp.bfloat16)


def mix(conv, y_local, z_gate, back, local_states, cdec, cum_g, segc, eb, gain):
    tok = conv.shape[0]
    nb = tok // STRETCH
    c_col = INNER // STATE + GROUPS
    return pl.pallas_call(
        mix_kernel,
        grid=(nb, GROUPS),
        in_specs=[
            pl.BlockSpec((STRETCH, STATE), lambda b, g: (b, c_col + g)),
            pl.BlockSpec((STRETCH, GROUP_COLS), lambda b, g: (b, g)),
            pl.BlockSpec((STRETCH, GROUP_COLS), lambda b, g: (b, g)),
            pl.BlockSpec((STATE, GROUP_COLS), lambda b, g: (0, g)),
            pl.BlockSpec((1, STATE, GROUP_COLS), lambda b, g: (b, 0, g)),
            pl.BlockSpec((1, 1, GROUP_COLS), lambda b, g: (b, 0, g)),
            pl.BlockSpec((1, STRETCH, PER_GROUP), lambda b, g: (g, b, 0)),
            pl.BlockSpec((STRETCH, 128), lambda b, g: (b, 0)),
            pl.BlockSpec((8, 128), lambda b, g: (b, 0)),
            pl.BlockSpec((1, GROUP_COLS), lambda b, g: (0, g)),
        ],
        out_specs=pl.BlockSpec((STRETCH, GROUP_COLS), lambda b, g: (b, g)),
        out_shape=jax.ShapeDtypeStruct((tok, INNER), jnp.bfloat16),
    )(conv, y_local, z_gate, back, local_states, cdec, cum_g, segc, eb, gain)


def scan_kernel(got_ref, out_ref):
    peers = got_ref.shape[0]

    def body(d, carry):
        out_ref[d] = carry.astype(jnp.bfloat16)
        decay = got_ref[d, STATE : STATE + 1, :].astype(jnp.float32) + got_ref[
            d, STATE + 1 : STATE + 2, :
        ].astype(jnp.float32)
        return decay * carry + got_ref[d, 0:STATE, :].astype(jnp.float32)

    lax.fori_loop(0, peers, body, jnp.zeros(out_ref.shape[1:], jnp.float32))


def swap_cores(value):
    return lax.ppermute(value, "core", [(0, 1), (1, 0)])


def tie(value, *after):
    def kernel(*refs):
        del refs

    return pl.pallas_call(
        kernel,
        in_specs=[pl.BlockSpec(memory_space=pl.ANY) for _ in range(1 + len(after))],
        out_specs=pl.BlockSpec(memory_space=pl.ANY),
        out_shape=jax.ShapeDtypeStruct(value.shape, value.dtype),
        input_output_aliases={0: 0},
    )(value, *after)


def compose(both, first_work, second_work):
    core = lax.axis_index("core")
    chips = lax.axis_size("chip")
    half = GROUP_COLS
    width = half // chips
    mine = lax.dynamic_index_in_dim(both, core, 0, keepdims=False)
    theirs = swap_cores(lax.dynamic_index_in_dim(both, 1 - core, 0, keepdims=False))
    first = jnp.where(core == 0, mine, theirs)
    second = jnp.where(core == 0, theirs, mine)
    first_decay = first[STATE:]
    chip_state = second[STATE:] * first[:STATE] + second[:STATE]
    chip_decay = first_decay * second[STATE:]
    decay_hi = chip_decay.astype(jnp.bfloat16)
    decay_lo = (chip_decay - decay_hi.astype(jnp.float32)).astype(jnp.bfloat16)
    payload = jnp.concatenate(
        [chip_state.astype(jnp.bfloat16), decay_hi, decay_lo], axis=0
    ).reshape(STATE + 2, chips, width).transpose(1, 0, 2)
    work = first_work()
    got = tie(lax.all_to_all(payload, "chip", split_axis=0, concat_axis=0, tiled=True), work)
    entering = pl.pallas_call(
        scan_kernel,
        out_shape=jax.ShapeDtypeStruct((chips, STATE, width), jnp.bfloat16),
    )(got)
    work = second_work(work)
    back = tie(lax.all_to_all(entering, "chip", split_axis=0, concat_axis=0, tiled=True), work)
    chip_in = back.transpose(1, 0, 2).reshape(STATE, half).astype(jnp.float32)
    later_in = first_decay * chip_in + first[:STATE]
    keep = jnp.where(core == 0, chip_in, later_in).astype(jnp.bfloat16)
    other = swap_cores(jnp.where(core == 0, later_in, chip_in).astype(jnp.bfloat16))
    hin = jnp.where(
        core == 0,
        jnp.concatenate([keep, other], axis=1),
        jnp.concatenate([other, keep], axis=1),
    )
    return hin, work


def local(xbc, z_gate, dt_raw, lengths, conv_weight, conv_bias, dt_bias, a_log, d_skip, norm_gain):
    tok = xbc.shape[0]
    nb = tok // STRETCH
    first_pos = (lax.axis_index("chip") * lax.axis_size("core") + lax.axis_index("core")) * tok
    rim_rows = shifted(xbc[tok - (CONV - 1) :], ("chip", "core"), 1)
    rim8 = jnp.concatenate([jnp.zeros((8 - (CONV - 1), CHANNELS), xbc.dtype), rim_rows], axis=0)
    ext_pos = first_pos - (CONV - 1) + jnp.arange(tok + CONV - 1)
    ext_seg = segment_of(ext_pos, lengths)
    target = ext_seg[CONV - 1 :]
    kept = [
        (ext_pos[tap : tap + tok] >= 0) & (ext_seg[tap : tap + tok] == target) for tap in range(CONV)
    ]
    masks = jnp.stack(kept, axis=1).astype(jnp.float32)
    masks = jnp.concatenate([masks, jnp.zeros((tok, 128 - CONV), jnp.float32)], axis=1)
    w8 = jnp.concatenate([conv_weight, jnp.zeros((8 - CONV, CHANNELS), jnp.float32)], axis=0)
    conv = conv_part(xbc, rim8, w8, conv_bias[None, :], masks)
    step = jax.nn.softplus(dt_raw.astype(jnp.float32) + dt_bias[None, :])
    log_decay = -step * jnp.exp(a_log)[None, :]
    cum = jnp.cumsum(log_decay.reshape(nb, STRETCH, HEADS), axis=1).reshape(tok, HEADS)
    segments = segment_of(first_pos + jnp.arange(tok), lengths)
    seg_before = segment_of(first_pos + jnp.arange(nb) * STRETCH - 1, lengths)
    seg_last = segments.reshape(nb, STRETCH)[:, -1]
    cum_last = cum.reshape(nb, STRETCH, HEADS)[:, -1, :]
    block_decay = jnp.where((seg_last == seg_before)[:, None], jnp.exp(cum_last), 0.0)

    cum_g = cum.reshape(tok, GROUPS, PER_GROUP).transpose(1, 0, 2)
    dt_g = step.reshape(tok, GROUPS, PER_GROUP).transpose(1, 0, 2)
    cumt_g = cum.T.reshape(GROUPS, PER_GROUP, tok)
    segc = jnp.broadcast_to(segments[:, None], (tok, 128)).astype(jnp.int32)
    segr = jnp.broadcast_to(segments[None, :], (8, tok)).astype(jnp.int32)
    eb = jnp.broadcast_to(seg_before[:, None, None], (nb, 8, 128)).reshape(nb * 8, 128)
    eb = eb.astype(jnp.int32)
    bt = conv[:, INNER : INNER + GROUPS * STATE].T
    bdec = jnp.repeat(block_decay, HEAD_DIM, axis=1)[:, None, :]

    local_states, cdec, both = block_states(bt, conv, dt_g, cum_g, segc, bdec)
    dsk = jnp.repeat(d_skip, HEAD_DIM)[None, :]
    def first_work():
        return intra_part(conv, dt_g, cum_g, cumt_g, segc, segr, dsk, 0)

    def second_work(done):
        return intra_part(conv, dt_g, cum_g, cumt_g, segc, segr, dsk, 1, done)

    back, y_local = compose(both, first_work, second_work)
    gain = norm_gain[None, :]
    return mix(conv, y_local, z_gate, back, local_states, cdec, cum_g, segc, eb, gain)


def solution(mesh):
    groups, peers = mesh.devices.shape
    split = Mesh(mesh.devices.reshape(groups, peers // 2, 2), ("group", "chip", "core"))
    rows = P(("group", "chip", "core"), None)
    return jax.shard_map(
        local,
        mesh=split,
        in_specs=(rows, rows, rows, P("group"), P(), P(), P(), P(), P(), P()),
        out_specs=rows,
        check_vma=False,
    )
```

```python
import jax
import jax.numpy as jnp
from jax import lax
from jax.experimental import pallas as pl
from jax.experimental.pallas import tpu as pltpu
from jax.sharding import Mesh, PartitionSpec as P

HEADS = 64
HEAD_DIM = 64
STATE = 256
GROUPS = 2
CONV = 4
STRETCH = 256
CHANNELS = 5120
INNER = HEADS * HEAD_DIM
PER_GROUP = HEADS // GROUPS
GROUP_COLS = INNER // GROUPS


def shifted(value, axis, by):
    peers = lax.axis_size(axis)
    pairs = [(i, i + by) for i in range(peers) if 0 <= i + by < peers]
    return lax.ppermute(value, axis, pairs)


def segment_of(positions, lengths):
    prompt_ends = jnp.cumsum(lengths)
    hits = (prompt_ends[None, :] <= positions[:, None]).astype(jnp.int32)
    return jnp.sum(hits, axis=1)


def expand_heads(v):
    heads = lax.broadcasted_iota(jnp.int32, (PER_GROUP, GROUP_COLS), 0)
    cols = lax.broadcasted_iota(jnp.int32, (PER_GROUP, GROUP_COLS), 1)
    spread = (cols // HEAD_DIM == heads).astype(jnp.bfloat16)
    hi = v.astype(jnp.bfloat16)
    rest = v - hi.astype(jnp.float32)
    mid = rest.astype(jnp.bfloat16)
    lo = (rest - mid.astype(jnp.float32)).astype(jnp.bfloat16)
    out = jnp.dot(hi, spread, preferred_element_type=jnp.float32)
    out = out + jnp.dot(mid, spread, preferred_element_type=jnp.float32)
    return out + jnp.dot(lo, spread, preferred_element_type=jnp.float32)


def silu(v):
    return v * (0.5 + 0.5 * jnp.tanh(0.5 * v))


CONV_COLS = 640


def conv_kernel(x_ref, rim_ref, w_ref, bias_ref, m_ref, out_ref):
    x = x_ref[...].astype(jnp.float32)
    rim = rim_ref[...].astype(jnp.float32)
    rows8 = lax.broadcasted_iota(jnp.int32, rim.shape, 0)
    summed = jnp.zeros(x.shape, jnp.float32)
    top = jnp.zeros(rim.shape, jnp.float32)
    for tap in range(CONV):
        by = CONV - 1 - tap
        wk = w_ref[tap : tap + 1, :]
        kept = m_ref[:, tap : tap + 1] > 0.0
        if by == 0:
            term = x
            top_term = x[0:8]
        else:
            term = pltpu.roll(x, by, 0)
            top_term = jnp.where(rows8 < by, pltpu.roll(rim, by, 0), term[0:8])
        summed = summed + jnp.where(kept, term * wk, 0.0)
        top = top + jnp.where(kept[0:8], top_term * wk, 0.0)
    out_ref[...] = silu(summed + bias_ref[...]).astype(jnp.bfloat16)
    out_ref[0:8, :] = silu(top + bias_ref[...]).astype(jnp.bfloat16)


def conv_part(xbc, rim8, w8, bias, masks):
    tok, chans = xbc.shape
    return pl.pallas_call(
        conv_kernel,
        grid=(chans // CONV_COLS,),
        in_specs=[
            pl.BlockSpec((tok, CONV_COLS), lambda c: (0, c)),
            pl.BlockSpec((8, CONV_COLS), lambda c: (0, c)),
            pl.BlockSpec((8, CONV_COLS), lambda c: (0, c)),
            pl.BlockSpec((1, CONV_COLS), lambda c: (0, c)),
            pl.BlockSpec((tok, 128), lambda c: (0, 0)),
        ],
        out_specs=pl.BlockSpec((tok, CONV_COLS), lambda c: (0, c)),
        out_shape=jax.ShapeDtypeStruct((tok, chans), jnp.bfloat16),
    )(xbc, rim8, w8, bias, masks)


def state_kernel(
    bt_ref, x_ref, dt_ref, cum_ref, segc_ref, bdec_ref, local_ref, cdec_ref, tot_ref,
    acc_ref, dec_ref,
):
    b = pl.program_id(1)

    @pl.when(b == 0)
    def _():
        acc_ref[...] = jnp.zeros(acc_ref.shape, jnp.float32)
        dec_ref[...] = jnp.ones(dec_ref.shape, jnp.float32)

    local_ref[0] = acc_ref[...]
    cdec_ref[0] = dec_ref[...]
    cum = cum_ref[0]
    step = dt_ref[0]
    segc = segc_ref[:, 0:1]
    last = cum[STRETCH - 1 : STRETCH, :]
    seg_last = segc[STRETCH - 1 : STRETCH, :]
    w = jnp.where(segc == seg_last, jnp.exp(last - cum), 0.0)
    scaled = (x_ref[...].astype(jnp.float32) * expand_heads(step)).astype(jnp.bfloat16)
    weighted = (scaled.astype(jnp.float32) * expand_heads(w)).astype(jnp.bfloat16)
    block_state = jnp.dot(bt_ref[...], weighted, preferred_element_type=jnp.float32)
    decay = bdec_ref[0]
    acc_ref[...] = decay * acc_ref[...] + block_state
    dec_ref[...] = dec_ref[...] * decay

    @pl.when(b == pl.num_programs(1) - 1)
    def _():
        tot_ref[0, 0:STATE, :] = acc_ref[...]
        tot_ref[0, STATE : STATE + 1, :] = dec_ref[...]


def block_states(bt, conv, dt_g, cum_g, segc, bdec):
    tok = conv.shape[0]
    nb = tok // STRETCH
    return pl.pallas_call(
        state_kernel,
        grid=(GROUPS, nb),
        in_specs=[
            pl.BlockSpec((STATE, STRETCH), lambda g, b: (g, b)),
            pl.BlockSpec((STRETCH, GROUP_COLS), lambda g, b: (b, g)),
            pl.BlockSpec((1, STRETCH, PER_GROUP), lambda g, b: (g, b, 0)),
            pl.BlockSpec((1, STRETCH, PER_GROUP), lambda g, b: (g, b, 0)),
            pl.BlockSpec((STRETCH, 128), lambda g, b: (b, 0)),
            pl.BlockSpec((1, 1, GROUP_COLS), lambda g, b: (b, 0, g)),
        ],
        out_specs=[
            pl.BlockSpec((1, STATE, GROUP_COLS), lambda g, b: (b, 0, g)),
            pl.BlockSpec((1, 1, GROUP_COLS), lambda g, b: (b, 0, g)),
            pl.BlockSpec((1, STATE + 1, GROUP_COLS), lambda g, b: (g, 0, 0)),
        ],
        out_shape=[
            jax.ShapeDtypeStruct((nb, STATE, INNER), jnp.float32),
            jax.ShapeDtypeStruct((nb, 1, INNER), jnp.float32),
            jax.ShapeDtypeStruct((GROUPS, STATE + 1, GROUP_COLS), jnp.float32),
        ],
        scratch_shapes=[
            pltpu.VMEM((STATE, GROUP_COLS), jnp.float32),
            pltpu.VMEM((1, GROUP_COLS), jnp.float32),
        ],
    )(bt, conv, dt_g, cum_g, segc, bdec)


def intra_kernel(
    c_ref, b_ref, x_ref, dt_ref, cum_ref, cumt_ref, segc_ref, segr_ref, dsk_ref, out_ref
):
    gram = lax.dot_general(
        c_ref[...], b_ref[...], (((1,), (1,)), ((), ())), preferred_element_type=jnp.float32
    )
    segc = segc_ref[:, 0:1]
    segr = segr_ref[0:1, :]
    rows = lax.broadcasted_iota(jnp.int32, (STRETCH, STRETCH), 0)
    cols = lax.broadcasted_iota(jnp.int32, (STRETCH, STRETCH), 1)
    gram = jnp.where((segc == segr) & (cols <= rows), gram, 0.0)
    cum = cum_ref[0]
    cumt = cumt_ref[0]
    step = dt_ref[0]
    for j in range(PER_GROUP):
        hc = slice(j * HEAD_DIM, (j + 1) * HEAD_DIM)
        gap = jnp.minimum(cum[:, j : j + 1] - cumt[j : j + 1, :], 0.0)
        weights = (gram * jnp.exp(gap)).astype(jnp.bfloat16)
        xf = x_ref[:, hc].astype(jnp.float32)
        scaled = (xf * step[:, j : j + 1]).astype(jnp.bfloat16)
        intra = jnp.dot(weights, scaled, preferred_element_type=jnp.float32)
        out_ref[:, hc] = intra + dsk_ref[:, hc] * xf


def intra_part(conv, dt_g, cum_g, cumt_g, segc, segr, dsk, g, into=None):
    tok = conv.shape[0]
    nb = tok // STRETCH
    b_col = INNER // STATE
    c_col = b_col + GROUPS
    operands = [conv, conv, conv, dt_g, cum_g, cumt_g, segc, segr, dsk]
    specs = [
        pl.BlockSpec((STRETCH, STATE), lambda b: (b, c_col + g)),
        pl.BlockSpec((STRETCH, STATE), lambda b: (b, b_col + g)),
        pl.BlockSpec((STRETCH, GROUP_COLS), lambda b: (b, g)),
        pl.BlockSpec((1, STRETCH, PER_GROUP), lambda b: (g, b, 0)),
        pl.BlockSpec((1, STRETCH, PER_GROUP), lambda b: (g, b, 0)),
        pl.BlockSpec((1, PER_GROUP, STRETCH), lambda b: (g, 0, b)),
        pl.BlockSpec((STRETCH, 128), lambda b: (b, 0)),
        pl.BlockSpec((8, STRETCH), lambda b: (0, b)),
        pl.BlockSpec((1, GROUP_COLS), lambda b: (0, g)),
    ]
    kernel = intra_kernel
    aliases = {}
    if into is not None:
        operands.append(into)
        specs.append(pl.BlockSpec(memory_space=pl.ANY))
        aliases = {len(operands) - 1: 0}

        def kernel(*refs):
            intra_kernel(*refs[:-2], refs[-1])

    return pl.pallas_call(
        kernel,
        grid=(nb,),
        in_specs=specs,
        out_specs=pl.BlockSpec((STRETCH, GROUP_COLS), lambda b: (b, g)),
        out_shape=jax.ShapeDtypeStruct((tok, INNER), jnp.float32),
        input_output_aliases=aliases,
    )(*operands)


def mix_kernel(
    c_ref, y_ref, z_ref, hin_ref, local_ref, cdec_ref, cum_ref, segc_ref, eb_ref, gain_ref,
    out_ref,
):
    state = cdec_ref[0] * hin_ref[...].astype(jnp.float32) + local_ref[0]
    segc = segc_ref[:, 0:1]
    entry = eb_ref[0:1, 0:1]
    in_weight = jnp.where(segc == entry, jnp.exp(cum_ref[0]), 0.0)
    inter = jnp.dot(c_ref[...], state.astype(jnp.bfloat16), preferred_element_type=jnp.float32)
    y = y_ref[...] + inter * expand_heads(in_weight)
    zf = z_ref[...].astype(jnp.float32)
    gated = y * silu(zf)
    mean_square = jnp.mean(gated * gated, axis=1, keepdims=True) + 1e-05
    out_ref[...] = (gated * lax.rsqrt(mean_square) * gain_ref[...]).astype(jnp.bfloat16)


def mix(conv, y_local, z_gate, back, local_states, cdec, cum_g, segc, eb, gain):
    tok = conv.shape[0]
    nb = tok // STRETCH
    c_col = INNER // STATE + GROUPS
    return pl.pallas_call(
        mix_kernel,
        grid=(nb, GROUPS),
        in_specs=[
            pl.BlockSpec((STRETCH, STATE), lambda b, g: (b, c_col + g)),
            pl.BlockSpec((STRETCH, GROUP_COLS), lambda b, g: (b, g)),
            pl.BlockSpec((STRETCH, GROUP_COLS), lambda b, g: (b, g)),
            pl.BlockSpec((STATE, GROUP_COLS), lambda b, g: (0, g)),
            pl.BlockSpec((1, STATE, GROUP_COLS), lambda b, g: (b, 0, g)),
            pl.BlockSpec((1, 1, GROUP_COLS), lambda b, g: (b, 0, g)),
            pl.BlockSpec((1, STRETCH, PER_GROUP), lambda b, g: (g, b, 0)),
            pl.BlockSpec((STRETCH, 128), lambda b, g: (b, 0)),
            pl.BlockSpec((8, 128), lambda b, g: (b, 0)),
            pl.BlockSpec((1, GROUP_COLS), lambda b, g: (0, g)),
        ],
        out_specs=pl.BlockSpec((STRETCH, GROUP_COLS), lambda b, g: (b, g)),
        out_shape=jax.ShapeDtypeStruct((tok, INNER), jnp.bfloat16),
    )(conv, y_local, z_gate, back, local_states, cdec, cum_g, segc, eb, gain)


def scan_kernel(got_ref, out_ref):
    peers = got_ref.shape[0]

    def body(d, carry):
        out_ref[d] = carry.astype(jnp.bfloat16)
        decay = got_ref[d, STATE : STATE + 1, :].astype(jnp.float32) + got_ref[
            d, STATE + 1 : STATE + 2, :
        ].astype(jnp.float32)
        return decay * carry + got_ref[d, 0:STATE, :].astype(jnp.float32)

    lax.fori_loop(0, peers, body, jnp.zeros(out_ref.shape[1:], jnp.float32))


def swap_cores(value):
    return lax.ppermute(value, "core", [(0, 1), (1, 0)])


def tie(value, *after):
    def kernel(*refs):
        del refs

    return pl.pallas_call(
        kernel,
        in_specs=[pl.BlockSpec(memory_space=pl.ANY) for _ in range(1 + len(after))],
        out_specs=pl.BlockSpec(memory_space=pl.ANY),
        out_shape=jax.ShapeDtypeStruct(value.shape, value.dtype),
        input_output_aliases={0: 0},
    )(value, *after)


def compose(both, first_work, second_work):
    core = lax.axis_index("core")
    chips = lax.axis_size("chip")
    half = GROUP_COLS
    width = half // chips
    mine = lax.dynamic_index_in_dim(both, core, 0, keepdims=False)
    theirs = swap_cores(lax.dynamic_index_in_dim(both, 1 - core, 0, keepdims=False))
    first = jnp.where(core == 0, mine, theirs)
    second = jnp.where(core == 0, theirs, mine)
    first_decay = first[STATE:]
    chip_state = second[STATE:] * first[:STATE] + second[:STATE]
    chip_decay = first_decay * second[STATE:]
    decay_hi = chip_decay.astype(jnp.bfloat16)
    decay_lo = (chip_decay - decay_hi.astype(jnp.float32)).astype(jnp.bfloat16)
    payload = jnp.concatenate(
        [chip_state.astype(jnp.bfloat16), decay_hi, decay_lo], axis=0
    ).reshape(STATE + 2, chips, width).transpose(1, 0, 2)
    work = first_work()
    got = tie(lax.all_to_all(payload, "chip", split_axis=0, concat_axis=0, tiled=True), work)
    entering = pl.pallas_call(
        scan_kernel,
        out_shape=jax.ShapeDtypeStruct((chips, STATE, width), jnp.bfloat16),
    )(got)
    work = second_work(work)
    back = tie(lax.all_to_all(entering, "chip", split_axis=0, concat_axis=0, tiled=True), work)
    chip_in = back.transpose(1, 0, 2).reshape(STATE, half).astype(jnp.float32)
    later_in = first_decay * chip_in + first[:STATE]
    keep = jnp.where(core == 0, chip_in, later_in).astype(jnp.bfloat16)
    other = swap_cores(jnp.where(core == 0, later_in, chip_in).astype(jnp.bfloat16))
    hin = jnp.where(
        core == 0,
        jnp.concatenate([keep, other], axis=1),
        jnp.concatenate([other, keep], axis=1),
    )
    return hin, work


def local(xbc, z_gate, dt_raw, lengths, conv_weight, conv_bias, dt_bias, a_log, d_skip, norm_gain):
    tok = xbc.shape[0]
    nb = tok // STRETCH
    first_pos = (lax.axis_index("chip") * lax.axis_size("core") + lax.axis_index("core")) * tok
    rim_rows = shifted(xbc[tok - (CONV - 1) :], ("chip", "core"), 1)
    rim8 = jnp.concatenate([jnp.zeros((8 - (CONV - 1), CHANNELS), xbc.dtype), rim_rows], axis=0)
    ext_pos = first_pos - (CONV - 1) + jnp.arange(tok + CONV - 1)
    ext_seg = segment_of(ext_pos, lengths)
    target = ext_seg[CONV - 1 :]
    kept = [
        (ext_pos[tap : tap + tok] >= 0) & (ext_seg[tap : tap + tok] == target) for tap in range(CONV)
    ]
    masks = jnp.stack(kept, axis=1).astype(jnp.float32)
    masks = jnp.concatenate([masks, jnp.zeros((tok, 128 - CONV), jnp.float32)], axis=1)
    w8 = jnp.concatenate([conv_weight, jnp.zeros((8 - CONV, CHANNELS), jnp.float32)], axis=0)
    conv = conv_part(xbc, rim8, w8, conv_bias[None, :], masks)
    step = jax.nn.softplus(dt_raw.astype(jnp.float32) + dt_bias[None, :])
    log_decay = -step * jnp.exp(a_log)[None, :]
    cum = jnp.cumsum(log_decay.reshape(nb, STRETCH, HEADS), axis=1).reshape(tok, HEADS)
    segments = segment_of(first_pos + jnp.arange(tok), lengths)
    seg_before = segment_of(first_pos + jnp.arange(nb) * STRETCH - 1, lengths)
    seg_last = segments.reshape(nb, STRETCH)[:, -1]
    cum_last = cum.reshape(nb, STRETCH, HEADS)[:, -1, :]
    block_decay = jnp.where((seg_last == seg_before)[:, None], jnp.exp(cum_last), 0.0)

    cum_g = cum.reshape(tok, GROUPS, PER_GROUP).transpose(1, 0, 2)
    dt_g = step.reshape(tok, GROUPS, PER_GROUP).transpose(1, 0, 2)
    cumt_g = cum.T.reshape(GROUPS, PER_GROUP, tok)
    segc = jnp.broadcast_to(segments[:, None], (tok, 128)).astype(jnp.int32)
    segr = jnp.broadcast_to(segments[None, :], (8, tok)).astype(jnp.int32)
    eb = jnp.broadcast_to(seg_before[:, None, None], (nb, 8, 128)).reshape(nb * 8, 128)
    eb = eb.astype(jnp.int32)
    bt = conv[:, INNER : INNER + GROUPS * STATE].T
    bdec = jnp.repeat(block_decay, HEAD_DIM, axis=1)[:, None, :]

    local_states, cdec, both = block_states(bt, conv, dt_g, cum_g, segc, bdec)
    dsk = jnp.repeat(d_skip, HEAD_DIM)[None, :]
    def first_work():
        return intra_part(conv, dt_g, cum_g, cumt_g, segc, segr, dsk, 0)

    def second_work(done):
        return intra_part(conv, dt_g, cum_g, cumt_g, segc, segr, dsk, 1, done)

    back, y_local = compose(both, first_work, second_work)
    gain = norm_gain[None, :]
    return mix(conv, y_local, z_gate, back, local_states, cdec, cum_g, segc, eb, gain)


def solution(mesh):
    groups, peers = mesh.devices.shape
    split = Mesh(mesh.devices.reshape(groups, peers // 2, 2), ("group", "chip", "core"))
    rows = P(("group", "chip", "core"), None)
    return jax.shard_map(
        local,
        mesh=split,
        in_specs=(rows, rows, rows, P("group"), P(), P(), P(), P(), P(), P()),
        out_specs=rows,
        check_vma=False,
    )
```

```python
import jax
import jax.numpy as jnp
from jax import lax
from jax.experimental import pallas as pl
from jax.experimental.pallas import tpu as pltpu
from jax.sharding import Mesh, PartitionSpec as P

HEADS = 64
HEAD_DIM = 64
STATE = 256
GROUPS = 2
CONV = 4
STRETCH = 256
CHANNELS = 5120
INNER = HEADS * HEAD_DIM
PER_GROUP = HEADS // GROUPS
GROUP_COLS = INNER // GROUPS


def shifted(value, axis, by):
    peers = lax.axis_size(axis)
    pairs = [(i, i + by) for i in range(peers) if 0 <= i + by < peers]
    return lax.ppermute(value, axis, pairs)


def segment_of(positions, lengths):
    prompt_ends = jnp.cumsum(lengths)
    hits = (prompt_ends[None, :] <= positions[:, None]).astype(jnp.int32)
    return jnp.sum(hits, axis=1)


def expand_heads(v):
    heads = lax.broadcasted_iota(jnp.int32, (PER_GROUP, GROUP_COLS), 0)
    cols = lax.broadcasted_iota(jnp.int32, (PER_GROUP, GROUP_COLS), 1)
    spread = (cols // HEAD_DIM == heads).astype(jnp.bfloat16)
    hi = v.astype(jnp.bfloat16)
    rest = v - hi.astype(jnp.float32)
    mid = rest.astype(jnp.bfloat16)
    lo = (rest - mid.astype(jnp.float32)).astype(jnp.bfloat16)
    out = jnp.dot(hi, spread, preferred_element_type=jnp.float32)
    out = out + jnp.dot(mid, spread, preferred_element_type=jnp.float32)
    return out + jnp.dot(lo, spread, preferred_element_type=jnp.float32)


CONV_COLS = 640


def conv_kernel(x_ref, rim_ref, w_ref, bias_ref, m_ref, out_ref):
    x = x_ref[...].astype(jnp.float32)
    rim = rim_ref[...].astype(jnp.float32)
    rows8 = lax.broadcasted_iota(jnp.int32, rim.shape, 0)
    summed = jnp.zeros(x.shape, jnp.float32)
    top = jnp.zeros(rim.shape, jnp.float32)
    for tap in range(CONV):
        by = CONV - 1 - tap
        wk = w_ref[tap : tap + 1, :]
        kept = m_ref[:, tap : tap + 1] > 0.0
        if by == 0:
            term = x
            top_term = x[0:8]
        else:
            term = pltpu.roll(x, by, 0)
            top_term = jnp.where(rows8 < by, pltpu.roll(rim, by, 0), term[0:8])
        summed = summed + jnp.where(kept, term * wk, 0.0)
        top = top + jnp.where(kept[0:8], top_term * wk, 0.0)
    out_ref[...] = jax.nn.silu(summed + bias_ref[...]).astype(jnp.bfloat16)
    out_ref[0:8, :] = jax.nn.silu(top + bias_ref[...]).astype(jnp.bfloat16)


def conv_part(xbc, rim8, w8, bias, masks):
    tok, chans = xbc.shape
    return pl.pallas_call(
        conv_kernel,
        grid=(chans // CONV_COLS,),
        in_specs=[
            pl.BlockSpec((tok, CONV_COLS), lambda c: (0, c)),
            pl.BlockSpec((8, CONV_COLS), lambda c: (0, c)),
            pl.BlockSpec((8, CONV_COLS), lambda c: (0, c)),
            pl.BlockSpec((1, CONV_COLS), lambda c: (0, c)),
            pl.BlockSpec((tok, 128), lambda c: (0, 0)),
        ],
        out_specs=pl.BlockSpec((tok, CONV_COLS), lambda c: (0, c)),
        out_shape=jax.ShapeDtypeStruct((tok, chans), jnp.bfloat16),
    )(xbc, rim8, w8, bias, masks)


def state_kernel(
    bt_ref, x_ref, dt_ref, cum_ref, segc_ref, bdec_ref, local_ref, cdec_ref, tot_ref,
    acc_ref, dec_ref,
):
    b = pl.program_id(1)

    @pl.when(b == 0)
    def _():
        acc_ref[...] = jnp.zeros(acc_ref.shape, jnp.float32)
        dec_ref[...] = jnp.ones(dec_ref.shape, jnp.float32)

    local_ref[0] = acc_ref[...]
    cdec_ref[0] = dec_ref[...]
    cum = cum_ref[0]
    step = dt_ref[0]
    segc = segc_ref[:, 0:1]
    last = cum[STRETCH - 1 : STRETCH, :]
    seg_last = segc[STRETCH - 1 : STRETCH, :]
    w = jnp.where(segc == seg_last, jnp.exp(last - cum), 0.0)
    scaled = (x_ref[...].astype(jnp.float32) * expand_heads(step)).astype(jnp.bfloat16)
    weighted = (scaled.astype(jnp.float32) * expand_heads(w)).astype(jnp.bfloat16)
    block_state = jnp.dot(bt_ref[...], weighted, preferred_element_type=jnp.float32)
    decay = bdec_ref[0]
    acc_ref[...] = decay * acc_ref[...] + block_state
    dec_ref[...] = dec_ref[...] * decay

    @pl.when(b == pl.num_programs(1) - 1)
    def _():
        tot_ref[0, 0:STATE, :] = acc_ref[...]
        tot_ref[0, STATE : STATE + 1, :] = dec_ref[...]


def half_state_kernel(
    core_ref, bt_ref, x_ref, dt_ref, cum_ref, segc_ref, bdec_ref, *rest
):
    local_ref, cdec_ref, tot_ref, acc_ref, dec_ref = rest[-5:]
    del core_ref
    b = pl.program_id(0)

    @pl.when(b == 0)
    def _():
        acc_ref[...] = jnp.zeros(acc_ref.shape, jnp.float32)
        dec_ref[...] = jnp.ones(dec_ref.shape, jnp.float32)

    local_ref[0] = acc_ref[...]
    cdec_ref[0] = dec_ref[...]
    cum = cum_ref[0]
    step = dt_ref[0]
    segc = segc_ref[:, 0:1]
    last = cum[STRETCH - 1 : STRETCH, :]
    seg_last = segc[STRETCH - 1 : STRETCH, :]
    w = jnp.where(segc == seg_last, jnp.exp(last - cum), 0.0)
    scaled = (x_ref[...].astype(jnp.float32) * expand_heads(step)).astype(jnp.bfloat16)
    weighted = (scaled.astype(jnp.float32) * expand_heads(w)).astype(jnp.bfloat16)
    block_state = jnp.dot(bt_ref[...], weighted, preferred_element_type=jnp.float32)
    decay = bdec_ref[0]
    acc_ref[...] = decay * acc_ref[...] + block_state
    dec_ref[...] = dec_ref[...] * decay

    @pl.when(b == pl.num_programs(0) - 1)
    def _():
        tot_ref[0:STATE, :] = acc_ref[...]
        tot_ref[STATE : STATE + 1, :] = dec_ref[...]


def half_states(bt, conv, dt_g, cum_g, segc, bdec, core_arr, which, prev=None):
    tok = conv.shape[0]
    nb = tok // STRETCH

    def grp(c):
        return (which + 1 + c[0]) % GROUPS

    operands = [bt, conv, dt_g, cum_g, segc, bdec]
    specs = [
        pl.BlockSpec((STATE, STRETCH), lambda b, c: (grp(c), b)),
        pl.BlockSpec((STRETCH, GROUP_COLS), lambda b, c: (b, grp(c))),
        pl.BlockSpec((1, STRETCH, PER_GROUP), lambda b, c: (grp(c), b, 0)),
        pl.BlockSpec((1, STRETCH, PER_GROUP), lambda b, c: (grp(c), b, 0)),
        pl.BlockSpec((STRETCH, 128), lambda b, c: (b, 0)),
        pl.BlockSpec((1, 1, GROUP_COLS), lambda b, c: (b, 0, grp(c))),
    ]
    aliases = {}
    if prev is not None:
        operands += list(prev)
        specs += [pl.BlockSpec(memory_space=pl.ANY), pl.BlockSpec(memory_space=pl.ANY)]
        aliases = {len(operands) - 1: 0, len(operands): 1}
    grid_spec = pltpu.PrefetchScalarGridSpec(
        num_scalar_prefetch=1,
        grid=(nb,),
        in_specs=specs,
        out_specs=[
            pl.BlockSpec((1, STATE, GROUP_COLS), lambda b, c: (b, 0, grp(c))),
            pl.BlockSpec((1, 1, GROUP_COLS), lambda b, c: (b, 0, grp(c))),
            pl.BlockSpec((STATE + 1, GROUP_COLS), lambda b, c: (0, 0)),
        ],
        scratch_shapes=[
            pltpu.VMEM((STATE, GROUP_COLS), jnp.float32),
            pltpu.VMEM((1, GROUP_COLS), jnp.float32),
        ],
    )
    return pl.pallas_call(
        half_state_kernel,
        grid_spec=grid_spec,
        out_shape=[
            jax.ShapeDtypeStruct((nb, STATE, INNER), jnp.float32),
            jax.ShapeDtypeStruct((nb, 1, INNER), jnp.float32),
            jax.ShapeDtypeStruct((STATE + 1, GROUP_COLS), jnp.float32),
        ],
        input_output_aliases=aliases,
    )(core_arr, *operands)


def intra_kernel(
    c_ref, b_ref, x_ref, dt_ref, cum_ref, cumt_ref, segc_ref, segr_ref, dsk_ref, out_ref
):
    gram = lax.dot_general(
        c_ref[...], b_ref[...], (((1,), (1,)), ((), ())), preferred_element_type=jnp.float32
    )
    segc = segc_ref[:, 0:1]
    segr = segr_ref[0:1, :]
    rows = lax.broadcasted_iota(jnp.int32, (STRETCH, STRETCH), 0)
    cols = lax.broadcasted_iota(jnp.int32, (STRETCH, STRETCH), 1)
    gram = jnp.where((segc == segr) & (cols <= rows), gram, 0.0)
    cum = cum_ref[0]
    cumt = cumt_ref[0]
    step = dt_ref[0]
    for j in range(PER_GROUP):
        hc = slice(j * HEAD_DIM, (j + 1) * HEAD_DIM)
        gap = jnp.minimum(cum[:, j : j + 1] - cumt[j : j + 1, :], 0.0)
        weights = (gram * jnp.exp(gap)).astype(jnp.bfloat16)
        xf = x_ref[:, hc].astype(jnp.float32)
        scaled = (xf * step[:, j : j + 1]).astype(jnp.bfloat16)
        intra = jnp.dot(weights, scaled, preferred_element_type=jnp.float32)
        out_ref[:, hc] = intra + dsk_ref[:, hc] * xf


def intra_part(conv, dt_g, cum_g, cumt_g, segc, segr, dsk, g, into=None):
    tok = conv.shape[0]
    nb = tok // STRETCH
    b_col = INNER // STATE
    c_col = b_col + GROUPS
    operands = [conv, conv, conv, dt_g, cum_g, cumt_g, segc, segr, dsk]
    specs = [
        pl.BlockSpec((STRETCH, STATE), lambda b: (b, c_col + g)),
        pl.BlockSpec((STRETCH, STATE), lambda b: (b, b_col + g)),
        pl.BlockSpec((STRETCH, GROUP_COLS), lambda b: (b, g)),
        pl.BlockSpec((1, STRETCH, PER_GROUP), lambda b: (g, b, 0)),
        pl.BlockSpec((1, STRETCH, PER_GROUP), lambda b: (g, b, 0)),
        pl.BlockSpec((1, PER_GROUP, STRETCH), lambda b: (g, 0, b)),
        pl.BlockSpec((STRETCH, 128), lambda b: (b, 0)),
        pl.BlockSpec((8, STRETCH), lambda b: (0, b)),
        pl.BlockSpec((1, GROUP_COLS), lambda b: (0, g)),
    ]
    kernel = intra_kernel
    aliases = {}
    if into is not None:
        operands.append(into)
        specs.append(pl.BlockSpec(memory_space=pl.ANY))
        aliases = {len(operands) - 1: 0}

        def kernel(*refs):
            intra_kernel(*refs[:-2], refs[-1])

    return pl.pallas_call(
        kernel,
        grid=(nb,),
        in_specs=specs,
        out_specs=pl.BlockSpec((STRETCH, GROUP_COLS), lambda b: (b, g)),
        out_shape=jax.ShapeDtypeStruct((tok, INNER), jnp.float32),
        input_output_aliases=aliases,
    )(*operands)


def mix_kernel(
    c_ref, y_ref, z_ref, hin_ref, local_ref, cdec_ref, cum_ref, segc_ref, eb_ref, gain_ref,
    out_ref,
):
    state = cdec_ref[0] * hin_ref[...].astype(jnp.float32) + local_ref[0]
    segc = segc_ref[:, 0:1]
    entry = eb_ref[0:1, 0:1]
    in_weight = jnp.where(segc == entry, jnp.exp(cum_ref[0]), 0.0)
    inter = jnp.dot(c_ref[...], state.astype(jnp.bfloat16), preferred_element_type=jnp.float32)
    y = y_ref[...] + inter * expand_heads(in_weight)
    zf = z_ref[...].astype(jnp.float32)
    gated = y * (zf * jax.nn.sigmoid(zf))
    mean_square = jnp.mean(gated * gated, axis=1, keepdims=True) + 1e-05
    out_ref[...] = (gated * lax.rsqrt(mean_square) * gain_ref[...]).astype(jnp.bfloat16)


def mix(conv, y_local, z_gate, back, local_states, cdec, cum_g, segc, eb, gain):
    tok = conv.shape[0]
    nb = tok // STRETCH
    c_col = INNER // STATE + GROUPS
    return pl.pallas_call(
        mix_kernel,
        grid=(nb, GROUPS),
        in_specs=[
            pl.BlockSpec((STRETCH, STATE), lambda b, g: (b, c_col + g)),
            pl.BlockSpec((STRETCH, GROUP_COLS), lambda b, g: (b, g)),
            pl.BlockSpec((STRETCH, GROUP_COLS), lambda b, g: (b, g)),
            pl.BlockSpec((STATE, GROUP_COLS), lambda b, g: (0, g)),
            pl.BlockSpec((1, STATE, GROUP_COLS), lambda b, g: (b, 0, g)),
            pl.BlockSpec((1, 1, GROUP_COLS), lambda b, g: (b, 0, g)),
            pl.BlockSpec((1, STRETCH, PER_GROUP), lambda b, g: (g, b, 0)),
            pl.BlockSpec((STRETCH, 128), lambda b, g: (b, 0)),
            pl.BlockSpec((8, 128), lambda b, g: (b, 0)),
            pl.BlockSpec((1, GROUP_COLS), lambda b, g: (0, g)),
        ],
        out_specs=pl.BlockSpec((STRETCH, GROUP_COLS), lambda b, g: (b, g)),
        out_shape=jax.ShapeDtypeStruct((tok, INNER), jnp.bfloat16),
    )(conv, y_local, z_gate, back, local_states, cdec, cum_g, segc, eb, gain)


def scan_kernel(got_ref, out_ref):
    peers = got_ref.shape[0]

    def body(d, carry):
        out_ref[d] = carry.astype(jnp.bfloat16)
        decay = got_ref[d, STATE : STATE + 1, :].astype(jnp.float32) + got_ref[
            d, STATE + 1 : STATE + 2, :
        ].astype(jnp.float32)
        return decay * carry + got_ref[d, 0:STATE, :].astype(jnp.float32)

    lax.fori_loop(0, peers, body, jnp.zeros(out_ref.shape[1:], jnp.float32))


def swap_cores(value):
    return lax.ppermute(value, "core", [(0, 1), (1, 0)])


def tie(value, *after):
    def kernel(*refs):
        del refs

    return pl.pallas_call(
        kernel,
        in_specs=[pl.BlockSpec(memory_space=pl.ANY) for _ in range(1 + len(after))],
        out_specs=pl.BlockSpec(memory_space=pl.ANY),
        out_shape=jax.ShapeDtypeStruct(value.shape, value.dtype),
        input_output_aliases={0: 0},
    )(value, *after)


def compose(for_other, mine, first_work, second_work):
    core = lax.axis_index("core")
    chips = lax.axis_size("chip")
    half = GROUP_COLS
    width = half // chips
    theirs = swap_cores(for_other)
    first = jnp.where(core == 0, mine, theirs)
    second = jnp.where(core == 0, theirs, mine)
    first_decay = first[STATE:]
    chip_state = second[STATE:] * first[:STATE] + second[:STATE]
    chip_decay = first_decay * second[STATE:]
    decay_hi = chip_decay.astype(jnp.bfloat16)
    decay_lo = (chip_decay - decay_hi.astype(jnp.float32)).astype(jnp.bfloat16)
    payload = jnp.concatenate(
        [chip_state.astype(jnp.bfloat16), decay_hi, decay_lo], axis=0
    ).reshape(STATE + 2, chips, width).transpose(1, 0, 2)
    work = first_work()
    got = tie(lax.all_to_all(payload, "chip", split_axis=0, concat_axis=0, tiled=True), work)
    entering = pl.pallas_call(
        scan_kernel,
        out_shape=jax.ShapeDtypeStruct((chips, STATE, width), jnp.bfloat16),
    )(got)
    work = second_work(work)
    back = tie(lax.all_to_all(entering, "chip", split_axis=0, concat_axis=0, tiled=True), work)
    chip_in = back.transpose(1, 0, 2).reshape(STATE, half).astype(jnp.float32)
    later_in = first_decay * chip_in + first[:STATE]
    keep = jnp.where(core == 0, chip_in, later_in).astype(jnp.bfloat16)
    other = swap_cores(jnp.where(core == 0, later_in, chip_in).astype(jnp.bfloat16))
    hin = jnp.where(
        core == 0,
        jnp.concatenate([keep, other], axis=1),
        jnp.concatenate([other, keep], axis=1),
    )
    return hin, work


def local(xbc, z_gate, dt_raw, lengths, conv_weight, conv_bias, dt_bias, a_log, d_skip, norm_gain):
    tok = xbc.shape[0]
    nb = tok // STRETCH
    first_pos = (lax.axis_index("chip") * lax.axis_size("core") + lax.axis_index("core")) * tok
    rim_rows = shifted(xbc[tok - (CONV - 1) :], ("chip", "core"), 1)
    rim8 = jnp.concatenate([jnp.zeros((8 - (CONV - 1), CHANNELS), xbc.dtype), rim_rows], axis=0)
    ext_pos = first_pos - (CONV - 1) + jnp.arange(tok + CONV - 1)
    ext_seg = segment_of(ext_pos, lengths)
    target = ext_seg[CONV - 1 :]
    kept = [
        (ext_pos[tap : tap + tok] >= 0) & (ext_seg[tap : tap + tok] == target) for tap in range(CONV)
    ]
    masks = jnp.stack(kept, axis=1).astype(jnp.float32)
    masks = jnp.concatenate([masks, jnp.zeros((tok, 128 - CONV), jnp.float32)], axis=1)
    w8 = jnp.concatenate([conv_weight, jnp.zeros((8 - CONV, CHANNELS), jnp.float32)], axis=0)
    conv = conv_part(xbc, rim8, w8, conv_bias[None, :], masks)
    step = jax.nn.softplus(dt_raw.astype(jnp.float32) + dt_bias[None, :])
    log_decay = -step * jnp.exp(a_log)[None, :]
    cum = jnp.cumsum(log_decay.reshape(nb, STRETCH, HEADS), axis=1).reshape(tok, HEADS)
    segments = segment_of(first_pos + jnp.arange(tok), lengths)
    seg_before = segment_of(first_pos + jnp.arange(nb) * STRETCH - 1, lengths)
    seg_last = segments.reshape(nb, STRETCH)[:, -1]
    cum_last = cum.reshape(nb, STRETCH, HEADS)[:, -1, :]
    block_decay = jnp.where((seg_last == seg_before)[:, None], jnp.exp(cum_last), 0.0)

    cum_g = cum.reshape(tok, GROUPS, PER_GROUP).transpose(1, 0, 2)
    dt_g = step.reshape(tok, GROUPS, PER_GROUP).transpose(1, 0, 2)
    cumt_g = cum.T.reshape(GROUPS, PER_GROUP, tok)
    segc = jnp.broadcast_to(segments[:, None], (tok, 128)).astype(jnp.int32)
    segr = jnp.broadcast_to(segments[None, :], (8, tok)).astype(jnp.int32)
    eb = jnp.broadcast_to(seg_before[:, None, None], (nb, 8, 128)).reshape(nb * 8, 128)
    eb = eb.astype(jnp.int32)
    bt = conv[:, INNER : INNER + GROUPS * STATE].T
    bdec = jnp.repeat(block_decay, HEAD_DIM, axis=1)[:, None, :]

    core_arr = lax.axis_index("core").astype(jnp.int32).reshape(1)
    local_a, cdec_a, for_other = half_states(bt, conv, dt_g, cum_g, segc, bdec, core_arr, 0)
    local_states, cdec, mine = half_states(
        bt, conv, dt_g, cum_g, segc, bdec, core_arr, 1, (local_a, cdec_a)
    )
    dsk = jnp.repeat(d_skip, HEAD_DIM)[None, :]
    def first_work():
        return intra_part(conv, dt_g, cum_g, cumt_g, segc, segr, dsk, 0)

    def second_work(done):
        return intra_part(conv, dt_g, cum_g, cumt_g, segc, segr, dsk, 1, done)

    back, y_local = compose(for_other, mine, first_work, second_work)
    gain = norm_gain[None, :]
    return mix(conv, y_local, z_gate, back, local_states, cdec, cum_g, segc, eb, gain)


def solution(mesh):
    groups, peers = mesh.devices.shape
    split = Mesh(mesh.devices.reshape(groups, peers // 2, 2), ("group", "chip", "core"))
    rows = P(("group", "chip", "core"), None)
    return jax.shard_map(
        local,
        mesh=split,
        in_specs=(rows, rows, rows, P("group"), P(), P(), P(), P(), P(), P()),
        out_specs=rows,
        check_vma=False,
    )
```

```python
import jax
import jax.numpy as jnp
from jax import lax
from jax.experimental import pallas as pl
from jax.experimental.pallas import tpu as pltpu
from jax.sharding import Mesh, PartitionSpec as P

HEADS = 64
HEAD_DIM = 64
STATE = 256
GROUPS = 2
CONV = 4
STRETCH = 256
CHANNELS = 5120
INNER = HEADS * HEAD_DIM
PER_GROUP = HEADS // GROUPS
GROUP_COLS = INNER // GROUPS


def shifted(value, axis, by):
    peers = lax.axis_size(axis)
    pairs = [(i, i + by) for i in range(peers) if 0 <= i + by < peers]
    return lax.ppermute(value, axis, pairs)


def segment_of(positions, lengths):
    prompt_ends = jnp.cumsum(lengths)
    hits = (prompt_ends[None, :] <= positions[:, None]).astype(jnp.int32)
    return jnp.sum(hits, axis=1)


def expand_heads(v):
    heads = lax.broadcasted_iota(jnp.int32, (PER_GROUP, GROUP_COLS), 0)
    cols = lax.broadcasted_iota(jnp.int32, (PER_GROUP, GROUP_COLS), 1)
    spread = (cols // HEAD_DIM == heads).astype(jnp.bfloat16)
    hi = v.astype(jnp.bfloat16)
    rest = v - hi.astype(jnp.float32)
    mid = rest.astype(jnp.bfloat16)
    lo = (rest - mid.astype(jnp.float32)).astype(jnp.bfloat16)
    out = jnp.dot(hi, spread, preferred_element_type=jnp.float32)
    out = out + jnp.dot(mid, spread, preferred_element_type=jnp.float32)
    return out + jnp.dot(lo, spread, preferred_element_type=jnp.float32)


CONV_COLS = 640


def conv_kernel(x_ref, rim_ref, w_ref, bias_ref, m_ref, out_ref):
    x = x_ref[...].astype(jnp.float32)
    rim = rim_ref[...].astype(jnp.float32)
    rows8 = lax.broadcasted_iota(jnp.int32, rim.shape, 0)
    summed = jnp.zeros(x.shape, jnp.float32)
    top = jnp.zeros(rim.shape, jnp.float32)
    for tap in range(CONV):
        by = CONV - 1 - tap
        wk = w_ref[tap : tap + 1, :]
        kept = m_ref[:, tap : tap + 1] > 0.0
        if by == 0:
            term = x
            top_term = x[0:8]
        else:
            term = pltpu.roll(x, by, 0)
            top_term = jnp.where(rows8 < by, pltpu.roll(rim, by, 0), term[0:8])
        summed = summed + jnp.where(kept, term * wk, 0.0)
        top = top + jnp.where(kept[0:8], top_term * wk, 0.0)
    out_ref[...] = jax.nn.silu(summed + bias_ref[...]).astype(jnp.bfloat16)
    out_ref[0:8, :] = jax.nn.silu(top + bias_ref[...]).astype(jnp.bfloat16)


def conv_part(xbc, rim8, w8, bias, masks):
    tok, chans = xbc.shape
    return pl.pallas_call(
        conv_kernel,
        grid=(chans // CONV_COLS,),
        in_specs=[
            pl.BlockSpec((tok, CONV_COLS), lambda c: (0, c)),
            pl.BlockSpec((8, CONV_COLS), lambda c: (0, c)),
            pl.BlockSpec((8, CONV_COLS), lambda c: (0, c)),
            pl.BlockSpec((1, CONV_COLS), lambda c: (0, c)),
            pl.BlockSpec((tok, 128), lambda c: (0, 0)),
        ],
        out_specs=pl.BlockSpec((tok, CONV_COLS), lambda c: (0, c)),
        out_shape=jax.ShapeDtypeStruct((tok, chans), jnp.bfloat16),
    )(xbc, rim8, w8, bias, masks)


def state_kernel(
    bt_ref, x_ref, dt_ref, cum_ref, segc_ref, bdec_ref, local_ref, cdec_ref, tot_ref,
    acc_ref, dec_ref,
):
    b = pl.program_id(1)

    @pl.when(b == 0)
    def _():
        acc_ref[...] = jnp.zeros(acc_ref.shape, jnp.float32)
        dec_ref[...] = jnp.ones(dec_ref.shape, jnp.float32)

    local_ref[0] = acc_ref[...]
    cdec_ref[0] = dec_ref[...]
    cum = cum_ref[0]
    step = dt_ref[0]
    segc = segc_ref[:, 0:1]
    last = cum[STRETCH - 1 : STRETCH, :]
    seg_last = segc[STRETCH - 1 : STRETCH, :]
    w = jnp.where(segc == seg_last, jnp.exp(last - cum), 0.0)
    scaled = (x_ref[...].astype(jnp.float32) * expand_heads(step)).astype(jnp.bfloat16)
    weighted = (scaled.astype(jnp.float32) * expand_heads(w)).astype(jnp.bfloat16)
    block_state = jnp.dot(bt_ref[...], weighted, preferred_element_type=jnp.float32)
    decay = bdec_ref[0]
    acc_ref[...] = decay * acc_ref[...] + block_state
    dec_ref[...] = dec_ref[...] * decay

    @pl.when(b == pl.num_programs(1) - 1)
    def _():
        tot_ref[0, 0:STATE, :] = acc_ref[...]
        tot_ref[0, STATE : STATE + 1, :] = dec_ref[...]


def half_state_kernel(
    core_ref, bt_ref, x_ref, dt_ref, cum_ref, segc_ref, bdec_ref, *rest
):
    local_ref, cdec_ref, tot_ref, acc_ref, dec_ref = rest[-5:]
    del core_ref
    b = pl.program_id(0)

    @pl.when(b == 0)
    def _():
        acc_ref[...] = jnp.zeros(acc_ref.shape, jnp.float32)
        dec_ref[...] = jnp.ones(dec_ref.shape, jnp.float32)

    local_ref[0] = acc_ref[...]
    cdec_ref[0] = dec_ref[...]
    cum = cum_ref[0]
    step = dt_ref[0]
    segc = segc_ref[:, 0:1]
    last = cum[STRETCH - 1 : STRETCH, :]
    seg_last = segc[STRETCH - 1 : STRETCH, :]
    w = jnp.where(segc == seg_last, jnp.exp(last - cum), 0.0)
    scaled = (x_ref[...].astype(jnp.float32) * expand_heads(step)).astype(jnp.bfloat16)
    weighted = (scaled.astype(jnp.float32) * expand_heads(w)).astype(jnp.bfloat16)
    block_state = jnp.dot(bt_ref[...], weighted, preferred_element_type=jnp.float32)
    decay = bdec_ref[0]
    acc_ref[...] = decay * acc_ref[...] + block_state
    dec_ref[...] = dec_ref[...] * decay

    @pl.when(b == pl.num_programs(0) - 1)
    def _():
        tot_ref[0:STATE, :] = acc_ref[...]
        tot_ref[STATE : STATE + 1, :] = dec_ref[...]


def half_states(bt, conv, dt_g, cum_g, segc, bdec, core_arr, which, prev=None):
    tok = conv.shape[0]
    nb = tok // STRETCH

    def grp(c):
        return (which + 1 + c[0]) % GROUPS

    operands = [bt, conv, dt_g, cum_g, segc, bdec]
    specs = [
        pl.BlockSpec((STATE, STRETCH), lambda b, c: (grp(c), b)),
        pl.BlockSpec((STRETCH, GROUP_COLS), lambda b, c: (b, grp(c))),
        pl.BlockSpec((1, STRETCH, PER_GROUP), lambda b, c: (grp(c), b, 0)),
        pl.BlockSpec((1, STRETCH, PER_GROUP), lambda b, c: (grp(c), b, 0)),
        pl.BlockSpec((STRETCH, 128), lambda b, c: (b, 0)),
        pl.BlockSpec((1, 1, GROUP_COLS), lambda b, c: (b, 0, grp(c))),
    ]
    aliases = {}
    if prev is not None:
        operands += list(prev)
        specs += [pl.BlockSpec(memory_space=pl.ANY), pl.BlockSpec(memory_space=pl.ANY)]
        aliases = {len(operands) - 1: 0, len(operands): 1}
    grid_spec = pltpu.PrefetchScalarGridSpec(
        num_scalar_prefetch=1,
        grid=(nb,),
        in_specs=specs,
        out_specs=[
            pl.BlockSpec((1, STATE, GROUP_COLS), lambda b, c: (b, 0, grp(c))),
            pl.BlockSpec((1, 1, GROUP_COLS), lambda b, c: (b, 0, grp(c))),
            pl.BlockSpec((STATE + 1, GROUP_COLS), lambda b, c: (0, 0)),
        ],
        scratch_shapes=[
            pltpu.VMEM((STATE, GROUP_COLS), jnp.float32),
            pltpu.VMEM((1, GROUP_COLS), jnp.float32),
        ],
    )
    return pl.pallas_call(
        half_state_kernel,
        grid_spec=grid_spec,
        out_shape=[
            jax.ShapeDtypeStruct((nb, STATE, INNER), jnp.float32),
            jax.ShapeDtypeStruct((nb, 1, INNER), jnp.float32),
            jax.ShapeDtypeStruct((STATE + 1, GROUP_COLS), jnp.float32),
        ],
        input_output_aliases=aliases,
    )(core_arr, *operands)


def intra_kernel(
    c_ref, b_ref, x_ref, dt_ref, cum_ref, cumt_ref, segc_ref, segr_ref, dsk_ref, out_ref
):
    gram = lax.dot_general(
        c_ref[...], b_ref[...], (((1,), (1,)), ((), ())), preferred_element_type=jnp.float32
    )
    segc = segc_ref[:, 0:1]
    segr = segr_ref[0:1, :]
    rows = lax.broadcasted_iota(jnp.int32, (STRETCH, STRETCH), 0)
    cols = lax.broadcasted_iota(jnp.int32, (STRETCH, STRETCH), 1)
    gram = jnp.where((segc == segr) & (cols <= rows), gram, 0.0)
    cum = cum_ref[0]
    cumt = cumt_ref[0]
    step = dt_ref[0]
    for j in range(PER_GROUP):
        hc = slice(j * HEAD_DIM, (j + 1) * HEAD_DIM)
        gap = jnp.minimum(cum[:, j : j + 1] - cumt[j : j + 1, :], 0.0)
        weights = (gram * jnp.exp(gap)).astype(jnp.bfloat16)
        xf = x_ref[:, hc].astype(jnp.float32)
        scaled = (xf * step[:, j : j + 1]).astype(jnp.bfloat16)
        intra = jnp.dot(weights, scaled, preferred_element_type=jnp.float32)
        out_ref[:, hc] = intra + dsk_ref[:, hc] * xf


def intra_part(conv, dt_g, cum_g, cumt_g, segc, segr, dsk, g, into=None):
    tok = conv.shape[0]
    nb = tok // STRETCH
    b_col = INNER // STATE
    c_col = b_col + GROUPS
    operands = [conv, conv, conv, dt_g, cum_g, cumt_g, segc, segr, dsk]
    specs = [
        pl.BlockSpec((STRETCH, STATE), lambda b: (b, c_col + g)),
        pl.BlockSpec((STRETCH, STATE), lambda b: (b, b_col + g)),
        pl.BlockSpec((STRETCH, GROUP_COLS), lambda b: (b, g)),
        pl.BlockSpec((1, STRETCH, PER_GROUP), lambda b: (g, b, 0)),
        pl.BlockSpec((1, STRETCH, PER_GROUP), lambda b: (g, b, 0)),
        pl.BlockSpec((1, PER_GROUP, STRETCH), lambda b: (g, 0, b)),
        pl.BlockSpec((STRETCH, 128), lambda b: (b, 0)),
        pl.BlockSpec((8, STRETCH), lambda b: (0, b)),
        pl.BlockSpec((1, GROUP_COLS), lambda b: (0, g)),
    ]
    kernel = intra_kernel
    aliases = {}
    if into is not None:
        operands.append(into)
        specs.append(pl.BlockSpec(memory_space=pl.ANY))
        aliases = {len(operands) - 1: 0}

        def kernel(*refs):
            intra_kernel(*refs[:-2], refs[-1])

    return pl.pallas_call(
        kernel,
        grid=(nb,),
        in_specs=specs,
        out_specs=pl.BlockSpec((STRETCH, GROUP_COLS), lambda b: (b, g)),
        out_shape=jax.ShapeDtypeStruct((tok, INNER), jnp.float32),
        input_output_aliases=aliases,
    )(*operands)


def mix_kernel(
    c_ref, y_ref, z_ref, hin_ref, local_ref, cdec_ref, cum_ref, segc_ref, eb_ref, gain_ref,
    out_ref,
):
    state = cdec_ref[0] * hin_ref[...].astype(jnp.float32) + local_ref[0]
    segc = segc_ref[:, 0:1]
    entry = eb_ref[0:1, 0:1]
    in_weight = jnp.where(segc == entry, jnp.exp(cum_ref[0]), 0.0)
    inter = jnp.dot(c_ref[...], state.astype(jnp.bfloat16), preferred_element_type=jnp.float32)
    y = y_ref[...] + inter * expand_heads(in_weight)
    zf = z_ref[...].astype(jnp.float32)
    gated = y * (zf * jax.nn.sigmoid(zf))
    mean_square = jnp.mean(gated * gated, axis=1, keepdims=True) + 1e-05
    out_ref[...] = (gated * lax.rsqrt(mean_square) * gain_ref[...]).astype(jnp.bfloat16)


def mix(conv, y_local, z_gate, hin, local_states, cdec, cum_g, segc, eb, gain, core_arr, which,
        prev=None):
    tok = conv.shape[0]
    nb = tok // STRETCH
    c_col = INNER // STATE + GROUPS

    def grp(c):
        return (which + c[0]) % GROUPS

    operands = [conv, y_local, z_gate, hin, local_states, cdec, cum_g, segc, eb, gain]
    specs = [
        pl.BlockSpec((STRETCH, STATE), lambda b, c: (b, c_col + grp(c))),
        pl.BlockSpec((STRETCH, GROUP_COLS), lambda b, c: (b, grp(c))),
        pl.BlockSpec((STRETCH, GROUP_COLS), lambda b, c: (b, grp(c))),
        pl.BlockSpec((STATE, GROUP_COLS), lambda b, c: (0, 0)),
        pl.BlockSpec((1, STATE, GROUP_COLS), lambda b, c: (b, 0, grp(c))),
        pl.BlockSpec((1, 1, GROUP_COLS), lambda b, c: (b, 0, grp(c))),
        pl.BlockSpec((1, STRETCH, PER_GROUP), lambda b, c: (grp(c), b, 0)),
        pl.BlockSpec((STRETCH, 128), lambda b, c: (b, 0)),
        pl.BlockSpec((8, 128), lambda b, c: (b, 0)),
        pl.BlockSpec((1, GROUP_COLS), lambda b, c: (0, grp(c))),
    ]
    kernel = mix_kernel
    aliases = {}
    if prev is not None:
        operands.append(prev)
        specs.append(pl.BlockSpec(memory_space=pl.ANY))
        aliases = {len(operands): 0}

        def kernel(*refs):
            mix_kernel(*refs[:-2], refs[-1])

    def with_core(core_ref, *refs):
        del core_ref
        kernel(*refs)

    grid_spec = pltpu.PrefetchScalarGridSpec(
        num_scalar_prefetch=1,
        grid=(nb,),
        in_specs=specs,
        out_specs=pl.BlockSpec((STRETCH, GROUP_COLS), lambda b, c: (b, grp(c))),
    )
    return pl.pallas_call(
        with_core,
        grid_spec=grid_spec,
        out_shape=jax.ShapeDtypeStruct((tok, INNER), jnp.bfloat16),
        input_output_aliases=aliases,
    )(core_arr, *operands)


def scan_kernel(got_ref, out_ref):
    peers = got_ref.shape[0]

    def body(d, carry):
        out_ref[d] = carry.astype(jnp.bfloat16)
        decay = got_ref[d, STATE : STATE + 1, :].astype(jnp.float32) + got_ref[
            d, STATE + 1 : STATE + 2, :
        ].astype(jnp.float32)
        return decay * carry + got_ref[d, 0:STATE, :].astype(jnp.float32)

    lax.fori_loop(0, peers, body, jnp.zeros(out_ref.shape[1:], jnp.float32))


def swap_cores(value):
    return lax.ppermute(value, "core", [(0, 1), (1, 0)])


def tie(value, *after):
    def kernel(*refs):
        del refs

    return pl.pallas_call(
        kernel,
        in_specs=[pl.BlockSpec(memory_space=pl.ANY) for _ in range(1 + len(after))],
        out_specs=pl.BlockSpec(memory_space=pl.ANY),
        out_shape=jax.ShapeDtypeStruct(value.shape, value.dtype),
        input_output_aliases={0: 0},
    )(value, *after)


def compose(for_other, mine, first_work, second_work):
    core = lax.axis_index("core")
    chips = lax.axis_size("chip")
    half = GROUP_COLS
    width = half // chips
    theirs = swap_cores(for_other)
    first = jnp.where(core == 0, mine, theirs)
    second = jnp.where(core == 0, theirs, mine)
    first_decay = first[STATE:]
    chip_state = second[STATE:] * first[:STATE] + second[:STATE]
    chip_decay = first_decay * second[STATE:]
    decay_hi = chip_decay.astype(jnp.bfloat16)
    decay_lo = (chip_decay - decay_hi.astype(jnp.float32)).astype(jnp.bfloat16)
    payload = jnp.concatenate(
        [chip_state.astype(jnp.bfloat16), decay_hi, decay_lo], axis=0
    ).reshape(STATE + 2, chips, width).transpose(1, 0, 2)
    work = first_work()
    got = tie(lax.all_to_all(payload, "chip", split_axis=0, concat_axis=0, tiled=True), work)
    entering = pl.pallas_call(
        scan_kernel,
        out_shape=jax.ShapeDtypeStruct((chips, STATE, width), jnp.bfloat16),
    )(got)
    work = second_work(work)
    back = tie(lax.all_to_all(entering, "chip", split_axis=0, concat_axis=0, tiled=True), work)
    chip_in = back.transpose(1, 0, 2).reshape(STATE, half).astype(jnp.float32)
    later_in = first_decay * chip_in + first[:STATE]
    keep = jnp.where(core == 0, chip_in, later_in).astype(jnp.bfloat16)
    other = swap_cores(jnp.where(core == 0, later_in, chip_in).astype(jnp.bfloat16))
    return keep, other, work


def local(xbc, z_gate, dt_raw, lengths, conv_weight, conv_bias, dt_bias, a_log, d_skip, norm_gain):
    tok = xbc.shape[0]
    nb = tok // STRETCH
    first_pos = (lax.axis_index("chip") * lax.axis_size("core") + lax.axis_index("core")) * tok
    rim_rows = shifted(xbc[tok - (CONV - 1) :], ("chip", "core"), 1)
    rim8 = jnp.concatenate([jnp.zeros((8 - (CONV - 1), CHANNELS), xbc.dtype), rim_rows], axis=0)
    ext_pos = first_pos - (CONV - 1) + jnp.arange(tok + CONV - 1)
    ext_seg = segment_of(ext_pos, lengths)
    target = ext_seg[CONV - 1 :]
    kept = [
        (ext_pos[tap : tap + tok] >= 0) & (ext_seg[tap : tap + tok] == target) for tap in range(CONV)
    ]
    masks = jnp.stack(kept, axis=1).astype(jnp.float32)
    masks = jnp.concatenate([masks, jnp.zeros((tok, 128 - CONV), jnp.float32)], axis=1)
    w8 = jnp.concatenate([conv_weight, jnp.zeros((8 - CONV, CHANNELS), jnp.float32)], axis=0)
    conv = conv_part(xbc, rim8, w8, conv_bias[None, :], masks)
    step = jax.nn.softplus(dt_raw.astype(jnp.float32) + dt_bias[None, :])
    log_decay = -step * jnp.exp(a_log)[None, :]
    cum = jnp.cumsum(log_decay.reshape(nb, STRETCH, HEADS), axis=1).reshape(tok, HEADS)
    segments = segment_of(first_pos + jnp.arange(tok), lengths)
    seg_before = segment_of(first_pos + jnp.arange(nb) * STRETCH - 1, lengths)
    seg_last = segments.reshape(nb, STRETCH)[:, -1]
    cum_last = cum.reshape(nb, STRETCH, HEADS)[:, -1, :]
    block_decay = jnp.where((seg_last == seg_before)[:, None], jnp.exp(cum_last), 0.0)

    cum_g = cum.reshape(tok, GROUPS, PER_GROUP).transpose(1, 0, 2)
    dt_g = step.reshape(tok, GROUPS, PER_GROUP).transpose(1, 0, 2)
    cumt_g = cum.T.reshape(GROUPS, PER_GROUP, tok)
    segc = jnp.broadcast_to(segments[:, None], (tok, 128)).astype(jnp.int32)
    segr = jnp.broadcast_to(segments[None, :], (8, tok)).astype(jnp.int32)
    eb = jnp.broadcast_to(seg_before[:, None, None], (nb, 8, 128)).reshape(nb * 8, 128)
    eb = eb.astype(jnp.int32)
    bt = conv[:, INNER : INNER + GROUPS * STATE].T
    bdec = jnp.repeat(block_decay, HEAD_DIM, axis=1)[:, None, :]

    core_arr = lax.axis_index("core").astype(jnp.int32).reshape(1)
    local_a, cdec_a, for_other = half_states(bt, conv, dt_g, cum_g, segc, bdec, core_arr, 0)
    local_states, cdec, mine = half_states(
        bt, conv, dt_g, cum_g, segc, bdec, core_arr, 1, (local_a, cdec_a)
    )
    dsk = jnp.repeat(d_skip, HEAD_DIM)[None, :]
    def first_work():
        return intra_part(conv, dt_g, cum_g, cumt_g, segc, segr, dsk, 0)

    def second_work(done):
        return intra_part(conv, dt_g, cum_g, cumt_g, segc, segr, dsk, 1, done)

    keep, other, y_local = compose(for_other, mine, first_work, second_work)
    gain = norm_gain[None, :]
    parts = (y_local, z_gate)
    rest = (local_states, cdec, cum_g, segc, eb, gain, core_arr)
    out = mix(conv, *parts, keep, *rest, 0)
    return mix(conv, *parts, other, *rest, 1, out)


def solution(mesh):
    groups, peers = mesh.devices.shape
    split = Mesh(mesh.devices.reshape(groups, peers // 2, 2), ("group", "chip", "core"))
    rows = P(("group", "chip", "core"), None)
    return jax.shard_map(
        local,
        mesh=split,
        in_specs=(rows, rows, rows, P("group"), P(), P(), P(), P(), P(), P()),
        out_specs=rows,
        check_vma=False,
    )
```

```python
import jax
import jax.numpy as jnp
from jax import lax
from jax.experimental import pallas as pl
from jax.experimental.pallas import tpu as pltpu
from jax.sharding import Mesh, PartitionSpec as P

HEADS = 64
HEAD_DIM = 64
STATE = 256
GROUPS = 2
CONV = 4
STRETCH = 256
CHANNELS = 5120
INNER = HEADS * HEAD_DIM
PER_GROUP = HEADS // GROUPS
GROUP_COLS = INNER // GROUPS


def shifted(value, axis, by):
    peers = lax.axis_size(axis)
    pairs = [(i, i + by) for i in range(peers) if 0 <= i + by < peers]
    return lax.ppermute(value, axis, pairs)


def segment_of(positions, lengths):
    prompt_ends = jnp.cumsum(lengths)
    hits = (prompt_ends[None, :] <= positions[:, None]).astype(jnp.int32)
    return jnp.sum(hits, axis=1)


def expand_heads(v):
    heads = lax.broadcasted_iota(jnp.int32, (PER_GROUP, GROUP_COLS), 0)
    cols = lax.broadcasted_iota(jnp.int32, (PER_GROUP, GROUP_COLS), 1)
    spread = (cols // HEAD_DIM == heads).astype(jnp.bfloat16)
    hi = v.astype(jnp.bfloat16)
    rest = v - hi.astype(jnp.float32)
    mid = rest.astype(jnp.bfloat16)
    lo = (rest - mid.astype(jnp.float32)).astype(jnp.bfloat16)
    out = jnp.dot(hi, spread, preferred_element_type=jnp.float32)
    out = out + jnp.dot(mid, spread, preferred_element_type=jnp.float32)
    return out + jnp.dot(lo, spread, preferred_element_type=jnp.float32)


CONV_COLS = 640


def conv_kernel(x_ref, rim_ref, w_ref, bias_ref, m_ref, out_ref):
    x = x_ref[...].astype(jnp.float32)
    rim = rim_ref[...].astype(jnp.float32)
    rows8 = lax.broadcasted_iota(jnp.int32, rim.shape, 0)
    summed = jnp.zeros(x.shape, jnp.float32)
    top = jnp.zeros(rim.shape, jnp.float32)
    for tap in range(CONV):
        by = CONV - 1 - tap
        wk = w_ref[tap : tap + 1, :]
        kept = m_ref[:, tap : tap + 1] > 0.0
        if by == 0:
            term = x
            top_term = x[0:8]
        else:
            term = pltpu.roll(x, by, 0)
            top_term = jnp.where(rows8 < by, pltpu.roll(rim, by, 0), term[0:8])
        summed = summed + jnp.where(kept, term * wk, 0.0)
        top = top + jnp.where(kept[0:8], top_term * wk, 0.0)
    out_ref[...] = jax.nn.silu(summed + bias_ref[...]).astype(jnp.bfloat16)
    out_ref[0:8, :] = jax.nn.silu(top + bias_ref[...]).astype(jnp.bfloat16)


def conv_part(xbc, rim8, w8, bias, masks):
    tok, chans = xbc.shape
    return pl.pallas_call(
        conv_kernel,
        grid=(chans // CONV_COLS,),
        in_specs=[
            pl.BlockSpec((tok, CONV_COLS), lambda c: (0, c)),
            pl.BlockSpec((8, CONV_COLS), lambda c: (0, c)),
            pl.BlockSpec((8, CONV_COLS), lambda c: (0, c)),
            pl.BlockSpec((1, CONV_COLS), lambda c: (0, c)),
            pl.BlockSpec((tok, 128), lambda c: (0, 0)),
        ],
        out_specs=pl.BlockSpec((tok, CONV_COLS), lambda c: (0, c)),
        out_shape=jax.ShapeDtypeStruct((tok, chans), jnp.bfloat16),
    )(xbc, rim8, w8, bias, masks)


def state_kernel(
    bt_ref, x_ref, dt_ref, cum_ref, segc_ref, bdec_ref, local_ref, cdec_ref, tot_ref,
    acc_ref, dec_ref,
):
    b = pl.program_id(1)

    @pl.when(b == 0)
    def _():
        acc_ref[...] = jnp.zeros(acc_ref.shape, jnp.float32)
        dec_ref[...] = jnp.ones(dec_ref.shape, jnp.float32)

    local_ref[0] = acc_ref[...]
    cdec_ref[0] = dec_ref[...]
    cum = cum_ref[0]
    step = dt_ref[0]
    segc = segc_ref[:, 0:1]
    last = cum[STRETCH - 1 : STRETCH, :]
    seg_last = segc[STRETCH - 1 : STRETCH, :]
    w = jnp.where(segc == seg_last, jnp.exp(last - cum), 0.0)
    scaled = (x_ref[...].astype(jnp.float32) * expand_heads(step)).astype(jnp.bfloat16)
    weighted = (scaled.astype(jnp.float32) * expand_heads(w)).astype(jnp.bfloat16)
    block_state = jnp.dot(bt_ref[...], weighted, preferred_element_type=jnp.float32)
    decay = bdec_ref[0]
    acc_ref[...] = decay * acc_ref[...] + block_state
    dec_ref[...] = dec_ref[...] * decay

    @pl.when(b == pl.num_programs(1) - 1)
    def _():
        tot_ref[0, 0:STATE, :] = acc_ref[...]
        tot_ref[0, STATE : STATE + 1, :] = dec_ref[...]


def half_state_kernel(
    core_ref, bt_ref, x_ref, dt_ref, cum_ref, segc_ref, bdec_ref, *rest
):
    local_ref, cdec_ref, tot_ref, acc_ref, dec_ref = rest[-5:]
    del core_ref
    b = pl.program_id(0)

    @pl.when(b == 0)
    def _():
        acc_ref[...] = jnp.zeros(acc_ref.shape, jnp.float32)
        dec_ref[...] = jnp.ones(dec_ref.shape, jnp.float32)

    local_ref[0] = acc_ref[...]
    cdec_ref[0] = dec_ref[...]
    cum = cum_ref[0]
    step = dt_ref[0]
    segc = segc_ref[:, 0:1]
    last = cum[STRETCH - 1 : STRETCH, :]
    seg_last = segc[STRETCH - 1 : STRETCH, :]
    w = jnp.where(segc == seg_last, jnp.exp(last - cum), 0.0)
    scaled = (x_ref[...].astype(jnp.float32) * expand_heads(step)).astype(jnp.bfloat16)
    weighted = (scaled.astype(jnp.float32) * expand_heads(w)).astype(jnp.bfloat16)
    block_state = jnp.dot(bt_ref[...], weighted, preferred_element_type=jnp.float32)
    decay = bdec_ref[0]
    acc_ref[...] = decay * acc_ref[...] + block_state
    dec_ref[...] = dec_ref[...] * decay

    @pl.when(b == pl.num_programs(0) - 1)
    def _():
        tot_ref[0:STATE, :] = acc_ref[...]
        tot_ref[STATE : STATE + 1, :] = dec_ref[...]


def half_states(bt, conv, dt_g, cum_g, segc, bdec, core_arr, which, prev=None):
    tok = conv.shape[0]
    nb = tok // STRETCH

    def grp(c):
        return (which + 1 + c[0]) % GROUPS

    operands = [bt, conv, dt_g, cum_g, segc, bdec]
    specs = [
        pl.BlockSpec((STATE, STRETCH), lambda b, c: (grp(c), b)),
        pl.BlockSpec((STRETCH, GROUP_COLS), lambda b, c: (b, grp(c))),
        pl.BlockSpec((1, STRETCH, PER_GROUP), lambda b, c: (grp(c), b, 0)),
        pl.BlockSpec((1, STRETCH, PER_GROUP), lambda b, c: (grp(c), b, 0)),
        pl.BlockSpec((STRETCH, 128), lambda b, c: (b, 0)),
        pl.BlockSpec((1, 1, GROUP_COLS), lambda b, c: (b, 0, grp(c))),
    ]
    aliases = {}
    if prev is not None:
        operands += list(prev)
        specs += [pl.BlockSpec(memory_space=pl.ANY), pl.BlockSpec(memory_space=pl.ANY)]
        aliases = {len(operands) - 1: 0, len(operands): 1}
    grid_spec = pltpu.PrefetchScalarGridSpec(
        num_scalar_prefetch=1,
        grid=(nb,),
        in_specs=specs,
        out_specs=[
            pl.BlockSpec((1, STATE, GROUP_COLS), lambda b, c: (b, 0, grp(c))),
            pl.BlockSpec((1, 1, GROUP_COLS), lambda b, c: (b, 0, grp(c))),
            pl.BlockSpec((STATE + 1, GROUP_COLS), lambda b, c: (0, 0)),
        ],
        scratch_shapes=[
            pltpu.VMEM((STATE, GROUP_COLS), jnp.float32),
            pltpu.VMEM((1, GROUP_COLS), jnp.float32),
        ],
    )
    return pl.pallas_call(
        half_state_kernel,
        grid_spec=grid_spec,
        out_shape=[
            jax.ShapeDtypeStruct((nb, STATE, INNER), jnp.float32),
            jax.ShapeDtypeStruct((nb, 1, INNER), jnp.float32),
            jax.ShapeDtypeStruct((STATE + 1, GROUP_COLS), jnp.float32),
        ],
        input_output_aliases=aliases,
    )(core_arr, *operands)


def intra_kernel(
    c_ref, b_ref, x_ref, dt_ref, cum_ref, cumt_ref, segc_ref, segr_ref, dsk_ref, out_ref
):
    gram = lax.dot_general(
        c_ref[...], b_ref[...], (((1,), (1,)), ((), ())), preferred_element_type=jnp.float32
    )
    segc = segc_ref[:, 0:1]
    segr = segr_ref[0:1, :]
    rows = lax.broadcasted_iota(jnp.int32, (STRETCH, STRETCH), 0)
    cols = lax.broadcasted_iota(jnp.int32, (STRETCH, STRETCH), 1)
    gram = jnp.where((segc == segr) & (cols <= rows), gram, 0.0)
    cum = cum_ref[0]
    cumt = cumt_ref[0]
    step = dt_ref[0]
    for j in range(PER_GROUP):
        hc = slice(j * HEAD_DIM, (j + 1) * HEAD_DIM)
        gap = jnp.minimum(cum[:, j : j + 1] - cumt[j : j + 1, :], 0.0)
        weights = (gram * jnp.exp(gap)).astype(jnp.bfloat16)
        xf = x_ref[:, hc].astype(jnp.float32)
        scaled = (xf * step[:, j : j + 1]).astype(jnp.bfloat16)
        intra = jnp.dot(weights, scaled, preferred_element_type=jnp.float32)
        out_ref[:, hc] = intra + dsk_ref[:, hc] * xf


def intra_part(conv, dt_g, cum_g, cumt_g, segc, segr, dsk, g, into=None):
    tok = conv.shape[0]
    nb = tok // STRETCH
    b_col = INNER // STATE
    c_col = b_col + GROUPS
    operands = [conv, conv, conv, dt_g, cum_g, cumt_g, segc, segr, dsk]
    specs = [
        pl.BlockSpec((STRETCH, STATE), lambda b: (b, c_col + g)),
        pl.BlockSpec((STRETCH, STATE), lambda b: (b, b_col + g)),
        pl.BlockSpec((STRETCH, GROUP_COLS), lambda b: (b, g)),
        pl.BlockSpec((1, STRETCH, PER_GROUP), lambda b: (g, b, 0)),
        pl.BlockSpec((1, STRETCH, PER_GROUP), lambda b: (g, b, 0)),
        pl.BlockSpec((1, PER_GROUP, STRETCH), lambda b: (g, 0, b)),
        pl.BlockSpec((STRETCH, 128), lambda b: (b, 0)),
        pl.BlockSpec((8, STRETCH), lambda b: (0, b)),
        pl.BlockSpec((1, GROUP_COLS), lambda b: (0, g)),
    ]
    kernel = intra_kernel
    aliases = {}
    if into is not None:
        operands.append(into)
        specs.append(pl.BlockSpec(memory_space=pl.ANY))
        aliases = {len(operands) - 1: 0}

        def kernel(*refs):
            intra_kernel(*refs[:-2], refs[-1])

    return pl.pallas_call(
        kernel,
        grid=(nb,),
        in_specs=specs,
        out_specs=pl.BlockSpec((STRETCH, GROUP_COLS), lambda b: (b, g)),
        out_shape=jax.ShapeDtypeStruct((tok, INNER), jnp.float32),
        input_output_aliases=aliases,
    )(*operands)


def mix_kernel(
    c_ref, y_ref, z_ref, hin_ref, local_ref, cdec_ref, cum_ref, segc_ref, eb_ref, gain_ref,
    out_ref,
):
    state = cdec_ref[0] * hin_ref[...].astype(jnp.float32) + local_ref[0]
    segc = segc_ref[:, 0:1]
    entry = eb_ref[0:1, 0:1]
    in_weight = jnp.where(segc == entry, jnp.exp(cum_ref[0]), 0.0)
    inter = jnp.dot(c_ref[...], state.astype(jnp.bfloat16), preferred_element_type=jnp.float32)
    y = y_ref[...] + inter * expand_heads(in_weight)
    zf = z_ref[...].astype(jnp.float32)
    gated = y * (zf * jax.nn.sigmoid(zf))
    mean_square = jnp.mean(gated * gated, axis=1, keepdims=True) + 1e-05
    out_ref[...] = (gated * lax.rsqrt(mean_square) * gain_ref[...]).astype(jnp.bfloat16)


def mix(conv, y_local, z_gate, hin, local_states, cdec, cum_g, segc, eb, gain, core_arr, which,
        prev=None):
    tok = conv.shape[0]
    nb = tok // STRETCH
    c_col = INNER // STATE + GROUPS

    def grp(c):
        return (which + c[0]) % GROUPS

    operands = [conv, y_local, z_gate, hin, local_states, cdec, cum_g, segc, eb, gain]
    specs = [
        pl.BlockSpec((STRETCH, STATE), lambda b, c: (b, c_col + grp(c))),
        pl.BlockSpec((STRETCH, GROUP_COLS), lambda b, c: (b, grp(c))),
        pl.BlockSpec((STRETCH, GROUP_COLS), lambda b, c: (b, grp(c))),
        pl.BlockSpec((STATE, GROUP_COLS), lambda b, c: (0, 0)),
        pl.BlockSpec((1, STATE, GROUP_COLS), lambda b, c: (b, 0, grp(c))),
        pl.BlockSpec((1, 1, GROUP_COLS), lambda b, c: (b, 0, grp(c))),
        pl.BlockSpec((1, STRETCH, PER_GROUP), lambda b, c: (grp(c), b, 0)),
        pl.BlockSpec((STRETCH, 128), lambda b, c: (b, 0)),
        pl.BlockSpec((8, 128), lambda b, c: (b, 0)),
        pl.BlockSpec((1, GROUP_COLS), lambda b, c: (0, grp(c))),
    ]
    kernel = mix_kernel
    aliases = {}
    if prev is not None:
        operands.append(prev)
        specs.append(pl.BlockSpec(memory_space=pl.ANY))
        aliases = {len(operands): 0}

        def kernel(*refs):
            mix_kernel(*refs[:-2], refs[-1])

    def with_core(core_ref, *refs):
        del core_ref
        kernel(*refs)

    grid_spec = pltpu.PrefetchScalarGridSpec(
        num_scalar_prefetch=1,
        grid=(nb,),
        in_specs=specs,
        out_specs=pl.BlockSpec((STRETCH, GROUP_COLS), lambda b, c: (b, grp(c))),
    )
    return pl.pallas_call(
        with_core,
        grid_spec=grid_spec,
        out_shape=jax.ShapeDtypeStruct((tok, INNER), jnp.bfloat16),
        input_output_aliases=aliases,
    )(core_arr, *operands)


def scan_kernel(got_ref, out_ref):
    peers = got_ref.shape[0]

    def body(d, carry):
        out_ref[d] = carry.astype(jnp.bfloat16)
        decay = got_ref[d, STATE : STATE + 1, :].astype(jnp.float32) + got_ref[
            d, STATE + 1 : STATE + 2, :
        ].astype(jnp.float32)
        return decay * carry + got_ref[d, 0:STATE, :].astype(jnp.float32)

    lax.fori_loop(0, peers, body, jnp.zeros(out_ref.shape[1:], jnp.float32))


def swap_cores(value):
    return lax.ppermute(value, "core", [(0, 1), (1, 0)])


def tie(value, *after):
    def kernel(*refs):
        del refs

    return pl.pallas_call(
        kernel,
        in_specs=[pl.BlockSpec(memory_space=pl.ANY) for _ in range(1 + len(after))],
        out_specs=pl.BlockSpec(memory_space=pl.ANY),
        out_shape=jax.ShapeDtypeStruct(value.shape, value.dtype),
        input_output_aliases={0: 0},
    )(value, *after)


def compose(for_other, mine, first_work, second_work):
    core = lax.axis_index("core")
    chips = lax.axis_size("chip")
    half = GROUP_COLS
    width = half // chips
    theirs = swap_cores(for_other)
    first = jnp.where(core == 0, mine, theirs)
    second = jnp.where(core == 0, theirs, mine)
    first_decay = first[STATE:]
    chip_state = second[STATE:] * first[:STATE] + second[:STATE]
    chip_decay = first_decay * second[STATE:]
    decay_hi = chip_decay.astype(jnp.bfloat16)
    decay_lo = (chip_decay - decay_hi.astype(jnp.float32)).astype(jnp.bfloat16)
    payload = jnp.concatenate(
        [chip_state.astype(jnp.bfloat16), decay_hi, decay_lo], axis=0
    ).reshape(STATE + 2, chips, width).transpose(1, 0, 2)
    work = first_work()
    got = tie(lax.all_to_all(payload, "chip", split_axis=0, concat_axis=0, tiled=True), work)
    entering = pl.pallas_call(
        scan_kernel,
        out_shape=jax.ShapeDtypeStruct((chips, STATE, width), jnp.bfloat16),
    )(got)
    work = second_work(work)
    back = tie(lax.all_to_all(entering, "chip", split_axis=0, concat_axis=0, tiled=True), work)
    chip_in = back.transpose(1, 0, 2).reshape(STATE, half).astype(jnp.float32)
    later_in = first_decay * chip_in + first[:STATE]
    keep = jnp.where(core == 0, chip_in, later_in).astype(jnp.bfloat16)
    other = swap_cores(jnp.where(core == 0, later_in, chip_in).astype(jnp.bfloat16))
    return keep, other, work


def local(xbc, z_gate, dt_raw, lengths, conv_weight, conv_bias, dt_bias, a_log, d_skip, norm_gain):
    tok = xbc.shape[0]
    nb = tok // STRETCH
    first_pos = (lax.axis_index("chip") * lax.axis_size("core") + lax.axis_index("core")) * tok
    rim_rows = shifted(xbc[tok - (CONV - 1) :], ("chip", "core"), 1)
    rim8 = jnp.zeros((8, CHANNELS), xbc.dtype)
    ext_pos = first_pos - (CONV - 1) + jnp.arange(tok + CONV - 1)
    ext_seg = segment_of(ext_pos, lengths)
    target = ext_seg[CONV - 1 :]
    kept = [
        (ext_pos[tap : tap + tok] >= 0) & (ext_seg[tap : tap + tok] == target) for tap in range(CONV)
    ]
    masks = jnp.stack(kept, axis=1).astype(jnp.float32)
    masks = jnp.concatenate([masks, jnp.zeros((tok, 128 - CONV), jnp.float32)], axis=1)
    w8 = jnp.concatenate([conv_weight, jnp.zeros((8 - CONV, CHANNELS), jnp.float32)], axis=0)
    conv = conv_part(xbc, rim8, w8, conv_bias[None, :], masks)
    head = jnp.concatenate([rim_rows, xbc[: CONV - 1]], axis=0).astype(jnp.float32)
    summed = conv_bias[None, :]
    for tap in range(CONV):
        term = head[tap : tap + CONV - 1] * conv_weight[tap][None, :]
        summed = summed + jnp.where(kept[tap][: CONV - 1, None], term, 0.0)
    conv = lax.dynamic_update_slice(conv, jax.nn.silu(summed).astype(jnp.bfloat16), (0, 0))
    step = jax.nn.softplus(dt_raw.astype(jnp.float32) + dt_bias[None, :])
    log_decay = -step * jnp.exp(a_log)[None, :]
    cum = jnp.cumsum(log_decay.reshape(nb, STRETCH, HEADS), axis=1).reshape(tok, HEADS)
    segments = segment_of(first_pos + jnp.arange(tok), lengths)
    seg_before = segment_of(first_pos + jnp.arange(nb) * STRETCH - 1, lengths)
    seg_last = segments.reshape(nb, STRETCH)[:, -1]
    cum_last = cum.reshape(nb, STRETCH, HEADS)[:, -1, :]
    block_decay = jnp.where((seg_last == seg_before)[:, None], jnp.exp(cum_last), 0.0)

    cum_g = cum.reshape(tok, GROUPS, PER_GROUP).transpose(1, 0, 2)
    dt_g = step.reshape(tok, GROUPS, PER_GROUP).transpose(1, 0, 2)
    cumt_g = cum.T.reshape(GROUPS, PER_GROUP, tok)
    segc = jnp.broadcast_to(segments[:, None], (tok, 128)).astype(jnp.int32)
    segr = jnp.broadcast_to(segments[None, :], (8, tok)).astype(jnp.int32)
    eb = jnp.broadcast_to(seg_before[:, None, None], (nb, 8, 128)).reshape(nb * 8, 128)
    eb = eb.astype(jnp.int32)
    bt = conv[:, INNER : INNER + GROUPS * STATE].T
    bdec = jnp.repeat(block_decay, HEAD_DIM, axis=1)[:, None, :]

    core_arr = lax.axis_index("core").astype(jnp.int32).reshape(1)
    local_a, cdec_a, for_other = half_states(bt, conv, dt_g, cum_g, segc, bdec, core_arr, 0)
    local_states, cdec, mine = half_states(
        bt, conv, dt_g, cum_g, segc, bdec, core_arr, 1, (local_a, cdec_a)
    )
    dsk = jnp.repeat(d_skip, HEAD_DIM)[None, :]
    def first_work():
        return intra_part(conv, dt_g, cum_g, cumt_g, segc, segr, dsk, 0)

    def second_work(done):
        return intra_part(conv, dt_g, cum_g, cumt_g, segc, segr, dsk, 1, done)

    keep, other, y_local = compose(for_other, mine, first_work, second_work)
    gain = norm_gain[None, :]
    parts = (y_local, z_gate)
    rest = (local_states, cdec, cum_g, segc, eb, gain, core_arr)
    out = mix(conv, *parts, keep, *rest, 0)
    return mix(conv, *parts, other, *rest, 1, out)


def solution(mesh):
    groups, peers = mesh.devices.shape
    split = Mesh(mesh.devices.reshape(groups, peers // 2, 2), ("group", "chip", "core"))
    rows = P(("group", "chip", "core"), None)
    return jax.shard_map(
        local,
        mesh=split,
        in_specs=(rows, rows, rows, P("group"), P(), P(), P(), P(), P(), P()),
        out_specs=rows,
        check_vma=False,
    )
```

```python
import jax
import jax.numpy as jnp
from jax import lax
from jax.experimental import pallas as pl
from jax.experimental.pallas import tpu as pltpu
from jax.sharding import Mesh, PartitionSpec as P

HEADS = 64
HEAD_DIM = 64
STATE = 256
GROUPS = 2
CONV = 4
STRETCH = 256
CHANNELS = 5120
INNER = HEADS * HEAD_DIM
PER_GROUP = HEADS // GROUPS
GROUP_COLS = INNER // GROUPS


def shifted(value, axis, by):
    peers = lax.axis_size(axis)
    pairs = [(i, i + by) for i in range(peers) if 0 <= i + by < peers]
    return lax.ppermute(value, axis, pairs)


def segment_of(positions, lengths):
    prompt_ends = jnp.cumsum(lengths)
    hits = (prompt_ends[None, :] <= positions[:, None]).astype(jnp.int32)
    return jnp.sum(hits, axis=1)


def expand_heads(v):
    heads = lax.broadcasted_iota(jnp.int32, (PER_GROUP, GROUP_COLS), 0)
    cols = lax.broadcasted_iota(jnp.int32, (PER_GROUP, GROUP_COLS), 1)
    spread = (cols // HEAD_DIM == heads).astype(jnp.bfloat16)
    hi = v.astype(jnp.bfloat16)
    rest = v - hi.astype(jnp.float32)
    mid = rest.astype(jnp.bfloat16)
    lo = (rest - mid.astype(jnp.float32)).astype(jnp.bfloat16)
    out = jnp.dot(hi, spread, preferred_element_type=jnp.float32)
    out = out + jnp.dot(mid, spread, preferred_element_type=jnp.float32)
    return out + jnp.dot(lo, spread, preferred_element_type=jnp.float32)


CONV_COLS = 640


def conv_kernel(x_ref, rim_ref, w_ref, bias_ref, m_ref, out_ref):
    x = x_ref[...].astype(jnp.float32)
    rim = rim_ref[...].astype(jnp.float32)
    rows8 = lax.broadcasted_iota(jnp.int32, rim.shape, 0)
    summed = jnp.zeros(x.shape, jnp.float32)
    top = jnp.zeros(rim.shape, jnp.float32)
    for tap in range(CONV):
        by = CONV - 1 - tap
        wk = w_ref[tap : tap + 1, :]
        kept = m_ref[:, tap : tap + 1] > 0.0
        if by == 0:
            term = x
            top_term = x[0:8]
        else:
            term = pltpu.roll(x, by, 0)
            top_term = jnp.where(rows8 < by, pltpu.roll(rim, by, 0), term[0:8])
        summed = summed + jnp.where(kept, term * wk, 0.0)
        top = top + jnp.where(kept[0:8], top_term * wk, 0.0)
    out_ref[...] = jax.nn.silu(summed + bias_ref[...]).astype(jnp.bfloat16)
    out_ref[0:8, :] = jax.nn.silu(top + bias_ref[...]).astype(jnp.bfloat16)


def conv_part(xbc, rim8, w8, bias, masks):
    tok, chans = xbc.shape
    return pl.pallas_call(
        conv_kernel,
        grid=(chans // CONV_COLS,),
        in_specs=[
            pl.BlockSpec((tok, CONV_COLS), lambda c: (0, c)),
            pl.BlockSpec((8, CONV_COLS), lambda c: (0, c)),
            pl.BlockSpec((CONV, CONV_COLS), lambda c: (0, c)),
            pl.BlockSpec((1, CONV_COLS), lambda c: (0, c)),
            pl.BlockSpec((tok, CONV), lambda c: (0, 0)),
        ],
        out_specs=pl.BlockSpec((tok, CONV_COLS), lambda c: (0, c)),
        out_shape=jax.ShapeDtypeStruct((tok, chans), jnp.bfloat16),
    )(xbc, rim8, w8, bias, masks)


def state_kernel(
    bt_ref, x_ref, dt_ref, cum_ref, segc_ref, bdec_ref, local_ref, cdec_ref, tot_ref,
    acc_ref, dec_ref,
):
    b = pl.program_id(1)

    @pl.when(b == 0)
    def _():
        acc_ref[...] = jnp.zeros(acc_ref.shape, jnp.float32)
        dec_ref[...] = jnp.ones(dec_ref.shape, jnp.float32)

    local_ref[0] = acc_ref[...]
    cdec_ref[0] = dec_ref[...]
    cum = cum_ref[0]
    step = dt_ref[0]
    segc = segc_ref[:, 0:1]
    last = cum[STRETCH - 1 : STRETCH, :]
    seg_last = segc[STRETCH - 1 : STRETCH, :]
    w = jnp.where(segc == seg_last, jnp.exp(last - cum), 0.0)
    scaled = (x_ref[...].astype(jnp.float32) * expand_heads(step)).astype(jnp.bfloat16)
    weighted = (scaled.astype(jnp.float32) * expand_heads(w)).astype(jnp.bfloat16)
    block_state = jnp.dot(bt_ref[...], weighted, preferred_element_type=jnp.float32)
    decay = bdec_ref[0]
    acc_ref[...] = decay * acc_ref[...] + block_state
    dec_ref[...] = dec_ref[...] * decay

    @pl.when(b == pl.num_programs(1) - 1)
    def _():
        tot_ref[0, 0:STATE, :] = acc_ref[...]
        tot_ref[0, STATE : STATE + 1, :] = dec_ref[...]


def half_state_kernel(
    core_ref, bt_ref, x_ref, dt_ref, cum_ref, segc_ref, bdec_ref, *rest
):
    local_ref, cdec_ref, tot_ref, acc_ref, dec_ref = rest[-5:]
    del core_ref
    b = pl.program_id(0)

    @pl.when(b == 0)
    def _():
        acc_ref[...] = jnp.zeros(acc_ref.shape, jnp.float32)
        dec_ref[...] = jnp.ones(dec_ref.shape, jnp.float32)

    local_ref[0] = acc_ref[...]
    cdec_ref[0] = dec_ref[...]
    cum = cum_ref[0]
    step = dt_ref[0]
    segc = segc_ref[:, 0:1]
    last = cum[STRETCH - 1 : STRETCH, :]
    seg_last = segc[STRETCH - 1 : STRETCH, :]
    w = jnp.where(segc == seg_last, jnp.exp(last - cum), 0.0)
    scaled = (x_ref[...].astype(jnp.float32) * expand_heads(step)).astype(jnp.bfloat16)
    weighted = (scaled.astype(jnp.float32) * expand_heads(w)).astype(jnp.bfloat16)
    block_state = jnp.dot(bt_ref[...], weighted, preferred_element_type=jnp.float32)
    decay = bdec_ref[0]
    acc_ref[...] = decay * acc_ref[...] + block_state
    dec_ref[...] = dec_ref[...] * decay

    @pl.when(b == pl.num_programs(0) - 1)
    def _():
        tot_ref[0:STATE, :] = acc_ref[...]
        tot_ref[STATE : STATE + 1, :] = dec_ref[...]


def half_states(bt, conv, dt_g, cum_g, segc, bdec, core_arr, which, prev=None):
    tok = conv.shape[0]
    nb = tok // STRETCH

    def grp(c):
        return (which + 1 + c[0]) % GROUPS

    operands = [bt, conv, dt_g, cum_g, segc, bdec]
    specs = [
        pl.BlockSpec((STATE, STRETCH), lambda b, c: (grp(c), b)),
        pl.BlockSpec((STRETCH, GROUP_COLS), lambda b, c: (b, grp(c))),
        pl.BlockSpec((1, STRETCH, PER_GROUP), lambda b, c: (grp(c), b, 0)),
        pl.BlockSpec((1, STRETCH, PER_GROUP), lambda b, c: (grp(c), b, 0)),
        pl.BlockSpec((STRETCH, 128), lambda b, c: (b, 0)),
        pl.BlockSpec((1, 1, GROUP_COLS), lambda b, c: (b, 0, grp(c))),
    ]
    aliases = {}
    if prev is not None:
        operands += list(prev)
        specs += [pl.BlockSpec(memory_space=pl.ANY), pl.BlockSpec(memory_space=pl.ANY)]
        aliases = {len(operands) - 1: 0, len(operands): 1}
    grid_spec = pltpu.PrefetchScalarGridSpec(
        num_scalar_prefetch=1,
        grid=(nb,),
        in_specs=specs,
        out_specs=[
            pl.BlockSpec((1, STATE, GROUP_COLS), lambda b, c: (b, 0, grp(c))),
            pl.BlockSpec((1, 1, GROUP_COLS), lambda b, c: (b, 0, grp(c))),
            pl.BlockSpec((STATE + 1, GROUP_COLS), lambda b, c: (0, 0)),
        ],
        scratch_shapes=[
            pltpu.VMEM((STATE, GROUP_COLS), jnp.float32),
            pltpu.VMEM((1, GROUP_COLS), jnp.float32),
        ],
    )
    return pl.pallas_call(
        half_state_kernel,
        grid_spec=grid_spec,
        out_shape=[
            jax.ShapeDtypeStruct((nb, STATE, INNER), jnp.float32),
            jax.ShapeDtypeStruct((nb, 1, INNER), jnp.float32),
            jax.ShapeDtypeStruct((STATE + 1, GROUP_COLS), jnp.float32),
        ],
        input_output_aliases=aliases,
    )(core_arr, *operands)


def intra_kernel(
    c_ref, b_ref, x_ref, dt_ref, cum_ref, cumt_ref, segc_ref, segr_ref, dsk_ref, out_ref
):
    gram = lax.dot_general(
        c_ref[...], b_ref[...], (((1,), (1,)), ((), ())), preferred_element_type=jnp.float32
    )
    segc = segc_ref[:, 0:1]
    segr = segr_ref[0:1, :]
    rows = lax.broadcasted_iota(jnp.int32, (STRETCH, STRETCH), 0)
    cols = lax.broadcasted_iota(jnp.int32, (STRETCH, STRETCH), 1)
    gram = jnp.where((segc == segr) & (cols <= rows), gram, 0.0)
    cum = cum_ref[0]
    cumt = cumt_ref[0]
    step = dt_ref[0]
    for j in range(PER_GROUP):
        hc = slice(j * HEAD_DIM, (j + 1) * HEAD_DIM)
        gap = jnp.minimum(cum[:, j : j + 1] - cumt[j : j + 1, :], 0.0)
        weights = (gram * jnp.exp(gap)).astype(jnp.bfloat16)
        xf = x_ref[:, hc].astype(jnp.float32)
        scaled = (xf * step[:, j : j + 1]).astype(jnp.bfloat16)
        intra = jnp.dot(weights, scaled, preferred_element_type=jnp.float32)
        out_ref[:, hc] = intra + dsk_ref[:, hc] * xf


def intra_part(conv, dt_g, cum_g, cumt_g, segc, segr, dsk, g, into=None):
    tok = conv.shape[0]
    nb = tok // STRETCH
    b_col = INNER // STATE
    c_col = b_col + GROUPS
    operands = [conv, conv, conv, dt_g, cum_g, cumt_g, segc, segr, dsk]
    specs = [
        pl.BlockSpec((STRETCH, STATE), lambda b: (b, c_col + g)),
        pl.BlockSpec((STRETCH, STATE), lambda b: (b, b_col + g)),
        pl.BlockSpec((STRETCH, GROUP_COLS), lambda b: (b, g)),
        pl.BlockSpec((1, STRETCH, PER_GROUP), lambda b: (g, b, 0)),
        pl.BlockSpec((1, STRETCH, PER_GROUP), lambda b: (g, b, 0)),
        pl.BlockSpec((1, PER_GROUP, STRETCH), lambda b: (g, 0, b)),
        pl.BlockSpec((STRETCH, 128), lambda b: (b, 0)),
        pl.BlockSpec((8, STRETCH), lambda b: (0, b)),
        pl.BlockSpec((1, GROUP_COLS), lambda b: (0, g)),
    ]
    kernel = intra_kernel
    aliases = {}
    if into is not None:
        operands.append(into)
        specs.append(pl.BlockSpec(memory_space=pl.ANY))
        aliases = {len(operands) - 1: 0}

        def kernel(*refs):
            intra_kernel(*refs[:-2], refs[-1])

    return pl.pallas_call(
        kernel,
        grid=(nb,),
        in_specs=specs,
        out_specs=pl.BlockSpec((STRETCH, GROUP_COLS), lambda b: (b, g)),
        out_shape=jax.ShapeDtypeStruct((tok, INNER), jnp.float32),
        input_output_aliases=aliases,
    )(*operands)


def mix_kernel(
    c_ref, y_ref, z_ref, hin_ref, local_ref, cdec_ref, cum_ref, segc_ref, eb_ref, gain_ref,
    out_ref,
):
    state = cdec_ref[0] * hin_ref[...].astype(jnp.float32) + local_ref[0]
    segc = segc_ref[:, 0:1]
    entry = eb_ref[0:1, 0:1]
    in_weight = jnp.where(segc == entry, jnp.exp(cum_ref[0]), 0.0)
    inter = jnp.dot(c_ref[...], state.astype(jnp.bfloat16), preferred_element_type=jnp.float32)
    y = y_ref[...] + inter * expand_heads(in_weight)
    zf = z_ref[...].astype(jnp.float32)
    gated = y * (zf * jax.nn.sigmoid(zf))
    mean_square = jnp.mean(gated * gated, axis=1, keepdims=True) + 1e-05
    out_ref[...] = (gated * lax.rsqrt(mean_square) * gain_ref[...]).astype(jnp.bfloat16)


def mix(conv, y_local, z_gate, hin, local_states, cdec, cum_g, segc, eb, gain, core_arr, which,
        prev=None):
    tok = conv.shape[0]
    nb = tok // STRETCH
    c_col = INNER // STATE + GROUPS

    def grp(c):
        return (which + c[0]) % GROUPS

    operands = [conv, y_local, z_gate, hin, local_states, cdec, cum_g, segc, eb, gain]
    specs = [
        pl.BlockSpec((STRETCH, STATE), lambda b, c: (b, c_col + grp(c))),
        pl.BlockSpec((STRETCH, GROUP_COLS), lambda b, c: (b, grp(c))),
        pl.BlockSpec((STRETCH, GROUP_COLS), lambda b, c: (b, grp(c))),
        pl.BlockSpec((STATE, GROUP_COLS), lambda b, c: (0, 0)),
        pl.BlockSpec((1, STATE, GROUP_COLS), lambda b, c: (b, 0, grp(c))),
        pl.BlockSpec((1, 1, GROUP_COLS), lambda b, c: (b, 0, grp(c))),
        pl.BlockSpec((1, STRETCH, PER_GROUP), lambda b, c: (grp(c), b, 0)),
        pl.BlockSpec((STRETCH, 128), lambda b, c: (b, 0)),
        pl.BlockSpec((8, 128), lambda b, c: (b, 0)),
        pl.BlockSpec((1, GROUP_COLS), lambda b, c: (0, grp(c))),
    ]
    kernel = mix_kernel
    aliases = {}
    if prev is not None:
        operands.append(prev)
        specs.append(pl.BlockSpec(memory_space=pl.ANY))
        aliases = {len(operands): 0}

        def kernel(*refs):
            mix_kernel(*refs[:-2], refs[-1])

    def with_core(core_ref, *refs):
        del core_ref
        kernel(*refs)

    grid_spec = pltpu.PrefetchScalarGridSpec(
        num_scalar_prefetch=1,
        grid=(nb,),
        in_specs=specs,
        out_specs=pl.BlockSpec((STRETCH, GROUP_COLS), lambda b, c: (b, grp(c))),
    )
    return pl.pallas_call(
        with_core,
        grid_spec=grid_spec,
        out_shape=jax.ShapeDtypeStruct((tok, INNER), jnp.bfloat16),
        input_output_aliases=aliases,
    )(core_arr, *operands)


def scan_kernel(got_ref, out_ref):
    peers = got_ref.shape[0]

    def body(d, carry):
        out_ref[d] = carry.astype(jnp.bfloat16)
        decay = got_ref[d, STATE : STATE + 1, :].astype(jnp.float32) + got_ref[
            d, STATE + 1 : STATE + 2, :
        ].astype(jnp.float32)
        return decay * carry + got_ref[d, 0:STATE, :].astype(jnp.float32)

    lax.fori_loop(0, peers, body, jnp.zeros(out_ref.shape[1:], jnp.float32))


def swap_cores(value):
    return lax.ppermute(value, "core", [(0, 1), (1, 0)])


def tie(value, *after):
    def kernel(*refs):
        del refs

    return pl.pallas_call(
        kernel,
        in_specs=[pl.BlockSpec(memory_space=pl.ANY) for _ in range(1 + len(after))],
        out_specs=pl.BlockSpec(memory_space=pl.ANY),
        out_shape=jax.ShapeDtypeStruct(value.shape, value.dtype),
        input_output_aliases={0: 0},
    )(value, *after)


def compose(for_other, mine, first_work, second_work):
    core = lax.axis_index("core")
    chips = lax.axis_size("chip")
    half = GROUP_COLS
    width = half // chips
    theirs = swap_cores(for_other)
    first = jnp.where(core == 0, mine, theirs)
    second = jnp.where(core == 0, theirs, mine)
    first_decay = first[STATE:]
    chip_state = second[STATE:] * first[:STATE] + second[:STATE]
    chip_decay = first_decay * second[STATE:]
    decay_hi = chip_decay.astype(jnp.bfloat16)
    decay_lo = (chip_decay - decay_hi.astype(jnp.float32)).astype(jnp.bfloat16)
    payload = jnp.concatenate(
        [chip_state.astype(jnp.bfloat16), decay_hi, decay_lo], axis=0
    ).reshape(STATE + 2, chips, width).transpose(1, 0, 2)
    work = first_work()
    got = tie(lax.all_to_all(payload, "chip", split_axis=0, concat_axis=0, tiled=True), work)
    entering = pl.pallas_call(
        scan_kernel,
        out_shape=jax.ShapeDtypeStruct((chips, STATE, width), jnp.bfloat16),
    )(got)
    work = second_work(work)
    back = tie(lax.all_to_all(entering, "chip", split_axis=0, concat_axis=0, tiled=True), work)
    chip_in = back.transpose(1, 0, 2).reshape(STATE, half).astype(jnp.float32)
    later_in = first_decay * chip_in + first[:STATE]
    keep = jnp.where(core == 0, chip_in, later_in).astype(jnp.bfloat16)
    other = swap_cores(jnp.where(core == 0, later_in, chip_in).astype(jnp.bfloat16))
    return keep, other, work


def local(xbc, z_gate, dt_raw, lengths, conv_weight, conv_bias, dt_bias, a_log, d_skip, norm_gain):
    tok = xbc.shape[0]
    nb = tok // STRETCH
    first_pos = (lax.axis_index("chip") * lax.axis_size("core") + lax.axis_index("core")) * tok
    rim_rows = shifted(xbc[tok - (CONV - 1) :], ("chip", "core"), 1)
    rim8 = jnp.concatenate([jnp.zeros((8 - (CONV - 1), CHANNELS), xbc.dtype), rim_rows], axis=0)
    ext_pos = first_pos - (CONV - 1) + jnp.arange(tok + CONV - 1)
    ext_seg = segment_of(ext_pos, lengths)
    target = ext_seg[CONV - 1 :]
    kept = [
        (ext_pos[tap : tap + tok] >= 0) & (ext_seg[tap : tap + tok] == target) for tap in range(CONV)
    ]
    masks = jnp.stack(kept, axis=1).astype(jnp.float32)
    conv = conv_part(xbc, rim8, conv_weight, conv_bias[None, :], masks)
    step = jax.nn.softplus(dt_raw.astype(jnp.float32) + dt_bias[None, :])
    log_decay = -step * jnp.exp(a_log)[None, :]
    cum = jnp.cumsum(log_decay.reshape(nb, STRETCH, HEADS), axis=1).reshape(tok, HEADS)
    segments = segment_of(first_pos + jnp.arange(tok), lengths)
    seg_before = segment_of(first_pos + jnp.arange(nb) * STRETCH - 1, lengths)
    seg_last = segments.reshape(nb, STRETCH)[:, -1]
    cum_last = cum.reshape(nb, STRETCH, HEADS)[:, -1, :]
    block_decay = jnp.where((seg_last == seg_before)[:, None], jnp.exp(cum_last), 0.0)

    cum_g = cum.reshape(tok, GROUPS, PER_GROUP).transpose(1, 0, 2)
    dt_g = step.reshape(tok, GROUPS, PER_GROUP).transpose(1, 0, 2)
    cumt_g = cum.T.reshape(GROUPS, PER_GROUP, tok)
    segc = jnp.broadcast_to(segments[:, None], (tok, 128)).astype(jnp.int32)
    segr = jnp.broadcast_to(segments[None, :], (8, tok)).astype(jnp.int32)
    eb = jnp.broadcast_to(seg_before[:, None, None], (nb, 8, 128)).reshape(nb * 8, 128)
    eb = eb.astype(jnp.int32)
    bt = conv[:, INNER : INNER + GROUPS * STATE].T
    bdec = jnp.repeat(block_decay, HEAD_DIM, axis=1)[:, None, :]

    core_arr = lax.axis_index("core").astype(jnp.int32).reshape(1)
    local_a, cdec_a, for_other = half_states(bt, conv, dt_g, cum_g, segc, bdec, core_arr, 0)
    local_states, cdec, mine = half_states(
        bt, conv, dt_g, cum_g, segc, bdec, core_arr, 1, (local_a, cdec_a)
    )
    dsk = jnp.repeat(d_skip, HEAD_DIM)[None, :]
    def first_work():
        return intra_part(conv, dt_g, cum_g, cumt_g, segc, segr, dsk, 0)

    def second_work(done):
        return intra_part(conv, dt_g, cum_g, cumt_g, segc, segr, dsk, 1, done)

    keep, other, y_local = compose(for_other, mine, first_work, second_work)
    gain = norm_gain[None, :]
    parts = (y_local, z_gate)
    rest = (local_states, cdec, cum_g, segc, eb, gain, core_arr)
    out = mix(conv, *parts, keep, *rest, 0)
    return mix(conv, *parts, other, *rest, 1, out)


def solution(mesh):
    groups, peers = mesh.devices.shape
    split = Mesh(mesh.devices.reshape(groups, peers // 2, 2), ("group", "chip", "core"))
    rows = P(("group", "chip", "core"), None)
    return jax.shard_map(
        local,
        mesh=split,
        in_specs=(rows, rows, rows, P("group"), P(), P(), P(), P(), P(), P()),
        out_specs=rows,
        check_vma=False,
    )
```

```python
import jax
import jax.numpy as jnp
from jax import lax
from jax.experimental import pallas as pl
from jax.experimental.pallas import tpu as pltpu
from jax.sharding import Mesh, PartitionSpec as P

HEADS = 64
HEAD_DIM = 64
STATE = 256
GROUPS = 2
CONV = 4
STRETCH = 256
CHANNELS = 5120
INNER = HEADS * HEAD_DIM
PER_GROUP = HEADS // GROUPS
GROUP_COLS = INNER // GROUPS


def shifted(value, axis, by):
    peers = lax.axis_size(axis)
    pairs = [(i, i + by) for i in range(peers) if 0 <= i + by < peers]
    return lax.ppermute(value, axis, pairs)


def segment_of(positions, lengths):
    prompt_ends = jnp.cumsum(lengths)
    hits = (prompt_ends[None, :] <= positions[:, None]).astype(jnp.int32)
    return jnp.sum(hits, axis=1)


def expand_heads(v):
    heads = lax.broadcasted_iota(jnp.int32, (PER_GROUP, GROUP_COLS), 0)
    cols = lax.broadcasted_iota(jnp.int32, (PER_GROUP, GROUP_COLS), 1)
    spread = (cols // HEAD_DIM == heads).astype(jnp.bfloat16)
    hi = v.astype(jnp.bfloat16)
    rest = v - hi.astype(jnp.float32)
    mid = rest.astype(jnp.bfloat16)
    lo = (rest - mid.astype(jnp.float32)).astype(jnp.bfloat16)
    out = jnp.dot(hi, spread, preferred_element_type=jnp.float32)
    out = out + jnp.dot(mid, spread, preferred_element_type=jnp.float32)
    return out + jnp.dot(lo, spread, preferred_element_type=jnp.float32)


CONV_COLS = 640


def conv_kernel(x_ref, rim_ref, w_ref, bias_ref, m_ref, out_ref):
    x = x_ref[...].astype(jnp.float32)
    rim = rim_ref[...].astype(jnp.float32)
    rows8 = lax.broadcasted_iota(jnp.int32, rim.shape, 0)
    summed = jnp.zeros(x.shape, jnp.float32)
    top = jnp.zeros(rim.shape, jnp.float32)
    for tap in range(CONV):
        by = CONV - 1 - tap
        wk = w_ref[tap : tap + 1, :]
        kept = m_ref[:, tap : tap + 1] > 0.0
        if by == 0:
            term = x
            top_term = x[0:8]
        else:
            term = pltpu.roll(x, by, 0)
            top_term = jnp.where(rows8 < by, pltpu.roll(rim, by, 0), term[0:8])
        summed = summed + jnp.where(kept, term * wk, 0.0)
        top = top + jnp.where(kept[0:8], top_term * wk, 0.0)
    out_ref[...] = jax.nn.silu(summed + bias_ref[...]).astype(jnp.bfloat16)
    out_ref[0:8, :] = jax.nn.silu(top + bias_ref[...]).astype(jnp.bfloat16)


def conv_part(xbc, rim8, w8, bias, masks):
    tok, chans = xbc.shape
    return pl.pallas_call(
        conv_kernel,
        grid=(chans // CONV_COLS,),
        in_specs=[
            pl.BlockSpec((tok, CONV_COLS), lambda c: (0, c)),
            pl.BlockSpec((8, CONV_COLS), lambda c: (0, c)),
            pl.BlockSpec((CONV, CONV_COLS), lambda c: (0, c)),
            pl.BlockSpec((1, CONV_COLS), lambda c: (0, c)),
            pl.BlockSpec((tok, CONV), lambda c: (0, 0)),
        ],
        out_specs=pl.BlockSpec((tok, CONV_COLS), lambda c: (0, c)),
        out_shape=jax.ShapeDtypeStruct((tok, chans), jnp.bfloat16),
    )(xbc, rim8, w8, bias, masks)


def state_kernel(
    bt_ref, x_ref, dt_ref, cum_ref, segc_ref, bdec_ref, local_ref, cdec_ref, tot_ref,
    acc_ref, dec_ref,
):
    b = pl.program_id(1)

    @pl.when(b == 0)
    def _():
        acc_ref[...] = jnp.zeros(acc_ref.shape, jnp.float32)
        dec_ref[...] = jnp.ones(dec_ref.shape, jnp.float32)

    local_ref[0] = acc_ref[...]
    cdec_ref[0] = dec_ref[...]
    cum = cum_ref[0]
    step = dt_ref[0]
    segc = segc_ref[:, 0:1]
    last = cum[STRETCH - 1 : STRETCH, :]
    seg_last = segc[STRETCH - 1 : STRETCH, :]
    w = jnp.where(segc == seg_last, jnp.exp(last - cum), 0.0)
    scaled = (x_ref[...].astype(jnp.float32) * expand_heads(step)).astype(jnp.bfloat16)
    weighted = (scaled.astype(jnp.float32) * expand_heads(w)).astype(jnp.bfloat16)
    block_state = jnp.dot(bt_ref[...], weighted, preferred_element_type=jnp.float32)
    decay = bdec_ref[0]
    acc_ref[...] = decay * acc_ref[...] + block_state
    dec_ref[...] = dec_ref[...] * decay

    @pl.when(b == pl.num_programs(1) - 1)
    def _():
        tot_ref[0, 0:STATE, :] = acc_ref[...]
        tot_ref[0, STATE : STATE + 1, :] = dec_ref[...]


def half_state_kernel(
    core_ref, bt_ref, x_ref, dt_ref, cum_ref, segc_ref, bdec_ref, *rest
):
    local_ref, cdec_ref, tot_ref, acc_ref, dec_ref = rest[-5:]
    del core_ref
    b = pl.program_id(0)

    @pl.when(b == 0)
    def _():
        acc_ref[...] = jnp.zeros(acc_ref.shape, jnp.float32)
        dec_ref[...] = jnp.ones(dec_ref.shape, jnp.float32)

    local_ref[0] = acc_ref[...]
    cdec_ref[0] = dec_ref[...]
    cum = cum_ref[0]
    step = dt_ref[0]
    segc = segc_ref[:, 0:1]
    last = cum[STRETCH - 1 : STRETCH, :]
    seg_last = segc[STRETCH - 1 : STRETCH, :]
    w = jnp.where(segc == seg_last, jnp.exp(last - cum), 0.0)
    scaled = (x_ref[...].astype(jnp.float32) * expand_heads(step)).astype(jnp.bfloat16)
    weighted = (scaled.astype(jnp.float32) * expand_heads(w)).astype(jnp.bfloat16)
    block_state = lax.dot_general(
        bt_ref[...], weighted, (((0,), (0,)), ((), ())), preferred_element_type=jnp.float32
    )
    decay = bdec_ref[0]
    acc_ref[...] = decay * acc_ref[...] + block_state
    dec_ref[...] = dec_ref[...] * decay

    @pl.when(b == pl.num_programs(0) - 1)
    def _():
        tot_ref[0:STATE, :] = acc_ref[...]
        tot_ref[STATE : STATE + 1, :] = dec_ref[...]


def half_states(bt, conv, dt_g, cum_g, segc, bdec, core_arr, which, prev=None):
    tok = conv.shape[0]
    nb = tok // STRETCH

    def grp(c):
        return (which + 1 + c[0]) % GROUPS

    operands = [bt, conv, dt_g, cum_g, segc, bdec]
    specs = [
        pl.BlockSpec((STRETCH, STATE), lambda b, c: (b, INNER // STATE + grp(c))),
        pl.BlockSpec((STRETCH, GROUP_COLS), lambda b, c: (b, grp(c))),
        pl.BlockSpec((1, STRETCH, PER_GROUP), lambda b, c: (grp(c), b, 0)),
        pl.BlockSpec((1, STRETCH, PER_GROUP), lambda b, c: (grp(c), b, 0)),
        pl.BlockSpec((STRETCH, 128), lambda b, c: (b, 0)),
        pl.BlockSpec((1, 1, GROUP_COLS), lambda b, c: (b, 0, grp(c))),
    ]
    aliases = {}
    if prev is not None:
        operands += list(prev)
        specs += [pl.BlockSpec(memory_space=pl.ANY), pl.BlockSpec(memory_space=pl.ANY)]
        aliases = {len(operands) - 1: 0, len(operands): 1}
    grid_spec = pltpu.PrefetchScalarGridSpec(
        num_scalar_prefetch=1,
        grid=(nb,),
        in_specs=specs,
        out_specs=[
            pl.BlockSpec((1, STATE, GROUP_COLS), lambda b, c: (b, 0, grp(c))),
            pl.BlockSpec((1, 1, GROUP_COLS), lambda b, c: (b, 0, grp(c))),
            pl.BlockSpec((STATE + 1, GROUP_COLS), lambda b, c: (0, 0)),
        ],
        scratch_shapes=[
            pltpu.VMEM((STATE, GROUP_COLS), jnp.float32),
            pltpu.VMEM((1, GROUP_COLS), jnp.float32),
        ],
    )
    return pl.pallas_call(
        half_state_kernel,
        grid_spec=grid_spec,
        out_shape=[
            jax.ShapeDtypeStruct((nb, STATE, INNER), jnp.float32),
            jax.ShapeDtypeStruct((nb, 1, INNER), jnp.float32),
            jax.ShapeDtypeStruct((STATE + 1, GROUP_COLS), jnp.float32),
        ],
        input_output_aliases=aliases,
    )(core_arr, *operands)


def intra_kernel(
    c_ref, b_ref, x_ref, dt_ref, cum_ref, cumt_ref, segc_ref, segr_ref, dsk_ref, out_ref
):
    gram = lax.dot_general(
        c_ref[...], b_ref[...], (((1,), (1,)), ((), ())), preferred_element_type=jnp.float32
    )
    segc = segc_ref[:, 0:1]
    segr = segr_ref[0:1, :]
    rows = lax.broadcasted_iota(jnp.int32, (STRETCH, STRETCH), 0)
    cols = lax.broadcasted_iota(jnp.int32, (STRETCH, STRETCH), 1)
    gram = jnp.where((segc == segr) & (cols <= rows), gram, 0.0)
    cum = cum_ref[0]
    cumt = cumt_ref[0]
    step = dt_ref[0]
    for j in range(PER_GROUP):
        hc = slice(j * HEAD_DIM, (j + 1) * HEAD_DIM)
        gap = jnp.minimum(cum[:, j : j + 1] - cumt[j : j + 1, :], 0.0)
        weights = (gram * jnp.exp(gap)).astype(jnp.bfloat16)
        xf = x_ref[:, hc].astype(jnp.float32)
        scaled = (xf * step[:, j : j + 1]).astype(jnp.bfloat16)
        intra = jnp.dot(weights, scaled, preferred_element_type=jnp.float32)
        out_ref[:, hc] = intra + dsk_ref[:, hc] * xf


def intra_part(conv, dt_g, cum_g, cumt_g, segc, segr, dsk, g, into=None):
    tok = conv.shape[0]
    nb = tok // STRETCH
    b_col = INNER // STATE
    c_col = b_col + GROUPS
    operands = [conv, conv, conv, dt_g, cum_g, cumt_g, segc, segr, dsk]
    specs = [
        pl.BlockSpec((STRETCH, STATE), lambda b: (b, c_col + g)),
        pl.BlockSpec((STRETCH, STATE), lambda b: (b, b_col + g)),
        pl.BlockSpec((STRETCH, GROUP_COLS), lambda b: (b, g)),
        pl.BlockSpec((1, STRETCH, PER_GROUP), lambda b: (g, b, 0)),
        pl.BlockSpec((1, STRETCH, PER_GROUP), lambda b: (g, b, 0)),
        pl.BlockSpec((1, PER_GROUP, STRETCH), lambda b: (g, 0, b)),
        pl.BlockSpec((STRETCH, 128), lambda b: (b, 0)),
        pl.BlockSpec((8, STRETCH), lambda b: (0, b)),
        pl.BlockSpec((1, GROUP_COLS), lambda b: (0, g)),
    ]
    kernel = intra_kernel
    aliases = {}
    if into is not None:
        operands.append(into)
        specs.append(pl.BlockSpec(memory_space=pl.ANY))
        aliases = {len(operands) - 1: 0}

        def kernel(*refs):
            intra_kernel(*refs[:-2], refs[-1])

    return pl.pallas_call(
        kernel,
        grid=(nb,),
        in_specs=specs,
        out_specs=pl.BlockSpec((STRETCH, GROUP_COLS), lambda b: (b, g)),
        out_shape=jax.ShapeDtypeStruct((tok, INNER), jnp.float32),
        input_output_aliases=aliases,
    )(*operands)


def mix_kernel(
    c_ref, y_ref, z_ref, hin_ref, local_ref, cdec_ref, cum_ref, segc_ref, eb_ref, gain_ref,
    out_ref,
):
    state = cdec_ref[0] * hin_ref[...].astype(jnp.float32) + local_ref[0]
    segc = segc_ref[:, 0:1]
    entry = eb_ref[0:1, 0:1]
    in_weight = jnp.where(segc == entry, jnp.exp(cum_ref[0]), 0.0)
    inter = jnp.dot(c_ref[...], state.astype(jnp.bfloat16), preferred_element_type=jnp.float32)
    y = y_ref[...] + inter * expand_heads(in_weight)
    zf = z_ref[...].astype(jnp.float32)
    gated = y * (zf * jax.nn.sigmoid(zf))
    mean_square = jnp.mean(gated * gated, axis=1, keepdims=True) + 1e-05
    out_ref[...] = (gated * lax.rsqrt(mean_square) * gain_ref[...]).astype(jnp.bfloat16)


def mix(conv, y_local, z_gate, hin, local_states, cdec, cum_g, segc, eb, gain, core_arr, which,
        prev=None):
    tok = conv.shape[0]
    nb = tok // STRETCH
    c_col = INNER // STATE + GROUPS

    def grp(c):
        return (which + c[0]) % GROUPS

    operands = [conv, y_local, z_gate, hin, local_states, cdec, cum_g, segc, eb, gain]
    specs = [
        pl.BlockSpec((STRETCH, STATE), lambda b, c: (b, c_col + grp(c))),
        pl.BlockSpec((STRETCH, GROUP_COLS), lambda b, c: (b, grp(c))),
        pl.BlockSpec((STRETCH, GROUP_COLS), lambda b, c: (b, grp(c))),
        pl.BlockSpec((STATE, GROUP_COLS), lambda b, c: (0, 0)),
        pl.BlockSpec((1, STATE, GROUP_COLS), lambda b, c: (b, 0, grp(c))),
        pl.BlockSpec((1, 1, GROUP_COLS), lambda b, c: (b, 0, grp(c))),
        pl.BlockSpec((1, STRETCH, PER_GROUP), lambda b, c: (grp(c), b, 0)),
        pl.BlockSpec((STRETCH, 128), lambda b, c: (b, 0)),
        pl.BlockSpec((8, 128), lambda b, c: (b, 0)),
        pl.BlockSpec((1, GROUP_COLS), lambda b, c: (0, grp(c))),
    ]
    kernel = mix_kernel
    aliases = {}
    if prev is not None:
        operands.append(prev)
        specs.append(pl.BlockSpec(memory_space=pl.ANY))
        aliases = {len(operands): 0}

        def kernel(*refs):
            mix_kernel(*refs[:-2], refs[-1])

    def with_core(core_ref, *refs):
        del core_ref
        kernel(*refs)

    grid_spec = pltpu.PrefetchScalarGridSpec(
        num_scalar_prefetch=1,
        grid=(nb,),
        in_specs=specs,
        out_specs=pl.BlockSpec((STRETCH, GROUP_COLS), lambda b, c: (b, grp(c))),
    )
    return pl.pallas_call(
        with_core,
        grid_spec=grid_spec,
        out_shape=jax.ShapeDtypeStruct((tok, INNER), jnp.bfloat16),
        input_output_aliases=aliases,
    )(core_arr, *operands)


def scan_kernel(got_ref, out_ref):
    peers = got_ref.shape[0]

    def body(d, carry):
        out_ref[d] = carry.astype(jnp.bfloat16)
        decay = got_ref[d, STATE : STATE + 1, :].astype(jnp.float32) + got_ref[
            d, STATE + 1 : STATE + 2, :
        ].astype(jnp.float32)
        return decay * carry + got_ref[d, 0:STATE, :].astype(jnp.float32)

    lax.fori_loop(0, peers, body, jnp.zeros(out_ref.shape[1:], jnp.float32))


def swap_cores(value):
    return lax.ppermute(value, "core", [(0, 1), (1, 0)])


def tie(value, *after):
    def kernel(*refs):
        del refs

    return pl.pallas_call(
        kernel,
        in_specs=[pl.BlockSpec(memory_space=pl.ANY) for _ in range(1 + len(after))],
        out_specs=pl.BlockSpec(memory_space=pl.ANY),
        out_shape=jax.ShapeDtypeStruct(value.shape, value.dtype),
        input_output_aliases={0: 0},
    )(value, *after)


def compose(for_other, mine, first_work, second_work):
    core = lax.axis_index("core")
    chips = lax.axis_size("chip")
    half = GROUP_COLS
    width = half // chips
    theirs = swap_cores(for_other)
    first = jnp.where(core == 0, mine, theirs)
    second = jnp.where(core == 0, theirs, mine)
    first_decay = first[STATE:]
    chip_state = second[STATE:] * first[:STATE] + second[:STATE]
    chip_decay = first_decay * second[STATE:]
    decay_hi = chip_decay.astype(jnp.bfloat16)
    decay_lo = (chip_decay - decay_hi.astype(jnp.float32)).astype(jnp.bfloat16)
    payload = jnp.concatenate(
        [chip_state.astype(jnp.bfloat16), decay_hi, decay_lo], axis=0
    ).reshape(STATE + 2, chips, width).transpose(1, 0, 2)
    work = first_work()
    got = tie(lax.all_to_all(payload, "chip", split_axis=0, concat_axis=0, tiled=True), work)
    entering = pl.pallas_call(
        scan_kernel,
        out_shape=jax.ShapeDtypeStruct((chips, STATE, width), jnp.bfloat16),
    )(got)
    work = second_work(work)
    back = tie(lax.all_to_all(entering, "chip", split_axis=0, concat_axis=0, tiled=True), work)
    chip_in = back.transpose(1, 0, 2).reshape(STATE, half).astype(jnp.float32)
    later_in = first_decay * chip_in + first[:STATE]
    keep = jnp.where(core == 0, chip_in, later_in).astype(jnp.bfloat16)
    other = swap_cores(jnp.where(core == 0, later_in, chip_in).astype(jnp.bfloat16))
    return keep, other, work


def local(xbc, z_gate, dt_raw, lengths, conv_weight, conv_bias, dt_bias, a_log, d_skip, norm_gain):
    tok = xbc.shape[0]
    nb = tok // STRETCH
    first_pos = (lax.axis_index("chip") * lax.axis_size("core") + lax.axis_index("core")) * tok
    rim_rows = shifted(xbc[tok - (CONV - 1) :], ("chip", "core"), 1)
    rim8 = jnp.concatenate([jnp.zeros((8 - (CONV - 1), CHANNELS), xbc.dtype), rim_rows], axis=0)
    ext_pos = first_pos - (CONV - 1) + jnp.arange(tok + CONV - 1)
    ext_seg = segment_of(ext_pos, lengths)
    target = ext_seg[CONV - 1 :]
    kept = [
        (ext_pos[tap : tap + tok] >= 0) & (ext_seg[tap : tap + tok] == target) for tap in range(CONV)
    ]
    masks = jnp.stack(kept, axis=1).astype(jnp.float32)
    conv = conv_part(xbc, rim8, conv_weight, conv_bias[None, :], masks)
    step = jax.nn.softplus(dt_raw.astype(jnp.float32) + dt_bias[None, :])
    log_decay = -step * jnp.exp(a_log)[None, :]
    cum = jnp.cumsum(log_decay.reshape(nb, STRETCH, HEADS), axis=1).reshape(tok, HEADS)
    segments = segment_of(first_pos + jnp.arange(tok), lengths)
    seg_before = segment_of(first_pos + jnp.arange(nb) * STRETCH - 1, lengths)
    seg_last = segments.reshape(nb, STRETCH)[:, -1]
    cum_last = cum.reshape(nb, STRETCH, HEADS)[:, -1, :]
    block_decay = jnp.where((seg_last == seg_before)[:, None], jnp.exp(cum_last), 0.0)

    cum_g = cum.reshape(tok, GROUPS, PER_GROUP).transpose(1, 0, 2)
    dt_g = step.reshape(tok, GROUPS, PER_GROUP).transpose(1, 0, 2)
    cumt_g = cum.T.reshape(GROUPS, PER_GROUP, tok)
    segc = jnp.broadcast_to(segments[:, None], (tok, 128)).astype(jnp.int32)
    segr = jnp.broadcast_to(segments[None, :], (8, tok)).astype(jnp.int32)
    eb = jnp.broadcast_to(seg_before[:, None, None], (nb, 8, 128)).reshape(nb * 8, 128)
    eb = eb.astype(jnp.int32)
    bdec = jnp.repeat(block_decay, HEAD_DIM, axis=1)[:, None, :]

    core_arr = lax.axis_index("core").astype(jnp.int32).reshape(1)
    local_a, cdec_a, for_other = half_states(conv, conv, dt_g, cum_g, segc, bdec, core_arr, 0)
    local_states, cdec, mine = half_states(
        conv, conv, dt_g, cum_g, segc, bdec, core_arr, 1, (local_a, cdec_a)
    )
    dsk = jnp.repeat(d_skip, HEAD_DIM)[None, :]
    def first_work():
        return intra_part(conv, dt_g, cum_g, cumt_g, segc, segr, dsk, 0)

    def second_work(done):
        return intra_part(conv, dt_g, cum_g, cumt_g, segc, segr, dsk, 1, done)

    keep, other, y_local = compose(for_other, mine, first_work, second_work)
    gain = norm_gain[None, :]
    parts = (y_local, z_gate)
    rest = (local_states, cdec, cum_g, segc, eb, gain, core_arr)
    out = mix(conv, *parts, keep, *rest, 0)
    return mix(conv, *parts, other, *rest, 1, out)


def solution(mesh):
    groups, peers = mesh.devices.shape
    split = Mesh(mesh.devices.reshape(groups, peers // 2, 2), ("group", "chip", "core"))
    rows = P(("group", "chip", "core"), None)
    return jax.shard_map(
        local,
        mesh=split,
        in_specs=(rows, rows, rows, P("group"), P(), P(), P(), P(), P(), P()),
        out_specs=rows,
        check_vma=False,
    )
```

```python
import jax
import jax.numpy as jnp
from jax import lax
from jax.experimental import pallas as pl
from jax.experimental.pallas import tpu as pltpu
from jax.sharding import Mesh, PartitionSpec as P

HEADS = 64
HEAD_DIM = 64
STATE = 256
GROUPS = 2
CONV = 4
STRETCH = 256
CHANNELS = 5120
INNER = HEADS * HEAD_DIM
PER_GROUP = HEADS // GROUPS
GROUP_COLS = INNER // GROUPS


def shifted(value, axis, by):
    peers = lax.axis_size(axis)
    pairs = [(i, i + by) for i in range(peers) if 0 <= i + by < peers]
    return lax.ppermute(value, axis, pairs)


def segment_of(positions, lengths):
    prompt_ends = jnp.cumsum(lengths)
    hits = (prompt_ends[None, :] <= positions[:, None]).astype(jnp.int32)
    return jnp.sum(hits, axis=1)


def expand_heads(v):
    heads = lax.broadcasted_iota(jnp.int32, (PER_GROUP, GROUP_COLS), 0)
    cols = lax.broadcasted_iota(jnp.int32, (PER_GROUP, GROUP_COLS), 1)
    spread = (cols // HEAD_DIM == heads).astype(jnp.bfloat16)
    hi = v.astype(jnp.bfloat16)
    rest = v - hi.astype(jnp.float32)
    mid = rest.astype(jnp.bfloat16)
    lo = (rest - mid.astype(jnp.float32)).astype(jnp.bfloat16)
    out = jnp.dot(hi, spread, preferred_element_type=jnp.float32)
    out = out + jnp.dot(mid, spread, preferred_element_type=jnp.float32)
    return out + jnp.dot(lo, spread, preferred_element_type=jnp.float32)


CONV_COLS = 640


def conv_kernel(x_ref, rim_ref, w_ref, bias_ref, m_ref, out_ref):
    x = x_ref[...].astype(jnp.float32)
    rim = rim_ref[...].astype(jnp.float32)
    rows8 = lax.broadcasted_iota(jnp.int32, rim.shape, 0)
    summed = jnp.zeros(x.shape, jnp.float32)
    top = jnp.zeros(rim.shape, jnp.float32)
    for tap in range(CONV):
        by = CONV - 1 - tap
        wk = w_ref[tap : tap + 1, :]
        kept = m_ref[:, tap : tap + 1] > 0.0
        if by == 0:
            term = x
            top_term = x[0:8]
        else:
            term = pltpu.roll(x, by, 0)
            top_term = jnp.where(rows8 < by, pltpu.roll(rim, by, 0), term[0:8])
        summed = summed + jnp.where(kept, term * wk, 0.0)
        top = top + jnp.where(kept[0:8], top_term * wk, 0.0)
    out_ref[...] = jax.nn.silu(summed + bias_ref[...]).astype(jnp.bfloat16)
    out_ref[0:8, :] = jax.nn.silu(top + bias_ref[...]).astype(jnp.bfloat16)


def conv_part(xbc, rim8, w8, bias, masks):
    tok, chans = xbc.shape
    return pl.pallas_call(
        conv_kernel,
        grid=(chans // CONV_COLS,),
        in_specs=[
            pl.BlockSpec((tok, CONV_COLS), lambda c: (0, c)),
            pl.BlockSpec((8, CONV_COLS), lambda c: (0, c)),
            pl.BlockSpec((CONV, CONV_COLS), lambda c: (0, c)),
            pl.BlockSpec((1, CONV_COLS), lambda c: (0, c)),
            pl.BlockSpec((tok, CONV), lambda c: (0, 0)),
        ],
        out_specs=pl.BlockSpec((tok, CONV_COLS), lambda c: (0, c)),
        out_shape=jax.ShapeDtypeStruct((tok, chans), jnp.bfloat16),
    )(xbc, rim8, w8, bias, masks)


def state_kernel(
    bt_ref, x_ref, dt_ref, cum_ref, segc_ref, bdec_ref, local_ref, cdec_ref, tot_ref,
    acc_ref, dec_ref,
):
    b = pl.program_id(1)

    @pl.when(b == 0)
    def _():
        acc_ref[...] = jnp.zeros(acc_ref.shape, jnp.float32)
        dec_ref[...] = jnp.ones(dec_ref.shape, jnp.float32)

    local_ref[0] = acc_ref[...]
    cdec_ref[0] = dec_ref[...]
    cum = cum_ref[0]
    step = dt_ref[0]
    segc = segc_ref[:, 0:1]
    last = cum[STRETCH - 1 : STRETCH, :]
    seg_last = segc[STRETCH - 1 : STRETCH, :]
    w = jnp.where(segc == seg_last, jnp.exp(last - cum), 0.0)
    scaled = (x_ref[...].astype(jnp.float32) * expand_heads(step)).astype(jnp.bfloat16)
    weighted = (scaled.astype(jnp.float32) * expand_heads(w)).astype(jnp.bfloat16)
    block_state = jnp.dot(bt_ref[...], weighted, preferred_element_type=jnp.float32)
    decay = bdec_ref[0]
    acc_ref[...] = decay * acc_ref[...] + block_state
    dec_ref[...] = dec_ref[...] * decay

    @pl.when(b == pl.num_programs(1) - 1)
    def _():
        tot_ref[0, 0:STATE, :] = acc_ref[...]
        tot_ref[0, STATE : STATE + 1, :] = dec_ref[...]


def half_state_kernel(
    core_ref, bt_ref, x_ref, dt_ref, cum_ref, segc_ref, bdec_ref, *rest
):
    local_ref, cdec_ref, tot_ref, acc_ref, dec_ref = rest[-5:]
    del core_ref
    b = pl.program_id(0)

    @pl.when(b == 0)
    def _():
        acc_ref[...] = jnp.zeros(acc_ref.shape, jnp.float32)
        dec_ref[...] = jnp.ones(dec_ref.shape, jnp.float32)

    local_ref[0] = acc_ref[...]
    cdec_ref[0] = dec_ref[...]
    cum = cum_ref[0]
    step = dt_ref[0]
    segc = segc_ref[:, 0:1]
    last = cum[STRETCH - 1 : STRETCH, :]
    seg_last = segc[STRETCH - 1 : STRETCH, :]
    w = jnp.where(segc == seg_last, jnp.exp(last - cum), 0.0)
    scaled = (x_ref[...].astype(jnp.float32) * expand_heads(step)).astype(jnp.bfloat16)
    weighted = (scaled.astype(jnp.float32) * expand_heads(w)).astype(jnp.bfloat16)
    block_state = lax.dot_general(
        bt_ref[...], weighted, (((0,), (0,)), ((), ())), preferred_element_type=jnp.float32
    )
    decay = bdec_ref[0]
    acc_ref[...] = decay * acc_ref[...] + block_state
    dec_ref[...] = dec_ref[...] * decay

    @pl.when(b == pl.num_programs(0) - 1)
    def _():
        tot_ref[0:STATE, :] = acc_ref[...]
        tot_ref[STATE : STATE + 1, :] = dec_ref[...]


def half_states(bt, conv, dt_g, cum_g, segc, bdec, core_arr, which, prev=None):
    tok = conv.shape[0]
    nb = tok // STRETCH

    def grp(c):
        return (which + 1 + c[0]) % GROUPS

    operands = [bt, conv, dt_g, cum_g, segc, bdec]
    specs = [
        pl.BlockSpec((STRETCH, STATE), lambda b, c: (b, INNER // STATE + grp(c))),
        pl.BlockSpec((STRETCH, GROUP_COLS), lambda b, c: (b, grp(c))),
        pl.BlockSpec((1, STRETCH, PER_GROUP), lambda b, c: (grp(c), b, 0)),
        pl.BlockSpec((1, STRETCH, PER_GROUP), lambda b, c: (grp(c), b, 0)),
        pl.BlockSpec((STRETCH, 128), lambda b, c: (b, 0)),
        pl.BlockSpec((1, 1, GROUP_COLS), lambda b, c: (b, 0, grp(c))),
    ]
    aliases = {}
    if prev is not None:
        operands += list(prev)
        specs += [pl.BlockSpec(memory_space=pl.ANY), pl.BlockSpec(memory_space=pl.ANY)]
        aliases = {len(operands) - 1: 0, len(operands): 1}
    grid_spec = pltpu.PrefetchScalarGridSpec(
        num_scalar_prefetch=1,
        grid=(nb,),
        in_specs=specs,
        out_specs=[
            pl.BlockSpec((1, STATE, GROUP_COLS), lambda b, c: (b, 0, grp(c))),
            pl.BlockSpec((1, 1, GROUP_COLS), lambda b, c: (b, 0, grp(c))),
            pl.BlockSpec((STATE + 1, GROUP_COLS), lambda b, c: (0, 0)),
        ],
        scratch_shapes=[
            pltpu.VMEM((STATE, GROUP_COLS), jnp.float32),
            pltpu.VMEM((1, GROUP_COLS), jnp.float32),
        ],
    )
    return pl.pallas_call(
        half_state_kernel,
        grid_spec=grid_spec,
        out_shape=[
            jax.ShapeDtypeStruct((nb, STATE, INNER), jnp.float32),
            jax.ShapeDtypeStruct((nb, 1, INNER), jnp.float32),
            jax.ShapeDtypeStruct((STATE + 1, GROUP_COLS), jnp.float32),
        ],
        input_output_aliases=aliases,
    )(core_arr, *operands)


def intra_kernel(
    c_ref, b_ref, x_ref, dt_ref, cum_ref, cumt_ref, segc_ref, segr_ref, dsk_ref, out_ref
):
    gram = lax.dot_general(
        c_ref[...], b_ref[...], (((1,), (1,)), ((), ())), preferred_element_type=jnp.float32
    )
    segc = segc_ref[:, 0:1]
    segr = segr_ref[0:1, :]
    rows = lax.broadcasted_iota(jnp.int32, (STRETCH, STRETCH), 0)
    cols = lax.broadcasted_iota(jnp.int32, (STRETCH, STRETCH), 1)
    gram = jnp.where((segc == segr) & (cols <= rows), gram, 0.0)
    cum = cum_ref[0]
    cumt = cumt_ref[0]
    step = dt_ref[0]
    for j in range(PER_GROUP):
        hc = slice(j * HEAD_DIM, (j + 1) * HEAD_DIM)
        gap = jnp.minimum(cum[:, j : j + 1] - cumt[j : j + 1, :], 0.0)
        weights = (gram * jnp.exp(gap)).astype(jnp.bfloat16)
        xf = x_ref[:, hc].astype(jnp.float32)
        scaled = (xf * step[:, j : j + 1]).astype(jnp.bfloat16)
        intra = jnp.dot(weights, scaled, preferred_element_type=jnp.float32)
        out_ref[:, hc] = intra + dsk_ref[:, hc] * xf


def intra_part(conv, dt_g, cum_g, cumt_g, segc, segr, dsk, g, into=None):
    tok = conv.shape[0]
    nb = tok // STRETCH
    b_col = INNER // STATE
    c_col = b_col + GROUPS
    operands = [conv, conv, conv, dt_g, cum_g, cumt_g, segc, segr, dsk]
    specs = [
        pl.BlockSpec((STRETCH, STATE), lambda b: (b, c_col + g)),
        pl.BlockSpec((STRETCH, STATE), lambda b: (b, b_col + g)),
        pl.BlockSpec((STRETCH, GROUP_COLS), lambda b: (b, g)),
        pl.BlockSpec((1, STRETCH, PER_GROUP), lambda b: (g, b, 0)),
        pl.BlockSpec((1, STRETCH, PER_GROUP), lambda b: (g, b, 0)),
        pl.BlockSpec((1, PER_GROUP, STRETCH), lambda b: (g, 0, b)),
        pl.BlockSpec((STRETCH, 128), lambda b: (b, 0)),
        pl.BlockSpec((8, STRETCH), lambda b: (0, b)),
        pl.BlockSpec((1, GROUP_COLS), lambda b: (0, g)),
    ]
    kernel = intra_kernel
    aliases = {}
    if into is not None:
        operands.append(into)
        specs.append(pl.BlockSpec(memory_space=pl.ANY))
        aliases = {len(operands) - 1: 0}

        def kernel(*refs):
            intra_kernel(*refs[:-2], refs[-1])

    return pl.pallas_call(
        kernel,
        grid=(nb,),
        in_specs=specs,
        out_specs=pl.BlockSpec((STRETCH, GROUP_COLS), lambda b: (b, g)),
        out_shape=jax.ShapeDtypeStruct((tok, INNER), jnp.float32),
        input_output_aliases=aliases,
    )(*operands)


def mix_kernel(
    c_ref, y_ref, z_ref, hin_ref, local_ref, cdec_ref, cum_ref, segc_ref, eb_ref, gain_ref,
    out_ref,
):
    state = cdec_ref[0] * hin_ref[...].astype(jnp.float32) + local_ref[0]
    segc = segc_ref[:, 0:1]
    entry = eb_ref[0:1, 0:1]
    in_weight = jnp.where(segc == entry, jnp.exp(cum_ref[0]), 0.0)
    inter = jnp.dot(c_ref[...], state.astype(jnp.bfloat16), preferred_element_type=jnp.float32)
    y = y_ref[...] + inter * expand_heads(in_weight)
    zf = z_ref[...].astype(jnp.float32)
    gated = y * (zf * jax.nn.sigmoid(zf))
    mean_square = jnp.mean(gated * gated, axis=1, keepdims=True) + 1e-05
    out_ref[...] = (gated * lax.rsqrt(mean_square) * gain_ref[...]).astype(jnp.bfloat16)


def mix(conv, y_local, z_gate, hin, local_states, cdec, cum_g, segc, eb, gain, core_arr, which,
        prev=None):
    tok = conv.shape[0]
    nb = tok // STRETCH
    c_col = INNER // STATE + GROUPS

    def grp(c):
        return (which + c[0]) % GROUPS

    operands = [conv, y_local, z_gate, hin, local_states, cdec, cum_g, segc, eb, gain]
    specs = [
        pl.BlockSpec((STRETCH, STATE), lambda b, c: (b, c_col + grp(c))),
        pl.BlockSpec((STRETCH, GROUP_COLS), lambda b, c: (b, grp(c))),
        pl.BlockSpec((STRETCH, GROUP_COLS), lambda b, c: (b, grp(c))),
        pl.BlockSpec((STATE, GROUP_COLS), lambda b, c: (0, 0)),
        pl.BlockSpec((1, STATE, GROUP_COLS), lambda b, c: (b, 0, grp(c))),
        pl.BlockSpec((1, 1, GROUP_COLS), lambda b, c: (b, 0, grp(c))),
        pl.BlockSpec((1, STRETCH, PER_GROUP), lambda b, c: (grp(c), b, 0)),
        pl.BlockSpec((STRETCH, 128), lambda b, c: (b, 0)),
        pl.BlockSpec((8, 128), lambda b, c: (b, 0)),
        pl.BlockSpec((1, GROUP_COLS), lambda b, c: (0, grp(c))),
    ]
    kernel = mix_kernel
    aliases = {}
    if prev is not None:
        operands.append(prev)
        specs.append(pl.BlockSpec(memory_space=pl.ANY))
        aliases = {len(operands): 0}

        def kernel(*refs):
            mix_kernel(*refs[:-2], refs[-1])

    def with_core(core_ref, *refs):
        del core_ref
        kernel(*refs)

    grid_spec = pltpu.PrefetchScalarGridSpec(
        num_scalar_prefetch=1,
        grid=(nb,),
        in_specs=specs,
        out_specs=pl.BlockSpec((STRETCH, GROUP_COLS), lambda b, c: (b, grp(c))),
    )
    return pl.pallas_call(
        with_core,
        grid_spec=grid_spec,
        out_shape=jax.ShapeDtypeStruct((tok, INNER), jnp.bfloat16),
        input_output_aliases=aliases,
    )(core_arr, *operands)


def scan_kernel(got_ref, out_ref):
    peers = got_ref.shape[0]

    def body(d, carry):
        out_ref[d] = carry.astype(jnp.bfloat16)
        decay = got_ref[d, STATE : STATE + 1, :].astype(jnp.float32) + got_ref[
            d, STATE + 1 : STATE + 2, :
        ].astype(jnp.float32)
        return decay * carry + got_ref[d, 0:STATE, :].astype(jnp.float32)

    lax.fori_loop(0, peers, body, jnp.zeros(out_ref.shape[1:], jnp.float32))


def swap_cores(value):
    return lax.ppermute(value, "core", [(0, 1), (1, 0)])


def tie(value, *after):
    def kernel(*refs):
        del refs

    return pl.pallas_call(
        kernel,
        in_specs=[pl.BlockSpec(memory_space=pl.ANY) for _ in range(1 + len(after))],
        out_specs=pl.BlockSpec(memory_space=pl.ANY),
        out_shape=jax.ShapeDtypeStruct(value.shape, value.dtype),
        input_output_aliases={0: 0},
    )(value, *after)


def compose(for_other, mine, first_work, second_work):
    core = lax.axis_index("core")
    chips = lax.axis_size("chip")
    half = GROUP_COLS
    width = half // chips
    theirs = swap_cores(for_other)
    first = jnp.where(core == 0, mine, theirs)
    second = jnp.where(core == 0, theirs, mine)
    first_decay = first[STATE:]
    chip_state = second[STATE:] * first[:STATE] + second[:STATE]
    chip_decay = first_decay * second[STATE:]
    decay_hi = chip_decay.astype(jnp.bfloat16)
    decay_lo = (chip_decay - decay_hi.astype(jnp.float32)).astype(jnp.bfloat16)
    payload = jnp.concatenate(
        [chip_state.astype(jnp.bfloat16), decay_hi, decay_lo], axis=0
    ).reshape(STATE + 2, chips, width).transpose(1, 0, 2)
    work = first_work()
    got = tie(lax.all_to_all(payload, "chip", split_axis=0, concat_axis=0, tiled=True), work)
    entering = pl.pallas_call(
        scan_kernel,
        out_shape=jax.ShapeDtypeStruct((chips, STATE, width), jnp.bfloat16),
    )(got)
    work = second_work(work)
    back = tie(lax.all_to_all(entering, "chip", split_axis=0, concat_axis=0, tiled=True), work)
    chip_in = back.transpose(1, 0, 2).reshape(STATE, half).astype(jnp.float32)
    later_in = first_decay * chip_in + first[:STATE]
    keep = jnp.where(core == 0, chip_in, later_in).astype(jnp.bfloat16)
    other = swap_cores(jnp.where(core == 0, later_in, chip_in).astype(jnp.bfloat16))
    return keep, other, work


def local(xbc, z_gate, dt_raw, lengths, conv_weight, conv_bias, dt_bias, a_log, d_skip, norm_gain):
    tok = xbc.shape[0]
    nb = tok // STRETCH
    first_pos = (lax.axis_index("chip") * lax.axis_size("core") + lax.axis_index("core")) * tok
    rim_rows = shifted(xbc[tok - (CONV - 1) :], ("chip", "core"), 1)
    rim8 = jnp.concatenate([jnp.zeros((8 - (CONV - 1), CHANNELS), xbc.dtype), rim_rows], axis=0)
    ext_pos = first_pos - (CONV - 1) + jnp.arange(tok + CONV - 1)
    ext_seg = segment_of(ext_pos, lengths)
    target = ext_seg[CONV - 1 :]
    kept = [
        (ext_pos[tap : tap + tok] >= 0) & (ext_seg[tap : tap + tok] == target) for tap in range(CONV)
    ]
    masks = jnp.stack(kept, axis=1).astype(jnp.float32)
    conv = conv_part(xbc, rim8, conv_weight, conv_bias[None, :], masks)
    raw_g = dt_raw.reshape(tok, GROUPS, PER_GROUP).transpose(1, 0, 2).astype(jnp.float32)
    dt_g = jax.nn.softplus(raw_g + dt_bias.reshape(GROUPS, 1, PER_GROUP))
    log_decay = -dt_g * jnp.exp(a_log).reshape(GROUPS, 1, PER_GROUP)
    cum_blocks = jnp.cumsum(log_decay.reshape(GROUPS, nb, STRETCH, PER_GROUP), axis=2)
    cum_g = cum_blocks.reshape(GROUPS, tok, PER_GROUP)
    segments = segment_of(first_pos + jnp.arange(tok), lengths)
    seg_before = segment_of(first_pos + jnp.arange(nb) * STRETCH - 1, lengths)
    seg_last = segments.reshape(nb, STRETCH)[:, -1]
    cum_last = cum_blocks[:, :, -1, :].transpose(1, 0, 2).reshape(nb, HEADS)
    block_decay = jnp.where((seg_last == seg_before)[:, None], jnp.exp(cum_last), 0.0)

    cumt_g = cum_g.transpose(0, 2, 1)
    segc = jnp.broadcast_to(segments[:, None], (tok, 128)).astype(jnp.int32)
    segr = jnp.broadcast_to(segments[None, :], (8, tok)).astype(jnp.int32)
    eb = jnp.broadcast_to(seg_before[:, None, None], (nb, 8, 128)).reshape(nb * 8, 128)
    eb = eb.astype(jnp.int32)
    bdec = jnp.repeat(block_decay, HEAD_DIM, axis=1)[:, None, :]

    core_arr = lax.axis_index("core").astype(jnp.int32).reshape(1)
    local_a, cdec_a, for_other = half_states(conv, conv, dt_g, cum_g, segc, bdec, core_arr, 0)
    local_states, cdec, mine = half_states(
        conv, conv, dt_g, cum_g, segc, bdec, core_arr, 1, (local_a, cdec_a)
    )
    dsk = jnp.repeat(d_skip, HEAD_DIM)[None, :]
    def first_work():
        return intra_part(conv, dt_g, cum_g, cumt_g, segc, segr, dsk, 0)

    def second_work(done):
        return intra_part(conv, dt_g, cum_g, cumt_g, segc, segr, dsk, 1, done)

    keep, other, y_local = compose(for_other, mine, first_work, second_work)
    gain = norm_gain[None, :]
    parts = (y_local, z_gate)
    rest = (local_states, cdec, cum_g, segc, eb, gain, core_arr)
    out = mix(conv, *parts, keep, *rest, 0)
    return mix(conv, *parts, other, *rest, 1, out)


def solution(mesh):
    groups, peers = mesh.devices.shape
    split = Mesh(mesh.devices.reshape(groups, peers // 2, 2), ("group", "chip", "core"))
    rows = P(("group", "chip", "core"), None)
    return jax.shard_map(
        local,
        mesh=split,
        in_specs=(rows, rows, rows, P("group"), P(), P(), P(), P(), P(), P()),
        out_specs=rows,
        check_vma=False,
    )
```

```python
import jax
import jax.numpy as jnp
from jax import lax
from jax.experimental import pallas as pl
from jax.experimental.pallas import tpu as pltpu
from jax.sharding import Mesh, PartitionSpec as P

HEADS = 64
HEAD_DIM = 64
STATE = 256
GROUPS = 2
CONV = 4
STRETCH = 256
CHANNELS = 5120
INNER = HEADS * HEAD_DIM
PER_GROUP = HEADS // GROUPS
GROUP_COLS = INNER // GROUPS


def shifted(value, axis, by):
    peers = lax.axis_size(axis)
    pairs = [(i, i + by) for i in range(peers) if 0 <= i + by < peers]
    return lax.ppermute(value, axis, pairs)


def segment_of(positions, lengths):
    prompt_ends = jnp.cumsum(lengths)
    hits = (prompt_ends[None, :] <= positions[:, None]).astype(jnp.int32)
    return jnp.sum(hits, axis=1)


def expand_heads(v):
    heads = lax.broadcasted_iota(jnp.int32, (PER_GROUP, GROUP_COLS), 0)
    cols = lax.broadcasted_iota(jnp.int32, (PER_GROUP, GROUP_COLS), 1)
    spread = (cols // HEAD_DIM == heads).astype(jnp.bfloat16)
    hi = v.astype(jnp.bfloat16)
    rest = v - hi.astype(jnp.float32)
    mid = rest.astype(jnp.bfloat16)
    lo = (rest - mid.astype(jnp.float32)).astype(jnp.bfloat16)
    out = jnp.dot(hi, spread, preferred_element_type=jnp.float32)
    out = out + jnp.dot(mid, spread, preferred_element_type=jnp.float32)
    return out + jnp.dot(lo, spread, preferred_element_type=jnp.float32)


CONV_COLS = 640


def conv_kernel(x_ref, rim_ref, w_ref, bias_ref, m_ref, out_ref):
    x = x_ref[...].astype(jnp.float32)
    rim = rim_ref[...].astype(jnp.float32)
    rows8 = lax.broadcasted_iota(jnp.int32, rim.shape, 0)
    summed = jnp.zeros(x.shape, jnp.float32)
    top = jnp.zeros(rim.shape, jnp.float32)
    for tap in range(CONV):
        by = CONV - 1 - tap
        wk = w_ref[tap : tap + 1, :]
        kept = m_ref[:, tap : tap + 1] > 0.0
        if by == 0:
            term = x
            top_term = x[0:8]
        else:
            term = pltpu.roll(x, by, 0)
            top_term = jnp.where(rows8 < by, pltpu.roll(rim, by, 0), term[0:8])
        summed = summed + jnp.where(kept, term * wk, 0.0)
        top = top + jnp.where(kept[0:8], top_term * wk, 0.0)
    out_ref[...] = jax.nn.silu(summed + bias_ref[...]).astype(jnp.bfloat16)
    out_ref[0:8, :] = jax.nn.silu(top + bias_ref[...]).astype(jnp.bfloat16)


def conv_part(xbc, rim8, w8, bias, masks):
    tok, chans = xbc.shape
    return pl.pallas_call(
        conv_kernel,
        grid=(chans // CONV_COLS,),
        in_specs=[
            pl.BlockSpec((tok, CONV_COLS), lambda c: (0, c)),
            pl.BlockSpec((8, CONV_COLS), lambda c: (0, c)),
            pl.BlockSpec((CONV, CONV_COLS), lambda c: (0, c)),
            pl.BlockSpec((1, CONV_COLS), lambda c: (0, c)),
            pl.BlockSpec((tok, CONV), lambda c: (0, 0)),
        ],
        out_specs=pl.BlockSpec((tok, CONV_COLS), lambda c: (0, c)),
        out_shape=jax.ShapeDtypeStruct((tok, chans), jnp.bfloat16),
    )(xbc, rim8, w8, bias, masks)


def state_kernel(
    bt_ref, x_ref, dt_ref, cum_ref, segc_ref, bdec_ref, local_ref, cdec_ref, tot_ref,
    acc_ref, dec_ref,
):
    b = pl.program_id(1)

    @pl.when(b == 0)
    def _():
        acc_ref[...] = jnp.zeros(acc_ref.shape, jnp.float32)
        dec_ref[...] = jnp.ones(dec_ref.shape, jnp.float32)

    local_ref[0] = acc_ref[...]
    cdec_ref[0] = dec_ref[...]
    cum = cum_ref[0]
    step = dt_ref[0]
    segc = segc_ref[:, 0:1]
    last = cum[STRETCH - 1 : STRETCH, :]
    seg_last = segc[STRETCH - 1 : STRETCH, :]
    w = jnp.where(segc == seg_last, jnp.exp(last - cum), 0.0)
    scaled = (x_ref[...].astype(jnp.float32) * expand_heads(step)).astype(jnp.bfloat16)
    weighted = (scaled.astype(jnp.float32) * expand_heads(w)).astype(jnp.bfloat16)
    block_state = jnp.dot(bt_ref[...], weighted, preferred_element_type=jnp.float32)
    decay = bdec_ref[0]
    acc_ref[...] = decay * acc_ref[...] + block_state
    dec_ref[...] = dec_ref[...] * decay

    @pl.when(b == pl.num_programs(1) - 1)
    def _():
        tot_ref[0, 0:STATE, :] = acc_ref[...]
        tot_ref[0, STATE : STATE + 1, :] = dec_ref[...]


def half_state_kernel(
    core_ref, bt_ref, x_ref, dt_ref, cum_ref, segc_ref, bdec_ref, *rest
):
    local_ref, cdec_ref, tot_ref, acc_ref, dec_ref = rest[-5:]
    del core_ref
    b = pl.program_id(0)

    @pl.when(b == 0)
    def _():
        acc_ref[...] = jnp.zeros(acc_ref.shape, jnp.float32)
        dec_ref[...] = jnp.ones(dec_ref.shape, jnp.float32)

    local_ref[0] = acc_ref[...]
    cdec_ref[0] = dec_ref[...]
    cum = cum_ref[0]
    step = dt_ref[0]
    segc = segc_ref[:, 0:1]
    last = cum[STRETCH - 1 : STRETCH, :]
    seg_last = segc[STRETCH - 1 : STRETCH, :]
    w = jnp.where(segc == seg_last, jnp.exp(last - cum), 0.0)
    scaled = (x_ref[...].astype(jnp.float32) * expand_heads(step)).astype(jnp.bfloat16)
    weighted = (scaled.astype(jnp.float32) * expand_heads(w)).astype(jnp.bfloat16)
    block_state = lax.dot_general(
        bt_ref[...], weighted, (((0,), (0,)), ((), ())), preferred_element_type=jnp.float32
    )
    decay = bdec_ref[0]
    acc_ref[...] = decay * acc_ref[...] + block_state
    dec_ref[...] = dec_ref[...] * decay

    @pl.when(b == pl.num_programs(0) - 1)
    def _():
        tot_ref[0:STATE, :] = acc_ref[...]
        tot_ref[STATE : STATE + 1, :] = dec_ref[...]


def half_states(bt, conv, dt_g, cum_g, segc, bdec, core_arr, which, prev=None):
    tok = conv.shape[0]
    nb = tok // STRETCH

    def grp(c):
        return (which + 1 + c[0]) % GROUPS

    operands = [bt, conv, dt_g, cum_g, segc, bdec]
    specs = [
        pl.BlockSpec((STRETCH, STATE), lambda b, c: (b, INNER // STATE + grp(c))),
        pl.BlockSpec((STRETCH, GROUP_COLS), lambda b, c: (b, grp(c))),
        pl.BlockSpec((1, STRETCH, PER_GROUP), lambda b, c: (grp(c), b, 0)),
        pl.BlockSpec((1, STRETCH, PER_GROUP), lambda b, c: (grp(c), b, 0)),
        pl.BlockSpec((STRETCH, 1), lambda b, c: (b, 0)),
        pl.BlockSpec((1, 1, GROUP_COLS), lambda b, c: (b, 0, grp(c))),
    ]
    aliases = {}
    if prev is not None:
        operands += list(prev)
        specs += [pl.BlockSpec(memory_space=pl.ANY), pl.BlockSpec(memory_space=pl.ANY)]
        aliases = {len(operands) - 1: 0, len(operands): 1}
    grid_spec = pltpu.PrefetchScalarGridSpec(
        num_scalar_prefetch=1,
        grid=(nb,),
        in_specs=specs,
        out_specs=[
            pl.BlockSpec((1, STATE, GROUP_COLS), lambda b, c: (b, 0, grp(c))),
            pl.BlockSpec((1, 1, GROUP_COLS), lambda b, c: (b, 0, grp(c))),
            pl.BlockSpec((STATE + 1, GROUP_COLS), lambda b, c: (0, 0)),
        ],
        scratch_shapes=[
            pltpu.VMEM((STATE, GROUP_COLS), jnp.float32),
            pltpu.VMEM((1, GROUP_COLS), jnp.float32),
        ],
    )
    return pl.pallas_call(
        half_state_kernel,
        grid_spec=grid_spec,
        out_shape=[
            jax.ShapeDtypeStruct((nb, STATE, INNER), jnp.float32),
            jax.ShapeDtypeStruct((nb, 1, INNER), jnp.float32),
            jax.ShapeDtypeStruct((STATE + 1, GROUP_COLS), jnp.float32),
        ],
        input_output_aliases=aliases,
    )(core_arr, *operands)


def intra_kernel(
    c_ref, b_ref, x_ref, dt_ref, cum_ref, cumt_ref, segc_ref, segr_ref, dsk_ref, out_ref
):
    gram = lax.dot_general(
        c_ref[...], b_ref[...], (((1,), (1,)), ((), ())), preferred_element_type=jnp.float32
    )
    segc = segc_ref[:, 0:1]
    segr = segr_ref[0:1, :]
    rows = lax.broadcasted_iota(jnp.int32, (STRETCH, STRETCH), 0)
    cols = lax.broadcasted_iota(jnp.int32, (STRETCH, STRETCH), 1)
    gram = jnp.where((segc == segr) & (cols <= rows), gram, 0.0)
    cum = cum_ref[0]
    cumt = cumt_ref[0]
    step = dt_ref[0]
    for j in range(PER_GROUP):
        hc = slice(j * HEAD_DIM, (j + 1) * HEAD_DIM)
        gap = jnp.minimum(cum[:, j : j + 1] - cumt[j : j + 1, :], 0.0)
        weights = (gram * jnp.exp(gap)).astype(jnp.bfloat16)
        xf = x_ref[:, hc].astype(jnp.float32)
        scaled = (xf * step[:, j : j + 1]).astype(jnp.bfloat16)
        intra = jnp.dot(weights, scaled, preferred_element_type=jnp.float32)
        out_ref[:, hc] = intra + dsk_ref[:, hc] * xf


def intra_part(conv, dt_g, cum_g, cumt_g, segc, segr, dsk, g, into=None):
    tok = conv.shape[0]
    nb = tok // STRETCH
    b_col = INNER // STATE
    c_col = b_col + GROUPS
    operands = [conv, conv, conv, dt_g, cum_g, cumt_g, segc, segr, dsk]
    specs = [
        pl.BlockSpec((STRETCH, STATE), lambda b: (b, c_col + g)),
        pl.BlockSpec((STRETCH, STATE), lambda b: (b, b_col + g)),
        pl.BlockSpec((STRETCH, GROUP_COLS), lambda b: (b, g)),
        pl.BlockSpec((1, STRETCH, PER_GROUP), lambda b: (g, b, 0)),
        pl.BlockSpec((1, STRETCH, PER_GROUP), lambda b: (g, b, 0)),
        pl.BlockSpec((1, PER_GROUP, STRETCH), lambda b: (g, 0, b)),
        pl.BlockSpec((STRETCH, 1), lambda b: (b, 0)),
        pl.BlockSpec((8, STRETCH), lambda b: (0, b)),
        pl.BlockSpec((1, GROUP_COLS), lambda b: (0, g)),
    ]
    kernel = intra_kernel
    aliases = {}
    if into is not None:
        operands.append(into)
        specs.append(pl.BlockSpec(memory_space=pl.ANY))
        aliases = {len(operands) - 1: 0}

        def kernel(*refs):
            intra_kernel(*refs[:-2], refs[-1])

    return pl.pallas_call(
        kernel,
        grid=(nb,),
        in_specs=specs,
        out_specs=pl.BlockSpec((STRETCH, GROUP_COLS), lambda b: (b, g)),
        out_shape=jax.ShapeDtypeStruct((tok, INNER), jnp.float32),
        input_output_aliases=aliases,
    )(*operands)


def mix_kernel(
    c_ref, y_ref, z_ref, hin_ref, local_ref, cdec_ref, cum_ref, segc_ref, eb_ref, gain_ref,
    out_ref,
):
    state = cdec_ref[0] * hin_ref[...].astype(jnp.float32) + local_ref[0]
    segc = segc_ref[:, 0:1]
    entry = eb_ref[0:1, 0:1]
    in_weight = jnp.where(segc == entry, jnp.exp(cum_ref[0]), 0.0)
    inter = jnp.dot(c_ref[...], state.astype(jnp.bfloat16), preferred_element_type=jnp.float32)
    y = y_ref[...] + inter * expand_heads(in_weight)
    zf = z_ref[...].astype(jnp.float32)
    gated = y * (zf * jax.nn.sigmoid(zf))
    mean_square = jnp.mean(gated * gated, axis=1, keepdims=True) + 1e-05
    out_ref[...] = (gated * lax.rsqrt(mean_square) * gain_ref[...]).astype(jnp.bfloat16)


def mix(conv, y_local, z_gate, hin, local_states, cdec, cum_g, segc, eb, gain, core_arr, which,
        prev=None):
    tok = conv.shape[0]
    nb = tok // STRETCH
    c_col = INNER // STATE + GROUPS

    def grp(c):
        return (which + c[0]) % GROUPS

    operands = [conv, y_local, z_gate, hin, local_states, cdec, cum_g, segc, eb, gain]
    specs = [
        pl.BlockSpec((STRETCH, STATE), lambda b, c: (b, c_col + grp(c))),
        pl.BlockSpec((STRETCH, GROUP_COLS), lambda b, c: (b, grp(c))),
        pl.BlockSpec((STRETCH, GROUP_COLS), lambda b, c: (b, grp(c))),
        pl.BlockSpec((STATE, GROUP_COLS), lambda b, c: (0, 0)),
        pl.BlockSpec((1, STATE, GROUP_COLS), lambda b, c: (b, 0, grp(c))),
        pl.BlockSpec((1, 1, GROUP_COLS), lambda b, c: (b, 0, grp(c))),
        pl.BlockSpec((1, STRETCH, PER_GROUP), lambda b, c: (grp(c), b, 0)),
        pl.BlockSpec((STRETCH, 1), lambda b, c: (b, 0)),
        pl.BlockSpec((8, 128), lambda b, c: (b, 0)),
        pl.BlockSpec((1, GROUP_COLS), lambda b, c: (0, grp(c))),
    ]
    kernel = mix_kernel
    aliases = {}
    if prev is not None:
        operands.append(prev)
        specs.append(pl.BlockSpec(memory_space=pl.ANY))
        aliases = {len(operands): 0}

        def kernel(*refs):
            mix_kernel(*refs[:-2], refs[-1])

    def with_core(core_ref, *refs):
        del core_ref
        kernel(*refs)

    grid_spec = pltpu.PrefetchScalarGridSpec(
        num_scalar_prefetch=1,
        grid=(nb,),
        in_specs=specs,
        out_specs=pl.BlockSpec((STRETCH, GROUP_COLS), lambda b, c: (b, grp(c))),
    )
    return pl.pallas_call(
        with_core,
        grid_spec=grid_spec,
        out_shape=jax.ShapeDtypeStruct((tok, INNER), jnp.bfloat16),
        input_output_aliases=aliases,
    )(core_arr, *operands)


def scan_kernel(got_ref, out_ref):
    peers = got_ref.shape[0]

    def body(d, carry):
        out_ref[d] = carry.astype(jnp.bfloat16)
        decay = got_ref[d, STATE : STATE + 1, :].astype(jnp.float32) + got_ref[
            d, STATE + 1 : STATE + 2, :
        ].astype(jnp.float32)
        return decay * carry + got_ref[d, 0:STATE, :].astype(jnp.float32)

    lax.fori_loop(0, peers, body, jnp.zeros(out_ref.shape[1:], jnp.float32))


def swap_cores(value):
    return lax.ppermute(value, "core", [(0, 1), (1, 0)])


def tie(value, *after):
    def kernel(*refs):
        del refs

    return pl.pallas_call(
        kernel,
        in_specs=[pl.BlockSpec(memory_space=pl.ANY) for _ in range(1 + len(after))],
        out_specs=pl.BlockSpec(memory_space=pl.ANY),
        out_shape=jax.ShapeDtypeStruct(value.shape, value.dtype),
        input_output_aliases={0: 0},
    )(value, *after)


def compose(for_other, mine, first_work, second_work):
    core = lax.axis_index("core")
    chips = lax.axis_size("chip")
    half = GROUP_COLS
    width = half // chips
    theirs = swap_cores(for_other)
    first = jnp.where(core == 0, mine, theirs)
    second = jnp.where(core == 0, theirs, mine)
    first_decay = first[STATE:]
    chip_state = second[STATE:] * first[:STATE] + second[:STATE]
    chip_decay = first_decay * second[STATE:]
    decay_hi = chip_decay.astype(jnp.bfloat16)
    decay_lo = (chip_decay - decay_hi.astype(jnp.float32)).astype(jnp.bfloat16)
    payload = jnp.concatenate(
        [chip_state.astype(jnp.bfloat16), decay_hi, decay_lo], axis=0
    ).reshape(STATE + 2, chips, width).transpose(1, 0, 2)
    work = first_work()
    got = tie(lax.all_to_all(payload, "chip", split_axis=0, concat_axis=0, tiled=True), work)
    entering = pl.pallas_call(
        scan_kernel,
        out_shape=jax.ShapeDtypeStruct((chips, STATE, width), jnp.bfloat16),
    )(got)
    work = second_work(work)
    back = tie(lax.all_to_all(entering, "chip", split_axis=0, concat_axis=0, tiled=True), work)
    chip_in = back.transpose(1, 0, 2).reshape(STATE, half).astype(jnp.float32)
    later_in = first_decay * chip_in + first[:STATE]
    keep = jnp.where(core == 0, chip_in, later_in).astype(jnp.bfloat16)
    other = swap_cores(jnp.where(core == 0, later_in, chip_in).astype(jnp.bfloat16))
    return keep, other, work


def local(xbc, z_gate, dt_raw, lengths, conv_weight, conv_bias, dt_bias, a_log, d_skip, norm_gain):
    tok = xbc.shape[0]
    nb = tok // STRETCH
    first_pos = (lax.axis_index("chip") * lax.axis_size("core") + lax.axis_index("core")) * tok
    rim_rows = shifted(xbc[tok - (CONV - 1) :], ("chip", "core"), 1)
    rim8 = jnp.concatenate([jnp.zeros((8 - (CONV - 1), CHANNELS), xbc.dtype), rim_rows], axis=0)
    ext_pos = first_pos - (CONV - 1) + jnp.arange(tok + CONV - 1)
    ext_seg = segment_of(ext_pos, lengths)
    target = ext_seg[CONV - 1 :]
    kept = [
        (ext_pos[tap : tap + tok] >= 0) & (ext_seg[tap : tap + tok] == target) for tap in range(CONV)
    ]
    masks = jnp.stack(kept, axis=1).astype(jnp.float32)
    conv = conv_part(xbc, rim8, conv_weight, conv_bias[None, :], masks)
    raw_g = dt_raw.reshape(tok, GROUPS, PER_GROUP).transpose(1, 0, 2).astype(jnp.float32)
    dt_g = jax.nn.softplus(raw_g + dt_bias.reshape(GROUPS, 1, PER_GROUP))
    log_decay = -dt_g * jnp.exp(a_log).reshape(GROUPS, 1, PER_GROUP)
    cum_blocks = jnp.cumsum(log_decay.reshape(GROUPS, nb, STRETCH, PER_GROUP), axis=2)
    cum_g = cum_blocks.reshape(GROUPS, tok, PER_GROUP)
    segments = segment_of(first_pos + jnp.arange(tok), lengths)
    seg_before = segment_of(first_pos + jnp.arange(nb) * STRETCH - 1, lengths)
    seg_last = segments.reshape(nb, STRETCH)[:, -1]
    cum_last = cum_blocks[:, :, -1, :].transpose(1, 0, 2).reshape(nb, HEADS)
    block_decay = jnp.where((seg_last == seg_before)[:, None], jnp.exp(cum_last), 0.0)

    cumt_g = cum_g.transpose(0, 2, 1)
    segc = segments[:, None].astype(jnp.int32)
    segr = jnp.broadcast_to(segments[None, :], (8, tok)).astype(jnp.int32)
    eb = jnp.broadcast_to(seg_before[:, None, None], (nb, 8, 128)).reshape(nb * 8, 128)
    eb = eb.astype(jnp.int32)
    bdec = jnp.repeat(block_decay, HEAD_DIM, axis=1)[:, None, :]

    core_arr = lax.axis_index("core").astype(jnp.int32).reshape(1)
    local_a, cdec_a, for_other = half_states(conv, conv, dt_g, cum_g, segc, bdec, core_arr, 0)
    local_states, cdec, mine = half_states(
        conv, conv, dt_g, cum_g, segc, bdec, core_arr, 1, (local_a, cdec_a)
    )
    dsk = jnp.repeat(d_skip, HEAD_DIM)[None, :]
    def first_work():
        return intra_part(conv, dt_g, cum_g, cumt_g, segc, segr, dsk, 0)

    def second_work(done):
        return intra_part(conv, dt_g, cum_g, cumt_g, segc, segr, dsk, 1, done)

    keep, other, y_local = compose(for_other, mine, first_work, second_work)
    gain = norm_gain[None, :]
    parts = (y_local, z_gate)
    rest = (local_states, cdec, cum_g, segc, eb, gain, core_arr)
    out = mix(conv, *parts, keep, *rest, 0)
    return mix(conv, *parts, other, *rest, 1, out)


def solution(mesh):
    groups, peers = mesh.devices.shape
    split = Mesh(mesh.devices.reshape(groups, peers // 2, 2), ("group", "chip", "core"))
    rows = P(("group", "chip", "core"), None)
    return jax.shard_map(
        local,
        mesh=split,
        in_specs=(rows, rows, rows, P("group"), P(), P(), P(), P(), P(), P()),
        out_specs=rows,
        check_vma=False,
    )
```

```python
import jax
import jax.numpy as jnp
from jax import lax
from jax.experimental import pallas as pl
from jax.experimental.pallas import tpu as pltpu
from jax.sharding import Mesh, PartitionSpec as P

HEADS = 64
HEAD_DIM = 64
STATE = 256
GROUPS = 2
CONV = 4
STRETCH = 256
CHANNELS = 5120
INNER = HEADS * HEAD_DIM
PER_GROUP = HEADS // GROUPS
GROUP_COLS = INNER // GROUPS


def shifted(value, axis, by):
    peers = lax.axis_size(axis)
    pairs = [(i, i + by) for i in range(peers) if 0 <= i + by < peers]
    return lax.ppermute(value, axis, pairs)


def segment_of(positions, lengths):
    prompt_ends = jnp.cumsum(lengths)
    hits = (prompt_ends[None, :] <= positions[:, None]).astype(jnp.int32)
    return jnp.sum(hits, axis=1)


def expand_heads(v):
    heads = lax.broadcasted_iota(jnp.int32, (PER_GROUP, GROUP_COLS), 0)
    cols = lax.broadcasted_iota(jnp.int32, (PER_GROUP, GROUP_COLS), 1)
    spread = (cols // HEAD_DIM == heads).astype(jnp.bfloat16)
    hi = v.astype(jnp.bfloat16)
    rest = v - hi.astype(jnp.float32)
    mid = rest.astype(jnp.bfloat16)
    lo = (rest - mid.astype(jnp.float32)).astype(jnp.bfloat16)
    out = jnp.dot(hi, spread, preferred_element_type=jnp.float32)
    out = out + jnp.dot(mid, spread, preferred_element_type=jnp.float32)
    return out + jnp.dot(lo, spread, preferred_element_type=jnp.float32)


CONV_COLS = 1280


def conv_kernel(x_ref, rim_ref, w_ref, bias_ref, m_ref, out_ref):
    x = x_ref[...].astype(jnp.float32)
    rim = rim_ref[...].astype(jnp.float32)
    rows8 = lax.broadcasted_iota(jnp.int32, rim.shape, 0)
    summed = jnp.zeros(x.shape, jnp.float32)
    top = jnp.zeros(rim.shape, jnp.float32)
    for tap in range(CONV):
        by = CONV - 1 - tap
        wk = w_ref[tap : tap + 1, :]
        kept = m_ref[:, tap : tap + 1] > 0.0
        if by == 0:
            term = x
            top_term = x[0:8]
        else:
            term = pltpu.roll(x, by, 0)
            top_term = jnp.where(rows8 < by, pltpu.roll(rim, by, 0), term[0:8])
        summed = summed + jnp.where(kept, term * wk, 0.0)
        top = top + jnp.where(kept[0:8], top_term * wk, 0.0)
    out_ref[...] = jax.nn.silu(summed + bias_ref[...]).astype(jnp.bfloat16)
    out_ref[0:8, :] = jax.nn.silu(top + bias_ref[...]).astype(jnp.bfloat16)


def conv_part(xbc, rim8, w8, bias, masks):
    tok, chans = xbc.shape
    return pl.pallas_call(
        conv_kernel,
        grid=(chans // CONV_COLS,),
        in_specs=[
            pl.BlockSpec((tok, CONV_COLS), lambda c: (0, c)),
            pl.BlockSpec((8, CONV_COLS), lambda c: (0, c)),
            pl.BlockSpec((CONV, CONV_COLS), lambda c: (0, c)),
            pl.BlockSpec((1, CONV_COLS), lambda c: (0, c)),
            pl.BlockSpec((tok, CONV), lambda c: (0, 0)),
        ],
        out_specs=pl.BlockSpec((tok, CONV_COLS), lambda c: (0, c)),
        out_shape=jax.ShapeDtypeStruct((tok, chans), jnp.bfloat16),
    )(xbc, rim8, w8, bias, masks)


def state_kernel(
    bt_ref, x_ref, dt_ref, cum_ref, segc_ref, bdec_ref, local_ref, cdec_ref, tot_ref,
    acc_ref, dec_ref,
):
    b = pl.program_id(1)

    @pl.when(b == 0)
    def _():
        acc_ref[...] = jnp.zeros(acc_ref.shape, jnp.float32)
        dec_ref[...] = jnp.ones(dec_ref.shape, jnp.float32)

    local_ref[0] = acc_ref[...]
    cdec_ref[0] = dec_ref[...]
    cum = cum_ref[0]
    step = dt_ref[0]
    segc = segc_ref[:, 0:1]
    last = cum[STRETCH - 1 : STRETCH, :]
    seg_last = segc[STRETCH - 1 : STRETCH, :]
    w = jnp.where(segc == seg_last, jnp.exp(last - cum), 0.0)
    scaled = (x_ref[...].astype(jnp.float32) * expand_heads(step)).astype(jnp.bfloat16)
    weighted = (scaled.astype(jnp.float32) * expand_heads(w)).astype(jnp.bfloat16)
    block_state = jnp.dot(bt_ref[...], weighted, preferred_element_type=jnp.float32)
    decay = bdec_ref[0]
    acc_ref[...] = decay * acc_ref[...] + block_state
    dec_ref[...] = dec_ref[...] * decay

    @pl.when(b == pl.num_programs(1) - 1)
    def _():
        tot_ref[0, 0:STATE, :] = acc_ref[...]
        tot_ref[0, STATE : STATE + 1, :] = dec_ref[...]


def half_state_kernel(
    core_ref, bt_ref, x_ref, dt_ref, cum_ref, segc_ref, bdec_ref, *rest
):
    local_ref, cdec_ref, tot_ref, acc_ref, dec_ref = rest[-5:]
    del core_ref
    b = pl.program_id(0)

    @pl.when(b == 0)
    def _():
        acc_ref[...] = jnp.zeros(acc_ref.shape, jnp.float32)
        dec_ref[...] = jnp.ones(dec_ref.shape, jnp.float32)

    local_ref[0] = acc_ref[...]
    cdec_ref[0] = dec_ref[...]
    cum = cum_ref[0]
    step = dt_ref[0]
    segc = segc_ref[:, 0:1]
    last = cum[STRETCH - 1 : STRETCH, :]
    seg_last = segc[STRETCH - 1 : STRETCH, :]
    w = jnp.where(segc == seg_last, jnp.exp(last - cum), 0.0)
    scaled = (x_ref[...].astype(jnp.float32) * expand_heads(step)).astype(jnp.bfloat16)
    weighted = (scaled.astype(jnp.float32) * expand_heads(w)).astype(jnp.bfloat16)
    block_state = lax.dot_general(
        bt_ref[...], weighted, (((0,), (0,)), ((), ())), preferred_element_type=jnp.float32
    )
    decay = bdec_ref[0]
    acc_ref[...] = decay * acc_ref[...] + block_state
    dec_ref[...] = dec_ref[...] * decay

    @pl.when(b == pl.num_programs(0) - 1)
    def _():
        tot_ref[0:STATE, :] = acc_ref[...]
        tot_ref[STATE : STATE + 1, :] = dec_ref[...]


def half_states(bt, conv, dt_g, cum_g, segc, bdec, core_arr, which, prev=None):
    tok = conv.shape[0]
    nb = tok // STRETCH

    def grp(c):
        return (which + 1 + c[0]) % GROUPS

    operands = [bt, conv, dt_g, cum_g, segc, bdec]
    specs = [
        pl.BlockSpec((STRETCH, STATE), lambda b, c: (b, INNER // STATE + grp(c))),
        pl.BlockSpec((STRETCH, GROUP_COLS), lambda b, c: (b, grp(c))),
        pl.BlockSpec((1, STRETCH, PER_GROUP), lambda b, c: (grp(c), b, 0)),
        pl.BlockSpec((1, STRETCH, PER_GROUP), lambda b, c: (grp(c), b, 0)),
        pl.BlockSpec((STRETCH, 128), lambda b, c: (b, 0)),
        pl.BlockSpec((1, 1, GROUP_COLS), lambda b, c: (b, 0, grp(c))),
    ]
    aliases = {}
    if prev is not None:
        operands += list(prev)
        specs += [pl.BlockSpec(memory_space=pl.ANY), pl.BlockSpec(memory_space=pl.ANY)]
        aliases = {len(operands) - 1: 0, len(operands): 1}
    grid_spec = pltpu.PrefetchScalarGridSpec(
        num_scalar_prefetch=1,
        grid=(nb,),
        in_specs=specs,
        out_specs=[
            pl.BlockSpec((1, STATE, GROUP_COLS), lambda b, c: (b, 0, grp(c))),
            pl.BlockSpec((1, 1, GROUP_COLS), lambda b, c: (b, 0, grp(c))),
            pl.BlockSpec((STATE + 1, GROUP_COLS), lambda b, c: (0, 0)),
        ],
        scratch_shapes=[
            pltpu.VMEM((STATE, GROUP_COLS), jnp.float32),
            pltpu.VMEM((1, GROUP_COLS), jnp.float32),
        ],
    )
    return pl.pallas_call(
        half_state_kernel,
        grid_spec=grid_spec,
        out_shape=[
            jax.ShapeDtypeStruct((nb, STATE, INNER), jnp.float32),
            jax.ShapeDtypeStruct((nb, 1, INNER), jnp.float32),
            jax.ShapeDtypeStruct((STATE + 1, GROUP_COLS), jnp.float32),
        ],
        input_output_aliases=aliases,
    )(core_arr, *operands)


def intra_kernel(
    c_ref, b_ref, x_ref, dt_ref, cum_ref, cumt_ref, segc_ref, segr_ref, dsk_ref, out_ref
):
    gram = lax.dot_general(
        c_ref[...], b_ref[...], (((1,), (1,)), ((), ())), preferred_element_type=jnp.float32
    )
    segc = segc_ref[:, 0:1]
    segr = segr_ref[0:1, :]
    rows = lax.broadcasted_iota(jnp.int32, (STRETCH, STRETCH), 0)
    cols = lax.broadcasted_iota(jnp.int32, (STRETCH, STRETCH), 1)
    gram = jnp.where((segc == segr) & (cols <= rows), gram, 0.0)
    cum = cum_ref[0]
    cumt = cumt_ref[0]
    step = dt_ref[0]
    for j in range(PER_GROUP):
        hc = slice(j * HEAD_DIM, (j + 1) * HEAD_DIM)
        gap = jnp.minimum(cum[:, j : j + 1] - cumt[j : j + 1, :], 0.0)
        weights = (gram * jnp.exp(gap)).astype(jnp.bfloat16)
        xf = x_ref[:, hc].astype(jnp.float32)
        scaled = (xf * step[:, j : j + 1]).astype(jnp.bfloat16)
        intra = jnp.dot(weights, scaled, preferred_element_type=jnp.float32)
        out_ref[:, hc] = intra + dsk_ref[:, hc] * xf


def intra_part(conv, dt_g, cum_g, cumt_g, segc, segr, dsk, g, into=None):
    tok = conv.shape[0]
    nb = tok // STRETCH
    b_col = INNER // STATE
    c_col = b_col + GROUPS
    operands = [conv, conv, conv, dt_g, cum_g, cumt_g, segc, segr, dsk]
    specs = [
        pl.BlockSpec((STRETCH, STATE), lambda b: (b, c_col + g)),
        pl.BlockSpec((STRETCH, STATE), lambda b: (b, b_col + g)),
        pl.BlockSpec((STRETCH, GROUP_COLS), lambda b: (b, g)),
        pl.BlockSpec((1, STRETCH, PER_GROUP), lambda b: (g, b, 0)),
        pl.BlockSpec((1, STRETCH, PER_GROUP), lambda b: (g, b, 0)),
        pl.BlockSpec((1, PER_GROUP, STRETCH), lambda b: (g, 0, b)),
        pl.BlockSpec((STRETCH, 128), lambda b: (b, 0)),
        pl.BlockSpec((8, STRETCH), lambda b: (0, b)),
        pl.BlockSpec((1, GROUP_COLS), lambda b: (0, g)),
    ]
    kernel = intra_kernel
    aliases = {}
    if into is not None:
        operands.append(into)
        specs.append(pl.BlockSpec(memory_space=pl.ANY))
        aliases = {len(operands) - 1: 0}

        def kernel(*refs):
            intra_kernel(*refs[:-2], refs[-1])

    return pl.pallas_call(
        kernel,
        grid=(nb,),
        in_specs=specs,
        out_specs=pl.BlockSpec((STRETCH, GROUP_COLS), lambda b: (b, g)),
        out_shape=jax.ShapeDtypeStruct((tok, INNER), jnp.float32),
        input_output_aliases=aliases,
    )(*operands)


def mix_kernel(
    c_ref, y_ref, z_ref, hin_ref, local_ref, cdec_ref, cum_ref, segc_ref, eb_ref, gain_ref,
    out_ref,
):
    state = cdec_ref[0] * hin_ref[...].astype(jnp.float32) + local_ref[0]
    segc = segc_ref[:, 0:1]
    entry = eb_ref[0:1, 0:1]
    in_weight = jnp.where(segc == entry, jnp.exp(cum_ref[0]), 0.0)
    inter = jnp.dot(c_ref[...], state.astype(jnp.bfloat16), preferred_element_type=jnp.float32)
    y = y_ref[...] + inter * expand_heads(in_weight)
    zf = z_ref[...].astype(jnp.float32)
    gated = y * (zf * jax.nn.sigmoid(zf))
    mean_square = jnp.mean(gated * gated, axis=1, keepdims=True) + 1e-05
    out_ref[...] = (gated * lax.rsqrt(mean_square) * gain_ref[...]).astype(jnp.bfloat16)


def mix(conv, y_local, z_gate, hin, local_states, cdec, cum_g, segc, eb, gain, core_arr, which,
        prev=None):
    tok = conv.shape[0]
    nb = tok // STRETCH
    c_col = INNER // STATE + GROUPS

    def grp(c):
        return (which + c[0]) % GROUPS

    operands = [conv, y_local, z_gate, hin, local_states, cdec, cum_g, segc, eb, gain]
    specs = [
        pl.BlockSpec((STRETCH, STATE), lambda b, c: (b, c_col + grp(c))),
        pl.BlockSpec((STRETCH, GROUP_COLS), lambda b, c: (b, grp(c))),
        pl.BlockSpec((STRETCH, GROUP_COLS), lambda b, c: (b, grp(c))),
        pl.BlockSpec((STATE, GROUP_COLS), lambda b, c: (0, 0)),
        pl.BlockSpec((1, STATE, GROUP_COLS), lambda b, c: (b, 0, grp(c))),
        pl.BlockSpec((1, 1, GROUP_COLS), lambda b, c: (b, 0, grp(c))),
        pl.BlockSpec((1, STRETCH, PER_GROUP), lambda b, c: (grp(c), b, 0)),
        pl.BlockSpec((STRETCH, 128), lambda b, c: (b, 0)),
        pl.BlockSpec((8, 128), lambda b, c: (b, 0)),
        pl.BlockSpec((1, GROUP_COLS), lambda b, c: (0, grp(c))),
    ]
    kernel = mix_kernel
    aliases = {}
    if prev is not None:
        operands.append(prev)
        specs.append(pl.BlockSpec(memory_space=pl.ANY))
        aliases = {len(operands): 0}

        def kernel(*refs):
            mix_kernel(*refs[:-2], refs[-1])

    def with_core(core_ref, *refs):
        del core_ref
        kernel(*refs)

    grid_spec = pltpu.PrefetchScalarGridSpec(
        num_scalar_prefetch=1,
        grid=(nb,),
        in_specs=specs,
        out_specs=pl.BlockSpec((STRETCH, GROUP_COLS), lambda b, c: (b, grp(c))),
    )
    return pl.pallas_call(
        with_core,
        grid_spec=grid_spec,
        out_shape=jax.ShapeDtypeStruct((tok, INNER), jnp.bfloat16),
        input_output_aliases=aliases,
    )(core_arr, *operands)


def scan_kernel(got_ref, out_ref):
    peers = got_ref.shape[0]

    def body(d, carry):
        out_ref[d] = carry.astype(jnp.bfloat16)
        decay = got_ref[d, STATE : STATE + 1, :].astype(jnp.float32) + got_ref[
            d, STATE + 1 : STATE + 2, :
        ].astype(jnp.float32)
        return decay * carry + got_ref[d, 0:STATE, :].astype(jnp.float32)

    lax.fori_loop(0, peers, body, jnp.zeros(out_ref.shape[1:], jnp.float32))


def swap_cores(value):
    return lax.ppermute(value, "core", [(0, 1), (1, 0)])


def tie(value, *after):
    def kernel(*refs):
        del refs

    return pl.pallas_call(
        kernel,
        in_specs=[pl.BlockSpec(memory_space=pl.ANY) for _ in range(1 + len(after))],
        out_specs=pl.BlockSpec(memory_space=pl.ANY),
        out_shape=jax.ShapeDtypeStruct(value.shape, value.dtype),
        input_output_aliases={0: 0},
    )(value, *after)


def compose(for_other, mine, first_work, second_work):
    core = lax.axis_index("core")
    chips = lax.axis_size("chip")
    half = GROUP_COLS
    width = half // chips
    theirs = swap_cores(for_other)
    first = jnp.where(core == 0, mine, theirs)
    second = jnp.where(core == 0, theirs, mine)
    first_decay = first[STATE:]
    chip_state = second[STATE:] * first[:STATE] + second[:STATE]
    chip_decay = first_decay * second[STATE:]
    decay_hi = chip_decay.astype(jnp.bfloat16)
    decay_lo = (chip_decay - decay_hi.astype(jnp.float32)).astype(jnp.bfloat16)
    payload = jnp.concatenate(
        [chip_state.astype(jnp.bfloat16), decay_hi, decay_lo], axis=0
    ).reshape(STATE + 2, chips, width).transpose(1, 0, 2)
    work = first_work()
    got = tie(lax.all_to_all(payload, "chip", split_axis=0, concat_axis=0, tiled=True), work)
    entering = pl.pallas_call(
        scan_kernel,
        out_shape=jax.ShapeDtypeStruct((chips, STATE, width), jnp.bfloat16),
    )(got)
    work = second_work(work)
    back = tie(lax.all_to_all(entering, "chip", split_axis=0, concat_axis=0, tiled=True), work)
    chip_in = back.transpose(1, 0, 2).reshape(STATE, half).astype(jnp.float32)
    later_in = first_decay * chip_in + first[:STATE]
    keep = jnp.where(core == 0, chip_in, later_in).astype(jnp.bfloat16)
    other = swap_cores(jnp.where(core == 0, later_in, chip_in).astype(jnp.bfloat16))
    return keep, other, work


def local(xbc, z_gate, dt_raw, lengths, conv_weight, conv_bias, dt_bias, a_log, d_skip, norm_gain):
    tok = xbc.shape[0]
    nb = tok // STRETCH
    first_pos = (lax.axis_index("chip") * lax.axis_size("core") + lax.axis_index("core")) * tok
    rim_rows = shifted(xbc[tok - (CONV - 1) :], ("chip", "core"), 1)
    rim8 = jnp.concatenate([jnp.zeros((8 - (CONV - 1), CHANNELS), xbc.dtype), rim_rows], axis=0)
    ext_pos = first_pos - (CONV - 1) + jnp.arange(tok + CONV - 1)
    ext_seg = segment_of(ext_pos, lengths)
    target = ext_seg[CONV - 1 :]
    kept = [
        (ext_pos[tap : tap + tok] >= 0) & (ext_seg[tap : tap + tok] == target) for tap in range(CONV)
    ]
    masks = jnp.stack(kept, axis=1).astype(jnp.float32)
    conv = conv_part(xbc, rim8, conv_weight, conv_bias[None, :], masks)
    raw_g = dt_raw.reshape(tok, GROUPS, PER_GROUP).transpose(1, 0, 2).astype(jnp.float32)
    dt_g = jax.nn.softplus(raw_g + dt_bias.reshape(GROUPS, 1, PER_GROUP))
    log_decay = -dt_g * jnp.exp(a_log).reshape(GROUPS, 1, PER_GROUP)
    cum_blocks = jnp.cumsum(log_decay.reshape(GROUPS, nb, STRETCH, PER_GROUP), axis=2)
    cum_g = cum_blocks.reshape(GROUPS, tok, PER_GROUP)
    segments = segment_of(first_pos + jnp.arange(tok), lengths)
    seg_before = segment_of(first_pos + jnp.arange(nb) * STRETCH - 1, lengths)
    seg_last = segments.reshape(nb, STRETCH)[:, -1]
    cum_last = cum_blocks[:, :, -1, :].transpose(1, 0, 2).reshape(nb, HEADS)
    block_decay = jnp.where((seg_last == seg_before)[:, None], jnp.exp(cum_last), 0.0)

    cumt_g = cum_g.transpose(0, 2, 1)
    segc = jnp.broadcast_to(segments[:, None], (tok, 128)).astype(jnp.int32)
    segr = jnp.broadcast_to(segments[None, :], (8, tok)).astype(jnp.int32)
    eb = jnp.broadcast_to(seg_before[:, None, None], (nb, 8, 128)).reshape(nb * 8, 128)
    eb = eb.astype(jnp.int32)
    bdec = jnp.repeat(block_decay, HEAD_DIM, axis=1)[:, None, :]

    core_arr = lax.axis_index("core").astype(jnp.int32).reshape(1)
    local_a, cdec_a, for_other = half_states(conv, conv, dt_g, cum_g, segc, bdec, core_arr, 0)
    local_states, cdec, mine = half_states(
        conv, conv, dt_g, cum_g, segc, bdec, core_arr, 1, (local_a, cdec_a)
    )
    dsk = jnp.repeat(d_skip, HEAD_DIM)[None, :]
    def first_work():
        return intra_part(conv, dt_g, cum_g, cumt_g, segc, segr, dsk, 0)

    def second_work(done):
        return intra_part(conv, dt_g, cum_g, cumt_g, segc, segr, dsk, 1, done)

    keep, other, y_local = compose(for_other, mine, first_work, second_work)
    gain = norm_gain[None, :]
    parts = (y_local, z_gate)
    rest = (local_states, cdec, cum_g, segc, eb, gain, core_arr)
    out = mix(conv, *parts, keep, *rest, 0)
    return mix(conv, *parts, other, *rest, 1, out)


def solution(mesh):
    groups, peers = mesh.devices.shape
    split = Mesh(mesh.devices.reshape(groups, peers // 2, 2), ("group", "chip", "core"))
    rows = P(("group", "chip", "core"), None)
    return jax.shard_map(
        local,
        mesh=split,
        in_specs=(rows, rows, rows, P("group"), P(), P(), P(), P(), P(), P()),
        out_specs=rows,
        check_vma=False,
    )
```

```python
import jax
import jax.numpy as jnp
from jax import lax
from jax.experimental import pallas as pl
from jax.experimental.pallas import tpu as pltpu
from jax.sharding import Mesh, PartitionSpec as P

HEADS = 64
HEAD_DIM = 64
STATE = 256
GROUPS = 2
CONV = 4
STRETCH = 256
CHANNELS = 5120
INNER = HEADS * HEAD_DIM
PER_GROUP = HEADS // GROUPS
GROUP_COLS = INNER // GROUPS


def shifted(value, axis, by):
    peers = lax.axis_size(axis)
    pairs = [(i, i + by) for i in range(peers) if 0 <= i + by < peers]
    return lax.ppermute(value, axis, pairs)


def segment_of(positions, lengths):
    prompt_ends = jnp.cumsum(lengths)
    hits = (prompt_ends[None, :] <= positions[:, None]).astype(jnp.int32)
    return jnp.sum(hits, axis=1)


def expand_heads(v):
    heads = lax.broadcasted_iota(jnp.int32, (PER_GROUP, GROUP_COLS), 0)
    cols = lax.broadcasted_iota(jnp.int32, (PER_GROUP, GROUP_COLS), 1)
    spread = (cols // HEAD_DIM == heads).astype(jnp.bfloat16)
    hi = v.astype(jnp.bfloat16)
    rest = v - hi.astype(jnp.float32)
    mid = rest.astype(jnp.bfloat16)
    lo = (rest - mid.astype(jnp.float32)).astype(jnp.bfloat16)
    out = jnp.dot(hi, spread, preferred_element_type=jnp.float32)
    out = out + jnp.dot(mid, spread, preferred_element_type=jnp.float32)
    return out + jnp.dot(lo, spread, preferred_element_type=jnp.float32)


CONV_COLS = 640


def conv_kernel(x_ref, rim_ref, w_ref, bias_ref, m_ref, out_ref):
    x = x_ref[...].astype(jnp.float32)
    rim = rim_ref[...].astype(jnp.float32)
    rows8 = lax.broadcasted_iota(jnp.int32, rim.shape, 0)
    summed = jnp.zeros(x.shape, jnp.float32)
    top = jnp.zeros(rim.shape, jnp.float32)
    for tap in range(CONV):
        by = CONV - 1 - tap
        wk = w_ref[tap : tap + 1, :]
        kept = m_ref[:, tap : tap + 1] > 0.0
        if by == 0:
            term = x
            top_term = x[0:8]
        else:
            term = pltpu.roll(x, by, 0)
            top_term = jnp.where(rows8 < by, pltpu.roll(rim, by, 0), term[0:8])
        summed = summed + jnp.where(kept, term * wk, 0.0)
        top = top + jnp.where(kept[0:8], top_term * wk, 0.0)
    out_ref[...] = jax.nn.silu(summed + bias_ref[...]).astype(jnp.bfloat16)
    out_ref[0:8, :] = jax.nn.silu(top + bias_ref[...]).astype(jnp.bfloat16)


def conv_part(xbc, rim8, w8, bias, masks):
    tok, chans = xbc.shape
    return pl.pallas_call(
        conv_kernel,
        grid=(chans // CONV_COLS,),
        in_specs=[
            pl.BlockSpec((tok, CONV_COLS), lambda c: (0, c)),
            pl.BlockSpec((8, CONV_COLS), lambda c: (0, c)),
            pl.BlockSpec((CONV, CONV_COLS), lambda c: (0, c)),
            pl.BlockSpec((1, CONV_COLS), lambda c: (0, c)),
            pl.BlockSpec((tok, CONV), lambda c: (0, 0)),
        ],
        out_specs=pl.BlockSpec((tok, CONV_COLS), lambda c: (0, c)),
        out_shape=jax.ShapeDtypeStruct((tok, chans), jnp.bfloat16),
    )(xbc, rim8, w8, bias, masks)


def state_kernel(
    bt_ref, x_ref, dt_ref, cum_ref, segc_ref, bdec_ref, local_ref, cdec_ref, tot_ref,
    acc_ref, dec_ref,
):
    b = pl.program_id(1)

    @pl.when(b == 0)
    def _():
        acc_ref[...] = jnp.zeros(acc_ref.shape, jnp.float32)
        dec_ref[...] = jnp.ones(dec_ref.shape, jnp.float32)

    local_ref[0] = acc_ref[...]
    cdec_ref[0] = dec_ref[...]
    cum = cum_ref[0]
    step = dt_ref[0]
    segc = segc_ref[:, 0:1]
    last = cum[STRETCH - 1 : STRETCH, :]
    seg_last = segc[STRETCH - 1 : STRETCH, :]
    w = jnp.where(segc == seg_last, jnp.exp(last - cum), 0.0)
    scaled = (x_ref[...].astype(jnp.float32) * expand_heads(step)).astype(jnp.bfloat16)
    weighted = (scaled.astype(jnp.float32) * expand_heads(w)).astype(jnp.bfloat16)
    block_state = jnp.dot(bt_ref[...], weighted, preferred_element_type=jnp.float32)
    decay = bdec_ref[0]
    acc_ref[...] = decay * acc_ref[...] + block_state
    dec_ref[...] = dec_ref[...] * decay

    @pl.when(b == pl.num_programs(1) - 1)
    def _():
        tot_ref[0, 0:STATE, :] = acc_ref[...]
        tot_ref[0, STATE : STATE + 1, :] = dec_ref[...]


def half_state_kernel(
    core_ref, bt_ref, x_ref, dt_ref, cum_ref, segc_ref, bdec_ref, *rest
):
    local_ref, cdec_ref, tot_ref, acc_ref, dec_ref = rest[-5:]
    del core_ref
    b = pl.program_id(0)

    @pl.when(b == 0)
    def _():
        acc_ref[...] = jnp.zeros(acc_ref.shape, jnp.float32)
        dec_ref[...] = jnp.ones(dec_ref.shape, jnp.float32)

    local_ref[0] = acc_ref[...]
    cdec_ref[0] = dec_ref[...]
    cum = cum_ref[0]
    step = dt_ref[0]
    segc = segc_ref[:, 0:1]
    last = cum[STRETCH - 1 : STRETCH, :]
    seg_last = segc[STRETCH - 1 : STRETCH, :]
    w = jnp.where(segc == seg_last, jnp.exp(last - cum), 0.0)
    scaled = (x_ref[...].astype(jnp.float32) * expand_heads(step)).astype(jnp.bfloat16)
    weighted = (scaled.astype(jnp.float32) * expand_heads(w)).astype(jnp.bfloat16)
    block_state = lax.dot_general(
        bt_ref[...], weighted, (((0,), (0,)), ((), ())), preferred_element_type=jnp.float32
    )
    decay = bdec_ref[0]
    acc_ref[...] = decay * acc_ref[...] + block_state
    dec_ref[...] = dec_ref[...] * decay

    @pl.when(b == pl.num_programs(0) - 1)
    def _():
        tot_ref[0:STATE, :] = acc_ref[...]
        tot_ref[STATE : STATE + 1, :] = dec_ref[...]


def half_states(bt, conv, dt_g, cum_g, segc, bdec, core_arr, which, prev=None):
    tok = conv.shape[0]
    nb = tok // STRETCH

    def grp(c):
        return (which + 1 + c[0]) % GROUPS

    operands = [bt, conv, dt_g, cum_g, segc, bdec]
    specs = [
        pl.BlockSpec((STRETCH, STATE), lambda b, c: (b, INNER // STATE + grp(c))),
        pl.BlockSpec((STRETCH, GROUP_COLS), lambda b, c: (b, grp(c))),
        pl.BlockSpec((1, STRETCH, PER_GROUP), lambda b, c: (grp(c), b, 0)),
        pl.BlockSpec((1, STRETCH, PER_GROUP), lambda b, c: (grp(c), b, 0)),
        pl.BlockSpec((STRETCH, 128), lambda b, c: (b, 0)),
        pl.BlockSpec((1, 1, GROUP_COLS), lambda b, c: (b, 0, grp(c))),
    ]
    aliases = {}
    if prev is not None:
        operands += list(prev)
        specs += [pl.BlockSpec(memory_space=pl.ANY), pl.BlockSpec(memory_space=pl.ANY)]
        aliases = {len(operands) - 1: 0, len(operands): 1}
    grid_spec = pltpu.PrefetchScalarGridSpec(
        num_scalar_prefetch=1,
        grid=(nb,),
        in_specs=specs,
        out_specs=[
            pl.BlockSpec((1, STATE, GROUP_COLS), lambda b, c: (b, 0, grp(c))),
            pl.BlockSpec((1, 1, GROUP_COLS), lambda b, c: (b, 0, grp(c))),
            pl.BlockSpec((STATE + 1, GROUP_COLS), lambda b, c: (0, 0)),
        ],
        scratch_shapes=[
            pltpu.VMEM((STATE, GROUP_COLS), jnp.float32),
            pltpu.VMEM((1, GROUP_COLS), jnp.float32),
        ],
    )
    return pl.pallas_call(
        half_state_kernel,
        grid_spec=grid_spec,
        out_shape=[
            jax.ShapeDtypeStruct((nb, STATE, INNER), jnp.float32),
            jax.ShapeDtypeStruct((nb, 1, INNER), jnp.float32),
            jax.ShapeDtypeStruct((STATE + 1, GROUP_COLS), jnp.float32),
        ],
        input_output_aliases=aliases,
    )(core_arr, *operands)


def intra_kernel(
    c_ref, b_ref, x_ref, dt_ref, cum_ref, cumt_ref, segc_ref, segr_ref, dsk_ref, out_ref
):
    gram = lax.dot_general(
        c_ref[...], b_ref[...], (((1,), (1,)), ((), ())), preferred_element_type=jnp.float32
    )
    segc = segc_ref[:, 0:1]
    segr = segr_ref[0:1, :]
    rows = lax.broadcasted_iota(jnp.int32, (STRETCH, STRETCH), 0)
    cols = lax.broadcasted_iota(jnp.int32, (STRETCH, STRETCH), 1)
    gram = jnp.where((segc == segr) & (cols <= rows), gram, 0.0)
    cum = cum_ref[0]
    cumt = cumt_ref[0]
    step = dt_ref[0]
    for j in range(PER_GROUP):
        hc = slice(j * HEAD_DIM, (j + 1) * HEAD_DIM)
        gap = jnp.minimum(cum[:, j : j + 1] - cumt[j : j + 1, :], 0.0)
        weights = (gram * jnp.exp(gap)).astype(jnp.bfloat16)
        xf = x_ref[:, hc].astype(jnp.float32)
        scaled = (xf * step[:, j : j + 1]).astype(jnp.bfloat16)
        intra = jnp.dot(weights, scaled, preferred_element_type=jnp.float32)
        out_ref[:, hc] = intra + dsk_ref[:, hc] * xf


def intra_part(conv, dt_g, cum_g, cumt_g, segc, segr, dsk, g, into=None):
    tok = conv.shape[0]
    nb = tok // STRETCH
    b_col = INNER // STATE
    c_col = b_col + GROUPS
    operands = [conv, conv, conv, dt_g, cum_g, cumt_g, segc, segr, dsk]
    specs = [
        pl.BlockSpec((STRETCH, STATE), lambda b: (b, c_col + g)),
        pl.BlockSpec((STRETCH, STATE), lambda b: (b, b_col + g)),
        pl.BlockSpec((STRETCH, GROUP_COLS), lambda b: (b, g)),
        pl.BlockSpec((1, STRETCH, PER_GROUP), lambda b: (g, b, 0)),
        pl.BlockSpec((1, STRETCH, PER_GROUP), lambda b: (g, b, 0)),
        pl.BlockSpec((1, PER_GROUP, STRETCH), lambda b: (g, 0, b)),
        pl.BlockSpec((STRETCH, 128), lambda b: (b, 0)),
        pl.BlockSpec((8, STRETCH), lambda b: (0, b)),
        pl.BlockSpec((1, GROUP_COLS), lambda b: (0, g)),
    ]
    kernel = intra_kernel
    aliases = {}
    if into is not None:
        operands.append(into)
        specs.append(pl.BlockSpec(memory_space=pl.ANY))
        aliases = {len(operands) - 1: 0}

        def kernel(*refs):
            intra_kernel(*refs[:-2], refs[-1])

    return pl.pallas_call(
        kernel,
        grid=(nb,),
        in_specs=specs,
        out_specs=pl.BlockSpec((STRETCH, GROUP_COLS), lambda b: (b, g)),
        out_shape=jax.ShapeDtypeStruct((tok, INNER), jnp.float32),
        input_output_aliases=aliases,
    )(*operands)


def mix_kernel(
    c_ref, y_ref, z_ref, hin_ref, local_ref, cdec_ref, cum_ref, segc_ref, eb_ref, gain_ref,
    out_ref,
):
    hin = hin_ref[...].astype(jnp.float32)
    state = jnp.where(pl.program_id(0) == 0, hin, cdec_ref[0] * hin + local_ref[0])
    segc = segc_ref[:, 0:1]
    entry = eb_ref[0:1, 0:1]
    in_weight = jnp.where(segc == entry, jnp.exp(cum_ref[0]), 0.0)
    inter = jnp.dot(c_ref[...], state.astype(jnp.bfloat16), preferred_element_type=jnp.float32)
    y = y_ref[...] + inter * expand_heads(in_weight)
    zf = z_ref[...].astype(jnp.float32)
    gated = y * (zf * jax.nn.sigmoid(zf))
    mean_square = jnp.mean(gated * gated, axis=1, keepdims=True) + 1e-05
    out_ref[...] = (gated * lax.rsqrt(mean_square) * gain_ref[...]).astype(jnp.bfloat16)


def mix(conv, y_local, z_gate, hin, local_states, cdec, cum_g, segc, eb, gain, core_arr, which,
        prev=None):
    tok = conv.shape[0]
    nb = tok // STRETCH
    c_col = INNER // STATE + GROUPS

    def grp(c):
        return (which + c[0]) % GROUPS

    operands = [conv, y_local, z_gate, hin, local_states, cdec, cum_g, segc, eb, gain]
    specs = [
        pl.BlockSpec((STRETCH, STATE), lambda b, c: (b, c_col + grp(c))),
        pl.BlockSpec((STRETCH, GROUP_COLS), lambda b, c: (b, grp(c))),
        pl.BlockSpec((STRETCH, GROUP_COLS), lambda b, c: (b, grp(c))),
        pl.BlockSpec((STATE, GROUP_COLS), lambda b, c: (0, 0)),
        pl.BlockSpec((1, STATE, GROUP_COLS), lambda b, c: (jnp.maximum(b, 1), 0, grp(c))),
        pl.BlockSpec((1, 1, GROUP_COLS), lambda b, c: (jnp.maximum(b, 1), 0, grp(c))),
        pl.BlockSpec((1, STRETCH, PER_GROUP), lambda b, c: (grp(c), b, 0)),
        pl.BlockSpec((STRETCH, 128), lambda b, c: (b, 0)),
        pl.BlockSpec((8, 128), lambda b, c: (b, 0)),
        pl.BlockSpec((1, GROUP_COLS), lambda b, c: (0, grp(c))),
    ]
    kernel = mix_kernel
    aliases = {}
    if prev is not None:
        operands.append(prev)
        specs.append(pl.BlockSpec(memory_space=pl.ANY))
        aliases = {len(operands): 0}

        def kernel(*refs):
            mix_kernel(*refs[:-2], refs[-1])

    def with_core(core_ref, *refs):
        del core_ref
        kernel(*refs)

    grid_spec = pltpu.PrefetchScalarGridSpec(
        num_scalar_prefetch=1,
        grid=(nb,),
        in_specs=specs,
        out_specs=pl.BlockSpec((STRETCH, GROUP_COLS), lambda b, c: (b, grp(c))),
    )
    return pl.pallas_call(
        with_core,
        grid_spec=grid_spec,
        out_shape=jax.ShapeDtypeStruct((tok, INNER), jnp.bfloat16),
        input_output_aliases=aliases,
    )(core_arr, *operands)


def scan_kernel(got_ref, out_ref):
    peers = got_ref.shape[0]

    def body(d, carry):
        out_ref[d] = carry.astype(jnp.bfloat16)
        decay = got_ref[d, STATE : STATE + 1, :].astype(jnp.float32) + got_ref[
            d, STATE + 1 : STATE + 2, :
        ].astype(jnp.float32)
        return decay * carry + got_ref[d, 0:STATE, :].astype(jnp.float32)

    lax.fori_loop(0, peers, body, jnp.zeros(out_ref.shape[1:], jnp.float32))


def swap_cores(value):
    return lax.ppermute(value, "core", [(0, 1), (1, 0)])


def tie(value, *after):
    def kernel(*refs):
        del refs

    return pl.pallas_call(
        kernel,
        in_specs=[pl.BlockSpec(memory_space=pl.ANY) for _ in range(1 + len(after))],
        out_specs=pl.BlockSpec(memory_space=pl.ANY),
        out_shape=jax.ShapeDtypeStruct(value.shape, value.dtype),
        input_output_aliases={0: 0},
    )(value, *after)


def compose(for_other, mine, first_work, second_work):
    core = lax.axis_index("core")
    chips = lax.axis_size("chip")
    half = GROUP_COLS
    width = half // chips
    theirs = swap_cores(for_other)
    first = jnp.where(core == 0, mine, theirs)
    second = jnp.where(core == 0, theirs, mine)
    first_decay = first[STATE:]
    chip_state = second[STATE:] * first[:STATE] + second[:STATE]
    chip_decay = first_decay * second[STATE:]
    decay_hi = chip_decay.astype(jnp.bfloat16)
    decay_lo = (chip_decay - decay_hi.astype(jnp.float32)).astype(jnp.bfloat16)
    payload = jnp.concatenate(
        [chip_state.astype(jnp.bfloat16), decay_hi, decay_lo], axis=0
    ).reshape(STATE + 2, chips, width).transpose(1, 0, 2)
    work = first_work()
    got = tie(lax.all_to_all(payload, "chip", split_axis=0, concat_axis=0, tiled=True), work)
    entering = pl.pallas_call(
        scan_kernel,
        out_shape=jax.ShapeDtypeStruct((chips, STATE, width), jnp.bfloat16),
    )(got)
    work = second_work(work)
    back = tie(lax.all_to_all(entering, "chip", split_axis=0, concat_axis=0, tiled=True), work)
    chip_in = back.transpose(1, 0, 2).reshape(STATE, half).astype(jnp.float32)
    later_in = first_decay * chip_in + first[:STATE]
    keep = jnp.where(core == 0, chip_in, later_in).astype(jnp.bfloat16)
    other = swap_cores(jnp.where(core == 0, later_in, chip_in).astype(jnp.bfloat16))
    return keep, other, work


def local(xbc, z_gate, dt_raw, lengths, conv_weight, conv_bias, dt_bias, a_log, d_skip, norm_gain):
    tok = xbc.shape[0]
    nb = tok // STRETCH
    first_pos = (lax.axis_index("chip") * lax.axis_size("core") + lax.axis_index("core")) * tok
    rim_rows = shifted(xbc[tok - (CONV - 1) :], ("chip", "core"), 1)
    rim8 = jnp.concatenate([jnp.zeros((8 - (CONV - 1), CHANNELS), xbc.dtype), rim_rows], axis=0)
    ext_pos = first_pos - (CONV - 1) + jnp.arange(tok + CONV - 1)
    ext_seg = segment_of(ext_pos, lengths)
    target = ext_seg[CONV - 1 :]
    kept = [
        (ext_pos[tap : tap + tok] >= 0) & (ext_seg[tap : tap + tok] == target) for tap in range(CONV)
    ]
    masks = jnp.stack(kept, axis=1).astype(jnp.float32)
    conv = conv_part(xbc, rim8, conv_weight, conv_bias[None, :], masks)
    raw_g = dt_raw.reshape(tok, GROUPS, PER_GROUP).transpose(1, 0, 2).astype(jnp.float32)
    dt_g = jax.nn.softplus(raw_g + dt_bias.reshape(GROUPS, 1, PER_GROUP))
    log_decay = -dt_g * jnp.exp(a_log).reshape(GROUPS, 1, PER_GROUP)
    cum_blocks = jnp.cumsum(log_decay.reshape(GROUPS, nb, STRETCH, PER_GROUP), axis=2)
    cum_g = cum_blocks.reshape(GROUPS, tok, PER_GROUP)
    segments = segment_of(first_pos + jnp.arange(tok), lengths)
    seg_before = segment_of(first_pos + jnp.arange(nb) * STRETCH - 1, lengths)
    seg_last = segments.reshape(nb, STRETCH)[:, -1]
    cum_last = cum_blocks[:, :, -1, :].transpose(1, 0, 2).reshape(nb, HEADS)
    block_decay = jnp.where((seg_last == seg_before)[:, None], jnp.exp(cum_last), 0.0)

    cumt_g = cum_g.transpose(0, 2, 1)
    segc = jnp.broadcast_to(segments[:, None], (tok, 128)).astype(jnp.int32)
    segr = jnp.broadcast_to(segments[None, :], (8, tok)).astype(jnp.int32)
    eb = jnp.broadcast_to(seg_before[:, None, None], (nb, 8, 128)).reshape(nb * 8, 128)
    eb = eb.astype(jnp.int32)
    bdec = jnp.repeat(block_decay, HEAD_DIM, axis=1)[:, None, :]

    core_arr = lax.axis_index("core").astype(jnp.int32).reshape(1)
    local_a, cdec_a, for_other = half_states(conv, conv, dt_g, cum_g, segc, bdec, core_arr, 0)
    local_states, cdec, mine = half_states(
        conv, conv, dt_g, cum_g, segc, bdec, core_arr, 1, (local_a, cdec_a)
    )
    dsk = jnp.repeat(d_skip, HEAD_DIM)[None, :]
    def first_work():
        return intra_part(conv, dt_g, cum_g, cumt_g, segc, segr, dsk, 0)

    def second_work(done):
        return intra_part(conv, dt_g, cum_g, cumt_g, segc, segr, dsk, 1, done)

    keep, other, y_local = compose(for_other, mine, first_work, second_work)
    gain = norm_gain[None, :]
    parts = (y_local, z_gate)
    rest = (local_states, cdec, cum_g, segc, eb, gain, core_arr)
    out = mix(conv, *parts, keep, *rest, 0)
    return mix(conv, *parts, other, *rest, 1, out)


def solution(mesh):
    groups, peers = mesh.devices.shape
    split = Mesh(mesh.devices.reshape(groups, peers // 2, 2), ("group", "chip", "core"))
    rows = P(("group", "chip", "core"), None)
    return jax.shard_map(
        local,
        mesh=split,
        in_specs=(rows, rows, rows, P("group"), P(), P(), P(), P(), P(), P()),
        out_specs=rows,
        check_vma=False,
    )
```

```python
import jax
import jax.numpy as jnp
from jax import lax
from jax.experimental import pallas as pl
from jax.experimental.pallas import tpu as pltpu
from jax.sharding import Mesh, PartitionSpec as P

HEADS = 64
HEAD_DIM = 64
STATE = 256
GROUPS = 2
CONV = 4
STRETCH = 256
CHANNELS = 5120
INNER = HEADS * HEAD_DIM
PER_GROUP = HEADS // GROUPS
GROUP_COLS = INNER // GROUPS


def shifted(value, axis, by):
    peers = lax.axis_size(axis)
    pairs = [(i, i + by) for i in range(peers) if 0 <= i + by < peers]
    return lax.ppermute(value, axis, pairs)


def segment_of(positions, lengths):
    prompt_ends = jnp.cumsum(lengths)
    hits = (prompt_ends[None, :] <= positions[:, None]).astype(jnp.int32)
    return jnp.sum(hits, axis=1)


def expand_heads(v):
    heads = lax.broadcasted_iota(jnp.int32, (PER_GROUP, GROUP_COLS), 0)
    cols = lax.broadcasted_iota(jnp.int32, (PER_GROUP, GROUP_COLS), 1)
    spread = (cols // HEAD_DIM == heads).astype(jnp.bfloat16)
    hi = v.astype(jnp.bfloat16)
    rest = v - hi.astype(jnp.float32)
    mid = rest.astype(jnp.bfloat16)
    lo = (rest - mid.astype(jnp.float32)).astype(jnp.bfloat16)
    out = jnp.dot(hi, spread, preferred_element_type=jnp.float32)
    out = out + jnp.dot(mid, spread, preferred_element_type=jnp.float32)
    return out + jnp.dot(lo, spread, preferred_element_type=jnp.float32)


CONV_COLS = 1024


def conv_kernel(x_ref, rim_ref, w_ref, bias_ref, m_ref, out_ref):
    x = x_ref[...].astype(jnp.float32)
    rim = rim_ref[...].astype(jnp.float32)
    rows8 = lax.broadcasted_iota(jnp.int32, rim.shape, 0)
    summed = jnp.zeros(x.shape, jnp.float32)
    top = jnp.zeros(rim.shape, jnp.float32)
    for tap in range(CONV):
        by = CONV - 1 - tap
        wk = w_ref[tap : tap + 1, :]
        kept = m_ref[:, tap : tap + 1] > 0.0
        if by == 0:
            term = x
            top_term = x[0:8]
        else:
            term = pltpu.roll(x, by, 0)
            top_term = jnp.where(rows8 < by, pltpu.roll(rim, by, 0), term[0:8])
        summed = summed + jnp.where(kept, term * wk, 0.0)
        top = top + jnp.where(kept[0:8], top_term * wk, 0.0)
    out_ref[...] = jax.nn.silu(summed + bias_ref[...]).astype(jnp.bfloat16)
    out_ref[0:8, :] = jax.nn.silu(top + bias_ref[...]).astype(jnp.bfloat16)


def conv_part(xbc, rim8, w8, bias, masks):
    tok, chans = xbc.shape
    return pl.pallas_call(
        conv_kernel,
        grid=(chans // CONV_COLS,),
        in_specs=[
            pl.BlockSpec((tok, CONV_COLS), lambda c: (0, c)),
            pl.BlockSpec((8, CONV_COLS), lambda c: (0, c)),
            pl.BlockSpec((CONV, CONV_COLS), lambda c: (0, c)),
            pl.BlockSpec((1, CONV_COLS), lambda c: (0, c)),
            pl.BlockSpec((tok, CONV), lambda c: (0, 0)),
        ],
        out_specs=pl.BlockSpec((tok, CONV_COLS), lambda c: (0, c)),
        out_shape=jax.ShapeDtypeStruct((tok, chans), jnp.bfloat16),
    )(xbc, rim8, w8, bias, masks)


def state_kernel(
    bt_ref, x_ref, dt_ref, cum_ref, segc_ref, bdec_ref, local_ref, cdec_ref, tot_ref,
    acc_ref, dec_ref,
):
    b = pl.program_id(1)

    @pl.when(b == 0)
    def _():
        acc_ref[...] = jnp.zeros(acc_ref.shape, jnp.float32)
        dec_ref[...] = jnp.ones(dec_ref.shape, jnp.float32)

    local_ref[0] = acc_ref[...]
    cdec_ref[0] = dec_ref[...]
    cum = cum_ref[0]
    step = dt_ref[0]
    segc = segc_ref[:, 0:1]
    last = cum[STRETCH - 1 : STRETCH, :]
    seg_last = segc[STRETCH - 1 : STRETCH, :]
    w = jnp.where(segc == seg_last, jnp.exp(last - cum), 0.0)
    scaled = (x_ref[...].astype(jnp.float32) * expand_heads(step)).astype(jnp.bfloat16)
    weighted = (scaled.astype(jnp.float32) * expand_heads(w)).astype(jnp.bfloat16)
    block_state = jnp.dot(bt_ref[...], weighted, preferred_element_type=jnp.float32)
    decay = bdec_ref[0]
    acc_ref[...] = decay * acc_ref[...] + block_state
    dec_ref[...] = dec_ref[...] * decay

    @pl.when(b == pl.num_programs(1) - 1)
    def _():
        tot_ref[0, 0:STATE, :] = acc_ref[...]
        tot_ref[0, STATE : STATE + 1, :] = dec_ref[...]


def half_state_kernel(
    core_ref, bt_ref, x_ref, dt_ref, cum_ref, segc_ref, bdec_ref, *rest
):
    local_ref, cdec_ref, tot_ref, acc_ref, dec_ref = rest[-5:]
    del core_ref
    b = pl.program_id(0)

    @pl.when(b == 0)
    def _():
        acc_ref[...] = jnp.zeros(acc_ref.shape, jnp.float32)
        dec_ref[...] = jnp.ones(dec_ref.shape, jnp.float32)

    local_ref[0] = acc_ref[...]
    cdec_ref[0] = dec_ref[...]
    cum = cum_ref[0]
    step = dt_ref[0]
    segc = segc_ref[:, 0:1]
    last = cum[STRETCH - 1 : STRETCH, :]
    seg_last = segc[STRETCH - 1 : STRETCH, :]
    w = jnp.where(segc == seg_last, jnp.exp(last - cum), 0.0)
    scaled = (x_ref[...].astype(jnp.float32) * expand_heads(step)).astype(jnp.bfloat16)
    weighted = (scaled.astype(jnp.float32) * expand_heads(w)).astype(jnp.bfloat16)
    block_state = lax.dot_general(
        bt_ref[...], weighted, (((0,), (0,)), ((), ())), preferred_element_type=jnp.float32
    )
    decay = bdec_ref[0]
    acc_ref[...] = decay * acc_ref[...] + block_state
    dec_ref[...] = dec_ref[...] * decay

    @pl.when(b == pl.num_programs(0) - 1)
    def _():
        tot_ref[0:STATE, :] = acc_ref[...]
        tot_ref[STATE : STATE + 1, :] = dec_ref[...]


def half_states(bt, conv, dt_g, cum_g, segc, bdec, core_arr, which, prev=None):
    tok = conv.shape[0]
    nb = tok // STRETCH

    def grp(c):
        return (which + 1 + c[0]) % GROUPS

    operands = [bt, conv, dt_g, cum_g, segc, bdec]
    specs = [
        pl.BlockSpec((STRETCH, STATE), lambda b, c: (b, INNER // STATE + grp(c))),
        pl.BlockSpec((STRETCH, GROUP_COLS), lambda b, c: (b, grp(c))),
        pl.BlockSpec((1, STRETCH, PER_GROUP), lambda b, c: (grp(c), b, 0)),
        pl.BlockSpec((1, STRETCH, PER_GROUP), lambda b, c: (grp(c), b, 0)),
        pl.BlockSpec((STRETCH, 128), lambda b, c: (b, 0)),
        pl.BlockSpec((1, 1, GROUP_COLS), lambda b, c: (b, 0, grp(c))),
    ]
    aliases = {}
    if prev is not None:
        operands += list(prev)
        specs += [pl.BlockSpec(memory_space=pl.ANY), pl.BlockSpec(memory_space=pl.ANY)]
        aliases = {len(operands) - 1: 0, len(operands): 1}
    grid_spec = pltpu.PrefetchScalarGridSpec(
        num_scalar_prefetch=1,
        grid=(nb,),
        in_specs=specs,
        out_specs=[
            pl.BlockSpec((1, STATE, GROUP_COLS), lambda b, c: (b, 0, grp(c))),
            pl.BlockSpec((1, 1, GROUP_COLS), lambda b, c: (b, 0, grp(c))),
            pl.BlockSpec((STATE + 1, GROUP_COLS), lambda b, c: (0, 0)),
        ],
        scratch_shapes=[
            pltpu.VMEM((STATE, GROUP_COLS), jnp.float32),
            pltpu.VMEM((1, GROUP_COLS), jnp.float32),
        ],
    )
    return pl.pallas_call(
        half_state_kernel,
        grid_spec=grid_spec,
        out_shape=[
            jax.ShapeDtypeStruct((nb, STATE, INNER), jnp.float32),
            jax.ShapeDtypeStruct((nb, 1, INNER), jnp.float32),
            jax.ShapeDtypeStruct((STATE + 1, GROUP_COLS), jnp.float32),
        ],
        input_output_aliases=aliases,
    )(core_arr, *operands)


def intra_kernel(
    c_ref, b_ref, x_ref, dt_ref, cum_ref, cumt_ref, segc_ref, segr_ref, dsk_ref, out_ref
):
    gram = lax.dot_general(
        c_ref[...], b_ref[...], (((1,), (1,)), ((), ())), preferred_element_type=jnp.float32
    )
    segc = segc_ref[:, 0:1]
    segr = segr_ref[0:1, :]
    rows = lax.broadcasted_iota(jnp.int32, (STRETCH, STRETCH), 0)
    cols = lax.broadcasted_iota(jnp.int32, (STRETCH, STRETCH), 1)
    gram = jnp.where((segc == segr) & (cols <= rows), gram, 0.0)
    cum = cum_ref[0]
    cumt = cumt_ref[0]
    step = dt_ref[0]
    for j in range(PER_GROUP):
        hc = slice(j * HEAD_DIM, (j + 1) * HEAD_DIM)
        gap = jnp.minimum(cum[:, j : j + 1] - cumt[j : j + 1, :], 0.0)
        weights = (gram * jnp.exp(gap)).astype(jnp.bfloat16)
        xf = x_ref[:, hc].astype(jnp.float32)
        scaled = (xf * step[:, j : j + 1]).astype(jnp.bfloat16)
        intra = jnp.dot(weights, scaled, preferred_element_type=jnp.float32)
        out_ref[:, hc] = intra + dsk_ref[:, hc] * xf


def intra_part(conv, dt_g, cum_g, cumt_g, segc, segr, dsk, g, into=None):
    tok = conv.shape[0]
    nb = tok // STRETCH
    b_col = INNER // STATE
    c_col = b_col + GROUPS
    operands = [conv, conv, conv, dt_g, cum_g, cumt_g, segc, segr, dsk]
    specs = [
        pl.BlockSpec((STRETCH, STATE), lambda b: (b, c_col + g)),
        pl.BlockSpec((STRETCH, STATE), lambda b: (b, b_col + g)),
        pl.BlockSpec((STRETCH, GROUP_COLS), lambda b: (b, g)),
        pl.BlockSpec((1, STRETCH, PER_GROUP), lambda b: (g, b, 0)),
        pl.BlockSpec((1, STRETCH, PER_GROUP), lambda b: (g, b, 0)),
        pl.BlockSpec((1, PER_GROUP, STRETCH), lambda b: (g, 0, b)),
        pl.BlockSpec((STRETCH, 128), lambda b: (b, 0)),
        pl.BlockSpec((8, STRETCH), lambda b: (0, b)),
        pl.BlockSpec((1, GROUP_COLS), lambda b: (0, g)),
    ]
    kernel = intra_kernel
    aliases = {}
    if into is not None:
        operands.append(into)
        specs.append(pl.BlockSpec(memory_space=pl.ANY))
        aliases = {len(operands) - 1: 0}

        def kernel(*refs):
            intra_kernel(*refs[:-2], refs[-1])

    return pl.pallas_call(
        kernel,
        grid=(nb,),
        in_specs=specs,
        out_specs=pl.BlockSpec((STRETCH, GROUP_COLS), lambda b: (b, g)),
        out_shape=jax.ShapeDtypeStruct((tok, INNER), jnp.float32),
        input_output_aliases=aliases,
    )(*operands)


def mix_kernel(
    c_ref, y_ref, z_ref, hin_ref, local_ref, cdec_ref, cum_ref, segc_ref, eb_ref, gain_ref,
    out_ref,
):
    state = cdec_ref[0] * hin_ref[...].astype(jnp.float32) + local_ref[0]
    segc = segc_ref[:, 0:1]
    entry = eb_ref[0:1, 0:1]
    in_weight = jnp.where(segc == entry, jnp.exp(cum_ref[0]), 0.0)
    inter = jnp.dot(c_ref[...], state.astype(jnp.bfloat16), preferred_element_type=jnp.float32)
    y = y_ref[...] + inter * expand_heads(in_weight)
    zf = z_ref[...].astype(jnp.float32)
    gated = y * (zf * jax.nn.sigmoid(zf))
    mean_square = jnp.mean(gated * gated, axis=1, keepdims=True) + 1e-05
    out_ref[...] = (gated * lax.rsqrt(mean_square) * gain_ref[...]).astype(jnp.bfloat16)


def mix(conv, y_local, z_gate, hin, local_states, cdec, cum_g, segc, eb, gain, core_arr, which,
        prev=None):
    tok = conv.shape[0]
    nb = tok // STRETCH
    c_col = INNER // STATE + GROUPS

    def grp(c):
        return (which + c[0]) % GROUPS

    operands = [conv, y_local, z_gate, hin, local_states, cdec, cum_g, segc, eb, gain]
    specs = [
        pl.BlockSpec((STRETCH, STATE), lambda b, c: (b, c_col + grp(c))),
        pl.BlockSpec((STRETCH, GROUP_COLS), lambda b, c: (b, grp(c))),
        pl.BlockSpec((STRETCH, GROUP_COLS), lambda b, c: (b, grp(c))),
        pl.BlockSpec((STATE, GROUP_COLS), lambda b, c: (0, 0)),
        pl.BlockSpec((1, STATE, GROUP_COLS), lambda b, c: (b, 0, grp(c))),
        pl.BlockSpec((1, 1, GROUP_COLS), lambda b, c: (b, 0, grp(c))),
        pl.BlockSpec((1, STRETCH, PER_GROUP), lambda b, c: (grp(c), b, 0)),
        pl.BlockSpec((STRETCH, 128), lambda b, c: (b, 0)),
        pl.BlockSpec((8, 128), lambda b, c: (b, 0)),
        pl.BlockSpec((1, GROUP_COLS), lambda b, c: (0, grp(c))),
    ]
    kernel = mix_kernel
    aliases = {}
    if prev is not None:
        operands.append(prev)
        specs.append(pl.BlockSpec(memory_space=pl.ANY))
        aliases = {len(operands): 0}

        def kernel(*refs):
            mix_kernel(*refs[:-2], refs[-1])

    def with_core(core_ref, *refs):
        del core_ref
        kernel(*refs)

    grid_spec = pltpu.PrefetchScalarGridSpec(
        num_scalar_prefetch=1,
        grid=(nb,),
        in_specs=specs,
        out_specs=pl.BlockSpec((STRETCH, GROUP_COLS), lambda b, c: (b, grp(c))),
    )
    return pl.pallas_call(
        with_core,
        grid_spec=grid_spec,
        out_shape=jax.ShapeDtypeStruct((tok, INNER), jnp.bfloat16),
        input_output_aliases=aliases,
    )(core_arr, *operands)


def scan_kernel(got_ref, out_ref):
    peers = got_ref.shape[0]

    def body(d, carry):
        out_ref[d] = carry.astype(jnp.bfloat16)
        decay = got_ref[d, STATE : STATE + 1, :].astype(jnp.float32) + got_ref[
            d, STATE + 1 : STATE + 2, :
        ].astype(jnp.float32)
        return decay * carry + got_ref[d, 0:STATE, :].astype(jnp.float32)

    lax.fori_loop(0, peers, body, jnp.zeros(out_ref.shape[1:], jnp.float32))


def swap_cores(value):
    return lax.ppermute(value, "core", [(0, 1), (1, 0)])


def tie(value, *after):
    def kernel(*refs):
        del refs

    return pl.pallas_call(
        kernel,
        in_specs=[pl.BlockSpec(memory_space=pl.ANY) for _ in range(1 + len(after))],
        out_specs=pl.BlockSpec(memory_space=pl.ANY),
        out_shape=jax.ShapeDtypeStruct(value.shape, value.dtype),
        input_output_aliases={0: 0},
    )(value, *after)


def compose(for_other, mine, first_work, second_work):
    core = lax.axis_index("core")
    chips = lax.axis_size("chip")
    half = GROUP_COLS
    width = half // chips
    theirs = swap_cores(for_other)
    first = jnp.where(core == 0, mine, theirs)
    second = jnp.where(core == 0, theirs, mine)
    first_decay = first[STATE:]
    chip_state = second[STATE:] * first[:STATE] + second[:STATE]
    chip_decay = first_decay * second[STATE:]
    decay_hi = chip_decay.astype(jnp.bfloat16)
    decay_lo = (chip_decay - decay_hi.astype(jnp.float32)).astype(jnp.bfloat16)
    payload = jnp.concatenate(
        [chip_state.astype(jnp.bfloat16), decay_hi, decay_lo], axis=0
    ).reshape(STATE + 2, chips, width).transpose(1, 0, 2)
    work = first_work()
    got = tie(lax.all_to_all(payload, "chip", split_axis=0, concat_axis=0, tiled=True), work)
    entering = pl.pallas_call(
        scan_kernel,
        out_shape=jax.ShapeDtypeStruct((chips, STATE, width), jnp.bfloat16),
    )(got)
    work = second_work(work)
    back = tie(lax.all_to_all(entering, "chip", split_axis=0, concat_axis=0, tiled=True), work)
    chip_in = back.transpose(1, 0, 2).reshape(STATE, half).astype(jnp.float32)
    later_in = first_decay * chip_in + first[:STATE]
    keep = jnp.where(core == 0, chip_in, later_in).astype(jnp.bfloat16)
    other = swap_cores(jnp.where(core == 0, later_in, chip_in).astype(jnp.bfloat16))
    return keep, other, work


def local(xbc, z_gate, dt_raw, lengths, conv_weight, conv_bias, dt_bias, a_log, d_skip, norm_gain):
    tok = xbc.shape[0]
    nb = tok // STRETCH
    first_pos = (lax.axis_index("chip") * lax.axis_size("core") + lax.axis_index("core")) * tok
    rim_rows = shifted(xbc[tok - (CONV - 1) :], ("chip", "core"), 1)
    rim8 = jnp.concatenate([jnp.zeros((8 - (CONV - 1), CHANNELS), xbc.dtype), rim_rows], axis=0)
    ext_pos = first_pos - (CONV - 1) + jnp.arange(tok + CONV - 1)
    ext_seg = segment_of(ext_pos, lengths)
    target = ext_seg[CONV - 1 :]
    kept = [
        (ext_pos[tap : tap + tok] >= 0) & (ext_seg[tap : tap + tok] == target) for tap in range(CONV)
    ]
    masks = jnp.stack(kept, axis=1).astype(jnp.float32)
    conv = conv_part(xbc, rim8, conv_weight, conv_bias[None, :], masks)
    raw_g = dt_raw.reshape(tok, GROUPS, PER_GROUP).transpose(1, 0, 2).astype(jnp.float32)
    dt_g = jax.nn.softplus(raw_g + dt_bias.reshape(GROUPS, 1, PER_GROUP))
    log_decay = -dt_g * jnp.exp(a_log).reshape(GROUPS, 1, PER_GROUP)
    cum_blocks = jnp.cumsum(log_decay.reshape(GROUPS, nb, STRETCH, PER_GROUP), axis=2)
    cum_g = cum_blocks.reshape(GROUPS, tok, PER_GROUP)
    segments = segment_of(first_pos + jnp.arange(tok), lengths)
    seg_before = segment_of(first_pos + jnp.arange(nb) * STRETCH - 1, lengths)
    seg_last = segments.reshape(nb, STRETCH)[:, -1]
    cum_last = cum_blocks[:, :, -1, :].transpose(1, 0, 2).reshape(nb, HEADS)
    block_decay = jnp.where((seg_last == seg_before)[:, None], jnp.exp(cum_last), 0.0)

    cumt_g = cum_g.transpose(0, 2, 1)
    segc = jnp.broadcast_to(segments[:, None], (tok, 128)).astype(jnp.int32)
    segr = jnp.broadcast_to(segments[None, :], (8, tok)).astype(jnp.int32)
    eb = jnp.broadcast_to(seg_before[:, None, None], (nb, 8, 128)).reshape(nb * 8, 128)
    eb = eb.astype(jnp.int32)
    bdec = jnp.repeat(block_decay, HEAD_DIM, axis=1)[:, None, :]

    core_arr = lax.axis_index("core").astype(jnp.int32).reshape(1)
    local_a, cdec_a, for_other = half_states(conv, conv, dt_g, cum_g, segc, bdec, core_arr, 0)
    local_states, cdec, mine = half_states(
        conv, conv, dt_g, cum_g, segc, bdec, core_arr, 1, (local_a, cdec_a)
    )
    dsk = jnp.repeat(d_skip, HEAD_DIM)[None, :]
    def first_work():
        return intra_part(conv, dt_g, cum_g, cumt_g, segc, segr, dsk, 0)

    def second_work(done):
        return intra_part(conv, dt_g, cum_g, cumt_g, segc, segr, dsk, 1, done)

    keep, other, y_local = compose(for_other, mine, first_work, second_work)
    gain = norm_gain[None, :]
    parts = (y_local, z_gate)
    rest = (local_states, cdec, cum_g, segc, eb, gain, core_arr)
    out = mix(conv, *parts, keep, *rest, 0)
    return mix(conv, *parts, other, *rest, 1, out)


def solution(mesh):
    groups, peers = mesh.devices.shape
    split = Mesh(mesh.devices.reshape(groups, peers // 2, 2), ("group", "chip", "core"))
    rows = P(("group", "chip", "core"), None)
    return jax.shard_map(
        local,
        mesh=split,
        in_specs=(rows, rows, rows, P("group"), P(), P(), P(), P(), P(), P()),
        out_specs=rows,
        check_vma=False,
    )
```
